32 devices in a mesh: tile: 8 (over z, core), deg: 4 (over y, x).
Axes of the slice: x: 2, y: 2, z: 4, core: 2. Of those that a mesh axis runs over, the one named last changes fastest.
Arguments:
- field: float32 [3, 8, 128, 512], P(None, None, 'tile', 'deg'), may hold values from -6 to 6
- flow: float32 [3, 8, 128, 512], P(None, None, 'tile', 'deg'), may hold values from -3 to 3
- match_ops: bfloat16 [32, 512, 512], P(('tile', 'deg')), may hold values from -0.5 to 20.5
- wave_of_slot: int32 [32], replicated, may hold values from 0 to 31, each once
Outputs:
- advanced: float32 [3, 8, 128, 512], P(None, None, 'tile', 'deg')
The draws below stay inside these ranges and needn't reach their ends.
Inputs may be any that keep to these rules, and one draw needn't show every extreme that they name: `wave_of_slot`: every wavenumber from 0 to 31 is named by exactly one slot.
All inputs are finite; a program needn't handle non-finite values.
Results may differ from the reference program's by a relative error of at most 0.00065.
Values may be sent and summed in bfloat16 or wider, within the bound.
No kernel may reach another device: no remote copies, remote signals or barrier semaphores. Data moves between devices by JAX's collectives and lax.ppermute only.
A program may use at most 64 MiB of HBM per device.

```python
import math
import jax
import jax.numpy as jnp
from jax import lax

P_SIZE = 8
LAYERS = 1
NR = 8
NA = 128
NB = 512
M = 32


def draw_match_ops(key, part):
    key_diag, key_off = jax.random.split(jax.random.fold_in(key, 17), 2)
    diagonal = jax.random.uniform(key_diag, (M, NB), jnp.float32, 8.0, 16.0)
    off_part = jnp.clip(0.2 * jax.random.normal(key_off, (M, NB, NB), jnp.float32), -0.45, 0.45)
    rows = jnp.arange(NB, dtype=jnp.int32)
    identity = (rows[:, None] == rows[None, :]).astype(jnp.float32)
    result = off_part * (1.0 - identity)[None] + identity[None] * diagonal[:, :, None]
    return result.astype(jnp.bfloat16)


def block_scale(key, shape, cuts, smallest, largest):
    level = 1.0
    for dim, shards_of in cuts:
        steps = jax.random.uniform(jax.random.fold_in(jax.random.fold_in(key, 6), dim), (shards_of,), jnp.float32, smallest / len(cuts), largest / len(cuts))
        level = level * jnp.repeat(jnp.exp(steps), shape[dim] // shards_of).reshape((-1,) + (1,) * (len(shape) - 1 - dim))
    return level


def normal_values(rng, shape, scale, limit, pieces=(), kind=jnp.bfloat16):
    drawn = jax.random.normal(rng, shape, jnp.float32) * scale
    if len(pieces) > 0:
        drawn = block_scale(rng, shape, pieces, -0.22, 0.18) * drawn
    return jnp.clip(drawn, min=-limit, max=limit).astype(kind)


def setup_inputs(seed: int = 0) -> dict:
    keys = jax.random.split(jax.random.key(seed), 5)
    field = normal_values(keys[0], (3, NR, NA, NB), 1.0, 6.0, ((2, 8), (3, 4)), jnp.float32)
    flow = normal_values(keys[1], (3, NR, NA, NB), 0.5, 3.0, ((2, 8), (3, 4)), jnp.float32)
    match_ops = draw_match_ops(jax.random.fold_in(keys[4], 71), 0)
    wave_of_slot = jax.random.permutation(keys[3], M).astype(jnp.int32)
    return {"field": field, "flow": flow, "match_ops": match_ops, "wave_of_slot": wave_of_slot}


diffusivity = 0.05
time_step = 0.01
highest = lax.Precision.HIGHEST
gll_interior = [0.2092992179024789, 0.5917001814331423, 0.8717401485096066]


def legendre_value(point, degree):
    previous = 1.0
    current = point
    for order in range(1, degree):
        following = ((2 * order + 1) * point * current - order * previous) / (order + 1)
        previous = current
        current = following
    return current


def gll_tables(count):
    degree = count - 1
    points = [-1.0] + [-value for value in reversed(gll_interior)] + list(gll_interior) + [1.0]
    values = [legendre_value(point, degree) for point in points]
    weights = [2.0 / (degree * (degree + 1) * value * value) for value in values]
    matrix = [[(values[row] / (values[col] * (points[row] - points[col])) if row != col else 0.0)
               for col in range(count)] for row in range(count)]
    matrix[0][0] = -degree * (degree + 1) / 4.0
    matrix[count - 1][count - 1] = degree * (degree + 1) / 4.0
    return points, weights, matrix


def apply_along(values, axis_pos, matrix):
    shape = values.shape
    blocks = values.reshape(shape[:axis_pos] + (shape[axis_pos] // P_SIZE, P_SIZE) + shape[axis_pos + 1:])
    letters = list("abcdefg"[:blocks.ndim])
    source = list(letters)
    source[axis_pos + 1] = "p"
    target = list(letters)
    target[axis_pos + 1] = "q"
    formula = "".join(source) + ",qp->" + "".join(target)
    return jnp.einsum(formula, blocks, matrix, precision=highest).reshape(shape)


def assemble_dim(values, axis_pos, left, right):
    shape = values.shape
    count = shape[axis_pos] // P_SIZE
    blocks = values.reshape(shape[:axis_pos] + (count, P_SIZE) + shape[axis_pos + 1:])
    edge_shape = shape[:axis_pos] + (1, 1) + shape[axis_pos + 1:]
    first = lax.slice_in_dim(blocks, 0, 1, axis=axis_pos + 1)
    last = lax.slice_in_dim(blocks, P_SIZE - 1, P_SIZE, axis=axis_pos + 1)
    before = jnp.concatenate([left.reshape(edge_shape), lax.slice_in_dim(last, 0, count - 1, axis=axis_pos)], axis=axis_pos)
    after = jnp.concatenate([lax.slice_in_dim(first, 1, count, axis=axis_pos), right.reshape(edge_shape)], axis=axis_pos)
    middle = lax.slice_in_dim(blocks, 1, P_SIZE - 1, axis=axis_pos + 1)
    joined = jnp.concatenate([first + before, middle, last + after], axis=axis_pos + 1)
    return joined.reshape(shape)


def assembled_weights(weights, count, lead, trail):
    position = jnp.arange(count * P_SIZE, dtype=jnp.int32)
    local_point = position % P_SIZE
    element = position // P_SIZE
    base = jnp.tile(weights, count)
    starts = jnp.where(local_point == 0, jnp.where(element > 0, 1.0, lead), 0.0) * weights[P_SIZE - 1]
    ends = jnp.where(local_point == P_SIZE - 1, jnp.where(element < count - 1, 1.0, trail), 0.0) * weights[0]
    return base + starts + ends


def phases(waves, elem_start, elem_count, span, points):
    element = elem_start + jnp.arange(elem_count * P_SIZE, dtype=jnp.int32) // P_SIZE
    whole = (waves[:, None] * (2 * element + 1)[None, :]) % span
    fraction = waves.astype(jnp.float32)[:, None] * jnp.tile(points, elem_count)[None, :]
    return (2.0 * math.pi / span) * (whole.astype(jnp.float32) + fraction)


def reference(field, flow, match_ops, wave_of_slot):
    points_list, weights_list, matrix_list = gll_tables(P_SIZE)
    points = jnp.asarray(points_list, jnp.float32)
    weights = jnp.asarray(weights_list, jnp.float32)
    dmat = jnp.asarray(matrix_list, jnp.float32)
    elems_a = NA // P_SIZE
    elems_b = NB // P_SIZE
    w_r = jnp.tile(weights, LAYERS)
    w_a = jnp.tile(weights, elems_a)
    w_b = jnp.tile(weights, elems_b)
    mass3 = w_r[:, None, None] * w_a[None, :, None] * w_b[None, None, :]
    surface_weight = w_a[:, None] * w_b[None, :]
    assembled = (assembled_weights(weights, LAYERS, 0.0, 0.0)[:, None, None]
                 * assembled_weights(weights, elems_a, 1.0, 1.0)[None, :, None]
                 * assembled_weights(weights, elems_b, 0.0, 0.0)[None, None, :])
    span = 2 * elems_a
    angle = phases(wave_of_slot, 0, elems_a, span, points)
    cosine = jnp.cos(angle)
    sine = jnp.sin(angle)
    analysis = (jnp.stack([cosine, sine], axis=1) * (w_a * (P_SIZE / NA))[None, None, :]).reshape(2 * M, NA)
    synthesis = jnp.stack([cosine.T, sine.T], axis=2).reshape(NA, 2 * M)
    flow_parts = [flow[0], flow[1], flow[2]]
    grad_flow = [[apply_along(flow_parts[component], direction, dmat) for direction in range(3)] for component in range(3)]

    def apply_one(operands):
        return jnp.dot(operands[1], operands[0].T, preferred_element_type=jnp.float32)

    def surface_flux(surface):
        coeff = jnp.dot(analysis, surface, precision=highest).reshape(M, 2, NB)
        owned = coeff.astype(jnp.bfloat16)
        mapped = lax.map(apply_one, (match_ops, owned))
        return -jnp.dot(synthesis, mapped.reshape(2 * M, NB), precision=highest)

    def tendency(parts):
        rhs = []
        for component in range(3):
            slopes = [apply_along(parts[component], direction, dmat) for direction in range(3)]
            stretch = parts[0] * grad_flow[component][0] + parts[1] * grad_flow[component][1] + parts[2] * grad_flow[component][2]
            carried = flow_parts[0] * slopes[0] + flow_parts[1] * slopes[1] + flow_parts[2] * slopes[2]
            spread = (apply_along(mass3 * slopes[0], 0, dmat.T) + apply_along(mass3 * slopes[1], 1, dmat.T)
                      + apply_along(mass3 * slopes[2], 2, dmat.T))
            rhs.append(mass3 * (stretch - carried) - diffusivity * spread)
        flux = surface_flux(parts[0][NR - 1])
        rhs[0] = rhs[0].at[NR - 1].add(diffusivity * surface_weight * flux)
        stacked = jnp.stack(rhs)
        plane_r = jnp.zeros_like(lax.slice_in_dim(stacked, 0, 1, axis=1))
        stacked = assemble_dim(stacked, 1, plane_r, plane_r)
        stacked = assemble_dim(stacked, 2, lax.slice_in_dim(stacked, NA - 1, NA, axis=2), lax.slice_in_dim(stacked, 0, 1, axis=2))
        plane_b = jnp.zeros_like(lax.slice_in_dim(stacked, 0, 1, axis=3))
        stacked = assemble_dim(stacked, 3, plane_b, plane_b)
        return stacked / assembled[None]

    section = field + time_step * tendency([field[0], field[1], field[2]])
    return 0.5 * (field + section + time_step * tendency([section[0], section[1], section[2]]))
```

```python
import math

import jax
import jax.numpy as jnp
from jax import lax
from jax.sharding import PartitionSpec as P

P_SIZE = 8


diffusivity = 0.05
time_step = 0.01
highest = lax.Precision.HIGHEST
gll_interior = [0.2092992179024789, 0.5917001814331423, 0.8717401485096066]


def padded_2(value, sides, width):
    for axis, dim in sides:
        size, length = (lax.axis_size(axis), value.shape[dim])
        up = [(i, (i + 1) % size) for i in range(size)]
        down = [(j, i) for i, j in up]
        last = lax.slice_in_dim(value, length - width, length, axis=dim)
        first = lax.slice_in_dim(value, 0, width, axis=dim)
        before = lax.ppermute(last, axis, up)
        after = lax.ppermute(first, axis, down)
        value = jnp.concatenate([before, value, after], axis=dim)
    return value


def legendre_value(point, degree):
    previous = 1.0
    current = point
    for order in range(1, degree):
        following = ((2 * order + 1) * point * current - order * previous) / (order + 1)
        previous = current
        current = following
    return current


def gll_tables(count):
    degree = count - 1
    points = [-1.0] + [-value for value in reversed(gll_interior)] + list(gll_interior) + [1.0]
    values = [legendre_value(point, degree) for point in points]
    weights = [2.0 / (degree * (degree + 1) * value * value) for value in values]
    matrix = [
        [
            values[row] / (values[col] * (points[row] - points[col])) if row != col else 0.0
            for col in range(count)
        ]
        for row in range(count)
    ]
    matrix[0][0] = -degree * (degree + 1) / 4.0
    matrix[count - 1][count - 1] = degree * (degree + 1) / 4.0
    return (points, weights, matrix)


def apply_along(values, axis_pos, matrix):
    shape = values.shape
    blocks = values.reshape(
        shape[:axis_pos] + (shape[axis_pos] // P_SIZE, P_SIZE) + shape[axis_pos + 1 :]
    )
    letters = list("abcdefg"[: blocks.ndim])
    source = list(letters)
    source[axis_pos + 1] = "p"
    target = list(letters)
    target[axis_pos + 1] = "q"
    formula = "".join(source) + ",qp->" + "".join(target)
    return jnp.einsum(formula, blocks, matrix, precision=highest).reshape(shape)


def assemble_dim(values, axis_pos, left, right):
    shape = values.shape
    count = shape[axis_pos] // P_SIZE
    blocks = values.reshape(shape[:axis_pos] + (count, P_SIZE) + shape[axis_pos + 1 :])
    edge_shape = shape[:axis_pos] + (1, 1) + shape[axis_pos + 1 :]
    first = lax.slice_in_dim(blocks, 0, 1, axis=axis_pos + 1)
    last = lax.slice_in_dim(blocks, P_SIZE - 1, P_SIZE, axis=axis_pos + 1)
    before = jnp.concatenate(
        [left.reshape(edge_shape), lax.slice_in_dim(last, 0, count - 1, axis=axis_pos)],
        axis=axis_pos,
    )
    after = jnp.concatenate(
        [lax.slice_in_dim(first, 1, count, axis=axis_pos), right.reshape(edge_shape)], axis=axis_pos
    )
    middle = lax.slice_in_dim(blocks, 1, P_SIZE - 1, axis=axis_pos + 1)
    joined = jnp.concatenate([first + before, middle, last + after], axis=axis_pos + 1)
    return joined.reshape(shape)


def assembled_weights(weights, count, lead, trail):
    position = jnp.arange(count * P_SIZE, dtype=jnp.int32)
    local_point = position % P_SIZE
    element = position // P_SIZE
    base = jnp.tile(weights, count)
    starts = (
        jnp.where(local_point == 0, jnp.where(element > 0, 1.0, lead), 0.0) * weights[P_SIZE - 1]
    )
    ends = (
        jnp.where(local_point == P_SIZE - 1, jnp.where(element < count - 1, 1.0, trail), 0.0)
        * weights[0]
    )
    return base + starts + ends


def phases(waves, elem_start, elem_count, span, points):
    element = elem_start + jnp.arange(elem_count * P_SIZE, dtype=jnp.int32) // P_SIZE
    whole = waves[:, None] * (2 * element + 1)[None, :] % span
    fraction = waves.astype(jnp.float32)[:, None] * jnp.tile(points, elem_count)[None, :]
    return 2.0 * math.pi / span * (whole.astype(jnp.float32) + fraction)


def phases_at(waves, position, span, points):
    element = position // P_SIZE
    whole = waves[:, None] * (2 * element + 1)[None, :] % span
    fraction = waves.astype(jnp.float32)[:, None] * points[position % P_SIZE][None, :]
    return 2.0 * math.pi / span * (whole.astype(jnp.float32) + fraction)


def shift_pairs(sizes, steps):
    count = sizes[0] * sizes[1]
    pairs = []
    for source in range(count):
        t, g = divmod(source, sizes[1])
        target = ((t + steps[0]) % sizes[0]) * sizes[1] + (g + steps[1]) % sizes[1]
        pairs.append((source, target))
    return pairs


def local(field, flow, match_ops, wave_of_slot):
    tiles = lax.axis_size("tile")
    groups = lax.axis_size("deg")
    both = ("tile", "deg")
    tile_index = lax.axis_index("tile")
    group_index = lax.axis_index("deg")
    radial_nodes = field.shape[1]
    na_dev = field.shape[2]
    nb_dev = field.shape[3]
    elems_a = na_dev // P_SIZE
    elems_b = nb_dev // P_SIZE
    nb = nb_dev * groups
    span = 2 * elems_a * tiles
    scale = P_SIZE / (na_dev * tiles)
    points_list, weights_list, matrix_list = gll_tables(P_SIZE)
    points = jnp.asarray(points_list, jnp.float32)
    weights = jnp.asarray(weights_list, jnp.float32)
    dmat = jnp.asarray(matrix_list, jnp.float32)
    block = jnp.kron(jnp.eye(elems_b, dtype=jnp.float32), dmat)
    lead = (group_index > 0).astype(jnp.float32)
    trail = (group_index < groups - 1).astype(jnp.float32)
    w_r = jnp.tile(weights, radial_nodes // P_SIZE)
    w_a = jnp.tile(weights, elems_a)
    w_b = jnp.tile(weights, elems_b)
    mass3 = w_r[:, None, None] * w_a[None, :, None] * w_b[None, None, :]
    assembled = (
        assembled_weights(weights, radial_nodes // P_SIZE, 0.0, 0.0)[:, None, None]
        * assembled_weights(weights, elems_a, 1.0, 1.0)[None, :, None]
        * assembled_weights(weights, elems_b, lead, trail)[None, None, :]
    )
    column_mask = jnp.concatenate([lead[None], jnp.ones((nb_dev,), jnp.float32), trail[None]])
    rows_ext = (tile_index * na_dev - 1 + jnp.arange(na_dev + 2, dtype=jnp.int32)) % (na_dev * tiles)
    cols_ext = group_index * nb_dev - 1 + jnp.arange(nb_dev + 2, dtype=jnp.int32)
    surface_ext = weights[rows_ext % P_SIZE][:, None] * weights[cols_ext % P_SIZE][None, :]

    def derive(values, direction, transpose):
        if direction == 2:
            table = block if transpose else block.T
            return jnp.dot(values, table, precision=highest)
        return apply_along(values, direction, dmat.T if transpose else dmat)

    flow_parts = [flow[0], flow[1], flow[2]]
    grad_flow = [
        [derive(flow_parts[component], direction, False) for direction in range(3)]
        for component in range(3)
    ]

    def surface_flux(surface):
        angle = phases(wave_of_slot, tile_index * elems_a, elems_a, span, points)
        table = (
            jnp.stack([jnp.cos(angle), jnp.sin(angle)], axis=1) * (w_a * scale)[None, None, :]
        ).reshape(-1, na_dev)
        partial = jnp.dot(table, surface, precision=highest).reshape(-1, 2, nb_dev)
        gathered = lax.all_to_all(partial, both, 0, 0, tiled=True)
        coeff = gathered.reshape(tiles, groups, 2, nb_dev).sum(axis=0)
        coeff = coeff.transpose(1, 0, 2).reshape(2, nb)
        owned = coeff.astype(jnp.bfloat16)
        mapped = jnp.einsum(
            "pq,cq->cp", match_ops[0], owned, preferred_element_type=jnp.float32
        )
        edged = jnp.concatenate([mapped[:, :1], mapped, mapped[:, -1:]], axis=1)
        pieces = jnp.stack(
            [edged[:, g * nb_dev : g * nb_dev + nb_dev + 2] for g in range(groups)], axis=0
        )
        sent = jnp.broadcast_to(pieces[None], (tiles,) + pieces.shape).reshape(
            tiles * groups, 2, nb_dev + 2
        )
        returned = lax.all_to_all(sent, both, 0, 0, tiled=True)
        angle = phases_at(wave_of_slot, rows_ext, span, points)
        synth = jnp.stack([jnp.cos(angle).T, jnp.sin(angle).T], axis=2).reshape(na_dev + 2, -1)
        flux = -jnp.dot(synth, returned.reshape(-1, nb_dev + 2), precision=highest)
        return diffusivity * surface_ext * flux

    def halo(stacked):
        a_lo = lax.slice_in_dim(stacked, 0, 1, axis=2)
        a_hi = lax.slice_in_dim(stacked, na_dev - 1, na_dev, axis=2)
        b_lo = lax.slice_in_dim(stacked, 0, 1, axis=3)
        b_hi = lax.slice_in_dim(stacked, nb_dev - 1, nb_dev, axis=3)
        sizes = (tiles, groups)
        from_up = lax.ppermute(a_hi, both, shift_pairs(sizes, (1, 0)))
        from_down = lax.ppermute(a_lo, both, shift_pairs(sizes, (-1, 0)))
        from_left = lax.ppermute(b_hi, both, shift_pairs(sizes, (0, 1)))
        from_right = lax.ppermute(b_lo, both, shift_pairs(sizes, (0, -1)))
        corner_ul = lax.ppermute(a_hi[:, :, :, -1:], both, shift_pairs(sizes, (1, 1)))
        corner_ur = lax.ppermute(a_hi[:, :, :, :1], both, shift_pairs(sizes, (1, -1)))
        corner_dl = lax.ppermute(a_lo[:, :, :, -1:], both, shift_pairs(sizes, (-1, 1)))
        corner_dr = lax.ppermute(a_lo[:, :, :, :1], both, shift_pairs(sizes, (-1, -1)))
        top = jnp.concatenate([corner_ul, from_up, corner_ur], axis=3)
        middle = jnp.concatenate([from_left, stacked, from_right], axis=3)
        bottom = jnp.concatenate([corner_dl, from_down, corner_dr], axis=3)
        return jnp.concatenate([top, middle, bottom], axis=2)

    def tendency(parts):
        rhs = []
        for component in range(3):
            slopes = [derive(parts[component], direction, False) for direction in range(3)]
            stretch = (
                parts[0] * grad_flow[component][0]
                + parts[1] * grad_flow[component][1]
                + parts[2] * grad_flow[component][2]
            )
            carried = (
                flow_parts[0] * slopes[0] + flow_parts[1] * slopes[1] + flow_parts[2] * slopes[2]
            )
            spread = (
                derive(mass3 * slopes[0], 0, True)
                + derive(mass3 * slopes[1], 1, True)
                + derive(mass3 * slopes[2], 2, True)
            )
            rhs.append(mass3 * (stretch - carried) - diffusivity * spread)
        flux_term = surface_flux(parts[0][radial_nodes - 1])
        stacked = jnp.stack(rhs)
        padded = halo(stacked)
        padded = padded.at[0, radial_nodes - 1].add(flux_term)
        plane_r = jnp.zeros_like(lax.slice_in_dim(padded, 0, 1, axis=1))
        padded = assemble_dim(padded, 1, plane_r, plane_r)
        padded = padded * column_mask
        along_a = assemble_dim(padded[:, :, 1:-1, :], 2, padded[:, :, 0:1, :], padded[:, :, -1:, :])
        along_b = assemble_dim(
            along_a[:, :, :, 1:-1], 3, along_a[:, :, :, 0:1], along_a[:, :, :, -1:]
        )
        return along_b / assembled[None]

    section = field + time_step * tendency([field[0], field[1], field[2]])
    return 0.5 * (field + section + time_step * tendency([section[0], section[1], section[2]]))


def solution(mesh):
    placed = (
        P(None, None, "tile", "deg"),
        P(None, None, "tile", "deg"),
        P(("tile", "deg"), None, None),
        P(),
    )
    return jax.shard_map(
        local, mesh=mesh, in_specs=placed, out_specs=P(None, None, "tile", "deg"), check_vma=False
    )
```

```python
import math

import numpy as np
import jax
import jax.numpy as jnp
from jax import lax
from jax.sharding import PartitionSpec as P
from jax.experimental import pallas as pl

P_SIZE = 8


diffusivity = 0.05
time_step = 0.01
highest = lax.Precision.HIGHEST
gll_interior = [0.2092992179024789, 0.5917001814331423, 0.8717401485096066]


def padded_2(value, sides, width):
    for axis, dim in sides:
        size, length = (lax.axis_size(axis), value.shape[dim])
        up = [(i, (i + 1) % size) for i in range(size)]
        down = [(j, i) for i, j in up]
        last = lax.slice_in_dim(value, length - width, length, axis=dim)
        first = lax.slice_in_dim(value, 0, width, axis=dim)
        before = lax.ppermute(last, axis, up)
        after = lax.ppermute(first, axis, down)
        value = jnp.concatenate([before, value, after], axis=dim)
    return value


def product(a, b):
    return jnp.dot(a, b, precision=highest, preferred_element_type=jnp.float32)


def gradient_kernel(flow_ref, mats_ref, out_ref):
    for component in range(3):
        x = flow_ref[component]
        out_ref[3 * component] = product(mats_ref[0], x)
        out_ref[3 * component + 1] = product(mats_ref[1], x)
        out_ref[3 * component + 2] = product(x, mats_ref[2])


def volume_kernel(parts_ref, flow_ref, grad_ref, mats_ref, mass_ref, out_ref):
    mass = mass_ref[...]
    p = [parts_ref[i] for i in range(3)]
    f = [flow_ref[i] for i in range(3)]
    for c in range(3):
        x = p[c]
        s0 = product(mats_ref[0], x)
        s1 = product(mats_ref[1], x)
        s2 = product(x, mats_ref[2])
        stretch = p[0] * grad_ref[3 * c] + p[1] * grad_ref[3 * c + 1] + p[2] * grad_ref[3 * c + 2]
        carried = f[0] * s0 + f[1] * s1 + f[2] * s2
        spread = (
            product(mats_ref[3], mass * s0)
            + product(mats_ref[4], mass * s1)
            + product(mass * s2, mats_ref[5])
        )
        out_ref[c] = mass * (stretch - carried) - diffusivity * spread


def derivative_tables(radial_nodes, na_dev, nb_dev):
    _, _, matrix_list = gll_tables(P_SIZE)
    dmat = np.asarray(matrix_list, np.float32)
    radial = np.kron(dmat, np.eye(na_dev, dtype=np.float32))
    first = np.kron(np.eye(radial_nodes * na_dev // P_SIZE, dtype=np.float32), dmat)
    second = np.kron(np.eye(nb_dev // P_SIZE, dtype=np.float32), dmat)
    return jnp.asarray(np.stack([radial, first, second.T, radial.T, first.T, second]))


def legendre_value(point, degree):
    previous = 1.0
    current = point
    for order in range(1, degree):
        following = ((2 * order + 1) * point * current - order * previous) / (order + 1)
        previous = current
        current = following
    return current


def gll_tables(count):
    degree = count - 1
    points = [-1.0] + [-value for value in reversed(gll_interior)] + list(gll_interior) + [1.0]
    values = [legendre_value(point, degree) for point in points]
    weights = [2.0 / (degree * (degree + 1) * value * value) for value in values]
    matrix = [
        [
            values[row] / (values[col] * (points[row] - points[col])) if row != col else 0.0
            for col in range(count)
        ]
        for row in range(count)
    ]
    matrix[0][0] = -degree * (degree + 1) / 4.0
    matrix[count - 1][count - 1] = degree * (degree + 1) / 4.0
    return (points, weights, matrix)


def apply_along(values, axis_pos, matrix):
    shape = values.shape
    blocks = values.reshape(
        shape[:axis_pos] + (shape[axis_pos] // P_SIZE, P_SIZE) + shape[axis_pos + 1 :]
    )
    letters = list("abcdefg"[: blocks.ndim])
    source = list(letters)
    source[axis_pos + 1] = "p"
    target = list(letters)
    target[axis_pos + 1] = "q"
    formula = "".join(source) + ",qp->" + "".join(target)
    return jnp.einsum(formula, blocks, matrix, precision=highest).reshape(shape)


def assemble_dim(values, axis_pos, left, right):
    shape = values.shape
    count = shape[axis_pos] // P_SIZE
    blocks = values.reshape(shape[:axis_pos] + (count, P_SIZE) + shape[axis_pos + 1 :])
    edge_shape = shape[:axis_pos] + (1, 1) + shape[axis_pos + 1 :]
    first = lax.slice_in_dim(blocks, 0, 1, axis=axis_pos + 1)
    last = lax.slice_in_dim(blocks, P_SIZE - 1, P_SIZE, axis=axis_pos + 1)
    before = jnp.concatenate(
        [left.reshape(edge_shape), lax.slice_in_dim(last, 0, count - 1, axis=axis_pos)],
        axis=axis_pos,
    )
    after = jnp.concatenate(
        [lax.slice_in_dim(first, 1, count, axis=axis_pos), right.reshape(edge_shape)], axis=axis_pos
    )
    middle = lax.slice_in_dim(blocks, 1, P_SIZE - 1, axis=axis_pos + 1)
    joined = jnp.concatenate([first + before, middle, last + after], axis=axis_pos + 1)
    return joined.reshape(shape)


def assembled_weights(weights, count, lead, trail):
    position = jnp.arange(count * P_SIZE, dtype=jnp.int32)
    local_point = position % P_SIZE
    element = position // P_SIZE
    base = jnp.tile(weights, count)
    starts = (
        jnp.where(local_point == 0, jnp.where(element > 0, 1.0, lead), 0.0) * weights[P_SIZE - 1]
    )
    ends = (
        jnp.where(local_point == P_SIZE - 1, jnp.where(element < count - 1, 1.0, trail), 0.0)
        * weights[0]
    )
    return base + starts + ends


def phases(waves, elem_start, elem_count, span, points):
    element = elem_start + jnp.arange(elem_count * P_SIZE, dtype=jnp.int32) // P_SIZE
    whole = waves[:, None] * (2 * element + 1)[None, :] % span
    fraction = waves.astype(jnp.float32)[:, None] * jnp.tile(points, elem_count)[None, :]
    return 2.0 * math.pi / span * (whole.astype(jnp.float32) + fraction)


def phases_at(waves, position, span, points):
    element = position // P_SIZE
    whole = waves[:, None] * (2 * element + 1)[None, :] % span
    fraction = waves.astype(jnp.float32)[:, None] * points[position % P_SIZE][None, :]
    return 2.0 * math.pi / span * (whole.astype(jnp.float32) + fraction)


def shift_pairs(sizes, steps):
    count = sizes[0] * sizes[1]
    pairs = []
    for source in range(count):
        t, g = divmod(source, sizes[1])
        target = ((t + steps[0]) % sizes[0]) * sizes[1] + (g + steps[1]) % sizes[1]
        pairs.append((source, target))
    return pairs


def local(field, flow, match_ops, wave_of_slot):
    tiles = lax.axis_size("tile")
    groups = lax.axis_size("deg")
    both = ("tile", "deg")
    tile_index = lax.axis_index("tile")
    group_index = lax.axis_index("deg")
    radial_nodes = field.shape[1]
    na_dev = field.shape[2]
    nb_dev = field.shape[3]
    elems_a = na_dev // P_SIZE
    elems_b = nb_dev // P_SIZE
    nb = nb_dev * groups
    span = 2 * elems_a * tiles
    scale = P_SIZE / (na_dev * tiles)
    points_list, weights_list, _ = gll_tables(P_SIZE)
    points = jnp.asarray(points_list, jnp.float32)
    weights = jnp.asarray(weights_list, jnp.float32)
    lead = (group_index > 0).astype(jnp.float32)
    trail = (group_index < groups - 1).astype(jnp.float32)
    w_r = jnp.tile(weights, radial_nodes // P_SIZE)
    w_a = jnp.tile(weights, elems_a)
    w_b = jnp.tile(weights, elems_b)
    mass3 = w_r[:, None, None] * w_a[None, :, None] * w_b[None, None, :]
    assembled = (
        assembled_weights(weights, radial_nodes // P_SIZE, 0.0, 0.0)[:, None, None]
        * assembled_weights(weights, elems_a, 1.0, 1.0)[None, :, None]
        * assembled_weights(weights, elems_b, lead, trail)[None, None, :]
    )
    column_mask = jnp.concatenate([lead[None], jnp.ones((nb_dev,), jnp.float32), trail[None]])
    rows_ext = (tile_index * na_dev - 1 + jnp.arange(na_dev + 2, dtype=jnp.int32)) % (na_dev * tiles)
    cols_ext = group_index * nb_dev - 1 + jnp.arange(nb_dev + 2, dtype=jnp.int32)
    surface_ext = weights[rows_ext % P_SIZE][:, None] * weights[cols_ext % P_SIZE][None, :]

    rows = radial_nodes * na_dev
    mats = derivative_tables(radial_nodes, na_dev, nb_dev)
    flat_mass = mass3.reshape(rows, nb_dev)
    flat_flow = flow.reshape(3, rows, nb_dev)
    grads = pl.pallas_call(
        gradient_kernel, out_shape=jax.ShapeDtypeStruct((9, rows, nb_dev), jnp.float32)
    )(flat_flow, mats)

    def surface_flux(surface):
        angle = phases(wave_of_slot, tile_index * elems_a, elems_a, span, points)
        table = (
            jnp.stack([jnp.cos(angle), jnp.sin(angle)], axis=1) * (w_a * scale)[None, None, :]
        ).reshape(-1, na_dev)
        partial = jnp.dot(table, surface, precision=highest).reshape(-1, 2, nb_dev)
        gathered = lax.all_to_all(partial, both, 0, 0, tiled=True)
        coeff = gathered.reshape(tiles, groups, 2, nb_dev).sum(axis=0)
        coeff = coeff.transpose(1, 0, 2).reshape(2, nb)
        owned = coeff.astype(jnp.bfloat16)
        mapped = jnp.einsum(
            "pq,cq->cp", match_ops[0], owned, preferred_element_type=jnp.float32
        )
        edged = jnp.concatenate([mapped[:, :1], mapped, mapped[:, -1:]], axis=1)
        pieces = jnp.stack(
            [edged[:, g * nb_dev : g * nb_dev + nb_dev + 2] for g in range(groups)], axis=0
        )
        sent = jnp.broadcast_to(pieces[None], (tiles,) + pieces.shape).reshape(
            tiles * groups, 2, nb_dev + 2
        )
        returned = lax.all_to_all(sent, both, 0, 0, tiled=True)
        angle = phases_at(wave_of_slot, rows_ext, span, points)
        synth = jnp.stack([jnp.cos(angle).T, jnp.sin(angle).T], axis=2).reshape(na_dev + 2, -1)
        flux = -jnp.dot(synth, returned.reshape(-1, nb_dev + 2), precision=highest)
        return diffusivity * surface_ext * flux

    def halo(stacked):
        a_lo = lax.slice_in_dim(stacked, 0, 1, axis=2)
        a_hi = lax.slice_in_dim(stacked, na_dev - 1, na_dev, axis=2)
        b_lo = lax.slice_in_dim(stacked, 0, 1, axis=3)
        b_hi = lax.slice_in_dim(stacked, nb_dev - 1, nb_dev, axis=3)
        sizes = (tiles, groups)
        from_up = lax.ppermute(a_hi, both, shift_pairs(sizes, (1, 0)))
        from_down = lax.ppermute(a_lo, both, shift_pairs(sizes, (-1, 0)))
        from_left = lax.ppermute(b_hi, both, shift_pairs(sizes, (0, 1)))
        from_right = lax.ppermute(b_lo, both, shift_pairs(sizes, (0, -1)))
        corner_ul = lax.ppermute(a_hi[:, :, :, -1:], both, shift_pairs(sizes, (1, 1)))
        corner_ur = lax.ppermute(a_hi[:, :, :, :1], both, shift_pairs(sizes, (1, -1)))
        corner_dl = lax.ppermute(a_lo[:, :, :, -1:], both, shift_pairs(sizes, (-1, 1)))
        corner_dr = lax.ppermute(a_lo[:, :, :, :1], both, shift_pairs(sizes, (-1, -1)))
        top = jnp.concatenate([corner_ul, from_up, corner_ur], axis=3)
        middle = jnp.concatenate([from_left, stacked, from_right], axis=3)
        bottom = jnp.concatenate([corner_dl, from_down, corner_dr], axis=3)
        return jnp.concatenate([top, middle, bottom], axis=2)

    def tendency(parts):
        stacked = pl.pallas_call(
            volume_kernel, out_shape=jax.ShapeDtypeStruct((3, rows, nb_dev), jnp.float32)
        )(parts.reshape(3, rows, nb_dev), flat_flow, grads, mats, flat_mass)
        stacked = stacked.reshape(parts.shape)
        flux_term = surface_flux(parts[0, radial_nodes - 1])
        padded = halo(stacked)
        padded = padded.at[0, radial_nodes - 1].add(flux_term)
        plane_r = jnp.zeros_like(lax.slice_in_dim(padded, 0, 1, axis=1))
        padded = assemble_dim(padded, 1, plane_r, plane_r)
        padded = padded * column_mask
        along_a = assemble_dim(padded[:, :, 1:-1, :], 2, padded[:, :, 0:1, :], padded[:, :, -1:, :])
        along_b = assemble_dim(
            along_a[:, :, :, 1:-1], 3, along_a[:, :, :, 0:1], along_a[:, :, :, -1:]
        )
        return along_b / assembled[None]

    section = field + time_step * tendency(field)
    return 0.5 * (field + section + time_step * tendency(section))


def solution(mesh):
    placed = (
        P(None, None, "tile", "deg"),
        P(None, None, "tile", "deg"),
        P(("tile", "deg"), None, None),
        P(),
    )
    return jax.shard_map(
        local, mesh=mesh, in_specs=placed, out_specs=P(None, None, "tile", "deg"), check_vma=False
    )
```

```python
import math

import numpy as np
import jax
import jax.numpy as jnp
from jax import lax
from jax.sharding import PartitionSpec as P
from jax.experimental import pallas as pl

P_SIZE = 8


diffusivity = 0.05
time_step = 0.01
highest = lax.Precision.HIGHEST
gll_interior = [0.2092992179024789, 0.5917001814331423, 0.8717401485096066]


def padded_2(value, sides, width):
    for axis, dim in sides:
        size, length = (lax.axis_size(axis), value.shape[dim])
        up = [(i, (i + 1) % size) for i in range(size)]
        down = [(j, i) for i, j in up]
        last = lax.slice_in_dim(value, length - width, length, axis=dim)
        first = lax.slice_in_dim(value, 0, width, axis=dim)
        before = lax.ppermute(last, axis, up)
        after = lax.ppermute(first, axis, down)
        value = jnp.concatenate([before, value, after], axis=dim)
    return value


def product(a, b):
    return jnp.dot(a, b, precision=highest, preferred_element_type=jnp.float32)


def gradient_kernel(flow_ref, mats_ref, out_ref):
    for component in range(3):
        x = flow_ref[component]
        out_ref[3 * component] = product(mats_ref[0], x)
        out_ref[3 * component + 1] = product(mats_ref[1], x)
        out_ref[3 * component + 2] = product(x, mats_ref[2])


def volume_kernel(parts_ref, flow_ref, grad_ref, mats_ref, mass_ref, out_ref):
    mass = mass_ref[...]
    p = [parts_ref[i] for i in range(3)]
    f = [flow_ref[i] for i in range(3)]
    for c in range(3):
        x = p[c]
        s0 = product(mats_ref[0], x)
        s1 = product(mats_ref[1], x)
        s2 = product(x, mats_ref[2])
        stretch = p[0] * grad_ref[3 * c] + p[1] * grad_ref[3 * c + 1] + p[2] * grad_ref[3 * c + 2]
        carried = f[0] * s0 + f[1] * s1 + f[2] * s2
        spread = (
            product(mats_ref[3], mass * s0)
            + product(mats_ref[4], mass * s1)
            + product(mass * s2, mats_ref[5])
        )
        out_ref[c] = mass * (stretch - carried) - diffusivity * spread


def derivative_tables(radial_nodes, na_dev, nb_dev):
    _, _, matrix_list = gll_tables(P_SIZE)
    dmat = np.asarray(matrix_list, np.float32)
    radial = np.kron(dmat, np.eye(na_dev, dtype=np.float32))
    first = np.kron(np.eye(radial_nodes * na_dev // P_SIZE, dtype=np.float32), dmat)
    second = np.kron(np.eye(nb_dev // P_SIZE, dtype=np.float32), dmat)
    return jnp.asarray(np.stack([radial, first, second.T, radial.T, first.T, second]))


def legendre_value(point, degree):
    previous = 1.0
    current = point
    for order in range(1, degree):
        following = ((2 * order + 1) * point * current - order * previous) / (order + 1)
        previous = current
        current = following
    return current


def gll_tables(count):
    degree = count - 1
    points = [-1.0] + [-value for value in reversed(gll_interior)] + list(gll_interior) + [1.0]
    values = [legendre_value(point, degree) for point in points]
    weights = [2.0 / (degree * (degree + 1) * value * value) for value in values]
    matrix = [
        [
            values[row] / (values[col] * (points[row] - points[col])) if row != col else 0.0
            for col in range(count)
        ]
        for row in range(count)
    ]
    matrix[0][0] = -degree * (degree + 1) / 4.0
    matrix[count - 1][count - 1] = degree * (degree + 1) / 4.0
    return (points, weights, matrix)


def apply_along(values, axis_pos, matrix):
    shape = values.shape
    blocks = values.reshape(
        shape[:axis_pos] + (shape[axis_pos] // P_SIZE, P_SIZE) + shape[axis_pos + 1 :]
    )
    letters = list("abcdefg"[: blocks.ndim])
    source = list(letters)
    source[axis_pos + 1] = "p"
    target = list(letters)
    target[axis_pos + 1] = "q"
    formula = "".join(source) + ",qp->" + "".join(target)
    return jnp.einsum(formula, blocks, matrix, precision=highest).reshape(shape)


def assemble_dim(values, axis_pos, left, right):
    shape = values.shape
    count = shape[axis_pos] // P_SIZE
    blocks = values.reshape(shape[:axis_pos] + (count, P_SIZE) + shape[axis_pos + 1 :])
    edge_shape = shape[:axis_pos] + (1, 1) + shape[axis_pos + 1 :]
    first = lax.slice_in_dim(blocks, 0, 1, axis=axis_pos + 1)
    last = lax.slice_in_dim(blocks, P_SIZE - 1, P_SIZE, axis=axis_pos + 1)
    before = jnp.concatenate(
        [left.reshape(edge_shape), lax.slice_in_dim(last, 0, count - 1, axis=axis_pos)],
        axis=axis_pos,
    )
    after = jnp.concatenate(
        [lax.slice_in_dim(first, 1, count, axis=axis_pos), right.reshape(edge_shape)], axis=axis_pos
    )
    middle = lax.slice_in_dim(blocks, 1, P_SIZE - 1, axis=axis_pos + 1)
    joined = jnp.concatenate([first + before, middle, last + after], axis=axis_pos + 1)
    return joined.reshape(shape)


def assembled_weights(weights, count, lead, trail):
    position = jnp.arange(count * P_SIZE, dtype=jnp.int32)
    local_point = position % P_SIZE
    element = position // P_SIZE
    base = jnp.tile(weights, count)
    starts = (
        jnp.where(local_point == 0, jnp.where(element > 0, 1.0, lead), 0.0) * weights[P_SIZE - 1]
    )
    ends = (
        jnp.where(local_point == P_SIZE - 1, jnp.where(element < count - 1, 1.0, trail), 0.0)
        * weights[0]
    )
    return base + starts + ends


def phases(waves, elem_start, elem_count, span, points):
    element = elem_start + jnp.arange(elem_count * P_SIZE, dtype=jnp.int32) // P_SIZE
    whole = waves[:, None] * (2 * element + 1)[None, :] % span
    fraction = waves.astype(jnp.float32)[:, None] * jnp.tile(points, elem_count)[None, :]
    return 2.0 * math.pi / span * (whole.astype(jnp.float32) + fraction)


def phases_at(waves, position, span, points):
    element = position // P_SIZE
    whole = waves[:, None] * (2 * element + 1)[None, :] % span
    fraction = waves.astype(jnp.float32)[:, None] * points[position % P_SIZE][None, :]
    return 2.0 * math.pi / span * (whole.astype(jnp.float32) + fraction)


def shift_pairs(sizes, steps):
    count = sizes[0] * sizes[1]
    pairs = []
    for source in range(count):
        t, g = divmod(source, sizes[1])
        target = ((t + steps[0]) % sizes[0]) * sizes[1] + (g + steps[1]) % sizes[1]
        pairs.append((source, target))
    return pairs


def local(field, flow, match_ops, wave_of_slot):
    tiles = lax.axis_size("tile")
    groups = lax.axis_size("deg")
    both = ("tile", "deg")
    tile_index = lax.axis_index("tile")
    group_index = lax.axis_index("deg")
    radial_nodes = field.shape[1]
    na_dev = field.shape[2]
    nb_dev = field.shape[3]
    elems_a = na_dev // P_SIZE
    elems_b = nb_dev // P_SIZE
    nb = nb_dev * groups
    span = 2 * elems_a * tiles
    scale = P_SIZE / (na_dev * tiles)
    points_list, weights_list, _ = gll_tables(P_SIZE)
    points = jnp.asarray(points_list, jnp.float32)
    weights = jnp.asarray(weights_list, jnp.float32)
    lead = (group_index > 0).astype(jnp.float32)
    trail = (group_index < groups - 1).astype(jnp.float32)
    w_r = jnp.tile(weights, radial_nodes // P_SIZE)
    w_a = jnp.tile(weights, elems_a)
    w_b = jnp.tile(weights, elems_b)
    mass3 = w_r[:, None, None] * w_a[None, :, None] * w_b[None, None, :]
    assembled = (
        assembled_weights(weights, radial_nodes // P_SIZE, 0.0, 0.0)[:, None, None]
        * assembled_weights(weights, elems_a, 1.0, 1.0)[None, :, None]
        * assembled_weights(weights, elems_b, lead, trail)[None, None, :]
    )
    column_mask = jnp.concatenate([lead[None], jnp.ones((nb_dev,), jnp.float32), trail[None]])
    rows_ext = (tile_index * na_dev - 1 + jnp.arange(na_dev + 2, dtype=jnp.int32)) % (na_dev * tiles)
    cols_ext = group_index * nb_dev - 1 + jnp.arange(nb_dev + 2, dtype=jnp.int32)
    surface_ext = weights[rows_ext % P_SIZE][:, None] * weights[cols_ext % P_SIZE][None, :]

    rows = radial_nodes * na_dev
    mats = derivative_tables(radial_nodes, na_dev, nb_dev)
    flat_mass = mass3.reshape(rows, nb_dev)
    flat_flow = flow.reshape(3, rows, nb_dev)
    grads = pl.pallas_call(
        gradient_kernel, out_shape=jax.ShapeDtypeStruct((9, rows, nb_dev), jnp.float32)
    )(flat_flow, mats)

    def owner_map(surface):
        angle = phases(wave_of_slot, tile_index * elems_a, elems_a, span, points)
        table = (
            jnp.stack([jnp.cos(angle), jnp.sin(angle)], axis=1) * (w_a * scale)[None, None, :]
        ).reshape(-1, na_dev)
        partial = jnp.dot(table, surface, precision=highest).reshape(-1, 2, nb_dev)
        gathered = lax.all_to_all(partial, both, 0, 0, tiled=True)
        coeff = gathered.reshape(tiles, groups, 2, nb_dev).sum(axis=0)
        coeff = coeff.transpose(1, 0, 2).reshape(2, nb)
        owned = coeff.astype(jnp.bfloat16)
        mapped = jnp.einsum(
            "pq,cq->cp", match_ops[0], owned, preferred_element_type=jnp.float32
        )
        edged = jnp.concatenate([mapped[:, :1], mapped, mapped[:, -1:]], axis=1)
        pieces = jnp.stack(
            [edged[:, g * nb_dev : g * nb_dev + nb_dev + 2] for g in range(groups)], axis=0
        )
        return jnp.broadcast_to(pieces[None], (tiles,) + pieces.shape).reshape(
            tiles, groups, 2 * (nb_dev + 2)
        )

    def flux_of(returned):
        angle = phases_at(wave_of_slot, rows_ext, span, points)
        synth = jnp.stack([jnp.cos(angle).T, jnp.sin(angle).T], axis=2).reshape(na_dev + 2, -1)
        flux = -jnp.dot(synth, returned.reshape(-1, nb_dev + 2), precision=highest)
        return diffusivity * surface_ext * flux

    mapped_len = 2 * (nb_dev + 2)
    slot_len = 3 * radial_nodes * max(nb_dev, na_dev)
    carried_halo = tiles >= 3 and groups >= 3 and tiles * groups <= 64

    def joint_exchange(sent, stacked):
        a_lo = lax.slice_in_dim(stacked, 0, 1, axis=2)
        a_hi = lax.slice_in_dim(stacked, na_dev - 1, na_dev, axis=2)
        b_lo = lax.slice_in_dim(stacked, 0, 1, axis=3)
        b_hi = lax.slice_in_dim(stacked, nb_dev - 1, nb_dev, axis=3)
        out_pieces = [
            ((1, 0), a_hi),
            ((-1, 0), a_lo),
            ((0, 1), b_hi),
            ((0, -1), b_lo),
            ((1, 1), a_hi[:, :, :, -1:]),
            ((1, -1), a_hi[:, :, :, :1]),
            ((-1, 1), a_lo[:, :, :, -1:]),
            ((-1, -1), a_lo[:, :, :, :1]),
        ]
        slots = jnp.zeros((tiles, groups, slot_len), jnp.float32)
        for (dt, dg), piece in out_pieces:
            flat = piece.reshape(1, 1, -1)
            flat = jnp.pad(flat, ((0, 0), (0, 0), (0, slot_len - flat.shape[2])))
            slots = lax.dynamic_update_slice(
                slots, flat, ((tile_index + dt) % tiles, (group_index + dg) % groups, 0)
            )
        message = jnp.concatenate([sent, slots], axis=2).reshape(tiles * groups, -1)
        received = lax.all_to_all(message, both, 0, 0, tiled=True).reshape(tiles, groups, -1)
        returned = received[:, :, :mapped_len].reshape(tiles * groups, 2, nb_dev + 2)

        def take(dt, dg, like):
            row = lax.dynamic_slice(
                received,
                ((tile_index - dt) % tiles, (group_index - dg) % groups, mapped_len),
                (1, 1, like.size),
            )
            return row.reshape(like.shape)

        from_up = take(1, 0, a_hi)
        from_down = take(-1, 0, a_lo)
        from_left = take(0, 1, b_hi)
        from_right = take(0, -1, b_lo)
        corner_ul = take(1, 1, a_hi[:, :, :, -1:])
        corner_ur = take(1, -1, a_hi[:, :, :, :1])
        corner_dl = take(-1, 1, a_lo[:, :, :, -1:])
        corner_dr = take(-1, -1, a_lo[:, :, :, :1])
        top = jnp.concatenate([corner_ul, from_up, corner_ur], axis=3)
        middle = jnp.concatenate([from_left, stacked, from_right], axis=3)
        bottom = jnp.concatenate([corner_dl, from_down, corner_dr], axis=3)
        return returned, jnp.concatenate([top, middle, bottom], axis=2)

    def halo(stacked):
        a_lo = lax.slice_in_dim(stacked, 0, 1, axis=2)
        a_hi = lax.slice_in_dim(stacked, na_dev - 1, na_dev, axis=2)
        b_lo = lax.slice_in_dim(stacked, 0, 1, axis=3)
        b_hi = lax.slice_in_dim(stacked, nb_dev - 1, nb_dev, axis=3)
        sizes = (tiles, groups)
        from_up = lax.ppermute(a_hi, both, shift_pairs(sizes, (1, 0)))
        from_down = lax.ppermute(a_lo, both, shift_pairs(sizes, (-1, 0)))
        from_left = lax.ppermute(b_hi, both, shift_pairs(sizes, (0, 1)))
        from_right = lax.ppermute(b_lo, both, shift_pairs(sizes, (0, -1)))
        corner_ul = lax.ppermute(a_hi[:, :, :, -1:], both, shift_pairs(sizes, (1, 1)))
        corner_ur = lax.ppermute(a_hi[:, :, :, :1], both, shift_pairs(sizes, (1, -1)))
        corner_dl = lax.ppermute(a_lo[:, :, :, -1:], both, shift_pairs(sizes, (-1, 1)))
        corner_dr = lax.ppermute(a_lo[:, :, :, :1], both, shift_pairs(sizes, (-1, -1)))
        top = jnp.concatenate([corner_ul, from_up, corner_ur], axis=3)
        middle = jnp.concatenate([from_left, stacked, from_right], axis=3)
        bottom = jnp.concatenate([corner_dl, from_down, corner_dr], axis=3)
        return jnp.concatenate([top, middle, bottom], axis=2)

    def tendency(parts):
        stacked = pl.pallas_call(
            volume_kernel, out_shape=jax.ShapeDtypeStruct((3, rows, nb_dev), jnp.float32)
        )(parts.reshape(3, rows, nb_dev), flat_flow, grads, mats, flat_mass)
        stacked = stacked.reshape(parts.shape)
        sent = owner_map(parts[0, radial_nodes - 1])
        if carried_halo:
            returned, padded = joint_exchange(sent, stacked)
        else:
            returned = lax.all_to_all(
                sent.reshape(tiles * groups, -1), both, 0, 0, tiled=True
            ).reshape(tiles * groups, 2, nb_dev + 2)
            padded = halo(stacked)
        flux_term = flux_of(returned)
        padded = padded.at[0, radial_nodes - 1].add(flux_term)
        plane_r = jnp.zeros_like(lax.slice_in_dim(padded, 0, 1, axis=1))
        padded = assemble_dim(padded, 1, plane_r, plane_r)
        padded = padded * column_mask
        along_a = assemble_dim(padded[:, :, 1:-1, :], 2, padded[:, :, 0:1, :], padded[:, :, -1:, :])
        along_b = assemble_dim(
            along_a[:, :, :, 1:-1], 3, along_a[:, :, :, 0:1], along_a[:, :, :, -1:]
        )
        return along_b / assembled[None]

    section = field + time_step * tendency(field)
    return 0.5 * (field + section + time_step * tendency(section))


def solution(mesh):
    placed = (
        P(None, None, "tile", "deg"),
        P(None, None, "tile", "deg"),
        P(("tile", "deg"), None, None),
        P(),
    )
    return jax.shard_map(
        local, mesh=mesh, in_specs=placed, out_specs=P(None, None, "tile", "deg"), check_vma=False
    )
```

```python
import math

import numpy as np
import jax
import jax.numpy as jnp
from jax import lax
from jax.sharding import PartitionSpec as P
from jax.experimental import pallas as pl

P_SIZE = 8


diffusivity = 0.05
time_step = 0.01
highest = lax.Precision.HIGHEST
gll_interior = [0.2092992179024789, 0.5917001814331423, 0.8717401485096066]


def padded_2(value, sides, width):
    for axis, dim in sides:
        size, length = (lax.axis_size(axis), value.shape[dim])
        up = [(i, (i + 1) % size) for i in range(size)]
        down = [(j, i) for i, j in up]
        last = lax.slice_in_dim(value, length - width, length, axis=dim)
        first = lax.slice_in_dim(value, 0, width, axis=dim)
        before = lax.ppermute(last, axis, up)
        after = lax.ppermute(first, axis, down)
        value = jnp.concatenate([before, value, after], axis=dim)
    return value


def product(a, b):
    return jnp.dot(a, b, precision=highest, preferred_element_type=jnp.float32)


def gradient_kernel(flow_ref, mats_ref, out_ref):
    for component in range(3):
        x = flow_ref[component]
        out_ref[3 * component] = product(mats_ref[0], x)
        out_ref[3 * component + 1] = product(mats_ref[1], x)
        out_ref[3 * component + 2] = product(x, mats_ref[2])


def volume_kernel(parts_ref, flow_ref, grad_ref, mats_ref, mass_ref, out_ref):
    mass = mass_ref[...]
    p = [parts_ref[i] for i in range(3)]
    f = [flow_ref[i] for i in range(3)]
    for c in range(3):
        x = p[c]
        s0 = product(mats_ref[0], x)
        s1 = product(mats_ref[1], x)
        s2 = product(x, mats_ref[2])
        stretch = p[0] * grad_ref[3 * c] + p[1] * grad_ref[3 * c + 1] + p[2] * grad_ref[3 * c + 2]
        carried = f[0] * s0 + f[1] * s1 + f[2] * s2
        spread = (
            product(mats_ref[3], mass * s0)
            + product(mats_ref[4], mass * s1)
            + product(mass * s2, mats_ref[5])
        )
        out_ref[c] = mass * (stretch - carried) - diffusivity * spread


def derivative_tables(radial_nodes, na_dev, nb_dev):
    _, _, matrix_list = gll_tables(P_SIZE)
    dmat = np.asarray(matrix_list, np.float32)
    radial = np.kron(dmat, np.eye(na_dev, dtype=np.float32))
    first = np.kron(np.eye(radial_nodes * na_dev // P_SIZE, dtype=np.float32), dmat)
    second = np.kron(np.eye(nb_dev // P_SIZE, dtype=np.float32), dmat)
    return jnp.asarray(np.stack([radial, first, second.T, radial.T, first.T, second]))


def legendre_value(point, degree):
    previous = 1.0
    current = point
    for order in range(1, degree):
        following = ((2 * order + 1) * point * current - order * previous) / (order + 1)
        previous = current
        current = following
    return current


def gll_tables(count):
    degree = count - 1
    points = [-1.0] + [-value for value in reversed(gll_interior)] + list(gll_interior) + [1.0]
    values = [legendre_value(point, degree) for point in points]
    weights = [2.0 / (degree * (degree + 1) * value * value) for value in values]
    matrix = [
        [
            values[row] / (values[col] * (points[row] - points[col])) if row != col else 0.0
            for col in range(count)
        ]
        for row in range(count)
    ]
    matrix[0][0] = -degree * (degree + 1) / 4.0
    matrix[count - 1][count - 1] = degree * (degree + 1) / 4.0
    return (points, weights, matrix)


def apply_along(values, axis_pos, matrix):
    shape = values.shape
    blocks = values.reshape(
        shape[:axis_pos] + (shape[axis_pos] // P_SIZE, P_SIZE) + shape[axis_pos + 1 :]
    )
    letters = list("abcdefg"[: blocks.ndim])
    source = list(letters)
    source[axis_pos + 1] = "p"
    target = list(letters)
    target[axis_pos + 1] = "q"
    formula = "".join(source) + ",qp->" + "".join(target)
    return jnp.einsum(formula, blocks, matrix, precision=highest).reshape(shape)


def assemble_dim(values, axis_pos, left, right):
    shape = values.shape
    count = shape[axis_pos] // P_SIZE
    blocks = values.reshape(shape[:axis_pos] + (count, P_SIZE) + shape[axis_pos + 1 :])
    edge_shape = shape[:axis_pos] + (1, 1) + shape[axis_pos + 1 :]
    first = lax.slice_in_dim(blocks, 0, 1, axis=axis_pos + 1)
    last = lax.slice_in_dim(blocks, P_SIZE - 1, P_SIZE, axis=axis_pos + 1)
    before = jnp.concatenate(
        [left.reshape(edge_shape), lax.slice_in_dim(last, 0, count - 1, axis=axis_pos)],
        axis=axis_pos,
    )
    after = jnp.concatenate(
        [lax.slice_in_dim(first, 1, count, axis=axis_pos), right.reshape(edge_shape)], axis=axis_pos
    )
    middle = lax.slice_in_dim(blocks, 1, P_SIZE - 1, axis=axis_pos + 1)
    joined = jnp.concatenate([first + before, middle, last + after], axis=axis_pos + 1)
    return joined.reshape(shape)


def assembled_weights(weights, count, lead, trail):
    position = jnp.arange(count * P_SIZE, dtype=jnp.int32)
    local_point = position % P_SIZE
    element = position // P_SIZE
    base = jnp.tile(weights, count)
    starts = (
        jnp.where(local_point == 0, jnp.where(element > 0, 1.0, lead), 0.0) * weights[P_SIZE - 1]
    )
    ends = (
        jnp.where(local_point == P_SIZE - 1, jnp.where(element < count - 1, 1.0, trail), 0.0)
        * weights[0]
    )
    return base + starts + ends


def phases(waves, elem_start, elem_count, span, points):
    element = elem_start + jnp.arange(elem_count * P_SIZE, dtype=jnp.int32) // P_SIZE
    whole = waves[:, None] * (2 * element + 1)[None, :] % span
    fraction = waves.astype(jnp.float32)[:, None] * jnp.tile(points, elem_count)[None, :]
    return 2.0 * math.pi / span * (whole.astype(jnp.float32) + fraction)


def phases_at(waves, position, span, points):
    element = position // P_SIZE
    whole = waves[:, None] * (2 * element + 1)[None, :] % span
    fraction = waves.astype(jnp.float32)[:, None] * points[position % P_SIZE][None, :]
    return 2.0 * math.pi / span * (whole.astype(jnp.float32) + fraction)


def shift_pairs(sizes, steps):
    count = sizes[0] * sizes[1]
    pairs = []
    for source in range(count):
        t, g = divmod(source, sizes[1])
        target = ((t + steps[0]) % sizes[0]) * sizes[1] + (g + steps[1]) % sizes[1]
        pairs.append((source, target))
    return pairs


def local(field, flow, match_ops, wave_of_slot):
    tiles = lax.axis_size("tile")
    groups = lax.axis_size("deg")
    both = ("tile", "deg")
    tile_index = lax.axis_index("tile")
    group_index = lax.axis_index("deg")
    radial_nodes = field.shape[1]
    na_dev = field.shape[2]
    nb_dev = field.shape[3]
    elems_a = na_dev // P_SIZE
    elems_b = nb_dev // P_SIZE
    nb = nb_dev * groups
    span = 2 * elems_a * tiles
    scale = P_SIZE / (na_dev * tiles)
    points_list, weights_list, _ = gll_tables(P_SIZE)
    points = jnp.asarray(points_list, jnp.float32)
    weights = jnp.asarray(weights_list, jnp.float32)
    lead = (group_index > 0).astype(jnp.float32)
    trail = (group_index < groups - 1).astype(jnp.float32)
    w_r = jnp.tile(weights, radial_nodes // P_SIZE)
    w_a = jnp.tile(weights, elems_a)
    w_b = jnp.tile(weights, elems_b)
    mass3 = w_r[:, None, None] * w_a[None, :, None] * w_b[None, None, :]
    assembled = (
        assembled_weights(weights, radial_nodes // P_SIZE, 0.0, 0.0)[:, None, None]
        * assembled_weights(weights, elems_a, 1.0, 1.0)[None, :, None]
        * assembled_weights(weights, elems_b, lead, trail)[None, None, :]
    )
    column_mask = jnp.concatenate([lead[None], jnp.ones((nb_dev,), jnp.float32), trail[None]])
    rows_ext = (tile_index * na_dev - 1 + jnp.arange(na_dev + 2, dtype=jnp.int32)) % (na_dev * tiles)
    cols_ext = group_index * nb_dev - 1 + jnp.arange(nb_dev + 2, dtype=jnp.int32)
    surface_ext = weights[rows_ext % P_SIZE][:, None] * weights[cols_ext % P_SIZE][None, :]

    rows = radial_nodes * na_dev
    mats = derivative_tables(radial_nodes, na_dev, nb_dev)
    flat_mass = mass3.reshape(rows, nb_dev)
    flat_flow = flow.reshape(3, rows, nb_dev)
    grads = pl.pallas_call(
        gradient_kernel, out_shape=jax.ShapeDtypeStruct((9, rows, nb_dev), jnp.float32)
    )(flat_flow, mats)

    def owner_map(surface):
        angle = phases(wave_of_slot, tile_index * elems_a, elems_a, span, points)
        table = (
            jnp.stack([jnp.cos(angle), jnp.sin(angle)], axis=1) * (w_a * scale)[None, None, :]
        ).reshape(-1, na_dev)
        partial = jnp.dot(table, surface, precision=highest).reshape(-1, 2, nb_dev)
        gathered = lax.all_to_all(partial, both, 0, 0, tiled=True)
        coeff = gathered.reshape(tiles, groups, 2, nb_dev).sum(axis=0)
        coeff = coeff.transpose(1, 0, 2).reshape(2, nb)
        owned = coeff.astype(jnp.bfloat16)
        mapped = jnp.einsum(
            "pq,cq->cp", match_ops[0], owned, preferred_element_type=jnp.float32
        )
        edged = jnp.concatenate([mapped[:, :1], mapped, mapped[:, -1:]], axis=1)
        pieces = jnp.stack(
            [edged[:, g * nb_dev : g * nb_dev + nb_dev + 2] for g in range(groups)], axis=0
        )
        return jnp.broadcast_to(pieces[None], (tiles,) + pieces.shape).reshape(
            tiles, groups, 2 * (nb_dev + 2)
        )

    def flux_of(returned):
        angle = phases_at(wave_of_slot, rows_ext, span, points)
        synth = jnp.stack([jnp.cos(angle).T, jnp.sin(angle).T], axis=2).reshape(na_dev + 2, -1)
        flux = -jnp.dot(synth, returned.reshape(-1, nb_dev + 2), precision=highest)
        return diffusivity * surface_ext * flux

    mapped_len = 2 * (nb_dev + 2)
    slot_len = 3 * radial_nodes * max(nb_dev, na_dev)
    carried_halo = tiles >= 3 and groups >= 3 and tiles * groups <= 64

    def joint_exchange(sent, stacked):
        a_lo = lax.slice_in_dim(stacked, 0, 1, axis=2)
        a_hi = lax.slice_in_dim(stacked, na_dev - 1, na_dev, axis=2)
        b_lo = lax.slice_in_dim(stacked, 0, 1, axis=3)
        b_hi = lax.slice_in_dim(stacked, nb_dev - 1, nb_dev, axis=3)
        out_pieces = [
            ((1, 0), a_hi),
            ((-1, 0), a_lo),
            ((0, 1), b_hi),
            ((0, -1), b_lo),
            ((1, 1), a_hi[:, :, :, -1:]),
            ((1, -1), a_hi[:, :, :, :1]),
            ((-1, 1), a_lo[:, :, :, -1:]),
            ((-1, -1), a_lo[:, :, :, :1]),
        ]
        slots = jnp.zeros((tiles, groups, slot_len), jnp.float32)
        for (dt, dg), piece in out_pieces:
            flat = piece.reshape(1, 1, -1)
            flat = jnp.pad(flat, ((0, 0), (0, 0), (0, slot_len - flat.shape[2])))
            slots = lax.dynamic_update_slice(
                slots, flat, ((tile_index + dt) % tiles, (group_index + dg) % groups, 0)
            )
        message = jnp.concatenate([sent, slots], axis=2).reshape(tiles * groups, -1)
        received = lax.all_to_all(message, both, 0, 0, tiled=True).reshape(tiles, groups, -1)
        returned = received[:, :, :mapped_len].reshape(tiles * groups, 2, nb_dev + 2)

        def take(dt, dg, like):
            row = lax.dynamic_slice(
                received,
                ((tile_index - dt) % tiles, (group_index - dg) % groups, mapped_len),
                (1, 1, like.size),
            )
            return row.reshape(like.shape)

        from_up = take(1, 0, a_hi)
        from_down = take(-1, 0, a_lo)
        from_left = take(0, 1, b_hi)
        from_right = take(0, -1, b_lo)
        corner_ul = take(1, 1, a_hi[:, :, :, -1:])
        corner_ur = take(1, -1, a_hi[:, :, :, :1])
        corner_dl = take(-1, 1, a_lo[:, :, :, -1:])
        corner_dr = take(-1, -1, a_lo[:, :, :, :1])
        top = jnp.concatenate([corner_ul, from_up, corner_ur], axis=3)
        middle = jnp.concatenate([from_left, stacked, from_right], axis=3)
        bottom = jnp.concatenate([corner_dl, from_down, corner_dr], axis=3)
        return returned, jnp.concatenate([top, middle, bottom], axis=2)

    def halo(stacked):
        a_lo = lax.slice_in_dim(stacked, 0, 1, axis=2)
        a_hi = lax.slice_in_dim(stacked, na_dev - 1, na_dev, axis=2)
        b_lo = lax.slice_in_dim(stacked, 0, 1, axis=3)
        b_hi = lax.slice_in_dim(stacked, nb_dev - 1, nb_dev, axis=3)
        sizes = (tiles, groups)
        from_up = lax.ppermute(a_hi, both, shift_pairs(sizes, (1, 0)))
        from_down = lax.ppermute(a_lo, both, shift_pairs(sizes, (-1, 0)))
        from_left = lax.ppermute(b_hi, both, shift_pairs(sizes, (0, 1)))
        from_right = lax.ppermute(b_lo, both, shift_pairs(sizes, (0, -1)))
        corner_ul = lax.ppermute(a_hi[:, :, :, -1:], both, shift_pairs(sizes, (1, 1)))
        corner_ur = lax.ppermute(a_hi[:, :, :, :1], both, shift_pairs(sizes, (1, -1)))
        corner_dl = lax.ppermute(a_lo[:, :, :, -1:], both, shift_pairs(sizes, (-1, 1)))
        corner_dr = lax.ppermute(a_lo[:, :, :, :1], both, shift_pairs(sizes, (-1, -1)))
        top = jnp.concatenate([corner_ul, from_up, corner_ur], axis=3)
        middle = jnp.concatenate([from_left, stacked, from_right], axis=3)
        bottom = jnp.concatenate([corner_dl, from_down, corner_dr], axis=3)
        return jnp.concatenate([top, middle, bottom], axis=2)

    def assemble_ext(padded):
        last = padded.ndim - 1
        padded = padded * column_mask
        along_a = assemble_dim(
            padded[..., 1:-1, :], last - 1, padded[..., 0:1, :], padded[..., -1:, :]
        )
        return assemble_dim(along_a[..., 1:-1], last, along_a[..., 0:1], along_a[..., -1:])

    def tendency(parts, surface):
        stacked = pl.pallas_call(
            volume_kernel, out_shape=jax.ShapeDtypeStruct((3, rows, nb_dev), jnp.float32)
        )(parts.reshape(3, rows, nb_dev), flat_flow, grads, mats, flat_mass)
        stacked = stacked.reshape(parts.shape)
        sent = owner_map(surface)
        if carried_halo:
            returned, padded = joint_exchange(sent, stacked)
        else:
            returned = lax.all_to_all(
                sent.reshape(tiles * groups, -1), both, 0, 0, tiled=True
            ).reshape(tiles * groups, 2, nb_dev + 2)
            padded = halo(stacked)
        flux_term = flux_of(returned)
        outer = padded[0, radial_nodes - 1] + flux_term
        outer_rate = assemble_ext(outer) / assembled[radial_nodes - 1]
        padded = padded.at[0, radial_nodes - 1].add(flux_term)
        plane_r = jnp.zeros_like(lax.slice_in_dim(padded, 0, 1, axis=1))
        padded = assemble_dim(padded, 1, plane_r, plane_r)
        return assemble_ext(padded) / assembled[None], outer_rate

    first_rate, first_outer = tendency(field, field[0, radial_nodes - 1])
    section = field + time_step * first_rate
    section_outer = field[0, radial_nodes - 1] + time_step * first_outer
    second_rate, _ = tendency(section, section_outer)
    return 0.5 * (field + section + time_step * second_rate)


def solution(mesh):
    placed = (
        P(None, None, "tile", "deg"),
        P(None, None, "tile", "deg"),
        P(("tile", "deg"), None, None),
        P(),
    )
    return jax.shard_map(
        local, mesh=mesh, in_specs=placed, out_specs=P(None, None, "tile", "deg"), check_vma=False
    )
```

```python
import math

import numpy as np
import jax
import jax.numpy as jnp
from jax import lax
from jax.sharding import PartitionSpec as P
from jax.experimental import pallas as pl

P_SIZE = 8


diffusivity = 0.05
time_step = 0.01
highest = lax.Precision.HIGHEST
gll_interior = [0.2092992179024789, 0.5917001814331423, 0.8717401485096066]


def padded_2(value, sides, width):
    for axis, dim in sides:
        size, length = (lax.axis_size(axis), value.shape[dim])
        up = [(i, (i + 1) % size) for i in range(size)]
        down = [(j, i) for i, j in up]
        last = lax.slice_in_dim(value, length - width, length, axis=dim)
        first = lax.slice_in_dim(value, 0, width, axis=dim)
        before = lax.ppermute(last, axis, up)
        after = lax.ppermute(first, axis, down)
        value = jnp.concatenate([before, value, after], axis=dim)
    return value


def product(a, b):
    return jnp.dot(a, b, precision=highest, preferred_element_type=jnp.float32)


def gradient_kernel(flow_ref, mats_ref, out_ref):
    for component in range(3):
        x = flow_ref[component]
        out_ref[3 * component] = product(mats_ref[0], x)
        out_ref[3 * component + 1] = product(mats_ref[1], x)
        out_ref[3 * component + 2] = product(x, mats_ref[2])


def volume_kernel(parts_ref, flow_ref, grad_ref, mats_ref, mass_ref, out_ref):
    mass = mass_ref[...]
    p = [parts_ref[i] for i in range(3)]
    f = [flow_ref[i] for i in range(3)]
    for c in range(3):
        x = p[c]
        s0 = product(mats_ref[0], x)
        s1 = product(mats_ref[1], x)
        s2 = product(x, mats_ref[2])
        stretch = p[0] * grad_ref[3 * c] + p[1] * grad_ref[3 * c + 1] + p[2] * grad_ref[3 * c + 2]
        carried = f[0] * s0 + f[1] * s1 + f[2] * s2
        spread = (
            product(mats_ref[3], mass * s0)
            + product(mats_ref[4], mass * s1)
            + product(mass * s2, mats_ref[5])
        )
        out_ref[c] = mass * (stretch - carried) - diffusivity * spread


def derivative_tables(radial_nodes, na_dev, nb_dev):
    _, _, matrix_list = gll_tables(P_SIZE)
    dmat = np.asarray(matrix_list, np.float32)
    radial = np.kron(dmat, np.eye(na_dev, dtype=np.float32))
    first = np.kron(np.eye(radial_nodes * na_dev // P_SIZE, dtype=np.float32), dmat)
    second = np.kron(np.eye(nb_dev // P_SIZE, dtype=np.float32), dmat)
    return jnp.asarray(np.stack([radial, first, second.T, radial.T, first.T, second]))


def legendre_value(point, degree):
    previous = 1.0
    current = point
    for order in range(1, degree):
        following = ((2 * order + 1) * point * current - order * previous) / (order + 1)
        previous = current
        current = following
    return current


def gll_tables(count):
    degree = count - 1
    points = [-1.0] + [-value for value in reversed(gll_interior)] + list(gll_interior) + [1.0]
    values = [legendre_value(point, degree) for point in points]
    weights = [2.0 / (degree * (degree + 1) * value * value) for value in values]
    matrix = [
        [
            values[row] / (values[col] * (points[row] - points[col])) if row != col else 0.0
            for col in range(count)
        ]
        for row in range(count)
    ]
    matrix[0][0] = -degree * (degree + 1) / 4.0
    matrix[count - 1][count - 1] = degree * (degree + 1) / 4.0
    return (points, weights, matrix)


def apply_along(values, axis_pos, matrix):
    shape = values.shape
    blocks = values.reshape(
        shape[:axis_pos] + (shape[axis_pos] // P_SIZE, P_SIZE) + shape[axis_pos + 1 :]
    )
    letters = list("abcdefg"[: blocks.ndim])
    source = list(letters)
    source[axis_pos + 1] = "p"
    target = list(letters)
    target[axis_pos + 1] = "q"
    formula = "".join(source) + ",qp->" + "".join(target)
    return jnp.einsum(formula, blocks, matrix, precision=highest).reshape(shape)


def assemble_dim(values, axis_pos, left, right):
    shape = values.shape
    count = shape[axis_pos] // P_SIZE
    blocks = values.reshape(shape[:axis_pos] + (count, P_SIZE) + shape[axis_pos + 1 :])
    edge_shape = shape[:axis_pos] + (1, 1) + shape[axis_pos + 1 :]
    first = lax.slice_in_dim(blocks, 0, 1, axis=axis_pos + 1)
    last = lax.slice_in_dim(blocks, P_SIZE - 1, P_SIZE, axis=axis_pos + 1)
    before = jnp.concatenate(
        [left.reshape(edge_shape), lax.slice_in_dim(last, 0, count - 1, axis=axis_pos)],
        axis=axis_pos,
    )
    after = jnp.concatenate(
        [lax.slice_in_dim(first, 1, count, axis=axis_pos), right.reshape(edge_shape)], axis=axis_pos
    )
    middle = lax.slice_in_dim(blocks, 1, P_SIZE - 1, axis=axis_pos + 1)
    joined = jnp.concatenate([first + before, middle, last + after], axis=axis_pos + 1)
    return joined.reshape(shape)


def assembled_weights(weights, count, lead, trail):
    position = jnp.arange(count * P_SIZE, dtype=jnp.int32)
    local_point = position % P_SIZE
    element = position // P_SIZE
    base = jnp.tile(weights, count)
    starts = (
        jnp.where(local_point == 0, jnp.where(element > 0, 1.0, lead), 0.0) * weights[P_SIZE - 1]
    )
    ends = (
        jnp.where(local_point == P_SIZE - 1, jnp.where(element < count - 1, 1.0, trail), 0.0)
        * weights[0]
    )
    return base + starts + ends


def phases(waves, elem_start, elem_count, span, points):
    element = elem_start + jnp.arange(elem_count * P_SIZE, dtype=jnp.int32) // P_SIZE
    whole = waves[:, None] * (2 * element + 1)[None, :] % span
    fraction = waves.astype(jnp.float32)[:, None] * jnp.tile(points, elem_count)[None, :]
    return 2.0 * math.pi / span * (whole.astype(jnp.float32) + fraction)


def phases_at(waves, position, span, points):
    element = position // P_SIZE
    whole = waves[:, None] * (2 * element + 1)[None, :] % span
    fraction = waves.astype(jnp.float32)[:, None] * points[position % P_SIZE][None, :]
    return 2.0 * math.pi / span * (whole.astype(jnp.float32) + fraction)


def shift_pairs(sizes, steps):
    count = sizes[0] * sizes[1]
    pairs = []
    for source in range(count):
        t, g = divmod(source, sizes[1])
        target = ((t + steps[0]) % sizes[0]) * sizes[1] + (g + steps[1]) % sizes[1]
        pairs.append((source, target))
    return pairs


def local(field, flow, match_ops, wave_of_slot):
    tiles = lax.axis_size("tile")
    groups = lax.axis_size("deg")
    both = ("tile", "deg")
    tile_index = lax.axis_index("tile")
    group_index = lax.axis_index("deg")
    radial_nodes = field.shape[1]
    na_dev = field.shape[2]
    nb_dev = field.shape[3]
    elems_a = na_dev // P_SIZE
    elems_b = nb_dev // P_SIZE
    nb = nb_dev * groups
    span = 2 * elems_a * tiles
    scale = P_SIZE / (na_dev * tiles)
    points_list, weights_list, _ = gll_tables(P_SIZE)
    points = jnp.asarray(points_list, jnp.float32)
    weights = jnp.asarray(weights_list, jnp.float32)
    lead = (group_index > 0).astype(jnp.float32)
    trail = (group_index < groups - 1).astype(jnp.float32)
    w_r = jnp.tile(weights, radial_nodes // P_SIZE)
    w_a = jnp.tile(weights, elems_a)
    w_b = jnp.tile(weights, elems_b)
    mass3 = w_r[:, None, None] * w_a[None, :, None] * w_b[None, None, :]
    assembled = (
        assembled_weights(weights, radial_nodes // P_SIZE, 0.0, 0.0)[:, None, None]
        * assembled_weights(weights, elems_a, 1.0, 1.0)[None, :, None]
        * assembled_weights(weights, elems_b, lead, trail)[None, None, :]
    )
    column_mask = jnp.concatenate([lead[None], jnp.ones((nb_dev,), jnp.float32), trail[None]])
    rows_ext = (tile_index * na_dev - 1 + jnp.arange(na_dev + 2, dtype=jnp.int32)) % (na_dev * tiles)
    cols_ext = group_index * nb_dev - 1 + jnp.arange(nb_dev + 2, dtype=jnp.int32)
    surface_ext = weights[rows_ext % P_SIZE][:, None] * weights[cols_ext % P_SIZE][None, :]

    rows = radial_nodes * na_dev
    mats = derivative_tables(radial_nodes, na_dev, nb_dev)
    flat_mass = mass3.reshape(rows, nb_dev)
    flat_flow = flow.reshape(3, rows, nb_dev)
    grads = pl.pallas_call(
        gradient_kernel, out_shape=jax.ShapeDtypeStruct((9, rows, nb_dev), jnp.float32)
    )(flat_flow, mats)

    def owner_map(surface):
        angle = phases(wave_of_slot, tile_index * elems_a, elems_a, span, points)
        table = (
            jnp.stack([jnp.cos(angle), jnp.sin(angle)], axis=1) * (w_a * scale)[None, None, :]
        ).reshape(-1, na_dev)
        partial = jnp.dot(table, surface, precision=highest).reshape(-1, 2, nb_dev)
        gathered = lax.all_to_all(partial, both, 0, 0, tiled=True)
        coeff = gathered.reshape(tiles, groups, 2, nb_dev).sum(axis=0)
        coeff = coeff.transpose(1, 0, 2).reshape(2, nb)
        owned = coeff.astype(jnp.bfloat16)
        mapped = jnp.einsum(
            "pq,cq->cp", match_ops[0], owned, preferred_element_type=jnp.float32
        )
        edged = jnp.concatenate([mapped[:, :1], mapped, mapped[:, -1:]], axis=1)
        pieces = jnp.stack(
            [edged[:, g * nb_dev : g * nb_dev + nb_dev + 2] for g in range(groups)], axis=0
        )
        return jnp.broadcast_to(pieces[None], (tiles,) + pieces.shape).reshape(
            tiles, groups, 2 * (nb_dev + 2)
        )

    def flux_of(returned):
        angle = phases_at(wave_of_slot, rows_ext, span, points)
        synth = jnp.stack([jnp.cos(angle).T, jnp.sin(angle).T], axis=2).reshape(na_dev + 2, -1)
        flux = -jnp.dot(synth, returned.reshape(-1, nb_dev + 2), precision=highest)
        return diffusivity * surface_ext * flux

    mapped_len = 2 * (nb_dev + 2)
    slot_len = 3 * radial_nodes * na_dev
    carried_halo = tiles >= 3 and groups >= 3 and tiles * groups <= 64

    def joint_exchange(sent, stacked):
        a_lo = lax.slice_in_dim(stacked, 0, 1, axis=2)
        a_hi = lax.slice_in_dim(stacked, na_dev - 1, na_dev, axis=2)
        b_lo = lax.slice_in_dim(stacked, 0, 1, axis=3)
        b_hi = lax.slice_in_dim(stacked, nb_dev - 1, nb_dev, axis=3)
        up = [(i, (i + 1) % tiles) for i in range(tiles)]
        down = [(j, i) for i, j in up]
        from_up = lax.ppermute(a_hi, "tile", up)
        from_down = lax.ppermute(a_lo, "tile", down)
        out_pieces = [
            ((0, 1), b_hi),
            ((0, -1), b_lo),
            ((1, 1), a_hi[:, :, :, -1:]),
            ((1, -1), a_hi[:, :, :, :1]),
            ((-1, 1), a_lo[:, :, :, -1:]),
            ((-1, -1), a_lo[:, :, :, :1]),
        ]
        slots = jnp.zeros((tiles, groups, slot_len), jnp.float32)
        for (dt, dg), piece in out_pieces:
            flat = piece.reshape(1, 1, -1)
            flat = jnp.pad(flat, ((0, 0), (0, 0), (0, slot_len - flat.shape[2])))
            slots = lax.dynamic_update_slice(
                slots, flat, ((tile_index + dt) % tiles, (group_index + dg) % groups, 0)
            )
        message = jnp.concatenate([sent, slots], axis=2).reshape(tiles * groups, -1)
        received = lax.all_to_all(message, both, 0, 0, tiled=True).reshape(tiles, groups, -1)
        returned = received[:, :, :mapped_len].reshape(tiles * groups, 2, nb_dev + 2)

        def take(dt, dg, like):
            row = lax.dynamic_slice(
                received,
                ((tile_index - dt) % tiles, (group_index - dg) % groups, mapped_len),
                (1, 1, like.size),
            )
            return row.reshape(like.shape)

        from_left = take(0, 1, b_hi)
        from_right = take(0, -1, b_lo)
        corner_ul = take(1, 1, a_hi[:, :, :, -1:])
        corner_ur = take(1, -1, a_hi[:, :, :, :1])
        corner_dl = take(-1, 1, a_lo[:, :, :, -1:])
        corner_dr = take(-1, -1, a_lo[:, :, :, :1])
        top = jnp.concatenate([corner_ul, from_up, corner_ur], axis=3)
        middle = jnp.concatenate([from_left, stacked, from_right], axis=3)
        bottom = jnp.concatenate([corner_dl, from_down, corner_dr], axis=3)
        return returned, jnp.concatenate([top, middle, bottom], axis=2)

    def halo(stacked):
        a_lo = lax.slice_in_dim(stacked, 0, 1, axis=2)
        a_hi = lax.slice_in_dim(stacked, na_dev - 1, na_dev, axis=2)
        b_lo = lax.slice_in_dim(stacked, 0, 1, axis=3)
        b_hi = lax.slice_in_dim(stacked, nb_dev - 1, nb_dev, axis=3)
        sizes = (tiles, groups)
        from_up = lax.ppermute(a_hi, both, shift_pairs(sizes, (1, 0)))
        from_down = lax.ppermute(a_lo, both, shift_pairs(sizes, (-1, 0)))
        from_left = lax.ppermute(b_hi, both, shift_pairs(sizes, (0, 1)))
        from_right = lax.ppermute(b_lo, both, shift_pairs(sizes, (0, -1)))
        corner_ul = lax.ppermute(a_hi[:, :, :, -1:], both, shift_pairs(sizes, (1, 1)))
        corner_ur = lax.ppermute(a_hi[:, :, :, :1], both, shift_pairs(sizes, (1, -1)))
        corner_dl = lax.ppermute(a_lo[:, :, :, -1:], both, shift_pairs(sizes, (-1, 1)))
        corner_dr = lax.ppermute(a_lo[:, :, :, :1], both, shift_pairs(sizes, (-1, -1)))
        top = jnp.concatenate([corner_ul, from_up, corner_ur], axis=3)
        middle = jnp.concatenate([from_left, stacked, from_right], axis=3)
        bottom = jnp.concatenate([corner_dl, from_down, corner_dr], axis=3)
        return jnp.concatenate([top, middle, bottom], axis=2)

    def assemble_ext(padded):
        last = padded.ndim - 1
        padded = padded * column_mask
        along_a = assemble_dim(
            padded[..., 1:-1, :], last - 1, padded[..., 0:1, :], padded[..., -1:, :]
        )
        return assemble_dim(along_a[..., 1:-1], last, along_a[..., 0:1], along_a[..., -1:])

    def tendency(parts, surface):
        stacked = pl.pallas_call(
            volume_kernel, out_shape=jax.ShapeDtypeStruct((3, rows, nb_dev), jnp.float32)
        )(parts.reshape(3, rows, nb_dev), flat_flow, grads, mats, flat_mass)
        stacked = stacked.reshape(parts.shape)
        sent = owner_map(surface)
        if carried_halo:
            returned, padded = joint_exchange(sent, stacked)
        else:
            returned = lax.all_to_all(
                sent.reshape(tiles * groups, -1), both, 0, 0, tiled=True
            ).reshape(tiles * groups, 2, nb_dev + 2)
            padded = halo(stacked)
        flux_term = flux_of(returned)
        outer = padded[0, radial_nodes - 1] + flux_term
        outer_rate = assemble_ext(outer) / assembled[radial_nodes - 1]
        padded = padded.at[0, radial_nodes - 1].add(flux_term)
        plane_r = jnp.zeros_like(lax.slice_in_dim(padded, 0, 1, axis=1))
        padded = assemble_dim(padded, 1, plane_r, plane_r)
        return assemble_ext(padded) / assembled[None], outer_rate

    first_rate, first_outer = tendency(field, field[0, radial_nodes - 1])
    section = field + time_step * first_rate
    section_outer = field[0, radial_nodes - 1] + time_step * first_outer
    second_rate, _ = tendency(section, section_outer)
    return 0.5 * (field + section + time_step * second_rate)


def solution(mesh):
    placed = (
        P(None, None, "tile", "deg"),
        P(None, None, "tile", "deg"),
        P(("tile", "deg"), None, None),
        P(),
    )
    return jax.shard_map(
        local, mesh=mesh, in_specs=placed, out_specs=P(None, None, "tile", "deg"), check_vma=False
    )
```

```python
import math

import numpy as np
import jax
import jax.numpy as jnp
from jax import lax
from jax.sharding import PartitionSpec as P
from jax.experimental import pallas as pl

P_SIZE = 8


diffusivity = 0.05
time_step = 0.01
highest = lax.Precision.HIGHEST
gll_interior = [0.2092992179024789, 0.5917001814331423, 0.8717401485096066]


def padded_2(value, sides, width):
    for axis, dim in sides:
        size, length = (lax.axis_size(axis), value.shape[dim])
        up = [(i, (i + 1) % size) for i in range(size)]
        down = [(j, i) for i, j in up]
        last = lax.slice_in_dim(value, length - width, length, axis=dim)
        first = lax.slice_in_dim(value, 0, width, axis=dim)
        before = lax.ppermute(last, axis, up)
        after = lax.ppermute(first, axis, down)
        value = jnp.concatenate([before, value, after], axis=dim)
    return value


def product(a, b):
    return jnp.dot(a, b, precision=highest, preferred_element_type=jnp.float32)


def gradient_kernel(flow_ref, mats_ref, out_ref):
    for component in range(3):
        x = flow_ref[component]
        out_ref[3 * component] = product(mats_ref[0], x)
        out_ref[3 * component + 1] = product(mats_ref[1], x)
        out_ref[3 * component + 2] = product(x, mats_ref[2])


def volume_kernel(parts_ref, flow_ref, grad_ref, mats_ref, mass_ref, out_ref, rows_ref, cols_ref):
    mass = mass_ref[...]
    p = [parts_ref[i] for i in range(3)]
    f = [flow_ref[i] for i in range(3)]
    planes = out_ref.shape[1] // rows_ref.shape[2]
    width = out_ref.shape[2]
    for c in range(3):
        x = p[c]
        s0 = product(mats_ref[0], x)
        s1 = product(mats_ref[1], x)
        s2 = product(x, mats_ref[2])
        stretch = p[0] * grad_ref[3 * c] + p[1] * grad_ref[3 * c + 1] + p[2] * grad_ref[3 * c + 2]
        carried = f[0] * s0 + f[1] * s1 + f[2] * s2
        spread = (
            product(mats_ref[3], mass * s0)
            + product(mats_ref[4], mass * s1)
            + product(mass * s2, mats_ref[5])
        )
        result = mass * (stretch - carried) - diffusivity * spread
        out_ref[c] = result
        turned = result.T
        cols_ref[0, c : c + 1, :] = turned[0:1, :]
        cols_ref[1, c : c + 1, :] = turned[width - 1 : width, :]
    for c in range(3):
        rows_ref[0, c] = out_ref[c, pl.ds(0, rows_ref.shape[2], stride=planes), :]
        rows_ref[1, c] = out_ref[c, pl.ds(planes - 1, rows_ref.shape[2], stride=planes), :]


def derivative_tables(radial_nodes, na_dev, nb_dev):
    _, _, matrix_list = gll_tables(P_SIZE)
    dmat = np.asarray(matrix_list, np.float32)
    radial = np.kron(dmat, np.eye(na_dev, dtype=np.float32))
    first = np.kron(np.eye(radial_nodes * na_dev // P_SIZE, dtype=np.float32), dmat)
    second = np.kron(np.eye(nb_dev // P_SIZE, dtype=np.float32), dmat)
    return jnp.asarray(np.stack([radial, first, second.T, radial.T, first.T, second]))


def legendre_value(point, degree):
    previous = 1.0
    current = point
    for order in range(1, degree):
        following = ((2 * order + 1) * point * current - order * previous) / (order + 1)
        previous = current
        current = following
    return current


def gll_tables(count):
    degree = count - 1
    points = [-1.0] + [-value for value in reversed(gll_interior)] + list(gll_interior) + [1.0]
    values = [legendre_value(point, degree) for point in points]
    weights = [2.0 / (degree * (degree + 1) * value * value) for value in values]
    matrix = [
        [
            values[row] / (values[col] * (points[row] - points[col])) if row != col else 0.0
            for col in range(count)
        ]
        for row in range(count)
    ]
    matrix[0][0] = -degree * (degree + 1) / 4.0
    matrix[count - 1][count - 1] = degree * (degree + 1) / 4.0
    return (points, weights, matrix)


def apply_along(values, axis_pos, matrix):
    shape = values.shape
    blocks = values.reshape(
        shape[:axis_pos] + (shape[axis_pos] // P_SIZE, P_SIZE) + shape[axis_pos + 1 :]
    )
    letters = list("abcdefg"[: blocks.ndim])
    source = list(letters)
    source[axis_pos + 1] = "p"
    target = list(letters)
    target[axis_pos + 1] = "q"
    formula = "".join(source) + ",qp->" + "".join(target)
    return jnp.einsum(formula, blocks, matrix, precision=highest).reshape(shape)


def assemble_dim(values, axis_pos, left, right):
    shape = values.shape
    count = shape[axis_pos] // P_SIZE
    blocks = values.reshape(shape[:axis_pos] + (count, P_SIZE) + shape[axis_pos + 1 :])
    edge_shape = shape[:axis_pos] + (1, 1) + shape[axis_pos + 1 :]
    first = lax.slice_in_dim(blocks, 0, 1, axis=axis_pos + 1)
    last = lax.slice_in_dim(blocks, P_SIZE - 1, P_SIZE, axis=axis_pos + 1)
    before = jnp.concatenate(
        [left.reshape(edge_shape), lax.slice_in_dim(last, 0, count - 1, axis=axis_pos)],
        axis=axis_pos,
    )
    after = jnp.concatenate(
        [lax.slice_in_dim(first, 1, count, axis=axis_pos), right.reshape(edge_shape)], axis=axis_pos
    )
    middle = lax.slice_in_dim(blocks, 1, P_SIZE - 1, axis=axis_pos + 1)
    joined = jnp.concatenate([first + before, middle, last + after], axis=axis_pos + 1)
    return joined.reshape(shape)


def assembled_weights(weights, count, lead, trail):
    position = jnp.arange(count * P_SIZE, dtype=jnp.int32)
    local_point = position % P_SIZE
    element = position // P_SIZE
    base = jnp.tile(weights, count)
    starts = (
        jnp.where(local_point == 0, jnp.where(element > 0, 1.0, lead), 0.0) * weights[P_SIZE - 1]
    )
    ends = (
        jnp.where(local_point == P_SIZE - 1, jnp.where(element < count - 1, 1.0, trail), 0.0)
        * weights[0]
    )
    return base + starts + ends


def phases(waves, elem_start, elem_count, span, points):
    element = elem_start + jnp.arange(elem_count * P_SIZE, dtype=jnp.int32) // P_SIZE
    whole = waves[:, None] * (2 * element + 1)[None, :] % span
    fraction = waves.astype(jnp.float32)[:, None] * jnp.tile(points, elem_count)[None, :]
    return 2.0 * math.pi / span * (whole.astype(jnp.float32) + fraction)


def phases_at(waves, position, span, points):
    element = position // P_SIZE
    whole = waves[:, None] * (2 * element + 1)[None, :] % span
    fraction = waves.astype(jnp.float32)[:, None] * points[position % P_SIZE][None, :]
    return 2.0 * math.pi / span * (whole.astype(jnp.float32) + fraction)


def shift_pairs(sizes, steps):
    count = sizes[0] * sizes[1]
    pairs = []
    for source in range(count):
        t, g = divmod(source, sizes[1])
        target = ((t + steps[0]) % sizes[0]) * sizes[1] + (g + steps[1]) % sizes[1]
        pairs.append((source, target))
    return pairs


def local(field, flow, match_ops, wave_of_slot):
    tiles = lax.axis_size("tile")
    groups = lax.axis_size("deg")
    both = ("tile", "deg")
    tile_index = lax.axis_index("tile")
    group_index = lax.axis_index("deg")
    radial_nodes = field.shape[1]
    na_dev = field.shape[2]
    nb_dev = field.shape[3]
    elems_a = na_dev // P_SIZE
    elems_b = nb_dev // P_SIZE
    nb = nb_dev * groups
    span = 2 * elems_a * tiles
    scale = P_SIZE / (na_dev * tiles)
    points_list, weights_list, _ = gll_tables(P_SIZE)
    points = jnp.asarray(points_list, jnp.float32)
    weights = jnp.asarray(weights_list, jnp.float32)
    lead = (group_index > 0).astype(jnp.float32)
    trail = (group_index < groups - 1).astype(jnp.float32)
    w_r = jnp.tile(weights, radial_nodes // P_SIZE)
    w_a = jnp.tile(weights, elems_a)
    w_b = jnp.tile(weights, elems_b)
    mass3 = w_r[:, None, None] * w_a[None, :, None] * w_b[None, None, :]
    assembled = (
        assembled_weights(weights, radial_nodes // P_SIZE, 0.0, 0.0)[:, None, None]
        * assembled_weights(weights, elems_a, 1.0, 1.0)[None, :, None]
        * assembled_weights(weights, elems_b, lead, trail)[None, None, :]
    )
    column_mask = jnp.concatenate([lead[None], jnp.ones((nb_dev,), jnp.float32), trail[None]])
    rows_ext = (tile_index * na_dev - 1 + jnp.arange(na_dev + 2, dtype=jnp.int32)) % (na_dev * tiles)
    cols_ext = group_index * nb_dev - 1 + jnp.arange(nb_dev + 2, dtype=jnp.int32)
    surface_ext = weights[rows_ext % P_SIZE][:, None] * weights[cols_ext % P_SIZE][None, :]

    rows = radial_nodes * na_dev
    mats = derivative_tables(radial_nodes, na_dev, nb_dev)
    flat_mass = mass3.reshape(rows, nb_dev)
    flat_flow = flow.reshape(3, rows, nb_dev)
    grads = pl.pallas_call(
        gradient_kernel, out_shape=jax.ShapeDtypeStruct((9, rows, nb_dev), jnp.float32)
    )(flat_flow, mats)

    def owner_map(surface):
        angle = phases(wave_of_slot, tile_index * elems_a, elems_a, span, points)
        table = (
            jnp.stack([jnp.cos(angle), jnp.sin(angle)], axis=1) * (w_a * scale)[None, None, :]
        ).reshape(-1, na_dev)
        partial = jnp.dot(table, surface, precision=highest).reshape(-1, 2, nb_dev)
        gathered = lax.all_to_all(partial, both, 0, 0, tiled=True)
        coeff = gathered.reshape(tiles, groups, 2, nb_dev).sum(axis=0)
        coeff = coeff.transpose(1, 0, 2).reshape(2, nb)
        owned = coeff.astype(jnp.bfloat16)
        mapped = jnp.einsum(
            "pq,cq->cp", match_ops[0], owned, preferred_element_type=jnp.float32
        )
        edged = jnp.concatenate([mapped[:, :1], mapped, mapped[:, -1:]], axis=1)
        pieces = jnp.stack(
            [edged[:, g * nb_dev : g * nb_dev + nb_dev + 2] for g in range(groups)], axis=0
        )
        return jnp.broadcast_to(pieces[None], (tiles,) + pieces.shape).reshape(
            tiles, groups, 2 * (nb_dev + 2)
        )

    def flux_of(returned):
        angle = phases_at(wave_of_slot, rows_ext, span, points)
        synth = jnp.stack([jnp.cos(angle).T, jnp.sin(angle).T], axis=2).reshape(na_dev + 2, -1)
        flux = -jnp.dot(synth, returned.reshape(-1, nb_dev + 2), precision=highest)
        return diffusivity * surface_ext * flux

    mapped_len = 2 * (nb_dev + 2)
    slot_len = 3 * radial_nodes * na_dev
    carried_halo = tiles >= 3 and groups >= 3 and tiles * groups <= 64

    def joint_exchange(sent, stacked, edge_rows, edge_cols):
        a_lo = edge_rows[0].reshape(3, radial_nodes, 1, nb_dev)
        a_hi = edge_rows[1].reshape(3, radial_nodes, 1, nb_dev)
        up = [(i, (i + 1) % tiles) for i in range(tiles)]
        down = [(j, i) for i, j in up]
        from_up = lax.ppermute(a_hi, "tile", up)
        from_down = lax.ppermute(a_lo, "tile", down)
        b_lo = edge_cols[0].reshape(1, 1, -1)
        b_hi = edge_cols[1].reshape(1, 1, -1)
        out_pieces = [
            ((0, 1), b_hi),
            ((0, -1), b_lo),
            ((1, 1), b_hi),
            ((1, -1), b_lo),
            ((-1, 1), b_hi),
            ((-1, -1), b_lo),
        ]
        slots = jnp.zeros((tiles, groups, slot_len), jnp.float32)
        for (dt, dg), flat in out_pieces:
            slots = lax.dynamic_update_slice(
                slots, flat, ((tile_index + dt) % tiles, (group_index + dg) % groups, 0)
            )
        message = jnp.concatenate([sent, slots], axis=2).reshape(tiles * groups, -1)
        received = lax.all_to_all(message, both, 0, 0, tiled=True).reshape(tiles, groups, -1)
        returned = received[:, :, :mapped_len].reshape(tiles * groups, 2, nb_dev + 2)

        def take(dt, dg):
            row = lax.dynamic_slice(
                received,
                ((tile_index - dt) % tiles, (group_index - dg) % groups, mapped_len),
                (1, 1, slot_len),
            )
            return row.reshape(3, radial_nodes, na_dev, 1)

        from_left = take(0, 1)
        from_right = take(0, -1)
        corner_ul = take(1, 1)[:, :, na_dev - 1 :, :]
        corner_ur = take(1, -1)[:, :, na_dev - 1 :, :]
        corner_dl = take(-1, 1)[:, :, :1, :]
        corner_dr = take(-1, -1)[:, :, :1, :]
        top = jnp.concatenate([corner_ul, from_up, corner_ur], axis=3)
        middle = jnp.concatenate([from_left, stacked, from_right], axis=3)
        bottom = jnp.concatenate([corner_dl, from_down, corner_dr], axis=3)
        return returned, jnp.concatenate([top, middle, bottom], axis=2)

    def halo(stacked):
        a_lo = lax.slice_in_dim(stacked, 0, 1, axis=2)
        a_hi = lax.slice_in_dim(stacked, na_dev - 1, na_dev, axis=2)
        b_lo = lax.slice_in_dim(stacked, 0, 1, axis=3)
        b_hi = lax.slice_in_dim(stacked, nb_dev - 1, nb_dev, axis=3)
        sizes = (tiles, groups)
        from_up = lax.ppermute(a_hi, both, shift_pairs(sizes, (1, 0)))
        from_down = lax.ppermute(a_lo, both, shift_pairs(sizes, (-1, 0)))
        from_left = lax.ppermute(b_hi, both, shift_pairs(sizes, (0, 1)))
        from_right = lax.ppermute(b_lo, both, shift_pairs(sizes, (0, -1)))
        corner_ul = lax.ppermute(a_hi[:, :, :, -1:], both, shift_pairs(sizes, (1, 1)))
        corner_ur = lax.ppermute(a_hi[:, :, :, :1], both, shift_pairs(sizes, (1, -1)))
        corner_dl = lax.ppermute(a_lo[:, :, :, -1:], both, shift_pairs(sizes, (-1, 1)))
        corner_dr = lax.ppermute(a_lo[:, :, :, :1], both, shift_pairs(sizes, (-1, -1)))
        top = jnp.concatenate([corner_ul, from_up, corner_ur], axis=3)
        middle = jnp.concatenate([from_left, stacked, from_right], axis=3)
        bottom = jnp.concatenate([corner_dl, from_down, corner_dr], axis=3)
        return jnp.concatenate([top, middle, bottom], axis=2)

    def assemble_ext(padded):
        last = padded.ndim - 1
        padded = padded * column_mask
        along_a = assemble_dim(
            padded[..., 1:-1, :], last - 1, padded[..., 0:1, :], padded[..., -1:, :]
        )
        return assemble_dim(along_a[..., 1:-1], last, along_a[..., 0:1], along_a[..., -1:])

    def tendency(parts, surface):
        stacked, edge_rows, edge_cols = pl.pallas_call(
            volume_kernel,
            out_shape=(
                jax.ShapeDtypeStruct((3, rows, nb_dev), jnp.float32),
                jax.ShapeDtypeStruct((2, 3, radial_nodes, nb_dev), jnp.float32),
                jax.ShapeDtypeStruct((2, 3, rows), jnp.float32),
            ),
        )(parts.reshape(3, rows, nb_dev), flat_flow, grads, mats, flat_mass)
        stacked = stacked.reshape(parts.shape)
        sent = owner_map(surface)
        if carried_halo:
            returned, padded = joint_exchange(sent, stacked, edge_rows, edge_cols)
        else:
            returned = lax.all_to_all(
                sent.reshape(tiles * groups, -1), both, 0, 0, tiled=True
            ).reshape(tiles * groups, 2, nb_dev + 2)
            padded = halo(stacked)
        flux_term = flux_of(returned)
        outer = padded[0, radial_nodes - 1] + flux_term
        outer_rate = assemble_ext(outer) / assembled[radial_nodes - 1]
        padded = padded.at[0, radial_nodes - 1].add(flux_term)
        plane_r = jnp.zeros_like(lax.slice_in_dim(padded, 0, 1, axis=1))
        padded = assemble_dim(padded, 1, plane_r, plane_r)
        return assemble_ext(padded) / assembled[None], outer_rate

    first_rate, first_outer = tendency(field, field[0, radial_nodes - 1])
    section = field + time_step * first_rate
    section_outer = field[0, radial_nodes - 1] + time_step * first_outer
    second_rate, _ = tendency(section, section_outer)
    return 0.5 * (field + section + time_step * second_rate)


def solution(mesh):
    placed = (
        P(None, None, "tile", "deg"),
        P(None, None, "tile", "deg"),
        P(("tile", "deg"), None, None),
        P(),
    )
    return jax.shard_map(
        local, mesh=mesh, in_specs=placed, out_specs=P(None, None, "tile", "deg"), check_vma=False
    )
```

```python
import math

import numpy as np
import jax
import jax.numpy as jnp
from jax import lax
from jax.sharding import PartitionSpec as P
from jax.experimental import pallas as pl

P_SIZE = 8


diffusivity = 0.05
time_step = 0.01
highest = lax.Precision.HIGHEST
gll_interior = [0.2092992179024789, 0.5917001814331423, 0.8717401485096066]


def padded_2(value, sides, width):
    for axis, dim in sides:
        size, length = (lax.axis_size(axis), value.shape[dim])
        up = [(i, (i + 1) % size) for i in range(size)]
        down = [(j, i) for i, j in up]
        last = lax.slice_in_dim(value, length - width, length, axis=dim)
        first = lax.slice_in_dim(value, 0, width, axis=dim)
        before = lax.ppermute(last, axis, up)
        after = lax.ppermute(first, axis, down)
        value = jnp.concatenate([before, value, after], axis=dim)
    return value


def product(a, b):
    return jnp.dot(a, b, precision=highest, preferred_element_type=jnp.float32)


def gradient_kernel(flow_ref, mats_ref, out_ref):
    for component in range(3):
        x = flow_ref[component]
        out_ref[3 * component] = product(mats_ref[0], x)
        out_ref[3 * component + 1] = product(mats_ref[1], x)
        out_ref[3 * component + 2] = product(x, mats_ref[2])


def volume_kernel(parts_ref, flow_ref, grad_ref, mats_ref, mass_ref, *outs):
    volume_body(parts_ref, flow_ref, grad_ref, mats_ref, mass_ref, *outs)


def first_volume_kernel(parts_ref, flow_ref, grad_ref, mats_ref, mass_ref, table_ref, *outs):
    volume_body(parts_ref, flow_ref, grad_ref, mats_ref, mass_ref, *outs[:3])
    depth = outs[0].shape[1] // outs[1].shape[2]
    surface = parts_ref[0, pl.ds(outs[0].shape[1] - depth, depth), :]
    outs[3][...] = product(table_ref[...], surface)


def volume_body(parts_ref, flow_ref, grad_ref, mats_ref, mass_ref, out_ref, rows_ref, cols_ref):
    mass = mass_ref[...]
    p = [parts_ref[i] for i in range(3)]
    f = [flow_ref[i] for i in range(3)]
    planes = out_ref.shape[1] // rows_ref.shape[2]
    width = out_ref.shape[2]
    for c in range(3):
        x = p[c]
        s0 = product(mats_ref[0], x)
        s1 = product(mats_ref[1], x)
        s2 = product(x, mats_ref[2])
        stretch = p[0] * grad_ref[3 * c] + p[1] * grad_ref[3 * c + 1] + p[2] * grad_ref[3 * c + 2]
        carried = f[0] * s0 + f[1] * s1 + f[2] * s2
        spread = (
            product(mats_ref[3], mass * s0)
            + product(mats_ref[4], mass * s1)
            + product(mass * s2, mats_ref[5])
        )
        result = mass * (stretch - carried) - diffusivity * spread
        out_ref[c] = result
        turned = result.T
        cols_ref[0, c : c + 1, :] = turned[0:1, :]
        cols_ref[1, c : c + 1, :] = turned[width - 1 : width, :]
    for c in range(3):
        rows_ref[0, c] = out_ref[c, pl.ds(0, rows_ref.shape[2], stride=planes), :]
        rows_ref[1, c] = out_ref[c, pl.ds(planes - 1, rows_ref.shape[2], stride=planes), :]


def derivative_tables(radial_nodes, na_dev, nb_dev):
    _, _, matrix_list = gll_tables(P_SIZE)
    dmat = np.asarray(matrix_list, np.float32)
    radial = np.kron(dmat, np.eye(na_dev, dtype=np.float32))
    first = np.kron(np.eye(radial_nodes * na_dev // P_SIZE, dtype=np.float32), dmat)
    second = np.kron(np.eye(nb_dev // P_SIZE, dtype=np.float32), dmat)
    return jnp.asarray(np.stack([radial, first, second.T, radial.T, first.T, second]))


def legendre_value(point, degree):
    previous = 1.0
    current = point
    for order in range(1, degree):
        following = ((2 * order + 1) * point * current - order * previous) / (order + 1)
        previous = current
        current = following
    return current


def gll_tables(count):
    degree = count - 1
    points = [-1.0] + [-value for value in reversed(gll_interior)] + list(gll_interior) + [1.0]
    values = [legendre_value(point, degree) for point in points]
    weights = [2.0 / (degree * (degree + 1) * value * value) for value in values]
    matrix = [
        [
            values[row] / (values[col] * (points[row] - points[col])) if row != col else 0.0
            for col in range(count)
        ]
        for row in range(count)
    ]
    matrix[0][0] = -degree * (degree + 1) / 4.0
    matrix[count - 1][count - 1] = degree * (degree + 1) / 4.0
    return (points, weights, matrix)


def apply_along(values, axis_pos, matrix):
    shape = values.shape
    blocks = values.reshape(
        shape[:axis_pos] + (shape[axis_pos] // P_SIZE, P_SIZE) + shape[axis_pos + 1 :]
    )
    letters = list("abcdefg"[: blocks.ndim])
    source = list(letters)
    source[axis_pos + 1] = "p"
    target = list(letters)
    target[axis_pos + 1] = "q"
    formula = "".join(source) + ",qp->" + "".join(target)
    return jnp.einsum(formula, blocks, matrix, precision=highest).reshape(shape)


def assemble_dim(values, axis_pos, left, right):
    shape = values.shape
    count = shape[axis_pos] // P_SIZE
    blocks = values.reshape(shape[:axis_pos] + (count, P_SIZE) + shape[axis_pos + 1 :])
    edge_shape = shape[:axis_pos] + (1, 1) + shape[axis_pos + 1 :]
    first = lax.slice_in_dim(blocks, 0, 1, axis=axis_pos + 1)
    last = lax.slice_in_dim(blocks, P_SIZE - 1, P_SIZE, axis=axis_pos + 1)
    before = jnp.concatenate(
        [left.reshape(edge_shape), lax.slice_in_dim(last, 0, count - 1, axis=axis_pos)],
        axis=axis_pos,
    )
    after = jnp.concatenate(
        [lax.slice_in_dim(first, 1, count, axis=axis_pos), right.reshape(edge_shape)], axis=axis_pos
    )
    middle = lax.slice_in_dim(blocks, 1, P_SIZE - 1, axis=axis_pos + 1)
    joined = jnp.concatenate([first + before, middle, last + after], axis=axis_pos + 1)
    return joined.reshape(shape)


def assembled_weights(weights, count, lead, trail):
    position = jnp.arange(count * P_SIZE, dtype=jnp.int32)
    local_point = position % P_SIZE
    element = position // P_SIZE
    base = jnp.tile(weights, count)
    starts = (
        jnp.where(local_point == 0, jnp.where(element > 0, 1.0, lead), 0.0) * weights[P_SIZE - 1]
    )
    ends = (
        jnp.where(local_point == P_SIZE - 1, jnp.where(element < count - 1, 1.0, trail), 0.0)
        * weights[0]
    )
    return base + starts + ends


def phases(waves, elem_start, elem_count, span, points):
    element = elem_start + jnp.arange(elem_count * P_SIZE, dtype=jnp.int32) // P_SIZE
    whole = waves[:, None] * (2 * element + 1)[None, :] % span
    fraction = waves.astype(jnp.float32)[:, None] * jnp.tile(points, elem_count)[None, :]
    return 2.0 * math.pi / span * (whole.astype(jnp.float32) + fraction)


def phases_at(waves, position, span, points):
    element = position // P_SIZE
    whole = waves[:, None] * (2 * element + 1)[None, :] % span
    fraction = waves.astype(jnp.float32)[:, None] * points[position % P_SIZE][None, :]
    return 2.0 * math.pi / span * (whole.astype(jnp.float32) + fraction)


def shift_pairs(sizes, steps):
    count = sizes[0] * sizes[1]
    pairs = []
    for source in range(count):
        t, g = divmod(source, sizes[1])
        target = ((t + steps[0]) % sizes[0]) * sizes[1] + (g + steps[1]) % sizes[1]
        pairs.append((source, target))
    return pairs


def local(field, flow, match_ops, wave_of_slot):
    tiles = lax.axis_size("tile")
    groups = lax.axis_size("deg")
    both = ("tile", "deg")
    tile_index = lax.axis_index("tile")
    group_index = lax.axis_index("deg")
    radial_nodes = field.shape[1]
    na_dev = field.shape[2]
    nb_dev = field.shape[3]
    elems_a = na_dev // P_SIZE
    elems_b = nb_dev // P_SIZE
    nb = nb_dev * groups
    span = 2 * elems_a * tiles
    scale = P_SIZE / (na_dev * tiles)
    points_list, weights_list, _ = gll_tables(P_SIZE)
    points = jnp.asarray(points_list, jnp.float32)
    weights = jnp.asarray(weights_list, jnp.float32)
    lead = (group_index > 0).astype(jnp.float32)
    trail = (group_index < groups - 1).astype(jnp.float32)
    w_r = jnp.tile(weights, radial_nodes // P_SIZE)
    w_a = jnp.tile(weights, elems_a)
    w_b = jnp.tile(weights, elems_b)
    mass3 = w_r[:, None, None] * w_a[None, :, None] * w_b[None, None, :]
    assembled = (
        assembled_weights(weights, radial_nodes // P_SIZE, 0.0, 0.0)[:, None, None]
        * assembled_weights(weights, elems_a, 1.0, 1.0)[None, :, None]
        * assembled_weights(weights, elems_b, lead, trail)[None, None, :]
    )
    column_mask = jnp.concatenate([lead[None], jnp.ones((nb_dev,), jnp.float32), trail[None]])
    rows_ext = (tile_index * na_dev - 1 + jnp.arange(na_dev + 2, dtype=jnp.int32)) % (na_dev * tiles)
    cols_ext = group_index * nb_dev - 1 + jnp.arange(nb_dev + 2, dtype=jnp.int32)
    surface_ext = weights[rows_ext % P_SIZE][:, None] * weights[cols_ext % P_SIZE][None, :]

    rows = radial_nodes * na_dev
    mats = derivative_tables(radial_nodes, na_dev, nb_dev)
    flat_mass = mass3.reshape(rows, nb_dev)
    flat_flow = flow.reshape(3, rows, nb_dev)
    grads = pl.pallas_call(
        gradient_kernel, out_shape=jax.ShapeDtypeStruct((9, rows, nb_dev), jnp.float32)
    )(flat_flow, mats)

    angle = phases(wave_of_slot, tile_index * elems_a, elems_a, span, points)
    analysis = (
        jnp.stack([jnp.cos(angle), jnp.sin(angle)], axis=1) * (w_a * scale)[None, None, :]
    ).reshape(-1, na_dev)

    def owner_map(partial):
        partial = partial.reshape(-1, 2, nb_dev)
        gathered = lax.all_to_all(partial, both, 0, 0, tiled=True)
        coeff = gathered.reshape(tiles, groups, 2, nb_dev).sum(axis=0)
        coeff = coeff.transpose(1, 0, 2).reshape(2, nb)
        owned = coeff.astype(jnp.bfloat16)
        mapped = jnp.einsum(
            "pq,cq->cp", match_ops[0], owned, preferred_element_type=jnp.float32
        )
        edged = jnp.concatenate([mapped[:, :1], mapped, mapped[:, -1:]], axis=1)
        pieces = jnp.stack(
            [edged[:, g * nb_dev : g * nb_dev + nb_dev + 2] for g in range(groups)], axis=0
        )
        return jnp.broadcast_to(pieces[None], (tiles,) + pieces.shape).reshape(
            tiles, groups, 2 * (nb_dev + 2)
        )

    def flux_of(returned):
        angle = phases_at(wave_of_slot, rows_ext, span, points)
        synth = jnp.stack([jnp.cos(angle).T, jnp.sin(angle).T], axis=2).reshape(na_dev + 2, -1)
        flux = -jnp.dot(synth, returned.reshape(-1, nb_dev + 2), precision=highest)
        return diffusivity * surface_ext * flux

    mapped_len = 2 * (nb_dev + 2)
    slot_len = 3 * radial_nodes * na_dev
    carried_halo = tiles >= 3 and groups >= 3 and tiles * groups <= 64

    def joint_exchange(sent, stacked, edge_rows, edge_cols):
        a_lo = edge_rows[0].reshape(3, radial_nodes, 1, nb_dev)
        a_hi = edge_rows[1].reshape(3, radial_nodes, 1, nb_dev)
        up = [(i, (i + 1) % tiles) for i in range(tiles)]
        down = [(j, i) for i, j in up]
        from_up = lax.ppermute(a_hi, "tile", up)
        from_down = lax.ppermute(a_lo, "tile", down)
        b_lo = edge_cols[0].reshape(1, 1, -1)
        b_hi = edge_cols[1].reshape(1, 1, -1)
        out_pieces = [
            ((0, 1), b_hi),
            ((0, -1), b_lo),
            ((1, 1), b_hi),
            ((1, -1), b_lo),
            ((-1, 1), b_hi),
            ((-1, -1), b_lo),
        ]
        slots = jnp.zeros((tiles, groups, slot_len), jnp.float32)
        for (dt, dg), flat in out_pieces:
            slots = lax.dynamic_update_slice(
                slots, flat, ((tile_index + dt) % tiles, (group_index + dg) % groups, 0)
            )
        message = jnp.concatenate([sent, slots], axis=2).reshape(tiles * groups, -1)
        received = lax.all_to_all(message, both, 0, 0, tiled=True).reshape(tiles, groups, -1)
        returned = received[:, :, :mapped_len].reshape(tiles * groups, 2, nb_dev + 2)

        def take(dt, dg):
            row = lax.dynamic_slice(
                received,
                ((tile_index - dt) % tiles, (group_index - dg) % groups, mapped_len),
                (1, 1, slot_len),
            )
            return row.reshape(3, radial_nodes, na_dev, 1)

        from_left = take(0, 1)
        from_right = take(0, -1)
        corner_ul = take(1, 1)[:, :, na_dev - 1 :, :]
        corner_ur = take(1, -1)[:, :, na_dev - 1 :, :]
        corner_dl = take(-1, 1)[:, :, :1, :]
        corner_dr = take(-1, -1)[:, :, :1, :]
        top = jnp.concatenate([corner_ul, from_up, corner_ur], axis=3)
        middle = jnp.concatenate([from_left, stacked, from_right], axis=3)
        bottom = jnp.concatenate([corner_dl, from_down, corner_dr], axis=3)
        return returned, jnp.concatenate([top, middle, bottom], axis=2)

    def halo(stacked):
        a_lo = lax.slice_in_dim(stacked, 0, 1, axis=2)
        a_hi = lax.slice_in_dim(stacked, na_dev - 1, na_dev, axis=2)
        b_lo = lax.slice_in_dim(stacked, 0, 1, axis=3)
        b_hi = lax.slice_in_dim(stacked, nb_dev - 1, nb_dev, axis=3)
        sizes = (tiles, groups)
        from_up = lax.ppermute(a_hi, both, shift_pairs(sizes, (1, 0)))
        from_down = lax.ppermute(a_lo, both, shift_pairs(sizes, (-1, 0)))
        from_left = lax.ppermute(b_hi, both, shift_pairs(sizes, (0, 1)))
        from_right = lax.ppermute(b_lo, both, shift_pairs(sizes, (0, -1)))
        corner_ul = lax.ppermute(a_hi[:, :, :, -1:], both, shift_pairs(sizes, (1, 1)))
        corner_ur = lax.ppermute(a_hi[:, :, :, :1], both, shift_pairs(sizes, (1, -1)))
        corner_dl = lax.ppermute(a_lo[:, :, :, -1:], both, shift_pairs(sizes, (-1, 1)))
        corner_dr = lax.ppermute(a_lo[:, :, :, :1], both, shift_pairs(sizes, (-1, -1)))
        top = jnp.concatenate([corner_ul, from_up, corner_ur], axis=3)
        middle = jnp.concatenate([from_left, stacked, from_right], axis=3)
        bottom = jnp.concatenate([corner_dl, from_down, corner_dr], axis=3)
        return jnp.concatenate([top, middle, bottom], axis=2)

    def assemble_ext(padded):
        last = padded.ndim - 1
        padded = padded * column_mask
        along_a = assemble_dim(
            padded[..., 1:-1, :], last - 1, padded[..., 0:1, :], padded[..., -1:, :]
        )
        return assemble_dim(along_a[..., 1:-1], last, along_a[..., 0:1], along_a[..., -1:])

    def tendency(parts, surface):
        shapes = (
            jax.ShapeDtypeStruct((3, rows, nb_dev), jnp.float32),
            jax.ShapeDtypeStruct((2, 3, radial_nodes, nb_dev), jnp.float32),
            jax.ShapeDtypeStruct((2, 3, rows), jnp.float32),
        )
        operands = (parts.reshape(3, rows, nb_dev), flat_flow, grads, mats, flat_mass)
        if surface is None:
            shapes = shapes + (jax.ShapeDtypeStruct(analysis.shape[:1] + (nb_dev,), jnp.float32),)
            stacked, edge_rows, edge_cols, partial = pl.pallas_call(
                first_volume_kernel, out_shape=shapes
            )(*operands, analysis)
        else:
            stacked, edge_rows, edge_cols = pl.pallas_call(volume_kernel, out_shape=shapes)(
                *operands
            )
            partial = jnp.dot(analysis, surface, precision=highest)
        stacked = stacked.reshape(parts.shape)
        sent = owner_map(partial)
        if carried_halo:
            returned, padded = joint_exchange(sent, stacked, edge_rows, edge_cols)
        else:
            returned = lax.all_to_all(
                sent.reshape(tiles * groups, -1), both, 0, 0, tiled=True
            ).reshape(tiles * groups, 2, nb_dev + 2)
            padded = halo(stacked)
        flux_term = flux_of(returned)
        outer = padded[0, radial_nodes - 1] + flux_term
        outer_rate = assemble_ext(outer) / assembled[radial_nodes - 1]
        padded = padded.at[0, radial_nodes - 1].add(flux_term)
        plane_r = jnp.zeros_like(lax.slice_in_dim(padded, 0, 1, axis=1))
        padded = assemble_dim(padded, 1, plane_r, plane_r)
        return assemble_ext(padded) / assembled[None], outer_rate

    first_rate, first_outer = tendency(field, None)
    section = field + time_step * first_rate
    section_outer = field[0, radial_nodes - 1] + time_step * first_outer
    second_rate, _ = tendency(section, section_outer)
    return 0.5 * (field + section + time_step * second_rate)


def solution(mesh):
    placed = (
        P(None, None, "tile", "deg"),
        P(None, None, "tile", "deg"),
        P(("tile", "deg"), None, None),
        P(),
    )
    return jax.shard_map(
        local, mesh=mesh, in_specs=placed, out_specs=P(None, None, "tile", "deg"), check_vma=False
    )
```

```python
import math

import numpy as np
import jax
import jax.numpy as jnp
from jax import lax
from jax.sharding import PartitionSpec as P
from jax.experimental import pallas as pl

P_SIZE = 8


diffusivity = 0.05
time_step = 0.01
highest = lax.Precision.HIGHEST
gll_interior = [0.2092992179024789, 0.5917001814331423, 0.8717401485096066]


def padded_2(value, sides, width):
    for axis, dim in sides:
        size, length = (lax.axis_size(axis), value.shape[dim])
        up = [(i, (i + 1) % size) for i in range(size)]
        down = [(j, i) for i, j in up]
        last = lax.slice_in_dim(value, length - width, length, axis=dim)
        first = lax.slice_in_dim(value, 0, width, axis=dim)
        before = lax.ppermute(last, axis, up)
        after = lax.ppermute(first, axis, down)
        value = jnp.concatenate([before, value, after], axis=dim)
    return value


def product(a, b):
    return jnp.dot(a, b, precision=highest, preferred_element_type=jnp.float32)


def gradient_kernel(flow_ref, mats_ref, out_ref):
    for component in range(3):
        x = flow_ref[component]
        out_ref[3 * component] = product(mats_ref[0], x)
        out_ref[3 * component + 1] = product(mats_ref[1], x)
        out_ref[3 * component + 2] = product(x, mats_ref[2])


def volume_kernel(parts_ref, flow_ref, grad_ref, mats_ref, mass_ref, *outs):
    volume_body(parts_ref, flow_ref, grad_ref, mats_ref, mass_ref, *outs)


def first_volume_kernel(parts_ref, flow_ref, grad_ref, mats_ref, mass_ref, table_ref, *outs):
    volume_body(parts_ref, flow_ref, grad_ref, mats_ref, mass_ref, *outs[:3])
    depth = outs[0].shape[1] // outs[1].shape[2]
    surface = parts_ref[0, pl.ds(outs[0].shape[1] - depth, depth), :]
    outs[3][...] = product(table_ref[...], surface)


def volume_body(parts_ref, flow_ref, grad_ref, mats_ref, mass_ref, out_ref, rows_ref, cols_ref):
    mass = mass_ref[...]
    p = [parts_ref[i] for i in range(3)]
    f = [flow_ref[i] for i in range(3)]
    planes = out_ref.shape[1] // rows_ref.shape[2]
    width = out_ref.shape[2]
    for c in range(3):
        x = p[c]
        s0 = product(mats_ref[0], x)
        s1 = product(mats_ref[1], x)
        s2 = product(x, mats_ref[2])
        stretch = p[0] * grad_ref[3 * c] + p[1] * grad_ref[3 * c + 1] + p[2] * grad_ref[3 * c + 2]
        carried = f[0] * s0 + f[1] * s1 + f[2] * s2
        spread = (
            product(mats_ref[3], mass * s0)
            + product(mats_ref[4], mass * s1)
            + product(mass * s2, mats_ref[5])
        )
        result = mass * (stretch - carried) - diffusivity * spread
        out_ref[c] = result
        turned = result.T
        cols_ref[0, c : c + 1, :] = turned[0:1, :]
        cols_ref[1, c : c + 1, :] = turned[width - 1 : width, :]
    for c in range(3):
        rows_ref[0, c] = out_ref[c, pl.ds(0, rows_ref.shape[2], stride=planes), :]
        rows_ref[1, c] = out_ref[c, pl.ds(planes - 1, rows_ref.shape[2], stride=planes), :]


def derivative_tables(radial_nodes, na_dev, nb_dev):
    _, _, matrix_list = gll_tables(P_SIZE)
    dmat = np.asarray(matrix_list, np.float32)
    radial = np.kron(dmat, np.eye(na_dev, dtype=np.float32))
    first = np.kron(np.eye(radial_nodes * na_dev // P_SIZE, dtype=np.float32), dmat)
    second = np.kron(np.eye(nb_dev // P_SIZE, dtype=np.float32), dmat)
    return jnp.asarray(np.stack([radial, first, second.T, radial.T, first.T, second]))


def legendre_value(point, degree):
    previous = 1.0
    current = point
    for order in range(1, degree):
        following = ((2 * order + 1) * point * current - order * previous) / (order + 1)
        previous = current
        current = following
    return current


def gll_tables(count):
    degree = count - 1
    points = [-1.0] + [-value for value in reversed(gll_interior)] + list(gll_interior) + [1.0]
    values = [legendre_value(point, degree) for point in points]
    weights = [2.0 / (degree * (degree + 1) * value * value) for value in values]
    matrix = [
        [
            values[row] / (values[col] * (points[row] - points[col])) if row != col else 0.0
            for col in range(count)
        ]
        for row in range(count)
    ]
    matrix[0][0] = -degree * (degree + 1) / 4.0
    matrix[count - 1][count - 1] = degree * (degree + 1) / 4.0
    return (points, weights, matrix)


def apply_along(values, axis_pos, matrix):
    shape = values.shape
    blocks = values.reshape(
        shape[:axis_pos] + (shape[axis_pos] // P_SIZE, P_SIZE) + shape[axis_pos + 1 :]
    )
    letters = list("abcdefg"[: blocks.ndim])
    source = list(letters)
    source[axis_pos + 1] = "p"
    target = list(letters)
    target[axis_pos + 1] = "q"
    formula = "".join(source) + ",qp->" + "".join(target)
    return jnp.einsum(formula, blocks, matrix, precision=highest).reshape(shape)


def assemble_dim(values, axis_pos, left, right):
    shape = values.shape
    count = shape[axis_pos] // P_SIZE
    blocks = values.reshape(shape[:axis_pos] + (count, P_SIZE) + shape[axis_pos + 1 :])
    edge_shape = shape[:axis_pos] + (1, 1) + shape[axis_pos + 1 :]
    first = lax.slice_in_dim(blocks, 0, 1, axis=axis_pos + 1)
    last = lax.slice_in_dim(blocks, P_SIZE - 1, P_SIZE, axis=axis_pos + 1)
    before = jnp.concatenate(
        [left.reshape(edge_shape), lax.slice_in_dim(last, 0, count - 1, axis=axis_pos)],
        axis=axis_pos,
    )
    after = jnp.concatenate(
        [lax.slice_in_dim(first, 1, count, axis=axis_pos), right.reshape(edge_shape)], axis=axis_pos
    )
    middle = lax.slice_in_dim(blocks, 1, P_SIZE - 1, axis=axis_pos + 1)
    joined = jnp.concatenate([first + before, middle, last + after], axis=axis_pos + 1)
    return joined.reshape(shape)


def assembled_weights(weights, count, lead, trail):
    position = jnp.arange(count * P_SIZE, dtype=jnp.int32)
    local_point = position % P_SIZE
    element = position // P_SIZE
    base = jnp.tile(weights, count)
    starts = (
        jnp.where(local_point == 0, jnp.where(element > 0, 1.0, lead), 0.0) * weights[P_SIZE - 1]
    )
    ends = (
        jnp.where(local_point == P_SIZE - 1, jnp.where(element < count - 1, 1.0, trail), 0.0)
        * weights[0]
    )
    return base + starts + ends


def static_assembled(weights, count, lead, trail):
    position = np.arange(count * P_SIZE)
    local_point = position % P_SIZE
    element = position // P_SIZE
    starts = np.where(local_point == 0, np.where(element > 0, 1.0, lead), 0.0) * weights[P_SIZE - 1]
    ends = np.where(local_point == P_SIZE - 1, np.where(element < count - 1, 1.0, trail), 0.0)
    return (np.tile(weights, count) + starts + ends * weights[0]).astype(np.float32)


def phases(waves, elem_start, elem_count, span, points):
    element = elem_start + jnp.arange(elem_count * P_SIZE, dtype=jnp.int32) // P_SIZE
    whole = waves[:, None] * (2 * element + 1)[None, :] % span
    fraction = waves.astype(jnp.float32)[:, None] * np.tile(points, elem_count)[None, :]
    return 2.0 * math.pi / span * (whole.astype(jnp.float32) + fraction)


def phases_at(waves, element, point_values, span):
    whole = waves[:, None] * (2 * element + 1)[None, :] % span
    fraction = waves.astype(jnp.float32)[:, None] * point_values[None, :]
    return 2.0 * math.pi / span * (whole.astype(jnp.float32) + fraction)


def shift_pairs(sizes, steps):
    count = sizes[0] * sizes[1]
    pairs = []
    for source in range(count):
        t, g = divmod(source, sizes[1])
        target = ((t + steps[0]) % sizes[0]) * sizes[1] + (g + steps[1]) % sizes[1]
        pairs.append((source, target))
    return pairs


def local(field, flow, match_ops, wave_of_slot):
    tiles = lax.axis_size("tile")
    groups = lax.axis_size("deg")
    both = ("tile", "deg")
    tile_index = lax.axis_index("tile")
    group_index = lax.axis_index("deg")
    radial_nodes = field.shape[1]
    na_dev = field.shape[2]
    nb_dev = field.shape[3]
    elems_a = na_dev // P_SIZE
    elems_b = nb_dev // P_SIZE
    nb = nb_dev * groups
    span = 2 * elems_a * tiles
    scale = P_SIZE / (na_dev * tiles)
    points_list, weights_list, _ = gll_tables(P_SIZE)
    points = np.asarray(points_list, np.float32)
    weights = np.asarray(weights_list, np.float32)
    lead = (group_index > 0).astype(jnp.float32)
    trail = (group_index < groups - 1).astype(jnp.float32)
    w_r = np.tile(weights, radial_nodes // P_SIZE)
    w_a = np.tile(weights, elems_a)
    w_b = np.tile(weights, elems_b)
    mass3 = w_r[:, None, None] * w_a[None, :, None] * w_b[None, None, :]
    b_first = np.zeros((nb_dev,), np.float32)
    b_first[0] = weights[P_SIZE - 1]
    b_last = np.zeros((nb_dev,), np.float32)
    b_last[nb_dev - 1] = weights[0]
    assembled_b = static_assembled(weights, elems_b, 0.0, 0.0) + lead * b_first + trail * b_last
    assembled = (
        (
            static_assembled(weights, radial_nodes // P_SIZE, 0.0, 0.0)[:, None]
            * static_assembled(weights, elems_a, 1.0, 1.0)[None, :]
        )[:, :, None]
        * assembled_b[None, None, :]
    )
    column_mask = jnp.concatenate([lead[None], jnp.ones((nb_dev,), jnp.float32), trail[None]])
    rows_ext = (tile_index * na_dev - 1 + jnp.arange(na_dev + 2, dtype=jnp.int32)) % (na_dev * tiles)
    row_points = (np.arange(na_dev + 2) - 1) % P_SIZE
    col_points = (np.arange(nb_dev + 2) - 1) % P_SIZE
    surface_ext = diffusivity * weights[row_points][:, None] * weights[col_points][None, :]

    rows = radial_nodes * na_dev
    mats = derivative_tables(radial_nodes, na_dev, nb_dev)
    flat_mass = mass3.reshape(rows, nb_dev)
    flat_flow = flow.reshape(3, rows, nb_dev)
    grads = pl.pallas_call(
        gradient_kernel, out_shape=jax.ShapeDtypeStruct((9, rows, nb_dev), jnp.float32)
    )(flat_flow, mats)

    angle = phases(wave_of_slot, tile_index * elems_a, elems_a, span, points)
    analysis = (
        jnp.stack([jnp.cos(angle), jnp.sin(angle)], axis=1) * (w_a * scale)[None, None, :]
    ).reshape(-1, na_dev)

    def owner_map(partial):
        partial = partial.reshape(-1, 2, nb_dev)
        gathered = lax.all_to_all(partial, both, 0, 0, tiled=True)
        coeff = gathered.reshape(tiles, groups, 2, nb_dev).sum(axis=0)
        coeff = coeff.transpose(1, 0, 2).reshape(2, nb)
        owned = coeff.astype(jnp.bfloat16)
        mapped = jnp.einsum(
            "pq,cq->cp", match_ops[0], owned, preferred_element_type=jnp.float32
        )
        edged = jnp.concatenate([mapped[:, :1], mapped, mapped[:, -1:]], axis=1)
        pieces = jnp.stack(
            [edged[:, g * nb_dev : g * nb_dev + nb_dev + 2] for g in range(groups)], axis=0
        )
        return jnp.broadcast_to(pieces[None], (tiles,) + pieces.shape).reshape(
            tiles, groups, 2 * (nb_dev + 2)
        )

    def flux_of(returned):
        angle = phases_at(wave_of_slot, rows_ext // P_SIZE, points[row_points], span)
        synth = jnp.stack([jnp.cos(angle).T, jnp.sin(angle).T], axis=2).reshape(na_dev + 2, -1)
        flux = -jnp.dot(synth, returned.reshape(-1, nb_dev + 2), precision=highest)
        return surface_ext * flux

    mapped_len = 2 * (nb_dev + 2)
    slot_len = 3 * radial_nodes * na_dev
    carried_halo = tiles >= 3 and groups >= 3 and tiles * groups <= 64

    def joint_exchange(sent, stacked, edge_rows, edge_cols):
        a_lo = edge_rows[0].reshape(3, radial_nodes, 1, nb_dev)
        a_hi = edge_rows[1].reshape(3, radial_nodes, 1, nb_dev)
        up = [(i, (i + 1) % tiles) for i in range(tiles)]
        down = [(j, i) for i, j in up]
        from_up = lax.ppermute(a_hi, "tile", up)
        from_down = lax.ppermute(a_lo, "tile", down)
        b_lo = edge_cols[0].reshape(1, 1, -1)
        b_hi = edge_cols[1].reshape(1, 1, -1)
        out_pieces = [
            ((0, 1), b_hi),
            ((0, -1), b_lo),
            ((1, 1), b_hi),
            ((1, -1), b_lo),
            ((-1, 1), b_hi),
            ((-1, -1), b_lo),
        ]
        slots = jnp.zeros((tiles, groups, slot_len), jnp.float32)
        for (dt, dg), flat in out_pieces:
            slots = lax.dynamic_update_slice(
                slots, flat, ((tile_index + dt) % tiles, (group_index + dg) % groups, 0)
            )
        message = jnp.concatenate([sent, slots], axis=2).reshape(tiles * groups, -1)
        received = lax.all_to_all(message, both, 0, 0, tiled=True).reshape(tiles, groups, -1)
        returned = received[:, :, :mapped_len].reshape(tiles * groups, 2, nb_dev + 2)

        def take(dt, dg):
            row = lax.dynamic_slice(
                received,
                ((tile_index - dt) % tiles, (group_index - dg) % groups, mapped_len),
                (1, 1, slot_len),
            )
            return row.reshape(3, radial_nodes, na_dev, 1)

        from_left = take(0, 1)
        from_right = take(0, -1)
        corner_ul = take(1, 1)[:, :, na_dev - 1 :, :]
        corner_ur = take(1, -1)[:, :, na_dev - 1 :, :]
        corner_dl = take(-1, 1)[:, :, :1, :]
        corner_dr = take(-1, -1)[:, :, :1, :]
        top = jnp.concatenate([corner_ul, from_up, corner_ur], axis=3)
        middle = jnp.concatenate([from_left, stacked, from_right], axis=3)
        bottom = jnp.concatenate([corner_dl, from_down, corner_dr], axis=3)
        return returned, jnp.concatenate([top, middle, bottom], axis=2)

    def halo(stacked):
        a_lo = lax.slice_in_dim(stacked, 0, 1, axis=2)
        a_hi = lax.slice_in_dim(stacked, na_dev - 1, na_dev, axis=2)
        b_lo = lax.slice_in_dim(stacked, 0, 1, axis=3)
        b_hi = lax.slice_in_dim(stacked, nb_dev - 1, nb_dev, axis=3)
        sizes = (tiles, groups)
        from_up = lax.ppermute(a_hi, both, shift_pairs(sizes, (1, 0)))
        from_down = lax.ppermute(a_lo, both, shift_pairs(sizes, (-1, 0)))
        from_left = lax.ppermute(b_hi, both, shift_pairs(sizes, (0, 1)))
        from_right = lax.ppermute(b_lo, both, shift_pairs(sizes, (0, -1)))
        corner_ul = lax.ppermute(a_hi[:, :, :, -1:], both, shift_pairs(sizes, (1, 1)))
        corner_ur = lax.ppermute(a_hi[:, :, :, :1], both, shift_pairs(sizes, (1, -1)))
        corner_dl = lax.ppermute(a_lo[:, :, :, -1:], both, shift_pairs(sizes, (-1, 1)))
        corner_dr = lax.ppermute(a_lo[:, :, :, :1], both, shift_pairs(sizes, (-1, -1)))
        top = jnp.concatenate([corner_ul, from_up, corner_ur], axis=3)
        middle = jnp.concatenate([from_left, stacked, from_right], axis=3)
        bottom = jnp.concatenate([corner_dl, from_down, corner_dr], axis=3)
        return jnp.concatenate([top, middle, bottom], axis=2)

    def assemble_ext(padded):
        last = padded.ndim - 1
        padded = padded * column_mask
        along_a = assemble_dim(
            padded[..., 1:-1, :], last - 1, padded[..., 0:1, :], padded[..., -1:, :]
        )
        return assemble_dim(along_a[..., 1:-1], last, along_a[..., 0:1], along_a[..., -1:])

    def tendency(parts, surface):
        shapes = (
            jax.ShapeDtypeStruct((3, rows, nb_dev), jnp.float32),
            jax.ShapeDtypeStruct((2, 3, radial_nodes, nb_dev), jnp.float32),
            jax.ShapeDtypeStruct((2, 3, rows), jnp.float32),
        )
        operands = (parts.reshape(3, rows, nb_dev), flat_flow, grads, mats, flat_mass)
        if surface is None:
            shapes = shapes + (jax.ShapeDtypeStruct(analysis.shape[:1] + (nb_dev,), jnp.float32),)
            stacked, edge_rows, edge_cols, partial = pl.pallas_call(
                first_volume_kernel, out_shape=shapes
            )(*operands, analysis)
        else:
            stacked, edge_rows, edge_cols = pl.pallas_call(volume_kernel, out_shape=shapes)(
                *operands
            )
            partial = jnp.dot(analysis, surface, precision=highest)
        stacked = stacked.reshape(parts.shape)
        sent = owner_map(partial)
        if carried_halo:
            returned, padded = joint_exchange(sent, stacked, edge_rows, edge_cols)
        else:
            returned = lax.all_to_all(
                sent.reshape(tiles * groups, -1), both, 0, 0, tiled=True
            ).reshape(tiles * groups, 2, nb_dev + 2)
            padded = halo(stacked)
        flux_term = flux_of(returned)
        outer = padded[0, radial_nodes - 1] + flux_term
        outer_rate = assemble_ext(outer) / assembled[radial_nodes - 1]
        padded = padded.at[0, radial_nodes - 1].add(flux_term)
        plane_r = jnp.zeros_like(lax.slice_in_dim(padded, 0, 1, axis=1))
        padded = assemble_dim(padded, 1, plane_r, plane_r)
        return assemble_ext(padded) / assembled[None], outer_rate

    first_rate, first_outer = tendency(field, None)
    section = field + time_step * first_rate
    section_outer = field[0, radial_nodes - 1] + time_step * first_outer
    second_rate, _ = tendency(section, section_outer)
    return 0.5 * (field + section + time_step * second_rate)


def solution(mesh):
    placed = (
        P(None, None, "tile", "deg"),
        P(None, None, "tile", "deg"),
        P(("tile", "deg"), None, None),
        P(),
    )
    return jax.shard_map(
        local, mesh=mesh, in_specs=placed, out_specs=P(None, None, "tile", "deg"), check_vma=False
    )
```

```python
import math

import numpy as np
import jax
import jax.numpy as jnp
from jax import lax
from jax.sharding import PartitionSpec as P
from jax.experimental import pallas as pl

P_SIZE = 8


diffusivity = 0.05
time_step = 0.01
highest = lax.Precision.HIGHEST
gll_interior = [0.2092992179024789, 0.5917001814331423, 0.8717401485096066]


def padded_2(value, sides, width):
    for axis, dim in sides:
        size, length = (lax.axis_size(axis), value.shape[dim])
        up = [(i, (i + 1) % size) for i in range(size)]
        down = [(j, i) for i, j in up]
        last = lax.slice_in_dim(value, length - width, length, axis=dim)
        first = lax.slice_in_dim(value, 0, width, axis=dim)
        before = lax.ppermute(last, axis, up)
        after = lax.ppermute(first, axis, down)
        value = jnp.concatenate([before, value, after], axis=dim)
    return value


def product(a, b):
    return jnp.dot(a, b, precision=highest, preferred_element_type=jnp.float32)


def gradient_kernel(flow_ref, mats_ref, out_ref):
    for component in range(3):
        x = flow_ref[component]
        out_ref[3 * component] = product(mats_ref[0], x)
        out_ref[3 * component + 1] = product(mats_ref[1], x)
        out_ref[3 * component + 2] = product(x, mats_ref[2])


def volume_kernel(parts_ref, flow_ref, grad_ref, mats_ref, mass_ref, *outs):
    volume_body(parts_ref, flow_ref, grad_ref, mats_ref, mass_ref, *outs)


def first_volume_kernel(parts_ref, flow_ref, grad_ref, mats_ref, mass_ref, table_ref, *outs):
    volume_body(parts_ref, flow_ref, grad_ref, mats_ref, mass_ref, *outs[:3])
    depth = outs[0].shape[1] // outs[1].shape[2]
    surface = parts_ref[0, pl.ds(outs[0].shape[1] - depth, depth), :]
    outs[3][...] = product(table_ref[...], surface)


def volume_body(parts_ref, flow_ref, grad_ref, mats_ref, mass_ref, out_ref, rows_ref, cols_ref):
    mass = mass_ref[...]
    p = [parts_ref[i] for i in range(3)]
    f = [flow_ref[i] for i in range(3)]
    planes = out_ref.shape[1] // rows_ref.shape[2]
    width = out_ref.shape[2]
    for c in range(3):
        x = p[c]
        s0 = product(mats_ref[0], x)
        s1 = product(mats_ref[1], x)
        s2 = product(x, mats_ref[2])
        stretch = p[0] * grad_ref[3 * c] + p[1] * grad_ref[3 * c + 1] + p[2] * grad_ref[3 * c + 2]
        carried = f[0] * s0 + f[1] * s1 + f[2] * s2
        spread = (
            product(mats_ref[3], mass * s0)
            + product(mats_ref[4], mass * s1)
            + product(mass * s2, mats_ref[5])
        )
        result = mass * (stretch - carried) - diffusivity * spread
        out_ref[c] = result
        turned = result.T
        cols_ref[0, c : c + 1, :] = turned[0:1, :]
        cols_ref[1, c : c + 1, :] = turned[width - 1 : width, :]
    for c in range(3):
        rows_ref[0, c] = out_ref[c, pl.ds(0, rows_ref.shape[2], stride=planes), :]
        rows_ref[1, c] = out_ref[c, pl.ds(planes - 1, rows_ref.shape[2], stride=planes), :]


def derivative_tables(radial_nodes, na_dev, nb_dev):
    _, _, matrix_list = gll_tables(P_SIZE)
    dmat = np.asarray(matrix_list, np.float32)
    radial = np.kron(dmat, np.eye(na_dev, dtype=np.float32))
    first = np.kron(np.eye(radial_nodes * na_dev // P_SIZE, dtype=np.float32), dmat)
    second = np.kron(np.eye(nb_dev // P_SIZE, dtype=np.float32), dmat)
    return jnp.asarray(np.stack([radial, first, second.T, radial.T, first.T, second]))


def legendre_value(point, degree):
    previous = 1.0
    current = point
    for order in range(1, degree):
        following = ((2 * order + 1) * point * current - order * previous) / (order + 1)
        previous = current
        current = following
    return current


def gll_tables(count):
    degree = count - 1
    points = [-1.0] + [-value for value in reversed(gll_interior)] + list(gll_interior) + [1.0]
    values = [legendre_value(point, degree) for point in points]
    weights = [2.0 / (degree * (degree + 1) * value * value) for value in values]
    matrix = [
        [
            values[row] / (values[col] * (points[row] - points[col])) if row != col else 0.0
            for col in range(count)
        ]
        for row in range(count)
    ]
    matrix[0][0] = -degree * (degree + 1) / 4.0
    matrix[count - 1][count - 1] = degree * (degree + 1) / 4.0
    return (points, weights, matrix)


def apply_along(values, axis_pos, matrix):
    shape = values.shape
    blocks = values.reshape(
        shape[:axis_pos] + (shape[axis_pos] // P_SIZE, P_SIZE) + shape[axis_pos + 1 :]
    )
    letters = list("abcdefg"[: blocks.ndim])
    source = list(letters)
    source[axis_pos + 1] = "p"
    target = list(letters)
    target[axis_pos + 1] = "q"
    formula = "".join(source) + ",qp->" + "".join(target)
    return jnp.einsum(formula, blocks, matrix, precision=highest).reshape(shape)


def assemble_dim(values, axis_pos, left, right):
    shape = values.shape
    count = shape[axis_pos] // P_SIZE
    blocks = values.reshape(shape[:axis_pos] + (count, P_SIZE) + shape[axis_pos + 1 :])
    edge_shape = shape[:axis_pos] + (1, 1) + shape[axis_pos + 1 :]
    first = lax.slice_in_dim(blocks, 0, 1, axis=axis_pos + 1)
    last = lax.slice_in_dim(blocks, P_SIZE - 1, P_SIZE, axis=axis_pos + 1)
    before = jnp.concatenate(
        [left.reshape(edge_shape), lax.slice_in_dim(last, 0, count - 1, axis=axis_pos)],
        axis=axis_pos,
    )
    after = jnp.concatenate(
        [lax.slice_in_dim(first, 1, count, axis=axis_pos), right.reshape(edge_shape)], axis=axis_pos
    )
    middle = lax.slice_in_dim(blocks, 1, P_SIZE - 1, axis=axis_pos + 1)
    joined = jnp.concatenate([first + before, middle, last + after], axis=axis_pos + 1)
    return joined.reshape(shape)


def assembled_weights(weights, count, lead, trail):
    position = jnp.arange(count * P_SIZE, dtype=jnp.int32)
    local_point = position % P_SIZE
    element = position // P_SIZE
    base = jnp.tile(weights, count)
    starts = (
        jnp.where(local_point == 0, jnp.where(element > 0, 1.0, lead), 0.0) * weights[P_SIZE - 1]
    )
    ends = (
        jnp.where(local_point == P_SIZE - 1, jnp.where(element < count - 1, 1.0, trail), 0.0)
        * weights[0]
    )
    return base + starts + ends


def static_assembled(weights, count, lead, trail):
    position = np.arange(count * P_SIZE)
    local_point = position % P_SIZE
    element = position // P_SIZE
    starts = np.where(local_point == 0, np.where(element > 0, 1.0, lead), 0.0) * weights[P_SIZE - 1]
    ends = np.where(local_point == P_SIZE - 1, np.where(element < count - 1, 1.0, trail), 0.0)
    return (np.tile(weights, count) + starts + ends * weights[0]).astype(np.float32)


def phases(waves, elem_start, elem_count, span, points):
    element = elem_start + jnp.arange(elem_count * P_SIZE, dtype=jnp.int32) // P_SIZE
    whole = waves[:, None] * (2 * element + 1)[None, :] % span
    fraction = waves.astype(jnp.float32)[:, None] * np.tile(points, elem_count)[None, :]
    return 2.0 * math.pi / span * (whole.astype(jnp.float32) + fraction)


def phases_at(waves, element, point_values, span):
    whole = waves[:, None] * (2 * element + 1)[None, :] % span
    fraction = waves.astype(jnp.float32)[:, None] * point_values[None, :]
    return 2.0 * math.pi / span * (whole.astype(jnp.float32) + fraction)


def shift_pairs(sizes, steps):
    count = sizes[0] * sizes[1]
    pairs = []
    for source in range(count):
        t, g = divmod(source, sizes[1])
        target = ((t + steps[0]) % sizes[0]) * sizes[1] + (g + steps[1]) % sizes[1]
        pairs.append((source, target))
    return pairs


def local(field, flow, match_ops, wave_of_slot):
    tiles = lax.axis_size("tile")
    groups = lax.axis_size("deg")
    both = ("tile", "deg")
    tile_index = lax.axis_index("tile")
    group_index = lax.axis_index("deg")
    radial_nodes = field.shape[1]
    na_dev = field.shape[2]
    nb_dev = field.shape[3]
    elems_a = na_dev // P_SIZE
    elems_b = nb_dev // P_SIZE
    nb = nb_dev * groups
    span = 2 * elems_a * tiles
    scale = P_SIZE / (na_dev * tiles)
    points_list, weights_list, _ = gll_tables(P_SIZE)
    points = np.asarray(points_list, np.float32)
    weights = np.asarray(weights_list, np.float32)
    lead = (group_index > 0).astype(jnp.float32)
    trail = (group_index < groups - 1).astype(jnp.float32)
    w_r = np.tile(weights, radial_nodes // P_SIZE)
    w_a = np.tile(weights, elems_a)
    w_b = np.tile(weights, elems_b)
    mass3 = w_r[:, None, None] * w_a[None, :, None] * w_b[None, None, :]
    b_first = np.zeros((nb_dev,), np.float32)
    b_first[0] = weights[P_SIZE - 1]
    b_last = np.zeros((nb_dev,), np.float32)
    b_last[nb_dev - 1] = weights[0]
    assembled_b = static_assembled(weights, elems_b, 0.0, 0.0) + lead * b_first + trail * b_last
    assembled = (
        (
            static_assembled(weights, radial_nodes // P_SIZE, 0.0, 0.0)[:, None]
            * static_assembled(weights, elems_a, 1.0, 1.0)[None, :]
        )[:, :, None]
        * assembled_b[None, None, :]
    )
    rows_ext = (tile_index * na_dev - 1 + jnp.arange(na_dev + 2, dtype=jnp.int32)) % (na_dev * tiles)
    row_points = (np.arange(na_dev + 2) - 1) % P_SIZE
    col_points = (np.arange(nb_dev + 2) - 1) % P_SIZE
    surface_ext = diffusivity * weights[row_points][:, None] * weights[col_points][None, :]

    rows = radial_nodes * na_dev
    mats = derivative_tables(radial_nodes, na_dev, nb_dev)
    flat_mass = mass3.reshape(rows, nb_dev)
    flat_flow = flow.reshape(3, rows, nb_dev)
    grads = pl.pallas_call(
        gradient_kernel, out_shape=jax.ShapeDtypeStruct((9, rows, nb_dev), jnp.float32)
    )(flat_flow, mats)

    angle = phases(wave_of_slot, tile_index * elems_a, elems_a, span, points)
    analysis = (
        jnp.stack([jnp.cos(angle), jnp.sin(angle)], axis=1) * (w_a * scale)[None, None, :]
    ).reshape(-1, na_dev)

    def owner_map(partial):
        partial = partial.reshape(-1, 2, nb_dev)
        gathered = lax.all_to_all(partial, both, 0, 0, tiled=True)
        coeff = gathered.reshape(tiles, groups, 2, nb_dev).sum(axis=0)
        coeff = coeff.transpose(1, 0, 2).reshape(2, nb)
        owned = coeff.astype(jnp.bfloat16)
        mapped = jnp.einsum(
            "pq,cq->cp", match_ops[0], owned, preferred_element_type=jnp.float32
        )
        edged = jnp.concatenate([mapped[:, :1], mapped, mapped[:, -1:]], axis=1)
        pieces = jnp.stack(
            [edged[:, g * nb_dev : g * nb_dev + nb_dev + 2] for g in range(groups)], axis=0
        )
        return jnp.broadcast_to(pieces[None], (tiles,) + pieces.shape).reshape(
            tiles, groups, 2 * (nb_dev + 2)
        )

    def flux_of(returned):
        angle = phases_at(wave_of_slot, rows_ext // P_SIZE, points[row_points], span)
        synth = jnp.stack([jnp.cos(angle).T, jnp.sin(angle).T], axis=2).reshape(na_dev + 2, -1)
        flux = -jnp.dot(synth, returned.reshape(-1, nb_dev + 2), precision=highest)
        return surface_ext * flux

    mapped_len = 2 * (nb_dev + 2)
    slot_len = 3 * radial_nodes * na_dev
    carried_halo = tiles >= 3 and groups >= 3 and tiles * groups <= 64

    def joint_exchange(sent, stacked, edge_rows, edge_cols):
        a_lo = edge_rows[0].reshape(3, radial_nodes, 1, nb_dev)
        a_hi = edge_rows[1].reshape(3, radial_nodes, 1, nb_dev)
        up = [(i, (i + 1) % tiles) for i in range(tiles)]
        down = [(j, i) for i, j in up]
        from_up = lax.ppermute(a_hi, "tile", up)
        from_down = lax.ppermute(a_lo, "tile", down)
        b_lo = edge_cols[0].reshape(1, 1, -1)
        b_hi = edge_cols[1].reshape(1, 1, -1)
        out_pieces = [
            ((0, 1), b_hi),
            ((0, -1), b_lo),
            ((1, 1), b_hi),
            ((1, -1), b_lo),
            ((-1, 1), b_hi),
            ((-1, -1), b_lo),
        ]
        slots = jnp.zeros((tiles, groups, slot_len), jnp.float32)
        for (dt, dg), flat in out_pieces:
            slots = lax.dynamic_update_slice(
                slots, flat, ((tile_index + dt) % tiles, (group_index + dg) % groups, 0)
            )
        message = jnp.concatenate([sent, slots], axis=2).reshape(tiles * groups, -1)
        received = lax.all_to_all(message, both, 0, 0, tiled=True).reshape(tiles, groups, -1)
        returned = received[:, :, :mapped_len].reshape(tiles * groups, 2, nb_dev + 2)

        def take(dt, dg):
            row = lax.dynamic_slice(
                received,
                ((tile_index - dt) % tiles, (group_index - dg) % groups, mapped_len),
                (1, 1, slot_len),
            )
            return row.reshape(3, radial_nodes, na_dev, 1)

        from_left = take(0, 1)
        from_right = take(0, -1)
        corner_ul = take(1, 1)[:, :, na_dev - 1 :, :]
        corner_ur = take(1, -1)[:, :, na_dev - 1 :, :]
        corner_dl = take(-1, 1)[:, :, :1, :]
        corner_dr = take(-1, -1)[:, :, :1, :]
        top = jnp.concatenate([corner_ul, from_up, corner_ur], axis=3)
        middle = jnp.concatenate([from_left, stacked, from_right], axis=3)
        bottom = jnp.concatenate([corner_dl, from_down, corner_dr], axis=3)
        return returned, jnp.concatenate([top, middle, bottom], axis=2)

    def halo(stacked):
        a_lo = lax.slice_in_dim(stacked, 0, 1, axis=2)
        a_hi = lax.slice_in_dim(stacked, na_dev - 1, na_dev, axis=2)
        b_lo = lax.slice_in_dim(stacked, 0, 1, axis=3)
        b_hi = lax.slice_in_dim(stacked, nb_dev - 1, nb_dev, axis=3)
        sizes = (tiles, groups)
        from_up = lax.ppermute(a_hi, both, shift_pairs(sizes, (1, 0)))
        from_down = lax.ppermute(a_lo, both, shift_pairs(sizes, (-1, 0)))
        from_left = lax.ppermute(b_hi, both, shift_pairs(sizes, (0, 1)))
        from_right = lax.ppermute(b_lo, both, shift_pairs(sizes, (0, -1)))
        corner_ul = lax.ppermute(a_hi[:, :, :, -1:], both, shift_pairs(sizes, (1, 1)))
        corner_ur = lax.ppermute(a_hi[:, :, :, :1], both, shift_pairs(sizes, (1, -1)))
        corner_dl = lax.ppermute(a_lo[:, :, :, -1:], both, shift_pairs(sizes, (-1, 1)))
        corner_dr = lax.ppermute(a_lo[:, :, :, :1], both, shift_pairs(sizes, (-1, -1)))
        top = jnp.concatenate([corner_ul, from_up, corner_ur], axis=3)
        middle = jnp.concatenate([from_left, stacked, from_right], axis=3)
        bottom = jnp.concatenate([corner_dl, from_down, corner_dr], axis=3)
        return jnp.concatenate([top, middle, bottom], axis=2)

    join_b = np.zeros((nb_dev + 2, nb_dev), np.float32)
    join_b[np.arange(nb_dev) + 1, np.arange(nb_dev)] = 1.0
    inner_first = np.arange(P_SIZE, nb_dev, P_SIZE)
    join_b[inner_first, inner_first] = 1.0
    inner_last = np.arange(P_SIZE - 1, nb_dev - 1, P_SIZE)
    join_b[inner_last + 2, inner_last] = 1.0
    edge_lead = np.zeros((nb_dev + 2, nb_dev), np.float32)
    edge_lead[0, 0] = 1.0
    edge_trail = np.zeros((nb_dev + 2, nb_dev), np.float32)
    edge_trail[nb_dev + 1, nb_dev - 1] = 1.0
    join_b = join_b + lead * edge_lead + trail * edge_trail

    def assemble_ext(padded):
        last = padded.ndim - 1
        along_a = assemble_dim(
            padded[..., 1:-1, :], last - 1, padded[..., 0:1, :], padded[..., -1:, :]
        )
        return jnp.dot(along_a, join_b, precision=highest)

    def tendency(parts, surface):
        shapes = (
            jax.ShapeDtypeStruct((3, rows, nb_dev), jnp.float32),
            jax.ShapeDtypeStruct((2, 3, radial_nodes, nb_dev), jnp.float32),
            jax.ShapeDtypeStruct((2, 3, rows), jnp.float32),
        )
        operands = (parts.reshape(3, rows, nb_dev), flat_flow, grads, mats, flat_mass)
        if surface is None:
            shapes = shapes + (jax.ShapeDtypeStruct(analysis.shape[:1] + (nb_dev,), jnp.float32),)
            stacked, edge_rows, edge_cols, partial = pl.pallas_call(
                first_volume_kernel, out_shape=shapes
            )(*operands, analysis)
        else:
            stacked, edge_rows, edge_cols = pl.pallas_call(volume_kernel, out_shape=shapes)(
                *operands
            )
            partial = jnp.dot(analysis, surface, precision=highest)
        stacked = stacked.reshape(parts.shape)
        sent = owner_map(partial)
        if carried_halo:
            returned, padded = joint_exchange(sent, stacked, edge_rows, edge_cols)
        else:
            returned = lax.all_to_all(
                sent.reshape(tiles * groups, -1), both, 0, 0, tiled=True
            ).reshape(tiles * groups, 2, nb_dev + 2)
            padded = halo(stacked)
        flux_term = flux_of(returned)
        outer = padded[0, radial_nodes - 1] + flux_term
        outer_rate = assemble_ext(outer) / assembled[radial_nodes - 1]
        padded = padded.at[0, radial_nodes - 1].add(flux_term)
        plane_r = jnp.zeros_like(lax.slice_in_dim(padded, 0, 1, axis=1))
        padded = assemble_dim(padded, 1, plane_r, plane_r)
        return assemble_ext(padded) / assembled[None], outer_rate

    first_rate, first_outer = tendency(field, None)
    section = field + time_step * first_rate
    section_outer = field[0, radial_nodes - 1] + time_step * first_outer
    second_rate, _ = tendency(section, section_outer)
    return 0.5 * (field + section + time_step * second_rate)


def solution(mesh):
    placed = (
        P(None, None, "tile", "deg"),
        P(None, None, "tile", "deg"),
        P(("tile", "deg"), None, None),
        P(),
    )
    return jax.shard_map(
        local, mesh=mesh, in_specs=placed, out_specs=P(None, None, "tile", "deg"), check_vma=False
    )
```

```python
import math

import numpy as np
import jax
import jax.numpy as jnp
from jax import lax
from jax.sharding import PartitionSpec as P
from jax.experimental import pallas as pl

P_SIZE = 8


diffusivity = 0.05
time_step = 0.01
highest = lax.Precision.HIGHEST
gll_interior = [0.2092992179024789, 0.5917001814331423, 0.8717401485096066]


def padded_2(value, sides, width):
    for axis, dim in sides:
        size, length = (lax.axis_size(axis), value.shape[dim])
        up = [(i, (i + 1) % size) for i in range(size)]
        down = [(j, i) for i, j in up]
        last = lax.slice_in_dim(value, length - width, length, axis=dim)
        first = lax.slice_in_dim(value, 0, width, axis=dim)
        before = lax.ppermute(last, axis, up)
        after = lax.ppermute(first, axis, down)
        value = jnp.concatenate([before, value, after], axis=dim)
    return value


def product(a, b):
    return jnp.dot(a, b, precision=highest, preferred_element_type=jnp.float32)


def gradient_kernel(flow_ref, mats_ref, out_ref):
    for component in range(3):
        x = flow_ref[component]
        out_ref[3 * component] = product(mats_ref[0], x)
        out_ref[3 * component + 1] = product(mats_ref[1], x)
        out_ref[3 * component + 2] = product(x, mats_ref[2])


def volume_kernel(parts_ref, flow_ref, grad_ref, mats_ref, mass_ref, *outs):
    volume_body(parts_ref, flow_ref, grad_ref, mats_ref, mass_ref, *outs)


def first_volume_kernel(parts_ref, flow_ref, grad_ref, mats_ref, mass_ref, table_ref, *outs):
    volume_body(parts_ref, flow_ref, grad_ref, mats_ref, mass_ref, *outs[:3])
    depth = outs[0].shape[1] // outs[1].shape[2]
    surface = parts_ref[0, pl.ds(outs[0].shape[1] - depth, depth), :]
    outs[3][...] = product(table_ref[...], surface)


def volume_body(parts_ref, flow_ref, grad_ref, mats_ref, mass_ref, out_ref, rows_ref, cols_ref):
    mass = mass_ref[...]
    p = [parts_ref[i] for i in range(3)]
    f = [flow_ref[i] for i in range(3)]
    planes = out_ref.shape[1] // rows_ref.shape[2]
    width = out_ref.shape[2]
    for c in range(3):
        x = p[c]
        s0 = product(mats_ref[0], x)
        s1 = product(mats_ref[1], x)
        s2 = product(x, mats_ref[2])
        stretch = p[0] * grad_ref[3 * c] + p[1] * grad_ref[3 * c + 1] + p[2] * grad_ref[3 * c + 2]
        carried = f[0] * s0 + f[1] * s1 + f[2] * s2
        spread = (
            product(mats_ref[3], mass * s0)
            + product(mats_ref[4], mass * s1)
            + product(mass * s2, mats_ref[5])
        )
        result = mass * (stretch - carried) - diffusivity * spread
        out_ref[c] = result
        turned = result.T
        cols_ref[0, c : c + 1, :] = turned[0:1, :]
        cols_ref[1, c : c + 1, :] = turned[width - 1 : width, :]
    for c in range(3):
        rows_ref[0, c] = out_ref[c, pl.ds(0, rows_ref.shape[2], stride=planes), :]
        rows_ref[1, c] = out_ref[c, pl.ds(planes - 1, rows_ref.shape[2], stride=planes), :]


def derivative_tables(radial_nodes, na_dev, nb_dev):
    _, _, matrix_list = gll_tables(P_SIZE)
    dmat = np.asarray(matrix_list, np.float32)
    radial = np.kron(dmat, np.eye(na_dev, dtype=np.float32))
    first = np.kron(np.eye(radial_nodes * na_dev // P_SIZE, dtype=np.float32), dmat)
    second = np.kron(np.eye(nb_dev // P_SIZE, dtype=np.float32), dmat)
    return jnp.asarray(np.stack([radial, first, second.T, radial.T, first.T, second]))


def legendre_value(point, degree):
    previous = 1.0
    current = point
    for order in range(1, degree):
        following = ((2 * order + 1) * point * current - order * previous) / (order + 1)
        previous = current
        current = following
    return current


def gll_tables(count):
    degree = count - 1
    points = [-1.0] + [-value for value in reversed(gll_interior)] + list(gll_interior) + [1.0]
    values = [legendre_value(point, degree) for point in points]
    weights = [2.0 / (degree * (degree + 1) * value * value) for value in values]
    matrix = [
        [
            values[row] / (values[col] * (points[row] - points[col])) if row != col else 0.0
            for col in range(count)
        ]
        for row in range(count)
    ]
    matrix[0][0] = -degree * (degree + 1) / 4.0
    matrix[count - 1][count - 1] = degree * (degree + 1) / 4.0
    return (points, weights, matrix)


def apply_along(values, axis_pos, matrix):
    shape = values.shape
    blocks = values.reshape(
        shape[:axis_pos] + (shape[axis_pos] // P_SIZE, P_SIZE) + shape[axis_pos + 1 :]
    )
    letters = list("abcdefg"[: blocks.ndim])
    source = list(letters)
    source[axis_pos + 1] = "p"
    target = list(letters)
    target[axis_pos + 1] = "q"
    formula = "".join(source) + ",qp->" + "".join(target)
    return jnp.einsum(formula, blocks, matrix, precision=highest).reshape(shape)


def assemble_dim(values, axis_pos, left, right):
    shape = values.shape
    count = shape[axis_pos] // P_SIZE
    blocks = values.reshape(shape[:axis_pos] + (count, P_SIZE) + shape[axis_pos + 1 :])
    edge_shape = shape[:axis_pos] + (1, 1) + shape[axis_pos + 1 :]
    first = lax.slice_in_dim(blocks, 0, 1, axis=axis_pos + 1)
    last = lax.slice_in_dim(blocks, P_SIZE - 1, P_SIZE, axis=axis_pos + 1)
    before = jnp.concatenate(
        [left.reshape(edge_shape), lax.slice_in_dim(last, 0, count - 1, axis=axis_pos)],
        axis=axis_pos,
    )
    after = jnp.concatenate(
        [lax.slice_in_dim(first, 1, count, axis=axis_pos), right.reshape(edge_shape)], axis=axis_pos
    )
    middle = lax.slice_in_dim(blocks, 1, P_SIZE - 1, axis=axis_pos + 1)
    joined = jnp.concatenate([first + before, middle, last + after], axis=axis_pos + 1)
    return joined.reshape(shape)


def assembled_weights(weights, count, lead, trail):
    position = jnp.arange(count * P_SIZE, dtype=jnp.int32)
    local_point = position % P_SIZE
    element = position // P_SIZE
    base = jnp.tile(weights, count)
    starts = (
        jnp.where(local_point == 0, jnp.where(element > 0, 1.0, lead), 0.0) * weights[P_SIZE - 1]
    )
    ends = (
        jnp.where(local_point == P_SIZE - 1, jnp.where(element < count - 1, 1.0, trail), 0.0)
        * weights[0]
    )
    return base + starts + ends


def static_assembled(weights, count, lead, trail):
    position = np.arange(count * P_SIZE)
    local_point = position % P_SIZE
    element = position // P_SIZE
    starts = np.where(local_point == 0, np.where(element > 0, 1.0, lead), 0.0) * weights[P_SIZE - 1]
    ends = np.where(local_point == P_SIZE - 1, np.where(element < count - 1, 1.0, trail), 0.0)
    return (np.tile(weights, count) + starts + ends * weights[0]).astype(np.float32)


def phases(waves, elem_start, elem_count, span, points):
    element = elem_start + jnp.arange(elem_count * P_SIZE, dtype=jnp.int32) // P_SIZE
    whole = waves[:, None] * (2 * element + 1)[None, :] % span
    fraction = waves.astype(jnp.float32)[:, None] * np.tile(points, elem_count)[None, :]
    return 2.0 * math.pi / span * (whole.astype(jnp.float32) + fraction)


def phases_at(waves, element, point_values, span):
    whole = waves[:, None] * (2 * element + 1)[None, :] % span
    fraction = waves.astype(jnp.float32)[:, None] * point_values[None, :]
    return 2.0 * math.pi / span * (whole.astype(jnp.float32) + fraction)


def shift_pairs(sizes, steps):
    count = sizes[0] * sizes[1]
    pairs = []
    for source in range(count):
        t, g = divmod(source, sizes[1])
        target = ((t + steps[0]) % sizes[0]) * sizes[1] + (g + steps[1]) % sizes[1]
        pairs.append((source, target))
    return pairs


def local(field, flow, match_ops, wave_of_slot):
    tiles = lax.axis_size("tile")
    groups = lax.axis_size("deg")
    both = ("tile", "deg")
    tile_index = lax.axis_index("tile")
    group_index = lax.axis_index("deg")
    radial_nodes = field.shape[1]
    na_dev = field.shape[2]
    nb_dev = field.shape[3]
    elems_a = na_dev // P_SIZE
    elems_b = nb_dev // P_SIZE
    nb = nb_dev * groups
    span = 2 * elems_a * tiles
    scale = P_SIZE / (na_dev * tiles)
    points_list, weights_list, _ = gll_tables(P_SIZE)
    points = np.asarray(points_list, np.float32)
    weights = np.asarray(weights_list, np.float32)
    lead = (group_index > 0).astype(jnp.float32)
    trail = (group_index < groups - 1).astype(jnp.float32)
    w_r = np.tile(weights, radial_nodes // P_SIZE)
    w_a = np.tile(weights, elems_a)
    w_b = np.tile(weights, elems_b)
    mass3 = w_r[:, None, None] * w_a[None, :, None] * w_b[None, None, :]
    b_first = np.zeros((nb_dev,), np.float32)
    b_first[0] = weights[P_SIZE - 1]
    b_last = np.zeros((nb_dev,), np.float32)
    b_last[nb_dev - 1] = weights[0]
    assembled_b = static_assembled(weights, elems_b, 0.0, 0.0) + lead * b_first + trail * b_last
    assembled = (
        (
            static_assembled(weights, radial_nodes // P_SIZE, 0.0, 0.0)[:, None]
            * static_assembled(weights, elems_a, 1.0, 1.0)[None, :]
        )[:, :, None]
        * assembled_b[None, None, :]
    )
    rows_ext = (tile_index * na_dev - 1 + jnp.arange(na_dev + 2, dtype=jnp.int32)) % (na_dev * tiles)
    row_points = (np.arange(na_dev + 2) - 1) % P_SIZE
    col_points = (np.arange(nb_dev + 2) - 1) % P_SIZE
    surface_ext = diffusivity * weights[row_points][:, None] * weights[col_points][None, :]

    rows = radial_nodes * na_dev
    mats = derivative_tables(radial_nodes, na_dev, nb_dev)
    flat_mass = mass3.reshape(rows, nb_dev)
    flat_flow = flow.reshape(3, rows, nb_dev)
    grads = pl.pallas_call(
        gradient_kernel, out_shape=jax.ShapeDtypeStruct((9, rows, nb_dev), jnp.float32)
    )(flat_flow, mats)

    angle = phases(wave_of_slot, tile_index * elems_a, elems_a, span, points)
    analysis = (
        jnp.stack([jnp.cos(angle), jnp.sin(angle)], axis=1) * (w_a * scale)[None, None, :]
    ).reshape(-1, na_dev)

    def owner_map(partial):
        partial = partial.reshape(-1, 2, nb_dev)
        gathered = lax.all_to_all(partial, both, 0, 0, tiled=True)
        coeff = gathered.reshape(tiles, groups, 2, nb_dev).sum(axis=0)
        coeff = coeff.transpose(1, 0, 2).reshape(2, nb)
        owned = coeff.astype(jnp.bfloat16)
        mapped = jnp.einsum(
            "pq,cq->cp", match_ops[0], owned, preferred_element_type=jnp.float32
        )
        chunks = []
        for g in range(groups):
            low = max(g * nb_dev - 1, 0)
            high = min((g + 1) * nb_dev, nb - 1)
            chunks.append(
                jnp.concatenate(
                    [
                        mapped[:, g * nb_dev : (g + 1) * nb_dev],
                        mapped[:, low : low + 1],
                        mapped[:, high : high + 1],
                    ],
                    axis=1,
                )
            )
        pieces = jnp.stack(chunks, axis=0)
        return jnp.broadcast_to(pieces[None], (tiles,) + pieces.shape).reshape(
            tiles, groups, 2 * (nb_dev + 2)
        )

    row_order = np.concatenate([np.arange(1, na_dev + 1), [0, na_dev + 1]])
    col_order = np.concatenate([np.arange(1, nb_dev + 1), [0, nb_dev + 1]])
    surface_ordered = surface_ext[row_order][:, col_order]

    def flux_of(returned):
        angle = phases_at(
            wave_of_slot, rows_ext[row_order] // P_SIZE, points[row_points[row_order]], span
        )
        synth = jnp.stack([jnp.cos(angle).T, jnp.sin(angle).T], axis=2).reshape(na_dev + 2, -1)
        flux = surface_ordered * -jnp.dot(
            synth, returned.reshape(-1, nb_dev + 2), precision=highest
        )
        a, b = na_dev, nb_dev
        return (
            flux[:a, :b],
            flux[a : a + 1, :b],
            flux[a + 1 :, :b],
            flux[:a, b : b + 1],
            flux[:a, b + 1 :],
            flux[a : a + 1, b : b + 1],
            flux[a : a + 1, b + 1 :],
            flux[a + 1 :, b : b + 1],
            flux[a + 1 :, b + 1 :],
        )

    mapped_len = 2 * (nb_dev + 2)
    slot_len = 3 * radial_nodes * na_dev
    carried_halo = tiles >= 3 and groups >= 3 and tiles * groups <= 64

    def joint_exchange(sent, stacked, edge_rows, edge_cols):
        a_lo = edge_rows[0].reshape(3, radial_nodes, 1, nb_dev)
        a_hi = edge_rows[1].reshape(3, radial_nodes, 1, nb_dev)
        up = [(i, (i + 1) % tiles) for i in range(tiles)]
        down = [(j, i) for i, j in up]
        from_up = lax.ppermute(a_hi, "tile", up)
        from_down = lax.ppermute(a_lo, "tile", down)
        b_lo = edge_cols[0].reshape(1, 1, -1)
        b_hi = edge_cols[1].reshape(1, 1, -1)
        out_pieces = [
            ((0, 1), b_hi),
            ((0, -1), b_lo),
            ((1, 1), b_hi),
            ((1, -1), b_lo),
            ((-1, 1), b_hi),
            ((-1, -1), b_lo),
        ]
        slots = jnp.zeros((tiles, groups, slot_len), jnp.float32)
        for (dt, dg), flat in out_pieces:
            slots = lax.dynamic_update_slice(
                slots, flat, ((tile_index + dt) % tiles, (group_index + dg) % groups, 0)
            )
        message = jnp.concatenate([sent, slots], axis=2).reshape(tiles * groups, -1)
        received = lax.all_to_all(message, both, 0, 0, tiled=True).reshape(tiles, groups, -1)
        returned = received[:, :, :mapped_len].reshape(tiles * groups, 2, nb_dev + 2)

        def take(dt, dg):
            row = lax.dynamic_slice(
                received,
                ((tile_index - dt) % tiles, (group_index - dg) % groups, mapped_len),
                (1, 1, slot_len),
            )
            return row.reshape(3, radial_nodes, na_dev, 1)

        from_left = take(0, 1)
        from_right = take(0, -1)
        corner_ul = take(1, 1)[:, :, na_dev - 1 :, :]
        corner_ur = take(1, -1)[:, :, na_dev - 1 :, :]
        corner_dl = take(-1, 1)[:, :, :1, :]
        corner_dr = take(-1, -1)[:, :, :1, :]
        return returned, (
            stacked, from_up, from_down, from_left, from_right,
            corner_ul, corner_ur, corner_dl, corner_dr,
        )

    def halo(stacked):
        a_lo = lax.slice_in_dim(stacked, 0, 1, axis=2)
        a_hi = lax.slice_in_dim(stacked, na_dev - 1, na_dev, axis=2)
        b_lo = lax.slice_in_dim(stacked, 0, 1, axis=3)
        b_hi = lax.slice_in_dim(stacked, nb_dev - 1, nb_dev, axis=3)
        sizes = (tiles, groups)
        from_up = lax.ppermute(a_hi, both, shift_pairs(sizes, (1, 0)))
        from_down = lax.ppermute(a_lo, both, shift_pairs(sizes, (-1, 0)))
        from_left = lax.ppermute(b_hi, both, shift_pairs(sizes, (0, 1)))
        from_right = lax.ppermute(b_lo, both, shift_pairs(sizes, (0, -1)))
        corner_ul = lax.ppermute(a_hi[:, :, :, -1:], both, shift_pairs(sizes, (1, 1)))
        corner_ur = lax.ppermute(a_hi[:, :, :, :1], both, shift_pairs(sizes, (1, -1)))
        corner_dl = lax.ppermute(a_lo[:, :, :, -1:], both, shift_pairs(sizes, (-1, 1)))
        corner_dr = lax.ppermute(a_lo[:, :, :, :1], both, shift_pairs(sizes, (-1, -1)))
        return (
            stacked, from_up, from_down, from_left, from_right,
            corner_ul, corner_ur, corner_dl, corner_dr,
        )

    join_b = np.zeros((nb_dev + 2, nb_dev), np.float32)
    join_b[np.arange(nb_dev) + 1, np.arange(nb_dev)] = 1.0
    inner_first = np.arange(P_SIZE, nb_dev, P_SIZE)
    join_b[inner_first, inner_first] = 1.0
    inner_last = np.arange(P_SIZE - 1, nb_dev - 1, P_SIZE)
    join_b[inner_last + 2, inner_last] = 1.0
    join_core = join_b[1:-1]
    lane_first = np.zeros((nb_dev,), np.float32)
    lane_first[0] = 1.0
    lane_last = np.zeros((nb_dev,), np.float32)
    lane_last[nb_dev - 1] = 1.0
    edge_left = lead * lane_first
    edge_right = trail * lane_last
    plane_mask = np.zeros((3, radial_nodes, 1, 1), np.float32)
    plane_mask[0, radial_nodes - 1] = 1.0

    def assemble_pieces(core, up, down, left, right, ul, ur, dl, dr):
        axis = core.ndim - 2
        along_a = assemble_dim(core, axis, up, down)
        side_left = assemble_dim(left, axis, ul, dl)
        side_right = assemble_dim(right, axis, ur, dr)
        return (
            jnp.dot(along_a, join_core, precision=highest)
            + side_left * edge_left
            + side_right * edge_right
        )

    def tendency(parts, surface):
        shapes = (
            jax.ShapeDtypeStruct((3, rows, nb_dev), jnp.float32),
            jax.ShapeDtypeStruct((2, 3, radial_nodes, nb_dev), jnp.float32),
            jax.ShapeDtypeStruct((2, 3, rows), jnp.float32),
        )
        operands = (parts.reshape(3, rows, nb_dev), flat_flow, grads, mats, flat_mass)
        if surface is None:
            shapes = shapes + (jax.ShapeDtypeStruct(analysis.shape[:1] + (nb_dev,), jnp.float32),)
            stacked, edge_rows, edge_cols, partial = pl.pallas_call(
                first_volume_kernel, out_shape=shapes
            )(*operands, analysis)
        else:
            stacked, edge_rows, edge_cols = pl.pallas_call(volume_kernel, out_shape=shapes)(
                *operands
            )
            partial = jnp.dot(analysis, surface, precision=highest)
        stacked = stacked.reshape(parts.shape)
        sent = owner_map(partial)
        if carried_halo:
            returned, pieces = joint_exchange(sent, stacked, edge_rows, edge_cols)
        else:
            returned = lax.all_to_all(
                sent.reshape(tiles * groups, -1), both, 0, 0, tiled=True
            ).reshape(tiles * groups, 2, nb_dev + 2)
            pieces = halo(stacked)
        flux_pieces = flux_of(returned)
        outer = [p[0, radial_nodes - 1] + f for p, f in zip(pieces, flux_pieces)]
        outer_rate = assemble_pieces(*outer) / assembled[radial_nodes - 1]
        whole = [p + plane_mask * f for p, f in zip(pieces, flux_pieces)]
        joined = assemble_pieces(*whole)
        if radial_nodes // P_SIZE > 1:
            plane_r = jnp.zeros_like(lax.slice_in_dim(joined, 0, 1, axis=1))
            joined = assemble_dim(joined, 1, plane_r, plane_r)
        return joined / assembled[None], outer_rate

    first_rate, first_outer = tendency(field, None)
    section = field + time_step * first_rate
    section_outer = field[0, radial_nodes - 1] + time_step * first_outer
    second_rate, _ = tendency(section, section_outer)
    return 0.5 * (field + section + time_step * second_rate)


def solution(mesh):
    placed = (
        P(None, None, "tile", "deg"),
        P(None, None, "tile", "deg"),
        P(("tile", "deg"), None, None),
        P(),
    )
    return jax.shard_map(
        local, mesh=mesh, in_specs=placed, out_specs=P(None, None, "tile", "deg"), check_vma=False
    )
```

```python
import math

import numpy as np
import jax
import jax.numpy as jnp
from jax import lax
from jax.sharding import PartitionSpec as P
from jax.experimental import pallas as pl

P_SIZE = 8


diffusivity = 0.05
time_step = 0.01
highest = lax.Precision.HIGHEST
gll_interior = [0.2092992179024789, 0.5917001814331423, 0.8717401485096066]


def padded_2(value, sides, width):
    for axis, dim in sides:
        size, length = (lax.axis_size(axis), value.shape[dim])
        up = [(i, (i + 1) % size) for i in range(size)]
        down = [(j, i) for i, j in up]
        last = lax.slice_in_dim(value, length - width, length, axis=dim)
        first = lax.slice_in_dim(value, 0, width, axis=dim)
        before = lax.ppermute(last, axis, up)
        after = lax.ppermute(first, axis, down)
        value = jnp.concatenate([before, value, after], axis=dim)
    return value


def product(a, b):
    return jnp.dot(a, b, precision=highest, preferred_element_type=jnp.float32)


def gradient_kernel(flow_ref, mats_ref, out_ref):
    for component in range(3):
        x = flow_ref[component]
        out_ref[3 * component] = product(mats_ref[0], x)
        out_ref[3 * component + 1] = product(mats_ref[1], x)
        out_ref[3 * component + 2] = product(x, mats_ref[2])


def volume_kernel(parts_ref, flow_ref, grad_ref, mats_ref, mass_ref, *outs):
    volume_body(parts_ref, flow_ref, grad_ref, mats_ref, mass_ref, *outs)


def first_volume_kernel(parts_ref, flow_ref, grad_ref, mats_ref, mass_ref, table_ref, *outs):
    volume_body(parts_ref, flow_ref, grad_ref, mats_ref, mass_ref, *outs[:3])
    depth = outs[0].shape[1] // outs[1].shape[2]
    surface = parts_ref[0, pl.ds(outs[0].shape[1] - depth, depth), :]
    outs[3][...] = product(table_ref[...], surface)


def volume_body(parts_ref, flow_ref, grad_ref, mats_ref, mass_ref, out_ref, rows_ref, cols_ref):
    mass = mass_ref[...]
    p = [parts_ref[i] for i in range(3)]
    f = [flow_ref[i] for i in range(3)]
    planes = out_ref.shape[1] // rows_ref.shape[2]
    width = out_ref.shape[2]
    for c in range(3):
        x = p[c]
        s0 = product(mats_ref[0], x)
        s1 = product(mats_ref[1], x)
        s2 = product(x, mats_ref[2])
        stretch = p[0] * grad_ref[3 * c] + p[1] * grad_ref[3 * c + 1] + p[2] * grad_ref[3 * c + 2]
        carried = f[0] * s0 + f[1] * s1 + f[2] * s2
        spread = (
            product(mats_ref[3], mass * s0)
            + product(mats_ref[4], mass * s1)
            + product(mass * s2, mats_ref[5])
        )
        result = mass * (stretch - carried) - diffusivity * spread
        out_ref[c] = result
        turned = result.T
        cols_ref[0, c : c + 1, :] = turned[0:1, :]
        cols_ref[1, c : c + 1, :] = turned[width - 1 : width, :]
    for c in range(3):
        rows_ref[0, c] = out_ref[c, pl.ds(0, rows_ref.shape[2], stride=planes), :]
        rows_ref[1, c] = out_ref[c, pl.ds(planes - 1, rows_ref.shape[2], stride=planes), :]


def derivative_tables(radial_nodes, na_dev, nb_dev):
    _, _, matrix_list = gll_tables(P_SIZE)
    dmat = np.asarray(matrix_list, np.float32)
    radial = np.kron(dmat, np.eye(na_dev, dtype=np.float32))
    first = np.kron(np.eye(radial_nodes * na_dev // P_SIZE, dtype=np.float32), dmat)
    second = np.kron(np.eye(nb_dev // P_SIZE, dtype=np.float32), dmat)
    return jnp.asarray(np.stack([radial, first, second.T, radial.T, first.T, second]))


def legendre_value(point, degree):
    previous = 1.0
    current = point
    for order in range(1, degree):
        following = ((2 * order + 1) * point * current - order * previous) / (order + 1)
        previous = current
        current = following
    return current


def gll_tables(count):
    degree = count - 1
    points = [-1.0] + [-value for value in reversed(gll_interior)] + list(gll_interior) + [1.0]
    values = [legendre_value(point, degree) for point in points]
    weights = [2.0 / (degree * (degree + 1) * value * value) for value in values]
    matrix = [
        [
            values[row] / (values[col] * (points[row] - points[col])) if row != col else 0.0
            for col in range(count)
        ]
        for row in range(count)
    ]
    matrix[0][0] = -degree * (degree + 1) / 4.0
    matrix[count - 1][count - 1] = degree * (degree + 1) / 4.0
    return (points, weights, matrix)


def apply_along(values, axis_pos, matrix):
    shape = values.shape
    blocks = values.reshape(
        shape[:axis_pos] + (shape[axis_pos] // P_SIZE, P_SIZE) + shape[axis_pos + 1 :]
    )
    letters = list("abcdefg"[: blocks.ndim])
    source = list(letters)
    source[axis_pos + 1] = "p"
    target = list(letters)
    target[axis_pos + 1] = "q"
    formula = "".join(source) + ",qp->" + "".join(target)
    return jnp.einsum(formula, blocks, matrix, precision=highest).reshape(shape)


def assemble_dim(values, axis_pos, left, right):
    shape = values.shape
    count = shape[axis_pos] // P_SIZE
    blocks = values.reshape(shape[:axis_pos] + (count, P_SIZE) + shape[axis_pos + 1 :])
    edge_shape = shape[:axis_pos] + (1, 1) + shape[axis_pos + 1 :]
    first = lax.slice_in_dim(blocks, 0, 1, axis=axis_pos + 1)
    last = lax.slice_in_dim(blocks, P_SIZE - 1, P_SIZE, axis=axis_pos + 1)
    before = jnp.concatenate(
        [left.reshape(edge_shape), lax.slice_in_dim(last, 0, count - 1, axis=axis_pos)],
        axis=axis_pos,
    )
    after = jnp.concatenate(
        [lax.slice_in_dim(first, 1, count, axis=axis_pos), right.reshape(edge_shape)], axis=axis_pos
    )
    middle = lax.slice_in_dim(blocks, 1, P_SIZE - 1, axis=axis_pos + 1)
    joined = jnp.concatenate([first + before, middle, last + after], axis=axis_pos + 1)
    return joined.reshape(shape)


def assembled_weights(weights, count, lead, trail):
    position = jnp.arange(count * P_SIZE, dtype=jnp.int32)
    local_point = position % P_SIZE
    element = position // P_SIZE
    base = jnp.tile(weights, count)
    starts = (
        jnp.where(local_point == 0, jnp.where(element > 0, 1.0, lead), 0.0) * weights[P_SIZE - 1]
    )
    ends = (
        jnp.where(local_point == P_SIZE - 1, jnp.where(element < count - 1, 1.0, trail), 0.0)
        * weights[0]
    )
    return base + starts + ends


def static_assembled(weights, count, lead, trail):
    position = np.arange(count * P_SIZE)
    local_point = position % P_SIZE
    element = position // P_SIZE
    starts = np.where(local_point == 0, np.where(element > 0, 1.0, lead), 0.0) * weights[P_SIZE - 1]
    ends = np.where(local_point == P_SIZE - 1, np.where(element < count - 1, 1.0, trail), 0.0)
    return (np.tile(weights, count) + starts + ends * weights[0]).astype(np.float32)


def phases(waves, elem_start, elem_count, span, points):
    element = elem_start + jnp.arange(elem_count * P_SIZE, dtype=jnp.int32) // P_SIZE
    whole = waves[:, None] * (2 * element + 1)[None, :] % span
    fraction = waves.astype(jnp.float32)[:, None] * np.tile(points, elem_count)[None, :]
    return 2.0 * math.pi / span * (whole.astype(jnp.float32) + fraction)


def phases_at(waves, element, point_values, span):
    whole = waves[:, None] * (2 * element + 1)[None, :] % span
    fraction = waves.astype(jnp.float32)[:, None] * point_values[None, :]
    return 2.0 * math.pi / span * (whole.astype(jnp.float32) + fraction)


def shift_pairs(sizes, steps):
    count = sizes[0] * sizes[1]
    pairs = []
    for source in range(count):
        t, g = divmod(source, sizes[1])
        target = ((t + steps[0]) % sizes[0]) * sizes[1] + (g + steps[1]) % sizes[1]
        pairs.append((source, target))
    return pairs


def local(field, flow, match_ops, wave_of_slot):
    tiles = lax.axis_size("tile")
    groups = lax.axis_size("deg")
    both = ("tile", "deg")
    tile_index = lax.axis_index("tile")
    group_index = lax.axis_index("deg")
    radial_nodes = field.shape[1]
    na_dev = field.shape[2]
    nb_dev = field.shape[3]
    elems_a = na_dev // P_SIZE
    elems_b = nb_dev // P_SIZE
    nb = nb_dev * groups
    span = 2 * elems_a * tiles
    scale = P_SIZE / (na_dev * tiles)
    points_list, weights_list, _ = gll_tables(P_SIZE)
    points = np.asarray(points_list, np.float32)
    weights = np.asarray(weights_list, np.float32)
    lead = (group_index > 0).astype(jnp.float32)
    trail = (group_index < groups - 1).astype(jnp.float32)
    w_r = np.tile(weights, radial_nodes // P_SIZE)
    w_a = np.tile(weights, elems_a)
    w_b = np.tile(weights, elems_b)
    mass3 = w_r[:, None, None] * w_a[None, :, None] * w_b[None, None, :]
    b_first = np.zeros((nb_dev,), np.float32)
    b_first[0] = weights[P_SIZE - 1]
    b_last = np.zeros((nb_dev,), np.float32)
    b_last[nb_dev - 1] = weights[0]
    assembled_b = static_assembled(weights, elems_b, 0.0, 0.0) + lead * b_first + trail * b_last
    assembled = (
        (
            static_assembled(weights, radial_nodes // P_SIZE, 0.0, 0.0)[:, None]
            * static_assembled(weights, elems_a, 1.0, 1.0)[None, :]
        )[:, :, None]
        * assembled_b[None, None, :]
    )
    rows_ext = (tile_index * na_dev - 1 + jnp.arange(na_dev + 2, dtype=jnp.int32)) % (na_dev * tiles)
    row_points = (np.arange(na_dev + 2) - 1) % P_SIZE
    col_points = (np.arange(nb_dev + 2) - 1) % P_SIZE
    surface_ext = diffusivity * weights[row_points][:, None] * weights[col_points][None, :]

    rows = radial_nodes * na_dev
    mats = derivative_tables(radial_nodes, na_dev, nb_dev)
    flat_mass = mass3.reshape(rows, nb_dev)
    flat_flow = flow.reshape(3, rows, nb_dev)
    grads = pl.pallas_call(
        gradient_kernel, out_shape=jax.ShapeDtypeStruct((9, rows, nb_dev), jnp.float32)
    )(flat_flow, mats)

    angle = phases(wave_of_slot, tile_index * elems_a, elems_a, span, points)
    analysis = (
        jnp.stack([jnp.cos(angle), jnp.sin(angle)], axis=1) * (w_a * scale)[None, None, :]
    ).reshape(-1, na_dev)

    def owner_map(partial):
        partial = partial.reshape(-1, 2, nb_dev)
        gathered = lax.all_to_all(partial, both, 0, 0, tiled=True)
        coeff = gathered.reshape(tiles, groups, 2, nb_dev).sum(axis=0)
        coeff = coeff.transpose(1, 0, 2).reshape(2, nb)
        owned = coeff.astype(jnp.bfloat16)
        mapped = jnp.einsum(
            "pq,cq->cp", match_ops[0], owned, preferred_element_type=jnp.float32
        )
        edged = jnp.concatenate([mapped[:, :1], mapped, mapped[:, -1:]], axis=1)
        pieces = jnp.stack(
            [edged[:, g * nb_dev : g * nb_dev + nb_dev + 2] for g in range(groups)], axis=0
        )
        return jnp.broadcast_to(pieces[None], (tiles,) + pieces.shape).reshape(
            tiles, groups, 2 * (nb_dev + 2)
        )

    def flux_of(returned):
        angle = phases_at(wave_of_slot, rows_ext // P_SIZE, points[row_points], span)
        synth = jnp.stack([jnp.cos(angle).T, jnp.sin(angle).T], axis=2).reshape(na_dev + 2, -1)
        flux = -jnp.dot(synth, returned.reshape(-1, nb_dev + 2), precision=highest)
        return surface_ext * flux

    mapped_len = 2 * (nb_dev + 2)
    slot_len = 3 * radial_nodes * na_dev
    carried_halo = tiles >= 3 and groups >= 3 and tiles * groups <= 64

    def joint_exchange(sent, stacked, edge_rows, edge_cols):
        a_lo = edge_rows[0].reshape(3, radial_nodes, 1, nb_dev)
        a_hi = edge_rows[1].reshape(3, radial_nodes, 1, nb_dev)
        up = [(i, (i + 1) % tiles) for i in range(tiles)]
        down = [(j, i) for i, j in up]
        from_up = lax.ppermute(a_hi, "tile", up)
        from_down = lax.ppermute(a_lo, "tile", down)
        b_lo = edge_cols[0].reshape(1, 1, -1)
        b_hi = edge_cols[1].reshape(1, 1, -1)
        out_pieces = [
            ((0, 1), b_hi),
            ((0, -1), b_lo),
            ((1, 1), b_hi),
            ((1, -1), b_lo),
            ((-1, 1), b_hi),
            ((-1, -1), b_lo),
        ]
        slots = jnp.zeros((tiles, groups, slot_len), jnp.float32)
        for (dt, dg), flat in out_pieces:
            slots = lax.dynamic_update_slice(
                slots, flat, ((tile_index + dt) % tiles, (group_index + dg) % groups, 0)
            )
        message = jnp.concatenate([sent, slots], axis=2).reshape(tiles * groups, -1)
        received = lax.all_to_all(message, both, 0, 0, tiled=True).reshape(tiles, groups, -1)
        returned = received[:, :, :mapped_len].reshape(tiles * groups, 2, nb_dev + 2)

        def take(dt, dg):
            row = lax.dynamic_slice(
                received,
                ((tile_index - dt) % tiles, (group_index - dg) % groups, mapped_len),
                (1, 1, slot_len),
            )
            return row.reshape(3, radial_nodes, na_dev, 1)

        from_left = take(0, 1)
        from_right = take(0, -1)
        corner_ul = take(1, 1)[:, :, na_dev - 1 :, :]
        corner_ur = take(1, -1)[:, :, na_dev - 1 :, :]
        corner_dl = take(-1, 1)[:, :, :1, :]
        corner_dr = take(-1, -1)[:, :, :1, :]
        top = jnp.concatenate([corner_ul, from_up, corner_ur], axis=3)
        middle = jnp.concatenate([from_left, stacked, from_right], axis=3)
        bottom = jnp.concatenate([corner_dl, from_down, corner_dr], axis=3)
        return returned, jnp.concatenate([top, middle, bottom], axis=2)

    def halo(stacked):
        a_lo = lax.slice_in_dim(stacked, 0, 1, axis=2)
        a_hi = lax.slice_in_dim(stacked, na_dev - 1, na_dev, axis=2)
        b_lo = lax.slice_in_dim(stacked, 0, 1, axis=3)
        b_hi = lax.slice_in_dim(stacked, nb_dev - 1, nb_dev, axis=3)
        sizes = (tiles, groups)
        from_up = lax.ppermute(a_hi, both, shift_pairs(sizes, (1, 0)))
        from_down = lax.ppermute(a_lo, both, shift_pairs(sizes, (-1, 0)))
        from_left = lax.ppermute(b_hi, both, shift_pairs(sizes, (0, 1)))
        from_right = lax.ppermute(b_lo, both, shift_pairs(sizes, (0, -1)))
        corner_ul = lax.ppermute(a_hi[:, :, :, -1:], both, shift_pairs(sizes, (1, 1)))
        corner_ur = lax.ppermute(a_hi[:, :, :, :1], both, shift_pairs(sizes, (1, -1)))
        corner_dl = lax.ppermute(a_lo[:, :, :, -1:], both, shift_pairs(sizes, (-1, 1)))
        corner_dr = lax.ppermute(a_lo[:, :, :, :1], both, shift_pairs(sizes, (-1, -1)))
        top = jnp.concatenate([corner_ul, from_up, corner_ur], axis=3)
        middle = jnp.concatenate([from_left, stacked, from_right], axis=3)
        bottom = jnp.concatenate([corner_dl, from_down, corner_dr], axis=3)
        return jnp.concatenate([top, middle, bottom], axis=2)

    join_b = np.zeros((nb_dev + 2, nb_dev), np.float32)
    join_b[np.arange(nb_dev) + 1, np.arange(nb_dev)] = 1.0
    inner_first = np.arange(P_SIZE, nb_dev, P_SIZE)
    join_b[inner_first, inner_first] = 1.0
    inner_last = np.arange(P_SIZE - 1, nb_dev - 1, P_SIZE)
    join_b[inner_last + 2, inner_last] = 1.0
    edge_lead = np.zeros((nb_dev + 2, nb_dev), np.float32)
    edge_lead[0, 0] = 1.0
    edge_trail = np.zeros((nb_dev + 2, nb_dev), np.float32)
    edge_trail[nb_dev + 1, nb_dev - 1] = 1.0
    join_b = join_b + lead * edge_lead + trail * edge_trail

    plane_mask = np.zeros((3, radial_nodes, 1, 1), np.float32)
    plane_mask[0, radial_nodes - 1] = 1.0

    def assemble_ext(padded):
        last = padded.ndim - 1
        along_a = assemble_dim(
            padded[..., 1:-1, :], last - 1, padded[..., 0:1, :], padded[..., -1:, :]
        )
        return jnp.dot(along_a, join_b, precision=highest)

    def tendency(parts, surface):
        shapes = (
            jax.ShapeDtypeStruct((3, rows, nb_dev), jnp.float32),
            jax.ShapeDtypeStruct((2, 3, radial_nodes, nb_dev), jnp.float32),
            jax.ShapeDtypeStruct((2, 3, rows), jnp.float32),
        )
        operands = (parts.reshape(3, rows, nb_dev), flat_flow, grads, mats, flat_mass)
        if surface is None:
            shapes = shapes + (jax.ShapeDtypeStruct(analysis.shape[:1] + (nb_dev,), jnp.float32),)
            stacked, edge_rows, edge_cols, partial = pl.pallas_call(
                first_volume_kernel, out_shape=shapes
            )(*operands, analysis)
        else:
            stacked, edge_rows, edge_cols = pl.pallas_call(volume_kernel, out_shape=shapes)(
                *operands
            )
            partial = jnp.dot(analysis, surface, precision=highest)
        stacked = stacked.reshape(parts.shape)
        sent = owner_map(partial)
        if carried_halo:
            returned, padded = joint_exchange(sent, stacked, edge_rows, edge_cols)
        else:
            returned = lax.all_to_all(
                sent.reshape(tiles * groups, -1), both, 0, 0, tiled=True
            ).reshape(tiles * groups, 2, nb_dev + 2)
            padded = halo(stacked)
        flux_term = flux_of(returned)
        outer = padded[0, radial_nodes - 1] + flux_term
        outer_rate = assemble_ext(outer) / assembled[radial_nodes - 1]
        padded = padded + plane_mask * flux_term
        plane_r = jnp.zeros_like(lax.slice_in_dim(padded, 0, 1, axis=1))
        padded = assemble_dim(padded, 1, plane_r, plane_r)
        return assemble_ext(padded) / assembled[None], outer_rate

    first_rate, first_outer = tendency(field, None)
    section = field + time_step * first_rate
    section_outer = field[0, radial_nodes - 1] + time_step * first_outer
    second_rate, _ = tendency(section, section_outer)
    return 0.5 * (field + section + time_step * second_rate)


def solution(mesh):
    placed = (
        P(None, None, "tile", "deg"),
        P(None, None, "tile", "deg"),
        P(("tile", "deg"), None, None),
        P(),
    )
    return jax.shard_map(
        local, mesh=mesh, in_specs=placed, out_specs=P(None, None, "tile", "deg"), check_vma=False
    )
```

```python
import math

import numpy as np
import jax
import jax.numpy as jnp
from jax import lax
from jax.sharding import PartitionSpec as P
from jax.experimental import pallas as pl

P_SIZE = 8


diffusivity = 0.05
time_step = 0.01
highest = lax.Precision.HIGHEST
gll_interior = [0.2092992179024789, 0.5917001814331423, 0.8717401485096066]


def padded_2(value, sides, width):
    for axis, dim in sides:
        size, length = (lax.axis_size(axis), value.shape[dim])
        up = [(i, (i + 1) % size) for i in range(size)]
        down = [(j, i) for i, j in up]
        last = lax.slice_in_dim(value, length - width, length, axis=dim)
        first = lax.slice_in_dim(value, 0, width, axis=dim)
        before = lax.ppermute(last, axis, up)
        after = lax.ppermute(first, axis, down)
        value = jnp.concatenate([before, value, after], axis=dim)
    return value


def product(a, b):
    return jnp.dot(a, b, precision=highest, preferred_element_type=jnp.float32)


def gradient_kernel(flow_ref, mats_ref, out_ref):
    for component in range(3):
        x = flow_ref[component]
        out_ref[3 * component] = product(mats_ref[0], x)
        out_ref[3 * component + 1] = product(mats_ref[1], x)
        out_ref[3 * component + 2] = product(x, mats_ref[2])


def volume_kernel(parts_ref, flow_ref, grad_ref, mats_ref, mass_ref, *outs):
    volume_body(parts_ref, flow_ref, grad_ref, mats_ref, mass_ref, *outs)


def first_volume_kernel(parts_ref, flow_ref, grad_ref, mats_ref, mass_ref, table_ref, *outs):
    volume_body(parts_ref, flow_ref, grad_ref, mats_ref, mass_ref, *outs[:3])
    depth = outs[0].shape[1] // outs[1].shape[2]
    surface = parts_ref[0, pl.ds(outs[0].shape[1] - depth, depth), :]
    outs[3][...] = product(table_ref[...], surface)


def second_volume_kernel(field_ref, rate_ref, flow_ref, grad_ref, mats_ref, mass_ref, *outs):
    section_ref = outs[3]
    section_ref[...] = field_ref[...] + time_step * rate_ref[...]
    volume_body(section_ref, flow_ref, grad_ref, mats_ref, mass_ref, *outs[:3])


def volume_body(parts_ref, flow_ref, grad_ref, mats_ref, mass_ref, out_ref, rows_ref, cols_ref):
    mass = mass_ref[...]
    p = [parts_ref[i] for i in range(3)]
    f = [flow_ref[i] for i in range(3)]
    planes = out_ref.shape[1] // rows_ref.shape[2]
    width = out_ref.shape[2]
    for c in range(3):
        x = p[c]
        s0 = product(mats_ref[0], x)
        s1 = product(mats_ref[1], x)
        s2 = product(x, mats_ref[2])
        stretch = p[0] * grad_ref[3 * c] + p[1] * grad_ref[3 * c + 1] + p[2] * grad_ref[3 * c + 2]
        carried = f[0] * s0 + f[1] * s1 + f[2] * s2
        spread = (
            product(mats_ref[3], mass * s0)
            + product(mats_ref[4], mass * s1)
            + product(mass * s2, mats_ref[5])
        )
        result = mass * (stretch - carried) - diffusivity * spread
        out_ref[c] = result
        turned = result.T
        cols_ref[0, c : c + 1, :] = turned[0:1, :]
        cols_ref[1, c : c + 1, :] = turned[width - 1 : width, :]
    for c in range(3):
        rows_ref[0, c] = out_ref[c, pl.ds(0, rows_ref.shape[2], stride=planes), :]
        rows_ref[1, c] = out_ref[c, pl.ds(planes - 1, rows_ref.shape[2], stride=planes), :]


def derivative_tables(radial_nodes, na_dev, nb_dev):
    _, _, matrix_list = gll_tables(P_SIZE)
    dmat = np.asarray(matrix_list, np.float32)
    radial = np.kron(dmat, np.eye(na_dev, dtype=np.float32))
    first = np.kron(np.eye(radial_nodes * na_dev // P_SIZE, dtype=np.float32), dmat)
    second = np.kron(np.eye(nb_dev // P_SIZE, dtype=np.float32), dmat)
    return jnp.asarray(np.stack([radial, first, second.T, radial.T, first.T, second]))


def legendre_value(point, degree):
    previous = 1.0
    current = point
    for order in range(1, degree):
        following = ((2 * order + 1) * point * current - order * previous) / (order + 1)
        previous = current
        current = following
    return current


def gll_tables(count):
    degree = count - 1
    points = [-1.0] + [-value for value in reversed(gll_interior)] + list(gll_interior) + [1.0]
    values = [legendre_value(point, degree) for point in points]
    weights = [2.0 / (degree * (degree + 1) * value * value) for value in values]
    matrix = [
        [
            values[row] / (values[col] * (points[row] - points[col])) if row != col else 0.0
            for col in range(count)
        ]
        for row in range(count)
    ]
    matrix[0][0] = -degree * (degree + 1) / 4.0
    matrix[count - 1][count - 1] = degree * (degree + 1) / 4.0
    return (points, weights, matrix)


def apply_along(values, axis_pos, matrix):
    shape = values.shape
    blocks = values.reshape(
        shape[:axis_pos] + (shape[axis_pos] // P_SIZE, P_SIZE) + shape[axis_pos + 1 :]
    )
    letters = list("abcdefg"[: blocks.ndim])
    source = list(letters)
    source[axis_pos + 1] = "p"
    target = list(letters)
    target[axis_pos + 1] = "q"
    formula = "".join(source) + ",qp->" + "".join(target)
    return jnp.einsum(formula, blocks, matrix, precision=highest).reshape(shape)


def assemble_dim(values, axis_pos, left, right):
    shape = values.shape
    count = shape[axis_pos] // P_SIZE
    blocks = values.reshape(shape[:axis_pos] + (count, P_SIZE) + shape[axis_pos + 1 :])
    edge_shape = shape[:axis_pos] + (1, 1) + shape[axis_pos + 1 :]
    first = lax.slice_in_dim(blocks, 0, 1, axis=axis_pos + 1)
    last = lax.slice_in_dim(blocks, P_SIZE - 1, P_SIZE, axis=axis_pos + 1)
    before = jnp.concatenate(
        [left.reshape(edge_shape), lax.slice_in_dim(last, 0, count - 1, axis=axis_pos)],
        axis=axis_pos,
    )
    after = jnp.concatenate(
        [lax.slice_in_dim(first, 1, count, axis=axis_pos), right.reshape(edge_shape)], axis=axis_pos
    )
    middle = lax.slice_in_dim(blocks, 1, P_SIZE - 1, axis=axis_pos + 1)
    joined = jnp.concatenate([first + before, middle, last + after], axis=axis_pos + 1)
    return joined.reshape(shape)


def assembled_weights(weights, count, lead, trail):
    position = jnp.arange(count * P_SIZE, dtype=jnp.int32)
    local_point = position % P_SIZE
    element = position // P_SIZE
    base = jnp.tile(weights, count)
    starts = (
        jnp.where(local_point == 0, jnp.where(element > 0, 1.0, lead), 0.0) * weights[P_SIZE - 1]
    )
    ends = (
        jnp.where(local_point == P_SIZE - 1, jnp.where(element < count - 1, 1.0, trail), 0.0)
        * weights[0]
    )
    return base + starts + ends


def static_assembled(weights, count, lead, trail):
    position = np.arange(count * P_SIZE)
    local_point = position % P_SIZE
    element = position // P_SIZE
    starts = np.where(local_point == 0, np.where(element > 0, 1.0, lead), 0.0) * weights[P_SIZE - 1]
    ends = np.where(local_point == P_SIZE - 1, np.where(element < count - 1, 1.0, trail), 0.0)
    return (np.tile(weights, count) + starts + ends * weights[0]).astype(np.float32)


def phases(waves, elem_start, elem_count, span, points):
    element = elem_start + jnp.arange(elem_count * P_SIZE, dtype=jnp.int32) // P_SIZE
    whole = waves[:, None] * (2 * element + 1)[None, :] % span
    fraction = waves.astype(jnp.float32)[:, None] * np.tile(points, elem_count)[None, :]
    return 2.0 * math.pi / span * (whole.astype(jnp.float32) + fraction)


def phases_at(waves, element, point_values, span):
    whole = waves[:, None] * (2 * element + 1)[None, :] % span
    fraction = waves.astype(jnp.float32)[:, None] * point_values[None, :]
    return 2.0 * math.pi / span * (whole.astype(jnp.float32) + fraction)


def shift_pairs(sizes, steps):
    count = sizes[0] * sizes[1]
    pairs = []
    for source in range(count):
        t, g = divmod(source, sizes[1])
        target = ((t + steps[0]) % sizes[0]) * sizes[1] + (g + steps[1]) % sizes[1]
        pairs.append((source, target))
    return pairs


def local(field, flow, match_ops, wave_of_slot):
    tiles = lax.axis_size("tile")
    groups = lax.axis_size("deg")
    both = ("tile", "deg")
    tile_index = lax.axis_index("tile")
    group_index = lax.axis_index("deg")
    radial_nodes = field.shape[1]
    na_dev = field.shape[2]
    nb_dev = field.shape[3]
    elems_a = na_dev // P_SIZE
    elems_b = nb_dev // P_SIZE
    nb = nb_dev * groups
    span = 2 * elems_a * tiles
    scale = P_SIZE / (na_dev * tiles)
    points_list, weights_list, _ = gll_tables(P_SIZE)
    points = np.asarray(points_list, np.float32)
    weights = np.asarray(weights_list, np.float32)
    lead = (group_index > 0).astype(jnp.float32)
    trail = (group_index < groups - 1).astype(jnp.float32)
    w_r = np.tile(weights, radial_nodes // P_SIZE)
    w_a = np.tile(weights, elems_a)
    w_b = np.tile(weights, elems_b)
    mass3 = w_r[:, None, None] * w_a[None, :, None] * w_b[None, None, :]
    b_first = np.zeros((nb_dev,), np.float32)
    b_first[0] = weights[P_SIZE - 1]
    b_last = np.zeros((nb_dev,), np.float32)
    b_last[nb_dev - 1] = weights[0]
    assembled_b = static_assembled(weights, elems_b, 0.0, 0.0) + lead * b_first + trail * b_last
    assembled = (
        (
            static_assembled(weights, radial_nodes // P_SIZE, 0.0, 0.0)[:, None]
            * static_assembled(weights, elems_a, 1.0, 1.0)[None, :]
        )[:, :, None]
        * assembled_b[None, None, :]
    )
    rows_ext = (tile_index * na_dev - 1 + jnp.arange(na_dev + 2, dtype=jnp.int32)) % (na_dev * tiles)
    row_points = (np.arange(na_dev + 2) - 1) % P_SIZE
    col_points = (np.arange(nb_dev + 2) - 1) % P_SIZE
    surface_ext = diffusivity * weights[row_points][:, None] * weights[col_points][None, :]

    rows = radial_nodes * na_dev
    mats = derivative_tables(radial_nodes, na_dev, nb_dev)
    flat_mass = mass3.reshape(rows, nb_dev)
    flat_flow = flow.reshape(3, rows, nb_dev)
    grads = pl.pallas_call(
        gradient_kernel, out_shape=jax.ShapeDtypeStruct((9, rows, nb_dev), jnp.float32)
    )(flat_flow, mats)

    angle = phases(wave_of_slot, tile_index * elems_a, elems_a, span, points)
    analysis = (
        jnp.stack([jnp.cos(angle), jnp.sin(angle)], axis=1) * (w_a * scale)[None, None, :]
    ).reshape(-1, na_dev)

    def owner_map(partial):
        partial = partial.reshape(-1, 2, nb_dev)
        gathered = lax.all_to_all(partial, both, 0, 0, tiled=True)
        coeff = gathered.reshape(tiles, groups, 2, nb_dev).sum(axis=0)
        coeff = coeff.transpose(1, 0, 2).reshape(2, nb)
        owned = coeff.astype(jnp.bfloat16)
        mapped = jnp.einsum(
            "pq,cq->cp", match_ops[0], owned, preferred_element_type=jnp.float32
        )
        edged = jnp.concatenate([mapped[:, :1], mapped, mapped[:, -1:]], axis=1)
        pieces = jnp.stack(
            [edged[:, g * nb_dev : g * nb_dev + nb_dev + 2] for g in range(groups)], axis=0
        )
        return jnp.broadcast_to(pieces[None], (tiles,) + pieces.shape).reshape(
            tiles, groups, 2 * (nb_dev + 2)
        )

    def flux_of(returned):
        angle = phases_at(wave_of_slot, rows_ext // P_SIZE, points[row_points], span)
        synth = jnp.stack([jnp.cos(angle).T, jnp.sin(angle).T], axis=2).reshape(na_dev + 2, -1)
        flux = -jnp.dot(synth, returned.reshape(-1, nb_dev + 2), precision=highest)
        return surface_ext * flux

    mapped_len = 2 * (nb_dev + 2)
    slot_len = 3 * radial_nodes * na_dev
    carried_halo = tiles >= 3 and groups >= 3 and tiles * groups <= 64

    def joint_exchange(sent, stacked, edge_rows, edge_cols):
        a_lo = edge_rows[0].reshape(3, radial_nodes, 1, nb_dev)
        a_hi = edge_rows[1].reshape(3, radial_nodes, 1, nb_dev)
        up = [(i, (i + 1) % tiles) for i in range(tiles)]
        down = [(j, i) for i, j in up]
        from_up = lax.ppermute(a_hi, "tile", up)
        from_down = lax.ppermute(a_lo, "tile", down)
        b_lo = edge_cols[0].reshape(1, 1, -1)
        b_hi = edge_cols[1].reshape(1, 1, -1)
        out_pieces = [
            ((0, 1), b_hi),
            ((0, -1), b_lo),
            ((1, 1), b_hi),
            ((1, -1), b_lo),
            ((-1, 1), b_hi),
            ((-1, -1), b_lo),
        ]
        slots = jnp.zeros((tiles, groups, slot_len), jnp.float32)
        for (dt, dg), flat in out_pieces:
            slots = lax.dynamic_update_slice(
                slots, flat, ((tile_index + dt) % tiles, (group_index + dg) % groups, 0)
            )
        message = jnp.concatenate([sent, slots], axis=2).reshape(tiles * groups, -1)
        received = lax.all_to_all(message, both, 0, 0, tiled=True).reshape(tiles, groups, -1)
        returned = received[:, :, :mapped_len].reshape(tiles * groups, 2, nb_dev + 2)

        def take(dt, dg):
            row = lax.dynamic_slice(
                received,
                ((tile_index - dt) % tiles, (group_index - dg) % groups, mapped_len),
                (1, 1, slot_len),
            )
            return row.reshape(3, radial_nodes, na_dev, 1)

        from_left = take(0, 1)
        from_right = take(0, -1)
        corner_ul = take(1, 1)[:, :, na_dev - 1 :, :]
        corner_ur = take(1, -1)[:, :, na_dev - 1 :, :]
        corner_dl = take(-1, 1)[:, :, :1, :]
        corner_dr = take(-1, -1)[:, :, :1, :]
        top = jnp.concatenate([corner_ul, from_up, corner_ur], axis=3)
        middle = jnp.concatenate([from_left, stacked, from_right], axis=3)
        bottom = jnp.concatenate([corner_dl, from_down, corner_dr], axis=3)
        return returned, jnp.concatenate([top, middle, bottom], axis=2)

    def halo(stacked):
        a_lo = lax.slice_in_dim(stacked, 0, 1, axis=2)
        a_hi = lax.slice_in_dim(stacked, na_dev - 1, na_dev, axis=2)
        b_lo = lax.slice_in_dim(stacked, 0, 1, axis=3)
        b_hi = lax.slice_in_dim(stacked, nb_dev - 1, nb_dev, axis=3)
        sizes = (tiles, groups)
        from_up = lax.ppermute(a_hi, both, shift_pairs(sizes, (1, 0)))
        from_down = lax.ppermute(a_lo, both, shift_pairs(sizes, (-1, 0)))
        from_left = lax.ppermute(b_hi, both, shift_pairs(sizes, (0, 1)))
        from_right = lax.ppermute(b_lo, both, shift_pairs(sizes, (0, -1)))
        corner_ul = lax.ppermute(a_hi[:, :, :, -1:], both, shift_pairs(sizes, (1, 1)))
        corner_ur = lax.ppermute(a_hi[:, :, :, :1], both, shift_pairs(sizes, (1, -1)))
        corner_dl = lax.ppermute(a_lo[:, :, :, -1:], both, shift_pairs(sizes, (-1, 1)))
        corner_dr = lax.ppermute(a_lo[:, :, :, :1], both, shift_pairs(sizes, (-1, -1)))
        top = jnp.concatenate([corner_ul, from_up, corner_ur], axis=3)
        middle = jnp.concatenate([from_left, stacked, from_right], axis=3)
        bottom = jnp.concatenate([corner_dl, from_down, corner_dr], axis=3)
        return jnp.concatenate([top, middle, bottom], axis=2)

    join_b = np.zeros((nb_dev + 2, nb_dev), np.float32)
    join_b[np.arange(nb_dev) + 1, np.arange(nb_dev)] = 1.0
    inner_first = np.arange(P_SIZE, nb_dev, P_SIZE)
    join_b[inner_first, inner_first] = 1.0
    inner_last = np.arange(P_SIZE - 1, nb_dev - 1, P_SIZE)
    join_b[inner_last + 2, inner_last] = 1.0
    edge_lead = np.zeros((nb_dev + 2, nb_dev), np.float32)
    edge_lead[0, 0] = 1.0
    edge_trail = np.zeros((nb_dev + 2, nb_dev), np.float32)
    edge_trail[nb_dev + 1, nb_dev - 1] = 1.0
    join_b = join_b + lead * edge_lead + trail * edge_trail

    plane_mask = np.zeros((3, radial_nodes, 1, 1), np.float32)
    plane_mask[0, radial_nodes - 1] = 1.0

    def assemble_ext(padded):
        last = padded.ndim - 1
        along_a = assemble_dim(
            padded[..., 1:-1, :], last - 1, padded[..., 0:1, :], padded[..., -1:, :]
        )
        return jnp.dot(along_a, join_b, precision=highest)

    def tendency(parts, surface, rate=None):
        shapes = (
            jax.ShapeDtypeStruct((3, rows, nb_dev), jnp.float32),
            jax.ShapeDtypeStruct((2, 3, radial_nodes, nb_dev), jnp.float32),
            jax.ShapeDtypeStruct((2, 3, rows), jnp.float32),
        )
        operands = (parts.reshape(3, rows, nb_dev), flat_flow, grads, mats, flat_mass)
        section = None
        if rate is not None:
            shapes = shapes + (jax.ShapeDtypeStruct((3, rows, nb_dev), jnp.float32),)
            stacked, edge_rows, edge_cols, section = pl.pallas_call(
                second_volume_kernel, out_shape=shapes
            )(parts.reshape(3, rows, nb_dev), rate.reshape(3, rows, nb_dev), *operands[1:])
            section = section.reshape(parts.shape)
            partial = jnp.dot(analysis, surface, precision=highest)
        elif surface is None:
            shapes = shapes + (jax.ShapeDtypeStruct(analysis.shape[:1] + (nb_dev,), jnp.float32),)
            stacked, edge_rows, edge_cols, partial = pl.pallas_call(
                first_volume_kernel, out_shape=shapes
            )(*operands, analysis)
        else:
            stacked, edge_rows, edge_cols = pl.pallas_call(volume_kernel, out_shape=shapes)(
                *operands
            )
            partial = jnp.dot(analysis, surface, precision=highest)
        stacked = stacked.reshape(parts.shape)
        sent = owner_map(partial)
        if carried_halo:
            returned, padded = joint_exchange(sent, stacked, edge_rows, edge_cols)
        else:
            returned = lax.all_to_all(
                sent.reshape(tiles * groups, -1), both, 0, 0, tiled=True
            ).reshape(tiles * groups, 2, nb_dev + 2)
            padded = halo(stacked)
        flux_term = flux_of(returned)
        outer = padded[0, radial_nodes - 1] + flux_term
        outer_rate = assemble_ext(outer) / assembled[radial_nodes - 1]
        padded = padded + plane_mask * flux_term
        plane_r = jnp.zeros_like(lax.slice_in_dim(padded, 0, 1, axis=1))
        padded = assemble_dim(padded, 1, plane_r, plane_r)
        return assemble_ext(padded) / assembled[None], outer_rate, section

    first_rate, first_outer, _ = tendency(field, None)
    section_outer = field[0, radial_nodes - 1] + time_step * first_outer
    second_rate, _, section = tendency(field, section_outer, first_rate)
    return 0.5 * (field + section + time_step * second_rate)


def solution(mesh):
    placed = (
        P(None, None, "tile", "deg"),
        P(None, None, "tile", "deg"),
        P(("tile", "deg"), None, None),
        P(),
    )
    return jax.shard_map(
        local, mesh=mesh, in_specs=placed, out_specs=P(None, None, "tile", "deg"), check_vma=False
    )
```

```python
import math

import numpy as np
import jax
import jax.numpy as jnp
from jax import lax
from jax.sharding import PartitionSpec as P
from jax.experimental import pallas as pl

P_SIZE = 8


diffusivity = 0.05
time_step = 0.01
highest = lax.Precision.HIGHEST
gll_interior = [0.2092992179024789, 0.5917001814331423, 0.8717401485096066]


def padded_2(value, sides, width):
    for axis, dim in sides:
        size, length = (lax.axis_size(axis), value.shape[dim])
        up = [(i, (i + 1) % size) for i in range(size)]
        down = [(j, i) for i, j in up]
        last = lax.slice_in_dim(value, length - width, length, axis=dim)
        first = lax.slice_in_dim(value, 0, width, axis=dim)
        before = lax.ppermute(last, axis, up)
        after = lax.ppermute(first, axis, down)
        value = jnp.concatenate([before, value, after], axis=dim)
    return value


def product(a, b):
    return jnp.dot(a, b, precision=highest, preferred_element_type=jnp.float32)


def gradient_kernel(flow_ref, mats_ref, out_ref):
    for component in range(3):
        x = flow_ref[component]
        out_ref[3 * component] = product(mats_ref[0], x)
        out_ref[3 * component + 1] = product(mats_ref[1], x)
        out_ref[3 * component + 2] = product(x, mats_ref[2])


def volume_kernel(parts_ref, flow_ref, grad_ref, mats_ref, mass_ref, *outs):
    volume_body(parts_ref, flow_ref, grad_ref, mats_ref, mass_ref, *outs)


def first_volume_kernel(parts_ref, flow_ref, grad_ref, mats_ref, mass_ref, table_ref, *outs):
    volume_body(parts_ref, flow_ref, grad_ref, mats_ref, mass_ref, *outs[:3])
    depth = outs[0].shape[1] // outs[1].shape[2]
    surface = parts_ref[0, pl.ds(outs[0].shape[1] - depth, depth), :]
    outs[3][...] = product(table_ref[...], surface)


def volume_body(parts_ref, flow_ref, grad_ref, mats_ref, mass_ref, out_ref, rows_ref, cols_ref):
    mass = mass_ref[...]
    p = [parts_ref[i] for i in range(3)]
    f = [flow_ref[i] for i in range(3)]
    planes = out_ref.shape[1] // rows_ref.shape[2]
    width = out_ref.shape[2]
    for c in range(3):
        x = p[c]
        s0 = product(mats_ref[0], x)
        s1 = product(mats_ref[1], x)
        s2 = product(x, mats_ref[2])
        stretch = p[0] * grad_ref[3 * c] + p[1] * grad_ref[3 * c + 1] + p[2] * grad_ref[3 * c + 2]
        carried = f[0] * s0 + f[1] * s1 + f[2] * s2
        spread = (
            product(mats_ref[3], mass * s0)
            + product(mats_ref[4], mass * s1)
            + product(mass * s2, mats_ref[5])
        )
        result = mass * (stretch - carried) - diffusivity * spread
        out_ref[c] = result
        turned = result.T
        cols_ref[0, c : c + 1, :] = turned[0:1, :]
        cols_ref[1, c : c + 1, :] = turned[width - 1 : width, :]
    for c in range(3):
        rows_ref[0, c] = out_ref[c, pl.ds(0, rows_ref.shape[2], stride=planes), :]
        rows_ref[1, c] = out_ref[c, pl.ds(planes - 1, rows_ref.shape[2], stride=planes), :]


def derivative_tables(radial_nodes, na_dev, nb_dev):
    _, _, matrix_list = gll_tables(P_SIZE)
    dmat = np.asarray(matrix_list, np.float32)
    radial = np.kron(dmat, np.eye(na_dev, dtype=np.float32))
    first = np.kron(np.eye(radial_nodes * na_dev // P_SIZE, dtype=np.float32), dmat)
    second = np.kron(np.eye(nb_dev // P_SIZE, dtype=np.float32), dmat)
    return jnp.asarray(np.stack([radial, first, second.T, radial.T, first.T, second]))


def legendre_value(point, degree):
    previous = 1.0
    current = point
    for order in range(1, degree):
        following = ((2 * order + 1) * point * current - order * previous) / (order + 1)
        previous = current
        current = following
    return current


def gll_tables(count):
    degree = count - 1
    points = [-1.0] + [-value for value in reversed(gll_interior)] + list(gll_interior) + [1.0]
    values = [legendre_value(point, degree) for point in points]
    weights = [2.0 / (degree * (degree + 1) * value * value) for value in values]
    matrix = [
        [
            values[row] / (values[col] * (points[row] - points[col])) if row != col else 0.0
            for col in range(count)
        ]
        for row in range(count)
    ]
    matrix[0][0] = -degree * (degree + 1) / 4.0
    matrix[count - 1][count - 1] = degree * (degree + 1) / 4.0
    return (points, weights, matrix)


def apply_along(values, axis_pos, matrix):
    shape = values.shape
    blocks = values.reshape(
        shape[:axis_pos] + (shape[axis_pos] // P_SIZE, P_SIZE) + shape[axis_pos + 1 :]
    )
    letters = list("abcdefg"[: blocks.ndim])
    source = list(letters)
    source[axis_pos + 1] = "p"
    target = list(letters)
    target[axis_pos + 1] = "q"
    formula = "".join(source) + ",qp->" + "".join(target)
    return jnp.einsum(formula, blocks, matrix, precision=highest).reshape(shape)


def assemble_dim(values, axis_pos, left, right):
    shape = values.shape
    count = shape[axis_pos] // P_SIZE
    blocks = values.reshape(shape[:axis_pos] + (count, P_SIZE) + shape[axis_pos + 1 :])
    edge_shape = shape[:axis_pos] + (1, 1) + shape[axis_pos + 1 :]
    first = lax.slice_in_dim(blocks, 0, 1, axis=axis_pos + 1)
    last = lax.slice_in_dim(blocks, P_SIZE - 1, P_SIZE, axis=axis_pos + 1)
    before = jnp.concatenate(
        [left.reshape(edge_shape), lax.slice_in_dim(last, 0, count - 1, axis=axis_pos)],
        axis=axis_pos,
    )
    after = jnp.concatenate(
        [lax.slice_in_dim(first, 1, count, axis=axis_pos), right.reshape(edge_shape)], axis=axis_pos
    )
    middle = lax.slice_in_dim(blocks, 1, P_SIZE - 1, axis=axis_pos + 1)
    joined = jnp.concatenate([first + before, middle, last + after], axis=axis_pos + 1)
    return joined.reshape(shape)


def assembled_weights(weights, count, lead, trail):
    position = jnp.arange(count * P_SIZE, dtype=jnp.int32)
    local_point = position % P_SIZE
    element = position // P_SIZE
    base = jnp.tile(weights, count)
    starts = (
        jnp.where(local_point == 0, jnp.where(element > 0, 1.0, lead), 0.0) * weights[P_SIZE - 1]
    )
    ends = (
        jnp.where(local_point == P_SIZE - 1, jnp.where(element < count - 1, 1.0, trail), 0.0)
        * weights[0]
    )
    return base + starts + ends


def static_assembled(weights, count, lead, trail):
    position = np.arange(count * P_SIZE)
    local_point = position % P_SIZE
    element = position // P_SIZE
    starts = np.where(local_point == 0, np.where(element > 0, 1.0, lead), 0.0) * weights[P_SIZE - 1]
    ends = np.where(local_point == P_SIZE - 1, np.where(element < count - 1, 1.0, trail), 0.0)
    return (np.tile(weights, count) + starts + ends * weights[0]).astype(np.float32)


def phases(waves, elem_start, elem_count, span, points):
    element = elem_start + jnp.arange(elem_count * P_SIZE, dtype=jnp.int32) // P_SIZE
    whole = waves[:, None] * (2 * element + 1)[None, :] % span
    fraction = waves.astype(jnp.float32)[:, None] * np.tile(points, elem_count)[None, :]
    return 2.0 * math.pi / span * (whole.astype(jnp.float32) + fraction)


def phases_at(waves, element, point_values, span):
    whole = waves[:, None] * (2 * element + 1)[None, :] % span
    fraction = waves.astype(jnp.float32)[:, None] * point_values[None, :]
    return 2.0 * math.pi / span * (whole.astype(jnp.float32) + fraction)


def shift_pairs(sizes, steps):
    count = sizes[0] * sizes[1]
    pairs = []
    for source in range(count):
        t, g = divmod(source, sizes[1])
        target = ((t + steps[0]) % sizes[0]) * sizes[1] + (g + steps[1]) % sizes[1]
        pairs.append((source, target))
    return pairs


def local(field, flow, match_ops, wave_of_slot):
    tiles = lax.axis_size("tile")
    groups = lax.axis_size("deg")
    both = ("tile", "deg")
    tile_index = lax.axis_index("tile")
    group_index = lax.axis_index("deg")
    radial_nodes = field.shape[1]
    na_dev = field.shape[2]
    nb_dev = field.shape[3]
    elems_a = na_dev // P_SIZE
    elems_b = nb_dev // P_SIZE
    nb = nb_dev * groups
    span = 2 * elems_a * tiles
    scale = P_SIZE / (na_dev * tiles)
    points_list, weights_list, _ = gll_tables(P_SIZE)
    points = np.asarray(points_list, np.float32)
    weights = np.asarray(weights_list, np.float32)
    lead = (group_index > 0).astype(jnp.float32)
    trail = (group_index < groups - 1).astype(jnp.float32)
    w_r = np.tile(weights, radial_nodes // P_SIZE)
    w_a = np.tile(weights, elems_a)
    w_b = np.tile(weights, elems_b)
    mass3 = w_r[:, None, None] * w_a[None, :, None] * w_b[None, None, :]
    b_first = np.zeros((nb_dev,), np.float32)
    b_first[0] = weights[P_SIZE - 1]
    b_last = np.zeros((nb_dev,), np.float32)
    b_last[nb_dev - 1] = weights[0]
    assembled_b = static_assembled(weights, elems_b, 0.0, 0.0) + lead * b_first + trail * b_last
    assembled = (
        (
            static_assembled(weights, radial_nodes // P_SIZE, 0.0, 0.0)[:, None]
            * static_assembled(weights, elems_a, 1.0, 1.0)[None, :]
        )[:, :, None]
        * assembled_b[None, None, :]
    )
    rows_ext = (tile_index * na_dev - 1 + jnp.arange(na_dev + 2, dtype=jnp.int32)) % (na_dev * tiles)
    row_points = (np.arange(na_dev + 2) - 1) % P_SIZE
    col_points = (np.arange(nb_dev + 2) - 1) % P_SIZE
    surface_ext = diffusivity * weights[row_points][:, None] * weights[col_points][None, :]

    rows = radial_nodes * na_dev
    mats = derivative_tables(radial_nodes, na_dev, nb_dev)
    flat_mass = mass3.reshape(rows, nb_dev)
    flat_flow = flow.reshape(3, rows, nb_dev)
    grads = pl.pallas_call(
        gradient_kernel, out_shape=jax.ShapeDtypeStruct((9, rows, nb_dev), jnp.float32)
    )(flat_flow, mats)

    angle = phases(wave_of_slot, tile_index * elems_a, elems_a, span, points)
    analysis = (
        jnp.stack([jnp.cos(angle), jnp.sin(angle)], axis=1) * (w_a * scale)[None, None, :]
    ).reshape(-1, na_dev)

    def owner_map(partial):
        partial = partial.reshape(-1, 2, nb_dev)
        gathered = lax.all_to_all(partial, both, 0, 0, tiled=True)
        coeff = gathered.reshape(tiles, groups, 2, nb_dev).sum(axis=0)
        coeff = coeff.transpose(1, 0, 2).reshape(2, nb)
        owned = coeff.astype(jnp.bfloat16)
        mapped = jnp.einsum(
            "pq,cq->cp", match_ops[0], owned, preferred_element_type=jnp.float32
        )
        edged = jnp.concatenate([mapped[:, :1], mapped, mapped[:, -1:]], axis=1)
        pieces = jnp.stack(
            [edged[:, g * nb_dev : g * nb_dev + nb_dev + 2] for g in range(groups)], axis=0
        )
        return jnp.broadcast_to(pieces[None], (tiles,) + pieces.shape).reshape(
            tiles, groups, 2 * (nb_dev + 2)
        )

    def flux_of(returned):
        angle = phases_at(wave_of_slot, rows_ext // P_SIZE, points[row_points], span)
        synth = jnp.stack([jnp.cos(angle).T, jnp.sin(angle).T], axis=2).reshape(na_dev + 2, -1)
        flux = -jnp.dot(synth, returned.reshape(-1, nb_dev + 2), precision=highest)
        return surface_ext * flux

    mapped_len = 2 * (nb_dev + 2)
    slot_len = 3 * radial_nodes * na_dev
    carried_halo = tiles >= 3 and groups >= 3 and tiles * groups <= 64

    def joint_exchange(sent, stacked, edge_rows, edge_cols):
        a_lo = edge_rows[0].reshape(3, radial_nodes, 1, nb_dev)
        a_hi = edge_rows[1].reshape(3, radial_nodes, 1, nb_dev)
        up = [(i, (i + 1) % tiles) for i in range(tiles)]
        down = [(j, i) for i, j in up]
        from_up = lax.ppermute(a_hi, "tile", up)
        from_down = lax.ppermute(a_lo, "tile", down)
        b_lo = edge_cols[0].reshape(1, 1, -1)
        b_hi = edge_cols[1].reshape(1, 1, -1)
        out_pieces = [
            ((0, 1), b_hi),
            ((0, -1), b_lo),
            ((1, 1), b_hi),
            ((1, -1), b_lo),
            ((-1, 1), b_hi),
            ((-1, -1), b_lo),
        ]
        slots = jnp.zeros((tiles, groups, slot_len), jnp.float32)
        for (dt, dg), flat in out_pieces:
            slots = lax.dynamic_update_slice(
                slots, flat, ((tile_index + dt) % tiles, (group_index + dg) % groups, 0)
            )
        message = jnp.concatenate([sent, slots], axis=2).reshape(tiles * groups, -1)
        received = lax.all_to_all(message, both, 0, 0, tiled=True).reshape(tiles, groups, -1)
        returned = received[:, :, :mapped_len].reshape(tiles * groups, 2, nb_dev + 2)

        def take(dt, dg):
            row = lax.dynamic_slice(
                received,
                ((tile_index - dt) % tiles, (group_index - dg) % groups, mapped_len),
                (1, 1, slot_len),
            )
            return row.reshape(3, radial_nodes, na_dev, 1)

        from_left = take(0, 1)
        from_right = take(0, -1)
        corner_ul = take(1, 1)[:, :, na_dev - 1 :, :]
        corner_ur = take(1, -1)[:, :, na_dev - 1 :, :]
        corner_dl = take(-1, 1)[:, :, :1, :]
        corner_dr = take(-1, -1)[:, :, :1, :]
        top = jnp.concatenate([corner_ul, from_up, corner_ur], axis=3)
        middle = jnp.concatenate([from_left, stacked, from_right], axis=3)
        bottom = jnp.concatenate([corner_dl, from_down, corner_dr], axis=3)
        return returned, jnp.concatenate([top, middle, bottom], axis=2)

    def halo(stacked):
        a_lo = lax.slice_in_dim(stacked, 0, 1, axis=2)
        a_hi = lax.slice_in_dim(stacked, na_dev - 1, na_dev, axis=2)
        b_lo = lax.slice_in_dim(stacked, 0, 1, axis=3)
        b_hi = lax.slice_in_dim(stacked, nb_dev - 1, nb_dev, axis=3)
        sizes = (tiles, groups)
        from_up = lax.ppermute(a_hi, both, shift_pairs(sizes, (1, 0)))
        from_down = lax.ppermute(a_lo, both, shift_pairs(sizes, (-1, 0)))
        from_left = lax.ppermute(b_hi, both, shift_pairs(sizes, (0, 1)))
        from_right = lax.ppermute(b_lo, both, shift_pairs(sizes, (0, -1)))
        corner_ul = lax.ppermute(a_hi[:, :, :, -1:], both, shift_pairs(sizes, (1, 1)))
        corner_ur = lax.ppermute(a_hi[:, :, :, :1], both, shift_pairs(sizes, (1, -1)))
        corner_dl = lax.ppermute(a_lo[:, :, :, -1:], both, shift_pairs(sizes, (-1, 1)))
        corner_dr = lax.ppermute(a_lo[:, :, :, :1], both, shift_pairs(sizes, (-1, -1)))
        top = jnp.concatenate([corner_ul, from_up, corner_ur], axis=3)
        middle = jnp.concatenate([from_left, stacked, from_right], axis=3)
        bottom = jnp.concatenate([corner_dl, from_down, corner_dr], axis=3)
        return jnp.concatenate([top, middle, bottom], axis=2)

    join_b = np.zeros((nb_dev + 2, nb_dev), np.float32)
    join_b[np.arange(nb_dev) + 1, np.arange(nb_dev)] = 1.0
    inner_first = np.arange(P_SIZE, nb_dev, P_SIZE)
    join_b[inner_first, inner_first] = 1.0
    inner_last = np.arange(P_SIZE - 1, nb_dev - 1, P_SIZE)
    join_b[inner_last + 2, inner_last] = 1.0
    edge_lead = np.zeros((nb_dev + 2, nb_dev), np.float32)
    edge_lead[0, 0] = 1.0
    edge_trail = np.zeros((nb_dev + 2, nb_dev), np.float32)
    edge_trail[nb_dev + 1, nb_dev - 1] = 1.0
    join_b = join_b + lead * edge_lead + trail * edge_trail


    def assemble_ext(padded):
        last = padded.ndim - 1
        along_a = assemble_dim(
            padded[..., 1:-1, :], last - 1, padded[..., 0:1, :], padded[..., -1:, :]
        )
        return jnp.dot(along_a, join_b, precision=highest)

    def tendency(parts, surface):
        shapes = (
            jax.ShapeDtypeStruct((3, rows, nb_dev), jnp.float32),
            jax.ShapeDtypeStruct((2, 3, radial_nodes, nb_dev), jnp.float32),
            jax.ShapeDtypeStruct((2, 3, rows), jnp.float32),
        )
        operands = (parts.reshape(3, rows, nb_dev), flat_flow, grads, mats, flat_mass)
        if surface is None:
            shapes = shapes + (jax.ShapeDtypeStruct(analysis.shape[:1] + (nb_dev,), jnp.float32),)
            stacked, edge_rows, edge_cols, partial = pl.pallas_call(
                first_volume_kernel, out_shape=shapes
            )(*operands, analysis)
        else:
            stacked, edge_rows, edge_cols = pl.pallas_call(volume_kernel, out_shape=shapes)(
                *operands
            )
            partial = jnp.einsum(
                "kca,ab->kcb", analysis.reshape(-1, 2, na_dev), surface, precision=highest
            )
        stacked = stacked.reshape(parts.shape)
        sent = owner_map(partial)
        if carried_halo:
            returned, padded = joint_exchange(sent, stacked, edge_rows, edge_cols)
        else:
            returned = lax.all_to_all(
                sent.reshape(tiles * groups, -1), both, 0, 0, tiled=True
            ).reshape(tiles * groups, 2, nb_dev + 2)
            padded = halo(stacked)
        flux_term = flux_of(returned)
        outer = padded[0, radial_nodes - 1] + flux_term
        outer_rate = assemble_ext(outer) / assembled[radial_nodes - 1]
        outer_plane = lax.slice_in_dim(padded[:1], radial_nodes - 1, radial_nodes, axis=1)
        first = jnp.concatenate(
            [padded[:1, : radial_nodes - 1], outer_plane + flux_term], axis=1
        )
        padded = jnp.concatenate([first, padded[1:]], axis=0)
        plane_r = jnp.zeros_like(lax.slice_in_dim(padded, 0, 1, axis=1))
        padded = assemble_dim(padded, 1, plane_r, plane_r)
        return assemble_ext(padded) / assembled[None], outer_rate

    first_rate, first_outer = tendency(field, None)
    section = field + time_step * first_rate
    section_outer = field[0, radial_nodes - 1] + time_step * first_outer
    second_rate, _ = tendency(section, section_outer)
    return 0.5 * (field + section + time_step * second_rate)


def solution(mesh):
    placed = (
        P(None, None, "tile", "deg"),
        P(None, None, "tile", "deg"),
        P(("tile", "deg"), None, None),
        P(),
    )
    return jax.shard_map(
        local, mesh=mesh, in_specs=placed, out_specs=P(None, None, "tile", "deg"), check_vma=False
    )
```

```python
import math

import numpy as np
import jax
import jax.numpy as jnp
from jax import lax
from jax.sharding import PartitionSpec as P
from jax.experimental import pallas as pl

P_SIZE = 8


diffusivity = 0.05
time_step = 0.01
highest = lax.Precision.HIGHEST
gll_interior = [0.2092992179024789, 0.5917001814331423, 0.8717401485096066]


def padded_2(value, sides, width):
    for axis, dim in sides:
        size, length = (lax.axis_size(axis), value.shape[dim])
        up = [(i, (i + 1) % size) for i in range(size)]
        down = [(j, i) for i, j in up]
        last = lax.slice_in_dim(value, length - width, length, axis=dim)
        first = lax.slice_in_dim(value, 0, width, axis=dim)
        before = lax.ppermute(last, axis, up)
        after = lax.ppermute(first, axis, down)
        value = jnp.concatenate([before, value, after], axis=dim)
    return value


def product(a, b):
    return jnp.dot(a, b, precision=highest, preferred_element_type=jnp.float32)


def gradient_kernel(flow_ref, mats_ref, out_ref):
    for component in range(3):
        x = flow_ref[component]
        out_ref[3 * component] = product(mats_ref[0], x)
        out_ref[3 * component + 1] = product(mats_ref[1], x)
        out_ref[3 * component + 2] = product(x, mats_ref[2])


def volume_kernel(parts_ref, flow_ref, grad_ref, mats_ref, mass_ref, *outs):
    volume_body(parts_ref, flow_ref, grad_ref, mats_ref, mass_ref, *outs)


def first_volume_kernel(parts_ref, flow_ref, mats_ref, mass_ref, table_ref, *outs):
    grad_ref = outs[4]
    gradient_kernel(flow_ref, mats_ref, grad_ref)
    volume_body(parts_ref, flow_ref, grad_ref, mats_ref, mass_ref, *outs[:3])
    depth = outs[0].shape[1] // outs[1].shape[2]
    surface = parts_ref[0, pl.ds(outs[0].shape[1] - depth, depth), :]
    outs[3][...] = product(table_ref[...], surface)


def volume_body(parts_ref, flow_ref, grad_ref, mats_ref, mass_ref, out_ref, rows_ref, cols_ref):
    mass = mass_ref[...]
    p = [parts_ref[i] for i in range(3)]
    f = [flow_ref[i] for i in range(3)]
    planes = out_ref.shape[1] // rows_ref.shape[2]
    width = out_ref.shape[2]
    for c in range(3):
        x = p[c]
        s0 = product(mats_ref[0], x)
        s1 = product(mats_ref[1], x)
        s2 = product(x, mats_ref[2])
        stretch = p[0] * grad_ref[3 * c] + p[1] * grad_ref[3 * c + 1] + p[2] * grad_ref[3 * c + 2]
        carried = f[0] * s0 + f[1] * s1 + f[2] * s2
        spread = (
            product(mats_ref[3], mass * s0)
            + product(mats_ref[4], mass * s1)
            + product(mass * s2, mats_ref[5])
        )
        result = mass * (stretch - carried) - diffusivity * spread
        out_ref[c] = result
        turned = result.T
        cols_ref[0, c : c + 1, :] = turned[0:1, :]
        cols_ref[1, c : c + 1, :] = turned[width - 1 : width, :]
    for c in range(3):
        rows_ref[0, c] = out_ref[c, pl.ds(0, rows_ref.shape[2], stride=planes), :]
        rows_ref[1, c] = out_ref[c, pl.ds(planes - 1, rows_ref.shape[2], stride=planes), :]


def derivative_tables(radial_nodes, na_dev, nb_dev):
    _, _, matrix_list = gll_tables(P_SIZE)
    dmat = np.asarray(matrix_list, np.float32)
    radial = np.kron(dmat, np.eye(na_dev, dtype=np.float32))
    first = np.kron(np.eye(radial_nodes * na_dev // P_SIZE, dtype=np.float32), dmat)
    second = np.kron(np.eye(nb_dev // P_SIZE, dtype=np.float32), dmat)
    return jnp.asarray(np.stack([radial, first, second.T, radial.T, first.T, second]))


def legendre_value(point, degree):
    previous = 1.0
    current = point
    for order in range(1, degree):
        following = ((2 * order + 1) * point * current - order * previous) / (order + 1)
        previous = current
        current = following
    return current


def gll_tables(count):
    degree = count - 1
    points = [-1.0] + [-value for value in reversed(gll_interior)] + list(gll_interior) + [1.0]
    values = [legendre_value(point, degree) for point in points]
    weights = [2.0 / (degree * (degree + 1) * value * value) for value in values]
    matrix = [
        [
            values[row] / (values[col] * (points[row] - points[col])) if row != col else 0.0
            for col in range(count)
        ]
        for row in range(count)
    ]
    matrix[0][0] = -degree * (degree + 1) / 4.0
    matrix[count - 1][count - 1] = degree * (degree + 1) / 4.0
    return (points, weights, matrix)


def apply_along(values, axis_pos, matrix):
    shape = values.shape
    blocks = values.reshape(
        shape[:axis_pos] + (shape[axis_pos] // P_SIZE, P_SIZE) + shape[axis_pos + 1 :]
    )
    letters = list("abcdefg"[: blocks.ndim])
    source = list(letters)
    source[axis_pos + 1] = "p"
    target = list(letters)
    target[axis_pos + 1] = "q"
    formula = "".join(source) + ",qp->" + "".join(target)
    return jnp.einsum(formula, blocks, matrix, precision=highest).reshape(shape)


def assemble_dim(values, axis_pos, left, right):
    shape = values.shape
    count = shape[axis_pos] // P_SIZE
    blocks = values.reshape(shape[:axis_pos] + (count, P_SIZE) + shape[axis_pos + 1 :])
    edge_shape = shape[:axis_pos] + (1, 1) + shape[axis_pos + 1 :]
    first = lax.slice_in_dim(blocks, 0, 1, axis=axis_pos + 1)
    last = lax.slice_in_dim(blocks, P_SIZE - 1, P_SIZE, axis=axis_pos + 1)
    before = jnp.concatenate(
        [left.reshape(edge_shape), lax.slice_in_dim(last, 0, count - 1, axis=axis_pos)],
        axis=axis_pos,
    )
    after = jnp.concatenate(
        [lax.slice_in_dim(first, 1, count, axis=axis_pos), right.reshape(edge_shape)], axis=axis_pos
    )
    middle = lax.slice_in_dim(blocks, 1, P_SIZE - 1, axis=axis_pos + 1)
    joined = jnp.concatenate([first + before, middle, last + after], axis=axis_pos + 1)
    return joined.reshape(shape)


def assembled_weights(weights, count, lead, trail):
    position = jnp.arange(count * P_SIZE, dtype=jnp.int32)
    local_point = position % P_SIZE
    element = position // P_SIZE
    base = jnp.tile(weights, count)
    starts = (
        jnp.where(local_point == 0, jnp.where(element > 0, 1.0, lead), 0.0) * weights[P_SIZE - 1]
    )
    ends = (
        jnp.where(local_point == P_SIZE - 1, jnp.where(element < count - 1, 1.0, trail), 0.0)
        * weights[0]
    )
    return base + starts + ends


def static_assembled(weights, count, lead, trail):
    position = np.arange(count * P_SIZE)
    local_point = position % P_SIZE
    element = position // P_SIZE
    starts = np.where(local_point == 0, np.where(element > 0, 1.0, lead), 0.0) * weights[P_SIZE - 1]
    ends = np.where(local_point == P_SIZE - 1, np.where(element < count - 1, 1.0, trail), 0.0)
    return (np.tile(weights, count) + starts + ends * weights[0]).astype(np.float32)


def phases(waves, elem_start, elem_count, span, points):
    element = elem_start + jnp.arange(elem_count * P_SIZE, dtype=jnp.int32) // P_SIZE
    whole = waves[:, None] * (2 * element + 1)[None, :] % span
    fraction = waves.astype(jnp.float32)[:, None] * np.tile(points, elem_count)[None, :]
    return 2.0 * math.pi / span * (whole.astype(jnp.float32) + fraction)


def phases_at(waves, element, point_values, span):
    whole = waves[:, None] * (2 * element + 1)[None, :] % span
    fraction = waves.astype(jnp.float32)[:, None] * point_values[None, :]
    return 2.0 * math.pi / span * (whole.astype(jnp.float32) + fraction)


def shift_pairs(sizes, steps):
    count = sizes[0] * sizes[1]
    pairs = []
    for source in range(count):
        t, g = divmod(source, sizes[1])
        target = ((t + steps[0]) % sizes[0]) * sizes[1] + (g + steps[1]) % sizes[1]
        pairs.append((source, target))
    return pairs


def local(field, flow, match_ops, wave_of_slot):
    tiles = lax.axis_size("tile")
    groups = lax.axis_size("deg")
    both = ("tile", "deg")
    tile_index = lax.axis_index("tile")
    group_index = lax.axis_index("deg")
    radial_nodes = field.shape[1]
    na_dev = field.shape[2]
    nb_dev = field.shape[3]
    elems_a = na_dev // P_SIZE
    elems_b = nb_dev // P_SIZE
    nb = nb_dev * groups
    span = 2 * elems_a * tiles
    scale = P_SIZE / (na_dev * tiles)
    points_list, weights_list, _ = gll_tables(P_SIZE)
    points = np.asarray(points_list, np.float32)
    weights = np.asarray(weights_list, np.float32)
    lead = (group_index > 0).astype(jnp.float32)
    trail = (group_index < groups - 1).astype(jnp.float32)
    w_r = np.tile(weights, radial_nodes // P_SIZE)
    w_a = np.tile(weights, elems_a)
    w_b = np.tile(weights, elems_b)
    mass3 = w_r[:, None, None] * w_a[None, :, None] * w_b[None, None, :]
    b_first = np.zeros((nb_dev,), np.float32)
    b_first[0] = weights[P_SIZE - 1]
    b_last = np.zeros((nb_dev,), np.float32)
    b_last[nb_dev - 1] = weights[0]
    assembled_b = static_assembled(weights, elems_b, 0.0, 0.0) + lead * b_first + trail * b_last
    assembled = (
        (
            static_assembled(weights, radial_nodes // P_SIZE, 0.0, 0.0)[:, None]
            * static_assembled(weights, elems_a, 1.0, 1.0)[None, :]
        )[:, :, None]
        * assembled_b[None, None, :]
    )
    rows_ext = (tile_index * na_dev - 1 + jnp.arange(na_dev + 2, dtype=jnp.int32)) % (na_dev * tiles)
    row_points = (np.arange(na_dev + 2) - 1) % P_SIZE
    col_points = (np.arange(nb_dev + 2) - 1) % P_SIZE
    surface_ext = diffusivity * weights[row_points][:, None] * weights[col_points][None, :]

    rows = radial_nodes * na_dev
    mats = derivative_tables(radial_nodes, na_dev, nb_dev)
    flat_mass = mass3.reshape(rows, nb_dev)
    flat_flow = flow.reshape(3, rows, nb_dev)

    angle = phases(wave_of_slot, tile_index * elems_a, elems_a, span, points)
    analysis = (
        jnp.stack([jnp.cos(angle), jnp.sin(angle)], axis=1) * (w_a * scale)[None, None, :]
    ).reshape(-1, na_dev)

    def owner_map(partial):
        partial = partial.reshape(-1, 2, nb_dev)
        gathered = lax.all_to_all(partial, both, 0, 0, tiled=True)
        coeff = gathered.reshape(tiles, groups, 2, nb_dev).sum(axis=0)
        coeff = coeff.transpose(1, 0, 2).reshape(2, nb)
        owned = coeff.astype(jnp.bfloat16)
        mapped = jnp.einsum(
            "pq,cq->cp", match_ops[0], owned, preferred_element_type=jnp.float32
        )
        edged = jnp.concatenate([mapped[:, :1], mapped, mapped[:, -1:]], axis=1)
        pieces = jnp.stack(
            [edged[:, g * nb_dev : g * nb_dev + nb_dev + 2] for g in range(groups)], axis=0
        )
        return jnp.broadcast_to(pieces[None], (tiles,) + pieces.shape).reshape(
            tiles, groups, 2 * (nb_dev + 2)
        )

    def flux_of(returned):
        angle = phases_at(wave_of_slot, rows_ext // P_SIZE, points[row_points], span)
        synth = jnp.stack([jnp.cos(angle).T, jnp.sin(angle).T], axis=2).reshape(na_dev + 2, -1)
        flux = -jnp.dot(synth, returned.reshape(-1, nb_dev + 2), precision=highest)
        return surface_ext * flux

    mapped_len = 2 * (nb_dev + 2)
    slot_len = 3 * radial_nodes * na_dev
    carried_halo = tiles >= 3 and groups >= 3 and tiles * groups <= 64

    def joint_exchange(sent, stacked, edge_rows, edge_cols):
        a_lo = edge_rows[0].reshape(3, radial_nodes, 1, nb_dev)
        a_hi = edge_rows[1].reshape(3, radial_nodes, 1, nb_dev)
        up = [(i, (i + 1) % tiles) for i in range(tiles)]
        down = [(j, i) for i, j in up]
        from_up = lax.ppermute(a_hi, "tile", up)
        from_down = lax.ppermute(a_lo, "tile", down)
        b_lo = edge_cols[0].reshape(1, 1, -1)
        b_hi = edge_cols[1].reshape(1, 1, -1)
        out_pieces = [
            ((0, 1), b_hi),
            ((0, -1), b_lo),
            ((1, 1), b_hi),
            ((1, -1), b_lo),
            ((-1, 1), b_hi),
            ((-1, -1), b_lo),
        ]
        slots = jnp.zeros((tiles, groups, slot_len), jnp.float32)
        for (dt, dg), flat in out_pieces:
            slots = lax.dynamic_update_slice(
                slots, flat, ((tile_index + dt) % tiles, (group_index + dg) % groups, 0)
            )
        message = jnp.concatenate([sent, slots], axis=2).reshape(tiles * groups, -1)
        received = lax.all_to_all(message, both, 0, 0, tiled=True).reshape(tiles, groups, -1)
        returned = received[:, :, :mapped_len].reshape(tiles * groups, 2, nb_dev + 2)

        def take(dt, dg):
            row = lax.dynamic_slice(
                received,
                ((tile_index - dt) % tiles, (group_index - dg) % groups, mapped_len),
                (1, 1, slot_len),
            )
            return row.reshape(3, radial_nodes, na_dev, 1)

        from_left = take(0, 1)
        from_right = take(0, -1)
        corner_ul = take(1, 1)[:, :, na_dev - 1 :, :]
        corner_ur = take(1, -1)[:, :, na_dev - 1 :, :]
        corner_dl = take(-1, 1)[:, :, :1, :]
        corner_dr = take(-1, -1)[:, :, :1, :]
        top = jnp.concatenate([corner_ul, from_up, corner_ur], axis=3)
        middle = jnp.concatenate([from_left, stacked, from_right], axis=3)
        bottom = jnp.concatenate([corner_dl, from_down, corner_dr], axis=3)
        return returned, jnp.concatenate([top, middle, bottom], axis=2)

    def halo(stacked):
        a_lo = lax.slice_in_dim(stacked, 0, 1, axis=2)
        a_hi = lax.slice_in_dim(stacked, na_dev - 1, na_dev, axis=2)
        b_lo = lax.slice_in_dim(stacked, 0, 1, axis=3)
        b_hi = lax.slice_in_dim(stacked, nb_dev - 1, nb_dev, axis=3)
        sizes = (tiles, groups)
        from_up = lax.ppermute(a_hi, both, shift_pairs(sizes, (1, 0)))
        from_down = lax.ppermute(a_lo, both, shift_pairs(sizes, (-1, 0)))
        from_left = lax.ppermute(b_hi, both, shift_pairs(sizes, (0, 1)))
        from_right = lax.ppermute(b_lo, both, shift_pairs(sizes, (0, -1)))
        corner_ul = lax.ppermute(a_hi[:, :, :, -1:], both, shift_pairs(sizes, (1, 1)))
        corner_ur = lax.ppermute(a_hi[:, :, :, :1], both, shift_pairs(sizes, (1, -1)))
        corner_dl = lax.ppermute(a_lo[:, :, :, -1:], both, shift_pairs(sizes, (-1, 1)))
        corner_dr = lax.ppermute(a_lo[:, :, :, :1], both, shift_pairs(sizes, (-1, -1)))
        top = jnp.concatenate([corner_ul, from_up, corner_ur], axis=3)
        middle = jnp.concatenate([from_left, stacked, from_right], axis=3)
        bottom = jnp.concatenate([corner_dl, from_down, corner_dr], axis=3)
        return jnp.concatenate([top, middle, bottom], axis=2)

    join_b = np.zeros((nb_dev + 2, nb_dev), np.float32)
    join_b[np.arange(nb_dev) + 1, np.arange(nb_dev)] = 1.0
    inner_first = np.arange(P_SIZE, nb_dev, P_SIZE)
    join_b[inner_first, inner_first] = 1.0
    inner_last = np.arange(P_SIZE - 1, nb_dev - 1, P_SIZE)
    join_b[inner_last + 2, inner_last] = 1.0
    edge_lead = np.zeros((nb_dev + 2, nb_dev), np.float32)
    edge_lead[0, 0] = 1.0
    edge_trail = np.zeros((nb_dev + 2, nb_dev), np.float32)
    edge_trail[nb_dev + 1, nb_dev - 1] = 1.0
    join_b = join_b + lead * edge_lead + trail * edge_trail

    plane_mask = np.zeros((3, radial_nodes, 1, 1), np.float32)
    plane_mask[0, radial_nodes - 1] = 1.0

    def assemble_ext(padded):
        last = padded.ndim - 1
        along_a = assemble_dim(
            padded[..., 1:-1, :], last - 1, padded[..., 0:1, :], padded[..., -1:, :]
        )
        return jnp.dot(along_a, join_b, precision=highest)

    shapes = (
        jax.ShapeDtypeStruct((3, rows, nb_dev), jnp.float32),
        jax.ShapeDtypeStruct((2, 3, radial_nodes, nb_dev), jnp.float32),
        jax.ShapeDtypeStruct((2, 3, rows), jnp.float32),
    )
    first_outs = pl.pallas_call(
        first_volume_kernel,
        out_shape=shapes
        + (
            jax.ShapeDtypeStruct(analysis.shape[:1] + (nb_dev,), jnp.float32),
            jax.ShapeDtypeStruct((9, rows, nb_dev), jnp.float32),
        ),
    )(field.reshape(3, rows, nb_dev), flat_flow, mats, flat_mass, analysis)
    grads = first_outs[4]

    def tendency(parts, surface):
        if surface is None:
            stacked, edge_rows, edge_cols, partial = first_outs[:4]
        else:
            stacked, edge_rows, edge_cols = pl.pallas_call(volume_kernel, out_shape=shapes)(
                parts.reshape(3, rows, nb_dev), flat_flow, grads, mats, flat_mass
            )
            partial = jnp.dot(analysis, surface, precision=highest)
        stacked = stacked.reshape(parts.shape)
        sent = owner_map(partial)
        if carried_halo:
            returned, padded = joint_exchange(sent, stacked, edge_rows, edge_cols)
        else:
            returned = lax.all_to_all(
                sent.reshape(tiles * groups, -1), both, 0, 0, tiled=True
            ).reshape(tiles * groups, 2, nb_dev + 2)
            padded = halo(stacked)
        flux_term = flux_of(returned)
        outer = padded[0, radial_nodes - 1] + flux_term
        outer_rate = assemble_ext(outer) / assembled[radial_nodes - 1]
        padded = padded + plane_mask * flux_term
        plane_r = jnp.zeros_like(lax.slice_in_dim(padded, 0, 1, axis=1))
        padded = assemble_dim(padded, 1, plane_r, plane_r)
        return assemble_ext(padded) / assembled[None], outer_rate

    first_rate, first_outer = tendency(field, None)
    section = field + time_step * first_rate
    section_outer = field[0, radial_nodes - 1] + time_step * first_outer
    second_rate, _ = tendency(section, section_outer)
    return 0.5 * (field + section + time_step * second_rate)


def solution(mesh):
    placed = (
        P(None, None, "tile", "deg"),
        P(None, None, "tile", "deg"),
        P(("tile", "deg"), None, None),
        P(),
    )
    return jax.shard_map(
        local, mesh=mesh, in_specs=placed, out_specs=P(None, None, "tile", "deg"), check_vma=False
    )
```

```python
import math

import numpy as np
import jax
import jax.numpy as jnp
from jax import lax
from jax.sharding import PartitionSpec as P
from jax.experimental import pallas as pl

P_SIZE = 8


diffusivity = 0.05
time_step = 0.01
highest = lax.Precision.HIGHEST
gll_interior = [0.2092992179024789, 0.5917001814331423, 0.8717401485096066]


def padded_2(value, sides, width):
    for axis, dim in sides:
        size, length = (lax.axis_size(axis), value.shape[dim])
        up = [(i, (i + 1) % size) for i in range(size)]
        down = [(j, i) for i, j in up]
        last = lax.slice_in_dim(value, length - width, length, axis=dim)
        first = lax.slice_in_dim(value, 0, width, axis=dim)
        before = lax.ppermute(last, axis, up)
        after = lax.ppermute(first, axis, down)
        value = jnp.concatenate([before, value, after], axis=dim)
    return value


def product(a, b):
    return jnp.dot(a, b, precision=highest, preferred_element_type=jnp.float32)


def gradient_kernel(flow_ref, mats_ref, out_ref):
    for component in range(3):
        x = flow_ref[component]
        out_ref[3 * component] = product(mats_ref[0], x)
        out_ref[3 * component + 1] = product(mats_ref[1], x)
        out_ref[3 * component + 2] = product(x, mats_ref[2])


def volume_kernel(parts_ref, flow_ref, grad_ref, mats_ref, mass_ref, *outs):
    volume_body(parts_ref, flow_ref, grad_ref, mats_ref, mass_ref, *outs)


def first_volume_kernel(parts_ref, flow_ref, mats_ref, mass_ref, table_ref, *outs):
    grad_ref = outs[4]
    gradient_kernel(flow_ref, mats_ref, grad_ref)
    volume_body(parts_ref, flow_ref, grad_ref, mats_ref, mass_ref, *outs[:3])
    depth = outs[0].shape[1] // outs[1].shape[2]
    surface = parts_ref[0, pl.ds(outs[0].shape[1] - depth, depth), :]
    outs[3][...] = product(table_ref[...], surface)


def volume_body(parts_ref, flow_ref, grad_ref, mats_ref, mass_ref, out_ref, rows_ref, cols_ref):
    mass = mass_ref[...]
    p = [parts_ref[i] for i in range(3)]
    f = [flow_ref[i] for i in range(3)]
    planes = out_ref.shape[1] // rows_ref.shape[2]
    width = out_ref.shape[2]
    for c in range(3):
        x = p[c]
        s0 = product(mats_ref[0], x)
        s1 = product(mats_ref[1], x)
        s2 = product(x, mats_ref[2])
        stretch = p[0] * grad_ref[3 * c] + p[1] * grad_ref[3 * c + 1] + p[2] * grad_ref[3 * c + 2]
        carried = f[0] * s0 + f[1] * s1 + f[2] * s2
        spread = (
            product(mats_ref[3], mass * s0)
            + product(mats_ref[4], mass * s1)
            + product(mass * s2, mats_ref[5])
        )
        result = mass * (stretch - carried) - diffusivity * spread
        out_ref[c] = result
        turned = result.T
        cols_ref[0, c : c + 1, :] = turned[0:1, :]
        cols_ref[1, c : c + 1, :] = turned[width - 1 : width, :]
    for c in range(3):
        rows_ref[0, c] = out_ref[c, pl.ds(0, rows_ref.shape[2], stride=planes), :]
        rows_ref[1, c] = out_ref[c, pl.ds(planes - 1, rows_ref.shape[2], stride=planes), :]


def derivative_tables(radial_nodes, na_dev, nb_dev):
    _, _, matrix_list = gll_tables(P_SIZE)
    dmat = np.asarray(matrix_list, np.float32)
    radial = np.kron(dmat, np.eye(na_dev, dtype=np.float32))
    first = np.kron(np.eye(radial_nodes * na_dev // P_SIZE, dtype=np.float32), dmat)
    second = np.kron(np.eye(nb_dev // P_SIZE, dtype=np.float32), dmat)
    return jnp.asarray(np.stack([radial, first, second.T, radial.T, first.T, second]))


def legendre_value(point, degree):
    previous = 1.0
    current = point
    for order in range(1, degree):
        following = ((2 * order + 1) * point * current - order * previous) / (order + 1)
        previous = current
        current = following
    return current


def gll_tables(count):
    degree = count - 1
    points = [-1.0] + [-value for value in reversed(gll_interior)] + list(gll_interior) + [1.0]
    values = [legendre_value(point, degree) for point in points]
    weights = [2.0 / (degree * (degree + 1) * value * value) for value in values]
    matrix = [
        [
            values[row] / (values[col] * (points[row] - points[col])) if row != col else 0.0
            for col in range(count)
        ]
        for row in range(count)
    ]
    matrix[0][0] = -degree * (degree + 1) / 4.0
    matrix[count - 1][count - 1] = degree * (degree + 1) / 4.0
    return (points, weights, matrix)


def apply_along(values, axis_pos, matrix):
    shape = values.shape
    blocks = values.reshape(
        shape[:axis_pos] + (shape[axis_pos] // P_SIZE, P_SIZE) + shape[axis_pos + 1 :]
    )
    letters = list("abcdefg"[: blocks.ndim])
    source = list(letters)
    source[axis_pos + 1] = "p"
    target = list(letters)
    target[axis_pos + 1] = "q"
    formula = "".join(source) + ",qp->" + "".join(target)
    return jnp.einsum(formula, blocks, matrix, precision=highest).reshape(shape)


def assemble_dim(values, axis_pos, left, right):
    shape = values.shape
    count = shape[axis_pos] // P_SIZE
    blocks = values.reshape(shape[:axis_pos] + (count, P_SIZE) + shape[axis_pos + 1 :])
    edge_shape = shape[:axis_pos] + (1, 1) + shape[axis_pos + 1 :]
    first = lax.slice_in_dim(blocks, 0, 1, axis=axis_pos + 1)
    last = lax.slice_in_dim(blocks, P_SIZE - 1, P_SIZE, axis=axis_pos + 1)
    before = jnp.concatenate(
        [left.reshape(edge_shape), lax.slice_in_dim(last, 0, count - 1, axis=axis_pos)],
        axis=axis_pos,
    )
    after = jnp.concatenate(
        [lax.slice_in_dim(first, 1, count, axis=axis_pos), right.reshape(edge_shape)], axis=axis_pos
    )
    middle = lax.slice_in_dim(blocks, 1, P_SIZE - 1, axis=axis_pos + 1)
    joined = jnp.concatenate([first + before, middle, last + after], axis=axis_pos + 1)
    return joined.reshape(shape)


def assembled_weights(weights, count, lead, trail):
    position = jnp.arange(count * P_SIZE, dtype=jnp.int32)
    local_point = position % P_SIZE
    element = position // P_SIZE
    base = jnp.tile(weights, count)
    starts = (
        jnp.where(local_point == 0, jnp.where(element > 0, 1.0, lead), 0.0) * weights[P_SIZE - 1]
    )
    ends = (
        jnp.where(local_point == P_SIZE - 1, jnp.where(element < count - 1, 1.0, trail), 0.0)
        * weights[0]
    )
    return base + starts + ends


def static_assembled(weights, count, lead, trail):
    position = np.arange(count * P_SIZE)
    local_point = position % P_SIZE
    element = position // P_SIZE
    starts = np.where(local_point == 0, np.where(element > 0, 1.0, lead), 0.0) * weights[P_SIZE - 1]
    ends = np.where(local_point == P_SIZE - 1, np.where(element < count - 1, 1.0, trail), 0.0)
    return (np.tile(weights, count) + starts + ends * weights[0]).astype(np.float32)


def phases(waves, elem_start, elem_count, span, points):
    element = elem_start + jnp.arange(elem_count * P_SIZE, dtype=jnp.int32) // P_SIZE
    whole = waves[:, None] * (2 * element + 1)[None, :] % span
    fraction = waves.astype(jnp.float32)[:, None] * np.tile(points, elem_count)[None, :]
    return 2.0 * math.pi / span * (whole.astype(jnp.float32) + fraction)


def phases_at(waves, element, point_values, span):
    whole = waves[:, None] * (2 * element + 1)[None, :] % span
    fraction = waves.astype(jnp.float32)[:, None] * point_values[None, :]
    return 2.0 * math.pi / span * (whole.astype(jnp.float32) + fraction)


def shift_pairs(sizes, steps):
    count = sizes[0] * sizes[1]
    pairs = []
    for source in range(count):
        t, g = divmod(source, sizes[1])
        target = ((t + steps[0]) % sizes[0]) * sizes[1] + (g + steps[1]) % sizes[1]
        pairs.append((source, target))
    return pairs


def local(field, flow, match_ops, wave_of_slot):
    tiles = lax.axis_size("tile")
    groups = lax.axis_size("deg")
    both = ("tile", "deg")
    tile_index = lax.axis_index("tile")
    group_index = lax.axis_index("deg")
    radial_nodes = field.shape[1]
    na_dev = field.shape[2]
    nb_dev = field.shape[3]
    elems_a = na_dev // P_SIZE
    elems_b = nb_dev // P_SIZE
    nb = nb_dev * groups
    span = 2 * elems_a * tiles
    scale = P_SIZE / (na_dev * tiles)
    points_list, weights_list, _ = gll_tables(P_SIZE)
    points = np.asarray(points_list, np.float32)
    weights = np.asarray(weights_list, np.float32)
    lead = (group_index > 0).astype(jnp.float32)
    trail = (group_index < groups - 1).astype(jnp.float32)
    w_r = np.tile(weights, radial_nodes // P_SIZE)
    w_a = np.tile(weights, elems_a)
    w_b = np.tile(weights, elems_b)
    mass3 = w_r[:, None, None] * w_a[None, :, None] * w_b[None, None, :]
    b_first = np.zeros((nb_dev,), np.float32)
    b_first[0] = weights[P_SIZE - 1]
    b_last = np.zeros((nb_dev,), np.float32)
    b_last[nb_dev - 1] = weights[0]
    assembled_b = static_assembled(weights, elems_b, 0.0, 0.0) + lead * b_first + trail * b_last
    assembled = (
        (
            static_assembled(weights, radial_nodes // P_SIZE, 0.0, 0.0)[:, None]
            * static_assembled(weights, elems_a, 1.0, 1.0)[None, :]
        )[:, :, None]
        * assembled_b[None, None, :]
    )
    rows_ext = (tile_index * na_dev - 1 + jnp.arange(na_dev + 2, dtype=jnp.int32)) % (na_dev * tiles)
    row_points = (np.arange(na_dev + 2) - 1) % P_SIZE
    col_points = (np.arange(nb_dev + 2) - 1) % P_SIZE
    surface_ext = diffusivity * weights[row_points][:, None] * weights[col_points][None, :]

    rows = radial_nodes * na_dev
    mats = derivative_tables(radial_nodes, na_dev, nb_dev)
    flat_mass = mass3.reshape(rows, nb_dev)
    flat_flow = flow.reshape(3, rows, nb_dev)

    angle = phases(wave_of_slot, tile_index * elems_a, elems_a, span, points)
    analysis = (
        jnp.stack([jnp.cos(angle), jnp.sin(angle)], axis=1) * (w_a * scale)[None, None, :]
    ).reshape(-1, na_dev)

    def owner_map(partial):
        partial = partial.reshape(-1, 2, nb_dev)
        gathered = lax.all_to_all(partial, both, 0, 0, tiled=True)
        coeff = gathered.reshape(tiles, groups, 2, nb_dev).sum(axis=0)
        coeff = coeff.transpose(1, 0, 2).reshape(2, nb)
        owned = coeff.astype(jnp.bfloat16)
        mapped = jnp.einsum(
            "pq,cq->cp", match_ops[0], owned, preferred_element_type=jnp.float32
        )
        edged = jnp.concatenate([mapped[:, :1], mapped, mapped[:, -1:]], axis=1)
        pieces = jnp.stack(
            [edged[:, g * nb_dev : g * nb_dev + nb_dev + 2] for g in range(groups)], axis=0
        )
        return jnp.broadcast_to(pieces[None], (tiles,) + pieces.shape).reshape(
            tiles, groups, 2 * (nb_dev + 2)
        )

    def flux_of(returned):
        angle = phases_at(wave_of_slot, rows_ext // P_SIZE, points[row_points], span)
        synth = jnp.stack([jnp.cos(angle).T, jnp.sin(angle).T], axis=2).reshape(na_dev + 2, -1)
        flux = -jnp.dot(synth, returned.reshape(-1, nb_dev + 2), precision=highest)
        return surface_ext * flux

    mapped_len = 2 * (nb_dev + 2)
    slot_len = 3 * radial_nodes * na_dev
    carried_halo = tiles >= 3 and groups >= 3 and tiles * groups <= 64

    def joint_exchange(sent, stacked, edge_rows, edge_cols):
        a_lo = edge_rows[0].reshape(3, radial_nodes, 1, nb_dev)
        a_hi = edge_rows[1].reshape(3, radial_nodes, 1, nb_dev)
        up = [(i, (i + 1) % tiles) for i in range(tiles)]
        down = [(j, i) for i, j in up]
        from_up = lax.ppermute(a_hi, "tile", up)
        from_down = lax.ppermute(a_lo, "tile", down)
        b_lo = edge_cols[0].reshape(1, 1, -1)
        b_hi = edge_cols[1].reshape(1, 1, -1)
        out_pieces = [
            ((0, 1), b_hi),
            ((0, -1), b_lo),
            ((1, 1), b_hi),
            ((1, -1), b_lo),
            ((-1, 1), b_hi),
            ((-1, -1), b_lo),
        ]
        slots = jnp.zeros((tiles * groups, 1, slot_len), jnp.float32)
        for (dt, dg), flat in out_pieces:
            target = ((tile_index + dt) % tiles) * groups + (group_index + dg) % groups
            slots = lax.dynamic_update_slice(slots, flat, (target, 0, 0))
        message = jnp.concatenate([sent.reshape(tiles * groups, 1, -1), slots], axis=2)
        received = lax.all_to_all(message, both, 0, 0, tiled=True)
        returned = received[:, 0, :mapped_len].reshape(tiles * groups, 2, nb_dev + 2)

        def take(dt, dg):
            source = ((tile_index - dt) % tiles) * groups + (group_index - dg) % groups
            row = lax.dynamic_slice(received, (source, 0, mapped_len), (1, 1, slot_len))
            return row.reshape(3, radial_nodes, na_dev, 1)

        from_left = take(0, 1)
        from_right = take(0, -1)
        corner_ul = take(1, 1)[:, :, na_dev - 1 :, :]
        corner_ur = take(1, -1)[:, :, na_dev - 1 :, :]
        corner_dl = take(-1, 1)[:, :, :1, :]
        corner_dr = take(-1, -1)[:, :, :1, :]
        top = jnp.concatenate([corner_ul, from_up, corner_ur], axis=3)
        middle = jnp.concatenate([from_left, stacked, from_right], axis=3)
        bottom = jnp.concatenate([corner_dl, from_down, corner_dr], axis=3)
        return returned, jnp.concatenate([top, middle, bottom], axis=2)

    def halo(stacked):
        a_lo = lax.slice_in_dim(stacked, 0, 1, axis=2)
        a_hi = lax.slice_in_dim(stacked, na_dev - 1, na_dev, axis=2)
        b_lo = lax.slice_in_dim(stacked, 0, 1, axis=3)
        b_hi = lax.slice_in_dim(stacked, nb_dev - 1, nb_dev, axis=3)
        sizes = (tiles, groups)
        from_up = lax.ppermute(a_hi, both, shift_pairs(sizes, (1, 0)))
        from_down = lax.ppermute(a_lo, both, shift_pairs(sizes, (-1, 0)))
        from_left = lax.ppermute(b_hi, both, shift_pairs(sizes, (0, 1)))
        from_right = lax.ppermute(b_lo, both, shift_pairs(sizes, (0, -1)))
        corner_ul = lax.ppermute(a_hi[:, :, :, -1:], both, shift_pairs(sizes, (1, 1)))
        corner_ur = lax.ppermute(a_hi[:, :, :, :1], both, shift_pairs(sizes, (1, -1)))
        corner_dl = lax.ppermute(a_lo[:, :, :, -1:], both, shift_pairs(sizes, (-1, 1)))
        corner_dr = lax.ppermute(a_lo[:, :, :, :1], both, shift_pairs(sizes, (-1, -1)))
        top = jnp.concatenate([corner_ul, from_up, corner_ur], axis=3)
        middle = jnp.concatenate([from_left, stacked, from_right], axis=3)
        bottom = jnp.concatenate([corner_dl, from_down, corner_dr], axis=3)
        return jnp.concatenate([top, middle, bottom], axis=2)

    join_b = np.zeros((nb_dev + 2, nb_dev), np.float32)
    join_b[np.arange(nb_dev) + 1, np.arange(nb_dev)] = 1.0
    inner_first = np.arange(P_SIZE, nb_dev, P_SIZE)
    join_b[inner_first, inner_first] = 1.0
    inner_last = np.arange(P_SIZE - 1, nb_dev - 1, P_SIZE)
    join_b[inner_last + 2, inner_last] = 1.0
    edge_lead = np.zeros((nb_dev + 2, nb_dev), np.float32)
    edge_lead[0, 0] = 1.0
    edge_trail = np.zeros((nb_dev + 2, nb_dev), np.float32)
    edge_trail[nb_dev + 1, nb_dev - 1] = 1.0
    join_b = join_b + lead * edge_lead + trail * edge_trail

    plane_mask = np.zeros((3, radial_nodes, 1, 1), np.float32)
    plane_mask[0, radial_nodes - 1] = 1.0

    def assemble_ext(padded):
        last = padded.ndim - 1
        along_a = assemble_dim(
            padded[..., 1:-1, :], last - 1, padded[..., 0:1, :], padded[..., -1:, :]
        )
        return jnp.dot(along_a, join_b, precision=highest)

    shapes = (
        jax.ShapeDtypeStruct((3, rows, nb_dev), jnp.float32),
        jax.ShapeDtypeStruct((2, 3, radial_nodes, nb_dev), jnp.float32),
        jax.ShapeDtypeStruct((2, 3, rows), jnp.float32),
    )
    first_outs = pl.pallas_call(
        first_volume_kernel,
        out_shape=shapes
        + (
            jax.ShapeDtypeStruct(analysis.shape[:1] + (nb_dev,), jnp.float32),
            jax.ShapeDtypeStruct((9, rows, nb_dev), jnp.float32),
        ),
    )(field.reshape(3, rows, nb_dev), flat_flow, mats, flat_mass, analysis)
    grads = first_outs[4]

    def tendency(parts, surface):
        if surface is None:
            stacked, edge_rows, edge_cols, partial = first_outs[:4]
        else:
            stacked, edge_rows, edge_cols = pl.pallas_call(volume_kernel, out_shape=shapes)(
                parts.reshape(3, rows, nb_dev), flat_flow, grads, mats, flat_mass
            )
            partial = jnp.dot(analysis, surface, precision=highest)
        stacked = stacked.reshape(parts.shape)
        sent = owner_map(partial)
        if carried_halo:
            returned, padded = joint_exchange(sent, stacked, edge_rows, edge_cols)
        else:
            returned = lax.all_to_all(
                sent.reshape(tiles * groups, -1), both, 0, 0, tiled=True
            ).reshape(tiles * groups, 2, nb_dev + 2)
            padded = halo(stacked)
        flux_term = flux_of(returned)
        outer = padded[0, radial_nodes - 1] + flux_term
        outer_rate = assemble_ext(outer) / assembled[radial_nodes - 1]
        padded = padded + plane_mask * flux_term
        plane_r = jnp.zeros_like(lax.slice_in_dim(padded, 0, 1, axis=1))
        padded = assemble_dim(padded, 1, plane_r, plane_r)
        return assemble_ext(padded) / assembled[None], outer_rate

    first_rate, first_outer = tendency(field, None)
    section = field + time_step * first_rate
    section_outer = field[0, radial_nodes - 1] + time_step * first_outer
    second_rate, _ = tendency(section, section_outer)
    return 0.5 * (field + section + time_step * second_rate)


def solution(mesh):
    placed = (
        P(None, None, "tile", "deg"),
        P(None, None, "tile", "deg"),
        P(("tile", "deg"), None, None),
        P(),
    )
    return jax.shard_map(
        local, mesh=mesh, in_specs=placed, out_specs=P(None, None, "tile", "deg"), check_vma=False
    )
```

```python
import math

import numpy as np
import jax
import jax.numpy as jnp
from jax import lax
from jax.sharding import PartitionSpec as P
from jax.experimental import pallas as pl

P_SIZE = 8


diffusivity = 0.05
time_step = 0.01
highest = lax.Precision.HIGHEST
gll_interior = [0.2092992179024789, 0.5917001814331423, 0.8717401485096066]


def padded_2(value, sides, width):
    for axis, dim in sides:
        size, length = (lax.axis_size(axis), value.shape[dim])
        up = [(i, (i + 1) % size) for i in range(size)]
        down = [(j, i) for i, j in up]
        last = lax.slice_in_dim(value, length - width, length, axis=dim)
        first = lax.slice_in_dim(value, 0, width, axis=dim)
        before = lax.ppermute(last, axis, up)
        after = lax.ppermute(first, axis, down)
        value = jnp.concatenate([before, value, after], axis=dim)
    return value


def product(a, b):
    return jnp.dot(a, b, precision=highest, preferred_element_type=jnp.float32)


def gradient_kernel(flow_ref, mats_ref, out_ref):
    for component in range(3):
        x = flow_ref[component]
        out_ref[3 * component] = product(mats_ref[0], x)
        out_ref[3 * component + 1] = product(mats_ref[1], x)
        out_ref[3 * component + 2] = product(x, mats_ref[2])


def volume_kernel(parts_ref, flow_ref, grad_ref, mats_ref, mass_ref, *outs):
    volume_body(parts_ref, flow_ref, grad_ref, mats_ref, mass_ref, *outs)


def first_volume_kernel(parts_ref, flow_ref, mats_ref, mass_ref, table_ref, *outs):
    grad_ref = outs[4]
    gradient_kernel(flow_ref, mats_ref, grad_ref)
    volume_body(parts_ref, flow_ref, grad_ref, mats_ref, mass_ref, *outs[:3])
    depth = outs[0].shape[1] // outs[1].shape[2]
    surface = parts_ref[0, pl.ds(outs[0].shape[1] - depth, depth), :]
    outs[3][...] = product(table_ref[...], surface)


def volume_body(parts_ref, flow_ref, grad_ref, mats_ref, mass_ref, out_ref, rows_ref, cols_ref):
    mass = mass_ref[...]
    p = [parts_ref[i] for i in range(3)]
    f = [flow_ref[i] for i in range(3)]
    planes = out_ref.shape[1] // rows_ref.shape[2]
    width = out_ref.shape[2]
    for c in range(3):
        x = p[c]
        s0 = product(mats_ref[0], x)
        s1 = product(mats_ref[1], x)
        s2 = product(x, mats_ref[2])
        stretch = p[0] * grad_ref[3 * c] + p[1] * grad_ref[3 * c + 1] + p[2] * grad_ref[3 * c + 2]
        carried = f[0] * s0 + f[1] * s1 + f[2] * s2
        spread = (
            product(mats_ref[3], mass * s0)
            + product(mats_ref[4], mass * s1)
            + product(mass * s2, mats_ref[5])
        )
        result = mass * (stretch - carried) - diffusivity * spread
        out_ref[c] = result
        turned = result.T
        cols_ref[0, c : c + 1, :] = turned[0:1, :]
        cols_ref[1, c : c + 1, :] = turned[width - 1 : width, :]
    for c in range(3):
        rows_ref[0, c] = out_ref[c, pl.ds(0, rows_ref.shape[2], stride=planes), :]
        rows_ref[1, c] = out_ref[c, pl.ds(planes - 1, rows_ref.shape[2], stride=planes), :]


def derivative_tables(radial_nodes, na_dev, nb_dev):
    _, _, matrix_list = gll_tables(P_SIZE)
    dmat = np.asarray(matrix_list, np.float32)
    radial = np.kron(dmat, np.eye(na_dev, dtype=np.float32))
    first = np.kron(np.eye(radial_nodes * na_dev // P_SIZE, dtype=np.float32), dmat)
    second = np.kron(np.eye(nb_dev // P_SIZE, dtype=np.float32), dmat)
    return jnp.asarray(np.stack([radial, first, second.T, radial.T, first.T, second]))


def legendre_value(point, degree):
    previous = 1.0
    current = point
    for order in range(1, degree):
        following = ((2 * order + 1) * point * current - order * previous) / (order + 1)
        previous = current
        current = following
    return current


def gll_tables(count):
    degree = count - 1
    points = [-1.0] + [-value for value in reversed(gll_interior)] + list(gll_interior) + [1.0]
    values = [legendre_value(point, degree) for point in points]
    weights = [2.0 / (degree * (degree + 1) * value * value) for value in values]
    matrix = [
        [
            values[row] / (values[col] * (points[row] - points[col])) if row != col else 0.0
            for col in range(count)
        ]
        for row in range(count)
    ]
    matrix[0][0] = -degree * (degree + 1) / 4.0
    matrix[count - 1][count - 1] = degree * (degree + 1) / 4.0
    return (points, weights, matrix)


def apply_along(values, axis_pos, matrix):
    shape = values.shape
    blocks = values.reshape(
        shape[:axis_pos] + (shape[axis_pos] // P_SIZE, P_SIZE) + shape[axis_pos + 1 :]
    )
    letters = list("abcdefg"[: blocks.ndim])
    source = list(letters)
    source[axis_pos + 1] = "p"
    target = list(letters)
    target[axis_pos + 1] = "q"
    formula = "".join(source) + ",qp->" + "".join(target)
    return jnp.einsum(formula, blocks, matrix, precision=highest).reshape(shape)


def assemble_dim(values, axis_pos, left, right):
    shape = values.shape
    count = shape[axis_pos] // P_SIZE
    blocks = values.reshape(shape[:axis_pos] + (count, P_SIZE) + shape[axis_pos + 1 :])
    edge_shape = shape[:axis_pos] + (1, 1) + shape[axis_pos + 1 :]
    first = lax.slice_in_dim(blocks, 0, 1, axis=axis_pos + 1)
    last = lax.slice_in_dim(blocks, P_SIZE - 1, P_SIZE, axis=axis_pos + 1)
    before = jnp.concatenate(
        [left.reshape(edge_shape), lax.slice_in_dim(last, 0, count - 1, axis=axis_pos)],
        axis=axis_pos,
    )
    after = jnp.concatenate(
        [lax.slice_in_dim(first, 1, count, axis=axis_pos), right.reshape(edge_shape)], axis=axis_pos
    )
    middle = lax.slice_in_dim(blocks, 1, P_SIZE - 1, axis=axis_pos + 1)
    joined = jnp.concatenate([first + before, middle, last + after], axis=axis_pos + 1)
    return joined.reshape(shape)


def assembled_weights(weights, count, lead, trail):
    position = jnp.arange(count * P_SIZE, dtype=jnp.int32)
    local_point = position % P_SIZE
    element = position // P_SIZE
    base = jnp.tile(weights, count)
    starts = (
        jnp.where(local_point == 0, jnp.where(element > 0, 1.0, lead), 0.0) * weights[P_SIZE - 1]
    )
    ends = (
        jnp.where(local_point == P_SIZE - 1, jnp.where(element < count - 1, 1.0, trail), 0.0)
        * weights[0]
    )
    return base + starts + ends


def static_assembled(weights, count, lead, trail):
    position = np.arange(count * P_SIZE)
    local_point = position % P_SIZE
    element = position // P_SIZE
    starts = np.where(local_point == 0, np.where(element > 0, 1.0, lead), 0.0) * weights[P_SIZE - 1]
    ends = np.where(local_point == P_SIZE - 1, np.where(element < count - 1, 1.0, trail), 0.0)
    return (np.tile(weights, count) + starts + ends * weights[0]).astype(np.float32)


def phases(waves, elem_start, elem_count, span, points):
    element = elem_start + jnp.arange(elem_count * P_SIZE, dtype=jnp.int32) // P_SIZE
    whole = waves[:, None] * (2 * element + 1)[None, :] % span
    fraction = waves.astype(jnp.float32)[:, None] * np.tile(points, elem_count)[None, :]
    return 2.0 * math.pi / span * (whole.astype(jnp.float32) + fraction)


def phases_at(waves, element, point_values, span):
    whole = waves[:, None] * (2 * element + 1)[None, :] % span
    fraction = waves.astype(jnp.float32)[:, None] * point_values[None, :]
    return 2.0 * math.pi / span * (whole.astype(jnp.float32) + fraction)


def shift_pairs(sizes, steps):
    count = sizes[0] * sizes[1]
    pairs = []
    for source in range(count):
        t, g = divmod(source, sizes[1])
        target = ((t + steps[0]) % sizes[0]) * sizes[1] + (g + steps[1]) % sizes[1]
        pairs.append((source, target))
    return pairs


def local(field, flow, match_ops, wave_of_slot):
    tiles = lax.axis_size("tile")
    groups = lax.axis_size("deg")
    both = ("tile", "deg")
    tile_index = lax.axis_index("tile")
    group_index = lax.axis_index("deg")
    radial_nodes = field.shape[1]
    na_dev = field.shape[2]
    nb_dev = field.shape[3]
    elems_a = na_dev // P_SIZE
    elems_b = nb_dev // P_SIZE
    nb = nb_dev * groups
    span = 2 * elems_a * tiles
    scale = P_SIZE / (na_dev * tiles)
    points_list, weights_list, _ = gll_tables(P_SIZE)
    points = np.asarray(points_list, np.float32)
    weights = np.asarray(weights_list, np.float32)
    lead = (group_index > 0).astype(jnp.float32)
    trail = (group_index < groups - 1).astype(jnp.float32)
    w_r = np.tile(weights, radial_nodes // P_SIZE)
    w_a = np.tile(weights, elems_a)
    w_b = np.tile(weights, elems_b)
    mass3 = w_r[:, None, None] * w_a[None, :, None] * w_b[None, None, :]
    b_first = np.zeros((nb_dev,), np.float32)
    b_first[0] = weights[P_SIZE - 1]
    b_last = np.zeros((nb_dev,), np.float32)
    b_last[nb_dev - 1] = weights[0]
    assembled_b = static_assembled(weights, elems_b, 0.0, 0.0) + lead * b_first + trail * b_last
    assembled = (
        (
            static_assembled(weights, radial_nodes // P_SIZE, 0.0, 0.0)[:, None]
            * static_assembled(weights, elems_a, 1.0, 1.0)[None, :]
        )[:, :, None]
        * assembled_b[None, None, :]
    )
    rows_ext = (tile_index * na_dev - 1 + jnp.arange(na_dev + 2, dtype=jnp.int32)) % (na_dev * tiles)
    row_points = (np.arange(na_dev + 2) - 1) % P_SIZE
    col_points = (np.arange(nb_dev + 2) - 1) % P_SIZE
    cols_ext = group_index * nb_dev - 1 + jnp.arange(nb_dev + 2, dtype=jnp.int32)

    def weight_at(index):
        point = index % P_SIZE
        total = jnp.zeros(index.shape, jnp.float32)
        for p in range(P_SIZE):
            total = total + jnp.where(point == p, float(weights[p]), 0.0)
        return total

    surface_ext = diffusivity * weight_at(rows_ext)[:, None] * weight_at(cols_ext)[None, :]

    rows = radial_nodes * na_dev
    mats = derivative_tables(radial_nodes, na_dev, nb_dev)
    flat_mass = mass3.reshape(rows, nb_dev)
    flat_flow = flow.reshape(3, rows, nb_dev)

    angle = phases(wave_of_slot, tile_index * elems_a, elems_a, span, points)
    analysis = (
        jnp.stack([jnp.cos(angle), jnp.sin(angle)], axis=1) * (w_a * scale)[None, None, :]
    ).reshape(-1, na_dev)

    def owner_map(partial):
        partial = partial.reshape(-1, 2, nb_dev)
        gathered = lax.all_to_all(partial, both, 0, 0, tiled=True)
        coeff = gathered.reshape(tiles, groups, 2, nb_dev).sum(axis=0)
        coeff = coeff.transpose(1, 0, 2).reshape(2, nb)
        owned = coeff.astype(jnp.bfloat16)
        mapped = jnp.einsum(
            "pq,cq->cp", match_ops[0], owned, preferred_element_type=jnp.float32
        )
        edged = jnp.concatenate([mapped[:, :1], mapped, mapped[:, -1:]], axis=1)
        pieces = jnp.stack(
            [edged[:, g * nb_dev : g * nb_dev + nb_dev + 2] for g in range(groups)], axis=0
        )
        return jnp.broadcast_to(pieces[None], (tiles,) + pieces.shape).reshape(
            tiles, groups, 2 * (nb_dev + 2)
        )

    def flux_of(returned):
        angle = phases_at(wave_of_slot, rows_ext // P_SIZE, points[row_points], span)
        synth = jnp.stack([jnp.cos(angle).T, jnp.sin(angle).T], axis=2).reshape(na_dev + 2, -1)
        flux = -jnp.dot(synth, returned.reshape(-1, nb_dev + 2), precision=highest)
        return surface_ext * flux

    mapped_len = 2 * (nb_dev + 2)
    slot_len = 3 * radial_nodes * na_dev
    carried_halo = tiles >= 3 and groups >= 3 and tiles * groups <= 64

    def joint_exchange(sent, stacked, edge_rows, edge_cols):
        a_lo = edge_rows[0].reshape(3, radial_nodes, 1, nb_dev)
        a_hi = edge_rows[1].reshape(3, radial_nodes, 1, nb_dev)
        up = [(i, (i + 1) % tiles) for i in range(tiles)]
        down = [(j, i) for i, j in up]
        from_up = lax.ppermute(a_hi, "tile", up)
        from_down = lax.ppermute(a_lo, "tile", down)
        b_lo = edge_cols[0].reshape(1, 1, -1)
        b_hi = edge_cols[1].reshape(1, 1, -1)
        out_pieces = [
            ((0, 1), b_hi),
            ((0, -1), b_lo),
            ((1, 1), b_hi),
            ((1, -1), b_lo),
            ((-1, 1), b_hi),
            ((-1, -1), b_lo),
        ]
        slots = jnp.zeros((tiles * groups, 1, slot_len), jnp.float32)
        for (dt, dg), flat in out_pieces:
            target = ((tile_index + dt) % tiles) * groups + (group_index + dg) % groups
            slots = lax.dynamic_update_slice(slots, flat, (target, 0, 0))
        message = jnp.concatenate([sent.reshape(tiles * groups, 1, -1), slots], axis=2)
        received = lax.all_to_all(message, both, 0, 0, tiled=True)
        returned = received[:, 0, :mapped_len].reshape(tiles * groups, 2, nb_dev + 2)

        def take(dt, dg):
            source = ((tile_index - dt) % tiles) * groups + (group_index - dg) % groups
            row = lax.dynamic_slice(received, (source, 0, mapped_len), (1, 1, slot_len))
            return row.reshape(3, radial_nodes, na_dev, 1)

        from_left = take(0, 1)
        from_right = take(0, -1)
        corner_ul = take(1, 1)[:, :, na_dev - 1 :, :]
        corner_ur = take(1, -1)[:, :, na_dev - 1 :, :]
        corner_dl = take(-1, 1)[:, :, :1, :]
        corner_dr = take(-1, -1)[:, :, :1, :]
        top = jnp.concatenate([corner_ul, from_up, corner_ur], axis=3)
        middle = jnp.concatenate([from_left, stacked, from_right], axis=3)
        bottom = jnp.concatenate([corner_dl, from_down, corner_dr], axis=3)
        return returned, jnp.concatenate([top, middle, bottom], axis=2)

    def halo(stacked):
        a_lo = lax.slice_in_dim(stacked, 0, 1, axis=2)
        a_hi = lax.slice_in_dim(stacked, na_dev - 1, na_dev, axis=2)
        b_lo = lax.slice_in_dim(stacked, 0, 1, axis=3)
        b_hi = lax.slice_in_dim(stacked, nb_dev - 1, nb_dev, axis=3)
        sizes = (tiles, groups)
        from_up = lax.ppermute(a_hi, both, shift_pairs(sizes, (1, 0)))
        from_down = lax.ppermute(a_lo, both, shift_pairs(sizes, (-1, 0)))
        from_left = lax.ppermute(b_hi, both, shift_pairs(sizes, (0, 1)))
        from_right = lax.ppermute(b_lo, both, shift_pairs(sizes, (0, -1)))
        corner_ul = lax.ppermute(a_hi[:, :, :, -1:], both, shift_pairs(sizes, (1, 1)))
        corner_ur = lax.ppermute(a_hi[:, :, :, :1], both, shift_pairs(sizes, (1, -1)))
        corner_dl = lax.ppermute(a_lo[:, :, :, -1:], both, shift_pairs(sizes, (-1, 1)))
        corner_dr = lax.ppermute(a_lo[:, :, :, :1], both, shift_pairs(sizes, (-1, -1)))
        top = jnp.concatenate([corner_ul, from_up, corner_ur], axis=3)
        middle = jnp.concatenate([from_left, stacked, from_right], axis=3)
        bottom = jnp.concatenate([corner_dl, from_down, corner_dr], axis=3)
        return jnp.concatenate([top, middle, bottom], axis=2)

    join_b = np.zeros((nb_dev + 2, nb_dev), np.float32)
    join_b[np.arange(nb_dev) + 1, np.arange(nb_dev)] = 1.0
    inner_first = np.arange(P_SIZE, nb_dev, P_SIZE)
    join_b[inner_first, inner_first] = 1.0
    inner_last = np.arange(P_SIZE - 1, nb_dev - 1, P_SIZE)
    join_b[inner_last + 2, inner_last] = 1.0
    edge_lead = np.zeros((nb_dev + 2, nb_dev), np.float32)
    edge_lead[0, 0] = 1.0
    edge_trail = np.zeros((nb_dev + 2, nb_dev), np.float32)
    edge_trail[nb_dev + 1, nb_dev - 1] = 1.0
    join_b = join_b + lead * edge_lead + trail * edge_trail

    mask_shape = (3, radial_nodes, 1, 1)
    outer_index = radial_nodes - 1 + jnp.minimum(tile_index, 0)
    plane_mask = jnp.where(
        (lax.broadcasted_iota(jnp.int32, mask_shape, 0) == 0)
        & (lax.broadcasted_iota(jnp.int32, mask_shape, 1) == outer_index),
        1.0,
        0.0,
    )

    def assemble_ext(padded):
        last = padded.ndim - 1
        along_a = assemble_dim(
            padded[..., 1:-1, :], last - 1, padded[..., 0:1, :], padded[..., -1:, :]
        )
        return jnp.dot(along_a, join_b, precision=highest)

    shapes = (
        jax.ShapeDtypeStruct((3, rows, nb_dev), jnp.float32),
        jax.ShapeDtypeStruct((2, 3, radial_nodes, nb_dev), jnp.float32),
        jax.ShapeDtypeStruct((2, 3, rows), jnp.float32),
    )
    first_outs = pl.pallas_call(
        first_volume_kernel,
        out_shape=shapes
        + (
            jax.ShapeDtypeStruct(analysis.shape[:1] + (nb_dev,), jnp.float32),
            jax.ShapeDtypeStruct((9, rows, nb_dev), jnp.float32),
        ),
    )(field.reshape(3, rows, nb_dev), flat_flow, mats, flat_mass, analysis)
    grads = first_outs[4]

    def tendency(parts, surface):
        if surface is None:
            stacked, edge_rows, edge_cols, partial = first_outs[:4]
        else:
            stacked, edge_rows, edge_cols = pl.pallas_call(volume_kernel, out_shape=shapes)(
                parts.reshape(3, rows, nb_dev), flat_flow, grads, mats, flat_mass
            )
            partial = jnp.dot(analysis, surface, precision=highest)
        stacked = stacked.reshape(parts.shape)
        sent = owner_map(partial)
        if carried_halo:
            returned, padded = joint_exchange(sent, stacked, edge_rows, edge_cols)
        else:
            returned = lax.all_to_all(
                sent.reshape(tiles * groups, -1), both, 0, 0, tiled=True
            ).reshape(tiles * groups, 2, nb_dev + 2)
            padded = halo(stacked)
        flux_term = flux_of(returned)
        outer = padded[0, radial_nodes - 1] + flux_term
        outer_rate = assemble_ext(outer) / assembled[radial_nodes - 1]
        padded = padded + plane_mask * flux_term
        plane_r = jnp.zeros_like(lax.slice_in_dim(padded, 0, 1, axis=1))
        padded = assemble_dim(padded, 1, plane_r, plane_r)
        return assemble_ext(padded) / assembled[None], outer_rate

    first_rate, first_outer = tendency(field, None)
    section = field + time_step * first_rate
    section_outer = field[0, radial_nodes - 1] + time_step * first_outer
    second_rate, _ = tendency(section, section_outer)
    return 0.5 * (field + section + time_step * second_rate)


def solution(mesh):
    placed = (
        P(None, None, "tile", "deg"),
        P(None, None, "tile", "deg"),
        P(("tile", "deg"), None, None),
        P(),
    )
    return jax.shard_map(
        local, mesh=mesh, in_specs=placed, out_specs=P(None, None, "tile", "deg"), check_vma=False
    )
```

```python
import math

import numpy as np
import jax
import jax.numpy as jnp
from jax import lax
from jax.sharding import PartitionSpec as P
from jax.experimental import pallas as pl

P_SIZE = 8


diffusivity = 0.05
time_step = 0.01
highest = lax.Precision.HIGHEST
gll_interior = [0.2092992179024789, 0.5917001814331423, 0.8717401485096066]


def padded_2(value, sides, width):
    for axis, dim in sides:
        size, length = (lax.axis_size(axis), value.shape[dim])
        up = [(i, (i + 1) % size) for i in range(size)]
        down = [(j, i) for i, j in up]
        last = lax.slice_in_dim(value, length - width, length, axis=dim)
        first = lax.slice_in_dim(value, 0, width, axis=dim)
        before = lax.ppermute(last, axis, up)
        after = lax.ppermute(first, axis, down)
        value = jnp.concatenate([before, value, after], axis=dim)
    return value


def product(a, b):
    return jnp.dot(a, b, precision=highest, preferred_element_type=jnp.float32)


def gradient_kernel(flow_ref, mats_ref, out_ref):
    for component in range(3):
        x = flow_ref[component]
        out_ref[3 * component] = product(mats_ref[0], x)
        out_ref[3 * component + 1] = product(mats_ref[1], x)
        out_ref[3 * component + 2] = product(x, mats_ref[2])


def volume_kernel(parts_ref, flow_ref, grad_ref, mats_ref, mass_ref, *outs):
    volume_body(parts_ref, flow_ref, grad_ref, mats_ref, mass_ref, *outs)


def first_volume_kernel(parts_ref, flow_ref, mats_ref, mass_ref, table_ref, *outs):
    grad_ref = outs[4]
    gradient_kernel(flow_ref, mats_ref, grad_ref)
    volume_body(parts_ref, flow_ref, grad_ref, mats_ref, mass_ref, *outs[:3])
    depth = outs[0].shape[1] // outs[1].shape[2]
    surface = parts_ref[0, pl.ds(outs[0].shape[1] - depth, depth), :]
    outs[3][...] = product(table_ref[...], surface)


def volume_body(parts_ref, flow_ref, grad_ref, mats_ref, mass_ref, out_ref, rows_ref, cols_ref):
    mass = mass_ref[...]
    p = [parts_ref[i] for i in range(3)]
    f = [flow_ref[i] for i in range(3)]
    planes = out_ref.shape[1] // rows_ref.shape[2]
    width = out_ref.shape[2]
    for c in range(3):
        x = p[c]
        s0 = product(mats_ref[0], x)
        s1 = product(mats_ref[1], x)
        s2 = product(x, mats_ref[2])
        stretch = p[0] * grad_ref[3 * c] + p[1] * grad_ref[3 * c + 1] + p[2] * grad_ref[3 * c + 2]
        carried = f[0] * s0 + f[1] * s1 + f[2] * s2
        spread = (
            product(mats_ref[3], mass * s0)
            + product(mats_ref[4], mass * s1)
            + product(mass * s2, mats_ref[5])
        )
        result = mass * (stretch - carried) - diffusivity * spread
        out_ref[c] = result
        turned = result.T
        cols_ref[0, c : c + 1, :] = turned[0:1, :]
        cols_ref[1, c : c + 1, :] = turned[width - 1 : width, :]
    for c in range(3):
        rows_ref[0, c] = out_ref[c, pl.ds(0, rows_ref.shape[2], stride=planes), :]
        rows_ref[1, c] = out_ref[c, pl.ds(planes - 1, rows_ref.shape[2], stride=planes), :]


def derivative_tables(radial_nodes, na_dev, nb_dev):
    _, _, matrix_list = gll_tables(P_SIZE)
    dmat = np.asarray(matrix_list, np.float32)
    radial = np.kron(dmat, np.eye(na_dev, dtype=np.float32))
    first = np.kron(np.eye(radial_nodes * na_dev // P_SIZE, dtype=np.float32), dmat)
    second = np.kron(np.eye(nb_dev // P_SIZE, dtype=np.float32), dmat)
    return jnp.asarray(np.stack([radial, first, second.T, radial.T, first.T, second]))


def legendre_value(point, degree):
    previous = 1.0
    current = point
    for order in range(1, degree):
        following = ((2 * order + 1) * point * current - order * previous) / (order + 1)
        previous = current
        current = following
    return current


def gll_tables(count):
    degree = count - 1
    points = [-1.0] + [-value for value in reversed(gll_interior)] + list(gll_interior) + [1.0]
    values = [legendre_value(point, degree) for point in points]
    weights = [2.0 / (degree * (degree + 1) * value * value) for value in values]
    matrix = [
        [
            values[row] / (values[col] * (points[row] - points[col])) if row != col else 0.0
            for col in range(count)
        ]
        for row in range(count)
    ]
    matrix[0][0] = -degree * (degree + 1) / 4.0
    matrix[count - 1][count - 1] = degree * (degree + 1) / 4.0
    return (points, weights, matrix)


def apply_along(values, axis_pos, matrix):
    shape = values.shape
    blocks = values.reshape(
        shape[:axis_pos] + (shape[axis_pos] // P_SIZE, P_SIZE) + shape[axis_pos + 1 :]
    )
    letters = list("abcdefg"[: blocks.ndim])
    source = list(letters)
    source[axis_pos + 1] = "p"
    target = list(letters)
    target[axis_pos + 1] = "q"
    formula = "".join(source) + ",qp->" + "".join(target)
    return jnp.einsum(formula, blocks, matrix, precision=highest).reshape(shape)


def assemble_dim(values, axis_pos, left, right):
    shape = values.shape
    count = shape[axis_pos] // P_SIZE
    blocks = values.reshape(shape[:axis_pos] + (count, P_SIZE) + shape[axis_pos + 1 :])
    edge_shape = shape[:axis_pos] + (1, 1) + shape[axis_pos + 1 :]
    first = lax.slice_in_dim(blocks, 0, 1, axis=axis_pos + 1)
    last = lax.slice_in_dim(blocks, P_SIZE - 1, P_SIZE, axis=axis_pos + 1)
    before = jnp.concatenate(
        [left.reshape(edge_shape), lax.slice_in_dim(last, 0, count - 1, axis=axis_pos)],
        axis=axis_pos,
    )
    after = jnp.concatenate(
        [lax.slice_in_dim(first, 1, count, axis=axis_pos), right.reshape(edge_shape)], axis=axis_pos
    )
    middle = lax.slice_in_dim(blocks, 1, P_SIZE - 1, axis=axis_pos + 1)
    joined = jnp.concatenate([first + before, middle, last + after], axis=axis_pos + 1)
    return joined.reshape(shape)


def assembled_weights(weights, count, lead, trail):
    position = jnp.arange(count * P_SIZE, dtype=jnp.int32)
    local_point = position % P_SIZE
    element = position // P_SIZE
    base = jnp.tile(weights, count)
    starts = (
        jnp.where(local_point == 0, jnp.where(element > 0, 1.0, lead), 0.0) * weights[P_SIZE - 1]
    )
    ends = (
        jnp.where(local_point == P_SIZE - 1, jnp.where(element < count - 1, 1.0, trail), 0.0)
        * weights[0]
    )
    return base + starts + ends


def static_assembled(weights, count, lead, trail):
    position = np.arange(count * P_SIZE)
    local_point = position % P_SIZE
    element = position // P_SIZE
    starts = np.where(local_point == 0, np.where(element > 0, 1.0, lead), 0.0) * weights[P_SIZE - 1]
    ends = np.where(local_point == P_SIZE - 1, np.where(element < count - 1, 1.0, trail), 0.0)
    return (np.tile(weights, count) + starts + ends * weights[0]).astype(np.float32)


def table_at(values, index):
    point = index % P_SIZE
    total = jnp.zeros(index.shape, jnp.float32)
    for p in range(P_SIZE):
        total = total + jnp.where(point == p, float(values[p]), 0.0)
    return total


def phases(waves, elem_start, elem_count, span, points):
    position = elem_start * P_SIZE + jnp.arange(elem_count * P_SIZE, dtype=jnp.int32)
    element = position // P_SIZE
    whole = waves[:, None] * (2 * element + 1)[None, :] % span
    fraction = waves.astype(jnp.float32)[:, None] * table_at(points, position)[None, :]
    return 2.0 * math.pi / span * (whole.astype(jnp.float32) + fraction)


def phases_at(waves, element, point_values, span):
    whole = waves[:, None] * (2 * element + 1)[None, :] % span
    fraction = waves.astype(jnp.float32)[:, None] * point_values[None, :]
    return 2.0 * math.pi / span * (whole.astype(jnp.float32) + fraction)


def shift_pairs(sizes, steps):
    count = sizes[0] * sizes[1]
    pairs = []
    for source in range(count):
        t, g = divmod(source, sizes[1])
        target = ((t + steps[0]) % sizes[0]) * sizes[1] + (g + steps[1]) % sizes[1]
        pairs.append((source, target))
    return pairs


def local(field, flow, match_ops, wave_of_slot):
    tiles = lax.axis_size("tile")
    groups = lax.axis_size("deg")
    both = ("tile", "deg")
    tile_index = lax.axis_index("tile")
    group_index = lax.axis_index("deg")
    radial_nodes = field.shape[1]
    na_dev = field.shape[2]
    nb_dev = field.shape[3]
    elems_a = na_dev // P_SIZE
    elems_b = nb_dev // P_SIZE
    nb = nb_dev * groups
    span = 2 * elems_a * tiles
    scale = P_SIZE / (na_dev * tiles)
    points_list, weights_list, _ = gll_tables(P_SIZE)
    points = np.asarray(points_list, np.float32)
    weights = np.asarray(weights_list, np.float32)
    lead = (group_index > 0).astype(jnp.float32)
    trail = (group_index < groups - 1).astype(jnp.float32)
    w_r = np.tile(weights, radial_nodes // P_SIZE)
    w_a = np.tile(weights, elems_a)
    w_b = np.tile(weights, elems_b)
    mass3 = w_r[:, None, None] * w_a[None, :, None] * w_b[None, None, :]
    b_first = np.zeros((nb_dev,), np.float32)
    b_first[0] = weights[P_SIZE - 1]
    b_last = np.zeros((nb_dev,), np.float32)
    b_last[nb_dev - 1] = weights[0]
    assembled_b = static_assembled(weights, elems_b, 0.0, 0.0) + lead * b_first + trail * b_last
    assembled = (
        (
            static_assembled(weights, radial_nodes // P_SIZE, 0.0, 0.0)[:, None]
            * static_assembled(weights, elems_a, 1.0, 1.0)[None, :]
        )[:, :, None]
        * assembled_b[None, None, :]
    )
    rows_ext = (tile_index * na_dev - 1 + jnp.arange(na_dev + 2, dtype=jnp.int32)) % (na_dev * tiles)
    row_points = (np.arange(na_dev + 2) - 1) % P_SIZE
    col_points = (np.arange(nb_dev + 2) - 1) % P_SIZE
    cols_ext = group_index * nb_dev - 1 + jnp.arange(nb_dev + 2, dtype=jnp.int32)

    def weight_at(index):
        return table_at(weights, index)

    surface_ext = diffusivity * weight_at(rows_ext)[:, None] * weight_at(cols_ext)[None, :]

    rows = radial_nodes * na_dev
    mats = derivative_tables(radial_nodes, na_dev, nb_dev)
    flat_mass = mass3.reshape(rows, nb_dev)
    flat_flow = flow.reshape(3, rows, nb_dev)

    angle = phases(wave_of_slot, tile_index * elems_a, elems_a, span, points)
    analysis = (
        jnp.stack([jnp.cos(angle), jnp.sin(angle)], axis=1)
        * (scale * weight_at(tile_index * na_dev + jnp.arange(na_dev, dtype=jnp.int32)))[
            None, None, :
        ]
    ).reshape(-1, na_dev)

    def owner_map(partial):
        partial = partial.reshape(-1, 2, nb_dev)
        gathered = lax.all_to_all(partial, both, 0, 0, tiled=True)
        coeff = gathered.reshape(tiles, groups, 2, nb_dev).sum(axis=0)
        coeff = coeff.transpose(1, 0, 2).reshape(2, nb)
        owned = coeff.astype(jnp.bfloat16)
        mapped = jnp.einsum(
            "pq,cq->cp", match_ops[0], owned, preferred_element_type=jnp.float32
        )
        edged = jnp.concatenate([mapped[:, :1], mapped, mapped[:, -1:]], axis=1)
        pieces = jnp.stack(
            [edged[:, g * nb_dev : g * nb_dev + nb_dev + 2] for g in range(groups)], axis=0
        )
        return jnp.broadcast_to(pieces[None], (tiles,) + pieces.shape).reshape(
            tiles, groups, 2 * (nb_dev + 2)
        )

    def flux_of(returned):
        angle = phases_at(wave_of_slot, rows_ext // P_SIZE, table_at(points, rows_ext), span)
        synth = jnp.stack([jnp.cos(angle).T, jnp.sin(angle).T], axis=2).reshape(na_dev + 2, -1)
        flux = -jnp.dot(synth, returned.reshape(-1, nb_dev + 2), precision=highest)
        return surface_ext * flux

    mapped_len = 2 * (nb_dev + 2)
    slot_len = 3 * radial_nodes * na_dev
    carried_halo = tiles >= 3 and groups >= 3 and tiles * groups <= 64

    def joint_exchange(sent, stacked, edge_rows, edge_cols):
        a_lo = edge_rows[0].reshape(3, radial_nodes, 1, nb_dev)
        a_hi = edge_rows[1].reshape(3, radial_nodes, 1, nb_dev)
        up = [(i, (i + 1) % tiles) for i in range(tiles)]
        down = [(j, i) for i, j in up]
        from_up = lax.ppermute(a_hi, "tile", up)
        from_down = lax.ppermute(a_lo, "tile", down)
        b_lo = edge_cols[0].reshape(1, 1, -1)
        b_hi = edge_cols[1].reshape(1, 1, -1)
        out_pieces = [
            ((0, 1), b_hi),
            ((0, -1), b_lo),
            ((1, 1), b_hi),
            ((1, -1), b_lo),
            ((-1, 1), b_hi),
            ((-1, -1), b_lo),
        ]
        slots = jnp.zeros((tiles * groups, 1, slot_len), jnp.float32)
        for (dt, dg), flat in out_pieces:
            target = ((tile_index + dt) % tiles) * groups + (group_index + dg) % groups
            slots = lax.dynamic_update_slice(slots, flat, (target, 0, 0))
        message = jnp.concatenate([sent.reshape(tiles * groups, 1, -1), slots], axis=2)
        received = lax.all_to_all(message, both, 0, 0, tiled=True)
        returned = received[:, 0, :mapped_len].reshape(tiles * groups, 2, nb_dev + 2)

        def take(dt, dg):
            source = ((tile_index - dt) % tiles) * groups + (group_index - dg) % groups
            row = lax.dynamic_slice(received, (source, 0, mapped_len), (1, 1, slot_len))
            return row.reshape(3, radial_nodes, na_dev, 1)

        from_left = take(0, 1)
        from_right = take(0, -1)
        corner_ul = take(1, 1)[:, :, na_dev - 1 :, :]
        corner_ur = take(1, -1)[:, :, na_dev - 1 :, :]
        corner_dl = take(-1, 1)[:, :, :1, :]
        corner_dr = take(-1, -1)[:, :, :1, :]
        top = jnp.concatenate([corner_ul, from_up, corner_ur], axis=3)
        middle = jnp.concatenate([from_left, stacked, from_right], axis=3)
        bottom = jnp.concatenate([corner_dl, from_down, corner_dr], axis=3)
        return returned, jnp.concatenate([top, middle, bottom], axis=2)

    def halo(stacked):
        a_lo = lax.slice_in_dim(stacked, 0, 1, axis=2)
        a_hi = lax.slice_in_dim(stacked, na_dev - 1, na_dev, axis=2)
        b_lo = lax.slice_in_dim(stacked, 0, 1, axis=3)
        b_hi = lax.slice_in_dim(stacked, nb_dev - 1, nb_dev, axis=3)
        sizes = (tiles, groups)
        from_up = lax.ppermute(a_hi, both, shift_pairs(sizes, (1, 0)))
        from_down = lax.ppermute(a_lo, both, shift_pairs(sizes, (-1, 0)))
        from_left = lax.ppermute(b_hi, both, shift_pairs(sizes, (0, 1)))
        from_right = lax.ppermute(b_lo, both, shift_pairs(sizes, (0, -1)))
        corner_ul = lax.ppermute(a_hi[:, :, :, -1:], both, shift_pairs(sizes, (1, 1)))
        corner_ur = lax.ppermute(a_hi[:, :, :, :1], both, shift_pairs(sizes, (1, -1)))
        corner_dl = lax.ppermute(a_lo[:, :, :, -1:], both, shift_pairs(sizes, (-1, 1)))
        corner_dr = lax.ppermute(a_lo[:, :, :, :1], both, shift_pairs(sizes, (-1, -1)))
        top = jnp.concatenate([corner_ul, from_up, corner_ur], axis=3)
        middle = jnp.concatenate([from_left, stacked, from_right], axis=3)
        bottom = jnp.concatenate([corner_dl, from_down, corner_dr], axis=3)
        return jnp.concatenate([top, middle, bottom], axis=2)

    join_b = np.zeros((nb_dev + 2, nb_dev), np.float32)
    join_b[np.arange(nb_dev) + 1, np.arange(nb_dev)] = 1.0
    inner_first = np.arange(P_SIZE, nb_dev, P_SIZE)
    join_b[inner_first, inner_first] = 1.0
    inner_last = np.arange(P_SIZE - 1, nb_dev - 1, P_SIZE)
    join_b[inner_last + 2, inner_last] = 1.0
    edge_lead = np.zeros((nb_dev + 2, nb_dev), np.float32)
    edge_lead[0, 0] = 1.0
    edge_trail = np.zeros((nb_dev + 2, nb_dev), np.float32)
    edge_trail[nb_dev + 1, nb_dev - 1] = 1.0
    join_b = join_b + lead * edge_lead + trail * edge_trail

    mask_shape = (3, radial_nodes, 1, 1)
    outer_index = radial_nodes - 1 + jnp.minimum(tile_index, 0)
    plane_mask = jnp.where(
        (lax.broadcasted_iota(jnp.int32, mask_shape, 0) == 0)
        & (lax.broadcasted_iota(jnp.int32, mask_shape, 1) == outer_index),
        1.0,
        0.0,
    )

    def assemble_ext(padded):
        last = padded.ndim - 1
        along_a = assemble_dim(
            padded[..., 1:-1, :], last - 1, padded[..., 0:1, :], padded[..., -1:, :]
        )
        return jnp.dot(along_a, join_b, precision=highest)

    shapes = (
        jax.ShapeDtypeStruct((3, rows, nb_dev), jnp.float32),
        jax.ShapeDtypeStruct((2, 3, radial_nodes, nb_dev), jnp.float32),
        jax.ShapeDtypeStruct((2, 3, rows), jnp.float32),
    )
    first_outs = pl.pallas_call(
        first_volume_kernel,
        out_shape=shapes
        + (
            jax.ShapeDtypeStruct(analysis.shape[:1] + (nb_dev,), jnp.float32),
            jax.ShapeDtypeStruct((9, rows, nb_dev), jnp.float32),
        ),
    )(field.reshape(3, rows, nb_dev), flat_flow, mats, flat_mass, analysis)
    grads = first_outs[4]

    def tendency(parts, surface):
        if surface is None:
            stacked, edge_rows, edge_cols, partial = first_outs[:4]
        else:
            stacked, edge_rows, edge_cols = pl.pallas_call(volume_kernel, out_shape=shapes)(
                parts.reshape(3, rows, nb_dev), flat_flow, grads, mats, flat_mass
            )
            partial = jnp.dot(analysis, surface, precision=highest)
        stacked = stacked.reshape(parts.shape)
        sent = owner_map(partial)
        if carried_halo:
            returned, padded = joint_exchange(sent, stacked, edge_rows, edge_cols)
        else:
            returned = lax.all_to_all(
                sent.reshape(tiles * groups, -1), both, 0, 0, tiled=True
            ).reshape(tiles * groups, 2, nb_dev + 2)
            padded = halo(stacked)
        flux_term = flux_of(returned)
        outer = padded[0, radial_nodes - 1] + flux_term
        outer_rate = assemble_ext(outer) / assembled[radial_nodes - 1]
        padded = padded + plane_mask * flux_term
        plane_r = jnp.zeros_like(lax.slice_in_dim(padded, 0, 1, axis=1))
        padded = assemble_dim(padded, 1, plane_r, plane_r)
        return assemble_ext(padded) / assembled[None], outer_rate

    first_rate, first_outer = tendency(field, None)
    section = field + time_step * first_rate
    section_outer = field[0, radial_nodes - 1] + time_step * first_outer
    second_rate, _ = tendency(section, section_outer)
    return 0.5 * (field + section + time_step * second_rate)


def solution(mesh):
    placed = (
        P(None, None, "tile", "deg"),
        P(None, None, "tile", "deg"),
        P(("tile", "deg"), None, None),
        P(),
    )
    return jax.shard_map(
        local, mesh=mesh, in_specs=placed, out_specs=P(None, None, "tile", "deg"), check_vma=False
    )
```

```python
import math

import numpy as np
import jax
import jax.numpy as jnp
from jax import lax
from jax.sharding import PartitionSpec as P
from jax.experimental import pallas as pl

P_SIZE = 8


diffusivity = 0.05
time_step = 0.01
highest = lax.Precision.HIGHEST
gll_interior = [0.2092992179024789, 0.5917001814331423, 0.8717401485096066]


def padded_2(value, sides, width):
    for axis, dim in sides:
        size, length = (lax.axis_size(axis), value.shape[dim])
        up = [(i, (i + 1) % size) for i in range(size)]
        down = [(j, i) for i, j in up]
        last = lax.slice_in_dim(value, length - width, length, axis=dim)
        first = lax.slice_in_dim(value, 0, width, axis=dim)
        before = lax.ppermute(last, axis, up)
        after = lax.ppermute(first, axis, down)
        value = jnp.concatenate([before, value, after], axis=dim)
    return value


def product(a, b):
    return jnp.dot(a, b, precision=highest, preferred_element_type=jnp.float32)


def gradient_kernel(flow_ref, mats_ref, out_ref):
    for component in range(3):
        x = flow_ref[component]
        out_ref[3 * component] = product(mats_ref[0], x)
        out_ref[3 * component + 1] = product(mats_ref[1], x)
        out_ref[3 * component + 2] = product(x, mats_ref[2])


def volume_kernel(parts_ref, flow_ref, grad_ref, mats_ref, mass_ref, *outs):
    volume_body(parts_ref, flow_ref, grad_ref, mats_ref, mass_ref, *outs)


def first_volume_kernel(parts_ref, flow_ref, mats_ref, mass_ref, table_ref, *outs):
    grad_ref = outs[4]
    gradient_kernel(flow_ref, mats_ref, grad_ref)
    volume_body(parts_ref, flow_ref, grad_ref, mats_ref, mass_ref, *outs[:3])
    depth = outs[0].shape[1] // outs[1].shape[2]
    surface = parts_ref[0, pl.ds(outs[0].shape[1] - depth, depth), :]
    outs[3][...] = product(table_ref[...], surface)


def volume_body(parts_ref, flow_ref, grad_ref, mats_ref, mass_ref, out_ref, rows_ref, cols_ref):
    mass = mass_ref[...]
    p = [parts_ref[i] for i in range(3)]
    f = [flow_ref[i] for i in range(3)]
    planes = out_ref.shape[1] // rows_ref.shape[2]
    width = out_ref.shape[2]
    for c in range(3):
        x = p[c]
        s0 = product(mats_ref[0], x)
        s1 = product(mats_ref[1], x)
        s2 = product(x, mats_ref[2])
        stretch = p[0] * grad_ref[3 * c] + p[1] * grad_ref[3 * c + 1] + p[2] * grad_ref[3 * c + 2]
        carried = f[0] * s0 + f[1] * s1 + f[2] * s2
        spread = (
            product(mats_ref[3], mass * s0)
            + product(mats_ref[4], mass * s1)
            + product(mass * s2, mats_ref[5])
        )
        result = mass * (stretch - carried) - diffusivity * spread
        out_ref[c] = result
        turned = result.T
        cols_ref[0, c : c + 1, :] = turned[0:1, :]
        cols_ref[1, c : c + 1, :] = turned[width - 1 : width, :]
    for c in range(3):
        rows_ref[0, c] = out_ref[c, pl.ds(0, rows_ref.shape[2], stride=planes), :]
        rows_ref[1, c] = out_ref[c, pl.ds(planes - 1, rows_ref.shape[2], stride=planes), :]


def derivative_tables(radial_nodes, na_dev, nb_dev):
    _, _, matrix_list = gll_tables(P_SIZE)
    dmat = np.asarray(matrix_list, np.float32)
    radial = np.kron(dmat, np.eye(na_dev, dtype=np.float32))
    first = np.kron(np.eye(radial_nodes * na_dev // P_SIZE, dtype=np.float32), dmat)
    second = np.kron(np.eye(nb_dev // P_SIZE, dtype=np.float32), dmat)
    return jnp.asarray(np.stack([radial, first, second.T, radial.T, first.T, second]))


def legendre_value(point, degree):
    previous = 1.0
    current = point
    for order in range(1, degree):
        following = ((2 * order + 1) * point * current - order * previous) / (order + 1)
        previous = current
        current = following
    return current


def gll_tables(count):
    degree = count - 1
    points = [-1.0] + [-value for value in reversed(gll_interior)] + list(gll_interior) + [1.0]
    values = [legendre_value(point, degree) for point in points]
    weights = [2.0 / (degree * (degree + 1) * value * value) for value in values]
    matrix = [
        [
            values[row] / (values[col] * (points[row] - points[col])) if row != col else 0.0
            for col in range(count)
        ]
        for row in range(count)
    ]
    matrix[0][0] = -degree * (degree + 1) / 4.0
    matrix[count - 1][count - 1] = degree * (degree + 1) / 4.0
    return (points, weights, matrix)


def apply_along(values, axis_pos, matrix):
    shape = values.shape
    blocks = values.reshape(
        shape[:axis_pos] + (shape[axis_pos] // P_SIZE, P_SIZE) + shape[axis_pos + 1 :]
    )
    letters = list("abcdefg"[: blocks.ndim])
    source = list(letters)
    source[axis_pos + 1] = "p"
    target = list(letters)
    target[axis_pos + 1] = "q"
    formula = "".join(source) + ",qp->" + "".join(target)
    return jnp.einsum(formula, blocks, matrix, precision=highest).reshape(shape)


def assemble_dim(values, axis_pos, left, right):
    shape = values.shape
    count = shape[axis_pos] // P_SIZE
    blocks = values.reshape(shape[:axis_pos] + (count, P_SIZE) + shape[axis_pos + 1 :])
    edge_shape = shape[:axis_pos] + (1, 1) + shape[axis_pos + 1 :]
    first = lax.slice_in_dim(blocks, 0, 1, axis=axis_pos + 1)
    last = lax.slice_in_dim(blocks, P_SIZE - 1, P_SIZE, axis=axis_pos + 1)
    before = jnp.concatenate(
        [left.reshape(edge_shape), lax.slice_in_dim(last, 0, count - 1, axis=axis_pos)],
        axis=axis_pos,
    )
    after = jnp.concatenate(
        [lax.slice_in_dim(first, 1, count, axis=axis_pos), right.reshape(edge_shape)], axis=axis_pos
    )
    middle = lax.slice_in_dim(blocks, 1, P_SIZE - 1, axis=axis_pos + 1)
    joined = jnp.concatenate([first + before, middle, last + after], axis=axis_pos + 1)
    return joined.reshape(shape)


def assembled_weights(weights, count, lead, trail):
    position = jnp.arange(count * P_SIZE, dtype=jnp.int32)
    local_point = position % P_SIZE
    element = position // P_SIZE
    base = jnp.tile(weights, count)
    starts = (
        jnp.where(local_point == 0, jnp.where(element > 0, 1.0, lead), 0.0) * weights[P_SIZE - 1]
    )
    ends = (
        jnp.where(local_point == P_SIZE - 1, jnp.where(element < count - 1, 1.0, trail), 0.0)
        * weights[0]
    )
    return base + starts + ends


def static_assembled(weights, count, lead, trail):
    position = np.arange(count * P_SIZE)
    local_point = position % P_SIZE
    element = position // P_SIZE
    starts = np.where(local_point == 0, np.where(element > 0, 1.0, lead), 0.0) * weights[P_SIZE - 1]
    ends = np.where(local_point == P_SIZE - 1, np.where(element < count - 1, 1.0, trail), 0.0)
    return (np.tile(weights, count) + starts + ends * weights[0]).astype(np.float32)


def table_at(values, index):
    point = index % P_SIZE
    total = jnp.zeros(index.shape, jnp.float32)
    for p in range(P_SIZE):
        total = total + jnp.where(point == p, float(values[p]), 0.0)
    return total


def phases(waves, elem_start, elem_count, span, points):
    position = elem_start * P_SIZE + jnp.arange(elem_count * P_SIZE, dtype=jnp.int32)
    element = position // P_SIZE
    whole = waves[:, None] * (2 * element + 1)[None, :] % span
    fraction = waves.astype(jnp.float32)[:, None] * table_at(points, position)[None, :]
    return 2.0 * math.pi / span * (whole.astype(jnp.float32) + fraction)


def phases_at(waves, element, point_values, span):
    whole = waves[:, None] * (2 * element + 1)[None, :] % span
    fraction = waves.astype(jnp.float32)[:, None] * point_values[None, :]
    return 2.0 * math.pi / span * (whole.astype(jnp.float32) + fraction)


def shift_pairs(sizes, steps):
    count = sizes[0] * sizes[1]
    pairs = []
    for source in range(count):
        t, g = divmod(source, sizes[1])
        target = ((t + steps[0]) % sizes[0]) * sizes[1] + (g + steps[1]) % sizes[1]
        pairs.append((source, target))
    return pairs


def local(field, flow, match_ops, wave_of_slot):
    tiles = lax.axis_size("tile")
    groups = lax.axis_size("deg")
    both = ("tile", "deg")
    tile_index = lax.axis_index("tile")
    group_index = lax.axis_index("deg")
    radial_nodes = field.shape[1]
    na_dev = field.shape[2]
    nb_dev = field.shape[3]
    elems_a = na_dev // P_SIZE
    elems_b = nb_dev // P_SIZE
    nb = nb_dev * groups
    span = 2 * elems_a * tiles
    scale = P_SIZE / (na_dev * tiles)
    points_list, weights_list, _ = gll_tables(P_SIZE)
    points = np.asarray(points_list, np.float32)
    weights = np.asarray(weights_list, np.float32)
    lead = (group_index > 0).astype(jnp.float32)
    trail = (group_index < groups - 1).astype(jnp.float32)
    w_r = np.tile(weights, radial_nodes // P_SIZE)
    w_a = np.tile(weights, elems_a)
    w_b = np.tile(weights, elems_b)
    mass3 = w_r[:, None, None] * w_a[None, :, None] * w_b[None, None, :]
    origin = jnp.minimum(tile_index, 0)

    def assembled_at(length, lead_value, trail_value):
        position = origin + jnp.arange(length, dtype=jnp.int32)
        local_point = position % P_SIZE
        element = position // P_SIZE
        count = length // P_SIZE
        starts = jnp.where(
            local_point == 0, jnp.where(element > 0, 1.0, lead_value), 0.0
        ) * float(weights[P_SIZE - 1])
        ends = jnp.where(
            local_point == P_SIZE - 1, jnp.where(element < count - 1, 1.0, trail_value), 0.0
        ) * float(weights[0])
        return table_at(weights, position) + starts + ends

    assembled = (
        (
            assembled_at(radial_nodes, 0.0, 0.0)[:, None]
            * assembled_at(na_dev, 1.0, 1.0)[None, :]
        )[:, :, None]
        * assembled_at(nb_dev, lead, trail)[None, None, :]
    )
    rows_ext = (tile_index * na_dev - 1 + jnp.arange(na_dev + 2, dtype=jnp.int32)) % (na_dev * tiles)
    row_points = (np.arange(na_dev + 2) - 1) % P_SIZE
    col_points = (np.arange(nb_dev + 2) - 1) % P_SIZE
    cols_ext = group_index * nb_dev - 1 + jnp.arange(nb_dev + 2, dtype=jnp.int32)

    def weight_at(index):
        return table_at(weights, index)

    surface_ext = diffusivity * weight_at(rows_ext)[:, None] * weight_at(cols_ext)[None, :]

    rows = radial_nodes * na_dev
    mats = derivative_tables(radial_nodes, na_dev, nb_dev)
    flat_mass = mass3.reshape(rows, nb_dev)
    flat_flow = flow.reshape(3, rows, nb_dev)

    angle = phases(wave_of_slot, tile_index * elems_a, elems_a, span, points)
    analysis = (
        jnp.stack([jnp.cos(angle), jnp.sin(angle)], axis=1)
        * (scale * weight_at(tile_index * na_dev + jnp.arange(na_dev, dtype=jnp.int32)))[
            None, None, :
        ]
    ).reshape(-1, na_dev)

    def owner_map(partial):
        partial = partial.reshape(-1, 2, nb_dev)
        gathered = lax.all_to_all(partial, both, 0, 0, tiled=True)
        coeff = gathered.reshape(tiles, groups, 2, nb_dev).sum(axis=0)
        coeff = coeff.transpose(1, 0, 2).reshape(2, nb)
        owned = coeff.astype(jnp.bfloat16)
        mapped = jnp.einsum(
            "pq,cq->cp", match_ops[0], owned, preferred_element_type=jnp.float32
        )
        edged = jnp.concatenate([mapped[:, :1], mapped, mapped[:, -1:]], axis=1)
        pieces = jnp.stack(
            [edged[:, g * nb_dev : g * nb_dev + nb_dev + 2] for g in range(groups)], axis=0
        )
        return jnp.broadcast_to(pieces[None], (tiles,) + pieces.shape).reshape(
            tiles, groups, 2 * (nb_dev + 2)
        )

    def flux_of(returned):
        angle = phases_at(wave_of_slot, rows_ext // P_SIZE, table_at(points, rows_ext), span)
        synth = jnp.stack([jnp.cos(angle).T, jnp.sin(angle).T], axis=2).reshape(na_dev + 2, -1)
        flux = -jnp.dot(synth, returned.reshape(-1, nb_dev + 2), precision=highest)
        return surface_ext * flux

    mapped_len = 2 * (nb_dev + 2)
    slot_len = 3 * radial_nodes * na_dev
    carried_halo = tiles >= 3 and groups >= 3 and tiles * groups <= 64

    def joint_exchange(sent, stacked, edge_rows, edge_cols):
        a_lo = edge_rows[0].reshape(3, radial_nodes, 1, nb_dev)
        a_hi = edge_rows[1].reshape(3, radial_nodes, 1, nb_dev)
        up = [(i, (i + 1) % tiles) for i in range(tiles)]
        down = [(j, i) for i, j in up]
        from_up = lax.ppermute(a_hi, "tile", up)
        from_down = lax.ppermute(a_lo, "tile", down)
        b_lo = edge_cols[0].reshape(1, 1, -1)
        b_hi = edge_cols[1].reshape(1, 1, -1)
        out_pieces = [
            ((0, 1), b_hi),
            ((0, -1), b_lo),
            ((1, 1), b_hi),
            ((1, -1), b_lo),
            ((-1, 1), b_hi),
            ((-1, -1), b_lo),
        ]
        slots = jnp.zeros((tiles * groups, 1, slot_len), jnp.float32)
        for (dt, dg), flat in out_pieces:
            target = ((tile_index + dt) % tiles) * groups + (group_index + dg) % groups
            slots = lax.dynamic_update_slice(slots, flat, (target, 0, 0))
        message = jnp.concatenate([sent.reshape(tiles * groups, 1, -1), slots], axis=2)
        received = lax.all_to_all(message, both, 0, 0, tiled=True)
        returned = received[:, 0, :mapped_len].reshape(tiles * groups, 2, nb_dev + 2)

        def take(dt, dg):
            source = ((tile_index - dt) % tiles) * groups + (group_index - dg) % groups
            row = lax.dynamic_slice(received, (source, 0, mapped_len), (1, 1, slot_len))
            return row.reshape(3, radial_nodes, na_dev, 1)

        from_left = take(0, 1)
        from_right = take(0, -1)
        corner_ul = take(1, 1)[:, :, na_dev - 1 :, :]
        corner_ur = take(1, -1)[:, :, na_dev - 1 :, :]
        corner_dl = take(-1, 1)[:, :, :1, :]
        corner_dr = take(-1, -1)[:, :, :1, :]
        top = jnp.concatenate([corner_ul, from_up, corner_ur], axis=3)
        middle = jnp.concatenate([from_left, stacked, from_right], axis=3)
        bottom = jnp.concatenate([corner_dl, from_down, corner_dr], axis=3)
        return returned, jnp.concatenate([top, middle, bottom], axis=2)

    def halo(stacked):
        a_lo = lax.slice_in_dim(stacked, 0, 1, axis=2)
        a_hi = lax.slice_in_dim(stacked, na_dev - 1, na_dev, axis=2)
        b_lo = lax.slice_in_dim(stacked, 0, 1, axis=3)
        b_hi = lax.slice_in_dim(stacked, nb_dev - 1, nb_dev, axis=3)
        sizes = (tiles, groups)
        from_up = lax.ppermute(a_hi, both, shift_pairs(sizes, (1, 0)))
        from_down = lax.ppermute(a_lo, both, shift_pairs(sizes, (-1, 0)))
        from_left = lax.ppermute(b_hi, both, shift_pairs(sizes, (0, 1)))
        from_right = lax.ppermute(b_lo, both, shift_pairs(sizes, (0, -1)))
        corner_ul = lax.ppermute(a_hi[:, :, :, -1:], both, shift_pairs(sizes, (1, 1)))
        corner_ur = lax.ppermute(a_hi[:, :, :, :1], both, shift_pairs(sizes, (1, -1)))
        corner_dl = lax.ppermute(a_lo[:, :, :, -1:], both, shift_pairs(sizes, (-1, 1)))
        corner_dr = lax.ppermute(a_lo[:, :, :, :1], both, shift_pairs(sizes, (-1, -1)))
        top = jnp.concatenate([corner_ul, from_up, corner_ur], axis=3)
        middle = jnp.concatenate([from_left, stacked, from_right], axis=3)
        bottom = jnp.concatenate([corner_dl, from_down, corner_dr], axis=3)
        return jnp.concatenate([top, middle, bottom], axis=2)

    join_b = np.zeros((nb_dev + 2, nb_dev), np.float32)
    join_b[np.arange(nb_dev) + 1, np.arange(nb_dev)] = 1.0
    inner_first = np.arange(P_SIZE, nb_dev, P_SIZE)
    join_b[inner_first, inner_first] = 1.0
    inner_last = np.arange(P_SIZE - 1, nb_dev - 1, P_SIZE)
    join_b[inner_last + 2, inner_last] = 1.0
    edge_lead = np.zeros((nb_dev + 2, nb_dev), np.float32)
    edge_lead[0, 0] = 1.0
    edge_trail = np.zeros((nb_dev + 2, nb_dev), np.float32)
    edge_trail[nb_dev + 1, nb_dev - 1] = 1.0
    join_b = join_b + lead * edge_lead + trail * edge_trail

    mask_shape = (3, radial_nodes, 1, 1)
    outer_index = radial_nodes - 1 + jnp.minimum(tile_index, 0)
    plane_mask = jnp.where(
        (lax.broadcasted_iota(jnp.int32, mask_shape, 0) == 0)
        & (lax.broadcasted_iota(jnp.int32, mask_shape, 1) == outer_index),
        1.0,
        0.0,
    )

    def assemble_ext(padded):
        last = padded.ndim - 1
        along_a = assemble_dim(
            padded[..., 1:-1, :], last - 1, padded[..., 0:1, :], padded[..., -1:, :]
        )
        return jnp.dot(along_a, join_b, precision=highest)

    shapes = (
        jax.ShapeDtypeStruct((3, rows, nb_dev), jnp.float32),
        jax.ShapeDtypeStruct((2, 3, radial_nodes, nb_dev), jnp.float32),
        jax.ShapeDtypeStruct((2, 3, rows), jnp.float32),
    )
    first_outs = pl.pallas_call(
        first_volume_kernel,
        out_shape=shapes
        + (
            jax.ShapeDtypeStruct(analysis.shape[:1] + (nb_dev,), jnp.float32),
            jax.ShapeDtypeStruct((9, rows, nb_dev), jnp.float32),
        ),
    )(field.reshape(3, rows, nb_dev), flat_flow, mats, flat_mass, analysis)
    grads = first_outs[4]

    def tendency(parts, surface):
        if surface is None:
            stacked, edge_rows, edge_cols, partial = first_outs[:4]
        else:
            stacked, edge_rows, edge_cols = pl.pallas_call(volume_kernel, out_shape=shapes)(
                parts.reshape(3, rows, nb_dev), flat_flow, grads, mats, flat_mass
            )
            partial = jnp.dot(analysis, surface, precision=highest)
        stacked = stacked.reshape(parts.shape)
        sent = owner_map(partial)
        if carried_halo:
            returned, padded = joint_exchange(sent, stacked, edge_rows, edge_cols)
        else:
            returned = lax.all_to_all(
                sent.reshape(tiles * groups, -1), both, 0, 0, tiled=True
            ).reshape(tiles * groups, 2, nb_dev + 2)
            padded = halo(stacked)
        flux_term = flux_of(returned)
        outer = padded[0, radial_nodes - 1] + flux_term
        outer_rate = assemble_ext(outer) / assembled[radial_nodes - 1]
        padded = padded + plane_mask * flux_term
        plane_r = jnp.zeros_like(lax.slice_in_dim(padded, 0, 1, axis=1))
        padded = assemble_dim(padded, 1, plane_r, plane_r)
        return assemble_ext(padded) / assembled[None], outer_rate

    first_rate, first_outer = tendency(field, None)
    section = field + time_step * first_rate
    section_outer = field[0, radial_nodes - 1] + time_step * first_outer
    second_rate, _ = tendency(section, section_outer)
    return 0.5 * (field + section + time_step * second_rate)


def solution(mesh):
    placed = (
        P(None, None, "tile", "deg"),
        P(None, None, "tile", "deg"),
        P(("tile", "deg"), None, None),
        P(),
    )
    return jax.shard_map(
        local, mesh=mesh, in_specs=placed, out_specs=P(None, None, "tile", "deg"), check_vma=False
    )
```

```python
import math

import numpy as np
import jax
import jax.numpy as jnp
from jax import lax
from jax.sharding import PartitionSpec as P
from jax.experimental import pallas as pl

P_SIZE = 8


diffusivity = 0.05
time_step = 0.01
highest = lax.Precision.HIGHEST
gll_interior = [0.2092992179024789, 0.5917001814331423, 0.8717401485096066]


def padded_2(value, sides, width):
    for axis, dim in sides:
        size, length = (lax.axis_size(axis), value.shape[dim])
        up = [(i, (i + 1) % size) for i in range(size)]
        down = [(j, i) for i, j in up]
        last = lax.slice_in_dim(value, length - width, length, axis=dim)
        first = lax.slice_in_dim(value, 0, width, axis=dim)
        before = lax.ppermute(last, axis, up)
        after = lax.ppermute(first, axis, down)
        value = jnp.concatenate([before, value, after], axis=dim)
    return value


def product(a, b):
    return jnp.dot(a, b, precision=highest, preferred_element_type=jnp.float32)


def gradient_kernel(flow_ref, mats_ref, out_ref):
    for component in range(3):
        x = flow_ref[component]
        out_ref[3 * component] = product(mats_ref[0], x)
        out_ref[3 * component + 1] = product(mats_ref[1], x)
        out_ref[3 * component + 2] = product(x, mats_ref[2])


def volume_kernel(parts_ref, flow_ref, grad_ref, mats_ref, mass_ref, *outs):
    volume_body(parts_ref, flow_ref, grad_ref, mats_ref, mass_ref, *outs)


def first_volume_kernel(parts_ref, flow_ref, mats_ref, mass_ref, table_ref, *outs):
    grad_ref = outs[4]
    gradient_kernel(flow_ref, mats_ref, grad_ref)
    volume_body(parts_ref, flow_ref, grad_ref, mats_ref, mass_ref, *outs[:3])
    depth = outs[0].shape[1] // outs[1].shape[2]
    surface = parts_ref[0, pl.ds(outs[0].shape[1] - depth, depth), :]
    outs[3][...] = product(table_ref[...], surface)


def volume_body(parts_ref, flow_ref, grad_ref, mats_ref, mass_ref, out_ref, rows_ref, cols_ref):
    mass = mass_ref[...]
    p = [parts_ref[i] for i in range(3)]
    f = [flow_ref[i] for i in range(3)]
    planes = out_ref.shape[1] // rows_ref.shape[2]
    width = out_ref.shape[2]
    for c in range(3):
        x = p[c]
        s0 = product(mats_ref[0], x)
        s1 = product(mats_ref[1], x)
        s2 = product(x, mats_ref[2])
        stretch = p[0] * grad_ref[3 * c] + p[1] * grad_ref[3 * c + 1] + p[2] * grad_ref[3 * c + 2]
        carried = f[0] * s0 + f[1] * s1 + f[2] * s2
        spread = (
            product(mats_ref[3], mass * s0)
            + product(mats_ref[4], mass * s1)
            + product(mass * s2, mats_ref[5])
        )
        result = mass * (stretch - carried) - diffusivity * spread
        out_ref[c] = result
        turned = result.T
        span_of = out_ref.shape[1]
        cols_ref[0, :, c * span_of : (c + 1) * span_of] = turned[0:1, :]
        cols_ref[1, :, c * span_of : (c + 1) * span_of] = turned[width - 1 : width, :]
    for c in range(3):
        rows_ref[0, c] = out_ref[c, pl.ds(0, rows_ref.shape[2], stride=planes), :]
        rows_ref[1, c] = out_ref[c, pl.ds(planes - 1, rows_ref.shape[2], stride=planes), :]


def derivative_tables(radial_nodes, na_dev, nb_dev):
    _, _, matrix_list = gll_tables(P_SIZE)
    dmat = np.asarray(matrix_list, np.float32)
    radial = np.kron(dmat, np.eye(na_dev, dtype=np.float32))
    first = np.kron(np.eye(radial_nodes * na_dev // P_SIZE, dtype=np.float32), dmat)
    second = np.kron(np.eye(nb_dev // P_SIZE, dtype=np.float32), dmat)
    return jnp.asarray(np.stack([radial, first, second.T, radial.T, first.T, second]))


def legendre_value(point, degree):
    previous = 1.0
    current = point
    for order in range(1, degree):
        following = ((2 * order + 1) * point * current - order * previous) / (order + 1)
        previous = current
        current = following
    return current


def gll_tables(count):
    degree = count - 1
    points = [-1.0] + [-value for value in reversed(gll_interior)] + list(gll_interior) + [1.0]
    values = [legendre_value(point, degree) for point in points]
    weights = [2.0 / (degree * (degree + 1) * value * value) for value in values]
    matrix = [
        [
            values[row] / (values[col] * (points[row] - points[col])) if row != col else 0.0
            for col in range(count)
        ]
        for row in range(count)
    ]
    matrix[0][0] = -degree * (degree + 1) / 4.0
    matrix[count - 1][count - 1] = degree * (degree + 1) / 4.0
    return (points, weights, matrix)


def apply_along(values, axis_pos, matrix):
    shape = values.shape
    blocks = values.reshape(
        shape[:axis_pos] + (shape[axis_pos] // P_SIZE, P_SIZE) + shape[axis_pos + 1 :]
    )
    letters = list("abcdefg"[: blocks.ndim])
    source = list(letters)
    source[axis_pos + 1] = "p"
    target = list(letters)
    target[axis_pos + 1] = "q"
    formula = "".join(source) + ",qp->" + "".join(target)
    return jnp.einsum(formula, blocks, matrix, precision=highest).reshape(shape)


def assemble_dim(values, axis_pos, left, right):
    shape = values.shape
    count = shape[axis_pos] // P_SIZE
    blocks = values.reshape(shape[:axis_pos] + (count, P_SIZE) + shape[axis_pos + 1 :])
    edge_shape = shape[:axis_pos] + (1, 1) + shape[axis_pos + 1 :]
    first = lax.slice_in_dim(blocks, 0, 1, axis=axis_pos + 1)
    last = lax.slice_in_dim(blocks, P_SIZE - 1, P_SIZE, axis=axis_pos + 1)
    before = jnp.concatenate(
        [left.reshape(edge_shape), lax.slice_in_dim(last, 0, count - 1, axis=axis_pos)],
        axis=axis_pos,
    )
    after = jnp.concatenate(
        [lax.slice_in_dim(first, 1, count, axis=axis_pos), right.reshape(edge_shape)], axis=axis_pos
    )
    middle = lax.slice_in_dim(blocks, 1, P_SIZE - 1, axis=axis_pos + 1)
    joined = jnp.concatenate([first + before, middle, last + after], axis=axis_pos + 1)
    return joined.reshape(shape)


def assembled_weights(weights, count, lead, trail):
    position = jnp.arange(count * P_SIZE, dtype=jnp.int32)
    local_point = position % P_SIZE
    element = position // P_SIZE
    base = jnp.tile(weights, count)
    starts = (
        jnp.where(local_point == 0, jnp.where(element > 0, 1.0, lead), 0.0) * weights[P_SIZE - 1]
    )
    ends = (
        jnp.where(local_point == P_SIZE - 1, jnp.where(element < count - 1, 1.0, trail), 0.0)
        * weights[0]
    )
    return base + starts + ends


def static_assembled(weights, count, lead, trail):
    position = np.arange(count * P_SIZE)
    local_point = position % P_SIZE
    element = position // P_SIZE
    starts = np.where(local_point == 0, np.where(element > 0, 1.0, lead), 0.0) * weights[P_SIZE - 1]
    ends = np.where(local_point == P_SIZE - 1, np.where(element < count - 1, 1.0, trail), 0.0)
    return (np.tile(weights, count) + starts + ends * weights[0]).astype(np.float32)


def table_at(values, index):
    point = index % P_SIZE
    total = jnp.zeros(index.shape, jnp.float32)
    for p in range(P_SIZE):
        total = total + jnp.where(point == p, float(values[p]), 0.0)
    return total


def phases(waves, elem_start, elem_count, span, points):
    position = elem_start * P_SIZE + jnp.arange(elem_count * P_SIZE, dtype=jnp.int32)
    element = position // P_SIZE
    whole = waves[:, None] * (2 * element + 1)[None, :] % span
    fraction = waves.astype(jnp.float32)[:, None] * table_at(points, position)[None, :]
    return 2.0 * math.pi / span * (whole.astype(jnp.float32) + fraction)


def phases_at(waves, element, point_values, span):
    whole = waves[:, None] * (2 * element + 1)[None, :] % span
    fraction = waves.astype(jnp.float32)[:, None] * point_values[None, :]
    return 2.0 * math.pi / span * (whole.astype(jnp.float32) + fraction)


def shift_pairs(sizes, steps):
    count = sizes[0] * sizes[1]
    pairs = []
    for source in range(count):
        t, g = divmod(source, sizes[1])
        target = ((t + steps[0]) % sizes[0]) * sizes[1] + (g + steps[1]) % sizes[1]
        pairs.append((source, target))
    return pairs


def local(field, flow, match_ops, wave_of_slot):
    tiles = lax.axis_size("tile")
    groups = lax.axis_size("deg")
    both = ("tile", "deg")
    tile_index = lax.axis_index("tile")
    group_index = lax.axis_index("deg")
    radial_nodes = field.shape[1]
    na_dev = field.shape[2]
    nb_dev = field.shape[3]
    elems_a = na_dev // P_SIZE
    elems_b = nb_dev // P_SIZE
    nb = nb_dev * groups
    span = 2 * elems_a * tiles
    scale = P_SIZE / (na_dev * tiles)
    points_list, weights_list, _ = gll_tables(P_SIZE)
    points = np.asarray(points_list, np.float32)
    weights = np.asarray(weights_list, np.float32)
    lead = (group_index > 0).astype(jnp.float32)
    trail = (group_index < groups - 1).astype(jnp.float32)
    w_r = np.tile(weights, radial_nodes // P_SIZE)
    w_a = np.tile(weights, elems_a)
    w_b = np.tile(weights, elems_b)
    mass3 = w_r[:, None, None] * w_a[None, :, None] * w_b[None, None, :]
    origin = jnp.minimum(tile_index, 0)

    def assembled_at(length, lead_value, trail_value):
        position = origin + jnp.arange(length, dtype=jnp.int32)
        local_point = position % P_SIZE
        element = position // P_SIZE
        count = length // P_SIZE
        starts = jnp.where(
            local_point == 0, jnp.where(element > 0, 1.0, lead_value), 0.0
        ) * float(weights[P_SIZE - 1])
        ends = jnp.where(
            local_point == P_SIZE - 1, jnp.where(element < count - 1, 1.0, trail_value), 0.0
        ) * float(weights[0])
        return table_at(weights, position) + starts + ends

    assembled = (
        (
            assembled_at(radial_nodes, 0.0, 0.0)[:, None]
            * assembled_at(na_dev, 1.0, 1.0)[None, :]
        )[:, :, None]
        * assembled_at(nb_dev, lead, trail)[None, None, :]
    )
    rows_ext = (tile_index * na_dev - 1 + jnp.arange(na_dev + 2, dtype=jnp.int32)) % (na_dev * tiles)
    row_points = (np.arange(na_dev + 2) - 1) % P_SIZE
    col_points = (np.arange(nb_dev + 2) - 1) % P_SIZE
    cols_ext = group_index * nb_dev - 1 + jnp.arange(nb_dev + 2, dtype=jnp.int32)

    def weight_at(index):
        return table_at(weights, index)

    surface_ext = diffusivity * weight_at(rows_ext)[:, None] * weight_at(cols_ext)[None, :]

    rows = radial_nodes * na_dev
    mats = derivative_tables(radial_nodes, na_dev, nb_dev)
    flat_mass = mass3.reshape(rows, nb_dev)
    flat_flow = flow.reshape(3, rows, nb_dev)

    angle = phases(wave_of_slot, tile_index * elems_a, elems_a, span, points)
    analysis = (
        jnp.stack([jnp.cos(angle), jnp.sin(angle)], axis=1)
        * (scale * weight_at(tile_index * na_dev + jnp.arange(na_dev, dtype=jnp.int32)))[
            None, None, :
        ]
    ).reshape(-1, na_dev)

    def owner_map(partial):
        partial = partial.reshape(-1, 2, nb_dev)
        gathered = lax.all_to_all(partial, both, 0, 0, tiled=True)
        coeff = gathered.reshape(tiles, groups, 2, nb_dev).sum(axis=0)
        coeff = coeff.transpose(1, 0, 2).reshape(2, nb)
        owned = coeff.astype(jnp.bfloat16)
        mapped = jnp.einsum(
            "pq,cq->cp", match_ops[0], owned, preferred_element_type=jnp.float32
        )
        edged = jnp.concatenate([mapped[:, :1], mapped, mapped[:, -1:]], axis=1)
        pieces = jnp.stack(
            [edged[:, g * nb_dev : g * nb_dev + nb_dev + 2] for g in range(groups)], axis=0
        )
        return jnp.broadcast_to(pieces[None], (tiles,) + pieces.shape).reshape(
            tiles, groups, 2 * (nb_dev + 2)
        )

    def flux_of(returned):
        angle = phases_at(wave_of_slot, rows_ext // P_SIZE, table_at(points, rows_ext), span)
        synth = jnp.stack([jnp.cos(angle).T, jnp.sin(angle).T], axis=2).reshape(na_dev + 2, -1)
        flux = -jnp.dot(synth, returned.reshape(-1, nb_dev + 2), precision=highest)
        return surface_ext * flux

    mapped_len = 2 * (nb_dev + 2)
    slot_len = 3 * radial_nodes * na_dev
    carried_halo = tiles >= 3 and groups >= 3 and tiles * groups <= 64

    def joint_exchange(sent, stacked, edge_rows, edge_cols):
        a_lo = edge_rows[0].reshape(3, radial_nodes, 1, nb_dev)
        a_hi = edge_rows[1].reshape(3, radial_nodes, 1, nb_dev)
        up = [(i, (i + 1) % tiles) for i in range(tiles)]
        down = [(j, i) for i, j in up]
        from_up = lax.ppermute(a_hi, "tile", up)
        from_down = lax.ppermute(a_lo, "tile", down)
        b_lo = edge_cols[0:1]
        b_hi = edge_cols[1:2]
        out_pieces = [
            ((0, 1), b_hi),
            ((0, -1), b_lo),
            ((1, 1), b_hi),
            ((1, -1), b_lo),
            ((-1, 1), b_hi),
            ((-1, -1), b_lo),
        ]
        slots = jnp.zeros((tiles * groups, 1, slot_len), jnp.float32)
        for (dt, dg), flat in out_pieces:
            target = ((tile_index + dt) % tiles) * groups + (group_index + dg) % groups
            slots = lax.dynamic_update_slice(slots, flat, (target, 0, 0))
        message = jnp.concatenate([sent.reshape(tiles * groups, 1, -1), slots], axis=2)
        received = lax.all_to_all(message, both, 0, 0, tiled=True)
        returned = received[:, 0, :mapped_len].reshape(tiles * groups, 2, nb_dev + 2)

        def take(dt, dg):
            source = ((tile_index - dt) % tiles) * groups + (group_index - dg) % groups
            row = lax.dynamic_slice(received, (source, 0, mapped_len), (1, 1, slot_len))
            return row.reshape(3, radial_nodes, na_dev, 1)

        from_left = take(0, 1)
        from_right = take(0, -1)
        corner_ul = take(1, 1)[:, :, na_dev - 1 :, :]
        corner_ur = take(1, -1)[:, :, na_dev - 1 :, :]
        corner_dl = take(-1, 1)[:, :, :1, :]
        corner_dr = take(-1, -1)[:, :, :1, :]
        top = jnp.concatenate([corner_ul, from_up, corner_ur], axis=3)
        middle = jnp.concatenate([from_left, stacked, from_right], axis=3)
        bottom = jnp.concatenate([corner_dl, from_down, corner_dr], axis=3)
        return returned, jnp.concatenate([top, middle, bottom], axis=2)

    def halo(stacked):
        a_lo = lax.slice_in_dim(stacked, 0, 1, axis=2)
        a_hi = lax.slice_in_dim(stacked, na_dev - 1, na_dev, axis=2)
        b_lo = lax.slice_in_dim(stacked, 0, 1, axis=3)
        b_hi = lax.slice_in_dim(stacked, nb_dev - 1, nb_dev, axis=3)
        sizes = (tiles, groups)
        from_up = lax.ppermute(a_hi, both, shift_pairs(sizes, (1, 0)))
        from_down = lax.ppermute(a_lo, both, shift_pairs(sizes, (-1, 0)))
        from_left = lax.ppermute(b_hi, both, shift_pairs(sizes, (0, 1)))
        from_right = lax.ppermute(b_lo, both, shift_pairs(sizes, (0, -1)))
        corner_ul = lax.ppermute(a_hi[:, :, :, -1:], both, shift_pairs(sizes, (1, 1)))
        corner_ur = lax.ppermute(a_hi[:, :, :, :1], both, shift_pairs(sizes, (1, -1)))
        corner_dl = lax.ppermute(a_lo[:, :, :, -1:], both, shift_pairs(sizes, (-1, 1)))
        corner_dr = lax.ppermute(a_lo[:, :, :, :1], both, shift_pairs(sizes, (-1, -1)))
        top = jnp.concatenate([corner_ul, from_up, corner_ur], axis=3)
        middle = jnp.concatenate([from_left, stacked, from_right], axis=3)
        bottom = jnp.concatenate([corner_dl, from_down, corner_dr], axis=3)
        return jnp.concatenate([top, middle, bottom], axis=2)

    join_b = np.zeros((nb_dev + 2, nb_dev), np.float32)
    join_b[np.arange(nb_dev) + 1, np.arange(nb_dev)] = 1.0
    inner_first = np.arange(P_SIZE, nb_dev, P_SIZE)
    join_b[inner_first, inner_first] = 1.0
    inner_last = np.arange(P_SIZE - 1, nb_dev - 1, P_SIZE)
    join_b[inner_last + 2, inner_last] = 1.0
    edge_lead = np.zeros((nb_dev + 2, nb_dev), np.float32)
    edge_lead[0, 0] = 1.0
    edge_trail = np.zeros((nb_dev + 2, nb_dev), np.float32)
    edge_trail[nb_dev + 1, nb_dev - 1] = 1.0
    join_b = join_b + lead * edge_lead + trail * edge_trail

    mask_shape = (3, radial_nodes, 1, 1)
    outer_index = radial_nodes - 1 + jnp.minimum(tile_index, 0)
    plane_mask = jnp.where(
        (lax.broadcasted_iota(jnp.int32, mask_shape, 0) == 0)
        & (lax.broadcasted_iota(jnp.int32, mask_shape, 1) == outer_index),
        1.0,
        0.0,
    )

    def assemble_ext(padded):
        last = padded.ndim - 1
        along_a = assemble_dim(
            padded[..., 1:-1, :], last - 1, padded[..., 0:1, :], padded[..., -1:, :]
        )
        return jnp.dot(along_a, join_b, precision=highest)

    shapes = (
        jax.ShapeDtypeStruct((3, rows, nb_dev), jnp.float32),
        jax.ShapeDtypeStruct((2, 3, radial_nodes, nb_dev), jnp.float32),
        jax.ShapeDtypeStruct((2, 1, 3 * rows), jnp.float32),
    )
    first_outs = pl.pallas_call(
        first_volume_kernel,
        out_shape=shapes
        + (
            jax.ShapeDtypeStruct(analysis.shape[:1] + (nb_dev,), jnp.float32),
            jax.ShapeDtypeStruct((9, rows, nb_dev), jnp.float32),
        ),
    )(field.reshape(3, rows, nb_dev), flat_flow, mats, flat_mass, analysis)
    grads = first_outs[4]

    def tendency(parts, surface):
        if surface is None:
            stacked, edge_rows, edge_cols, partial = first_outs[:4]
        else:
            stacked, edge_rows, edge_cols = pl.pallas_call(volume_kernel, out_shape=shapes)(
                parts.reshape(3, rows, nb_dev), flat_flow, grads, mats, flat_mass
            )
            partial = jnp.dot(analysis, surface, precision=highest)
        stacked = stacked.reshape(parts.shape)
        sent = owner_map(partial)
        if carried_halo:
            returned, padded = joint_exchange(sent, stacked, edge_rows, edge_cols)
        else:
            returned = lax.all_to_all(
                sent.reshape(tiles * groups, -1), both, 0, 0, tiled=True
            ).reshape(tiles * groups, 2, nb_dev + 2)
            padded = halo(stacked)
        flux_term = flux_of(returned)
        outer = padded[0, radial_nodes - 1] + flux_term
        outer_rate = assemble_ext(outer) / assembled[radial_nodes - 1]
        padded = padded + plane_mask * flux_term
        plane_r = jnp.zeros_like(lax.slice_in_dim(padded, 0, 1, axis=1))
        padded = assemble_dim(padded, 1, plane_r, plane_r)
        return assemble_ext(padded) / assembled[None], outer_rate

    first_rate, first_outer = tendency(field, None)
    section = field + time_step * first_rate
    section_outer = field[0, radial_nodes - 1] + time_step * first_outer
    second_rate, _ = tendency(section, section_outer)
    return 0.5 * (field + section + time_step * second_rate)


def solution(mesh):
    placed = (
        P(None, None, "tile", "deg"),
        P(None, None, "tile", "deg"),
        P(("tile", "deg"), None, None),
        P(),
    )
    return jax.shard_map(
        local, mesh=mesh, in_specs=placed, out_specs=P(None, None, "tile", "deg"), check_vma=False
    )
```

```python
import math

import numpy as np
import jax
import jax.numpy as jnp
from jax import lax
from jax.sharding import PartitionSpec as P
from jax.experimental import pallas as pl

P_SIZE = 8


diffusivity = 0.05
time_step = 0.01
highest = lax.Precision.HIGHEST
gll_interior = [0.2092992179024789, 0.5917001814331423, 0.8717401485096066]


def padded_2(value, sides, width):
    for axis, dim in sides:
        size, length = (lax.axis_size(axis), value.shape[dim])
        up = [(i, (i + 1) % size) for i in range(size)]
        down = [(j, i) for i, j in up]
        last = lax.slice_in_dim(value, length - width, length, axis=dim)
        first = lax.slice_in_dim(value, 0, width, axis=dim)
        before = lax.ppermute(last, axis, up)
        after = lax.ppermute(first, axis, down)
        value = jnp.concatenate([before, value, after], axis=dim)
    return value


def product(a, b):
    return jnp.dot(a, b, precision=lax.Precision.HIGH, preferred_element_type=jnp.float32)


def gradient_kernel(flow_ref, mats_ref, out_ref):
    for component in range(3):
        x = flow_ref[component]
        out_ref[3 * component] = product(mats_ref[0], x)
        out_ref[3 * component + 1] = product(mats_ref[1], x)
        out_ref[3 * component + 2] = product(x, mats_ref[2])


def volume_kernel(parts_ref, flow_ref, grad_ref, mats_ref, mass_ref, *outs):
    volume_body(parts_ref, flow_ref, grad_ref, mats_ref, mass_ref, *outs)


def first_volume_kernel(parts_ref, flow_ref, mats_ref, mass_ref, table_ref, *outs):
    grad_ref = outs[4]
    gradient_kernel(flow_ref, mats_ref, grad_ref)
    volume_body(parts_ref, flow_ref, grad_ref, mats_ref, mass_ref, *outs[:3])
    depth = outs[0].shape[1] // outs[1].shape[2]
    surface = parts_ref[0, pl.ds(outs[0].shape[1] - depth, depth), :]
    outs[3][...] = product(table_ref[...], surface)


def volume_body(parts_ref, flow_ref, grad_ref, mats_ref, mass_ref, out_ref, rows_ref, cols_ref):
    mass = mass_ref[...]
    p = [parts_ref[i] for i in range(3)]
    f = [flow_ref[i] for i in range(3)]
    planes = out_ref.shape[1] // rows_ref.shape[2]
    width = out_ref.shape[2]
    for c in range(3):
        x = p[c]
        s0 = product(mats_ref[0], x)
        s1 = product(mats_ref[1], x)
        s2 = product(x, mats_ref[2])
        stretch = p[0] * grad_ref[3 * c] + p[1] * grad_ref[3 * c + 1] + p[2] * grad_ref[3 * c + 2]
        carried = f[0] * s0 + f[1] * s1 + f[2] * s2
        spread = (
            product(mats_ref[3], mass * s0)
            + product(mats_ref[4], mass * s1)
            + product(mass * s2, mats_ref[5])
        )
        result = mass * (stretch - carried) - diffusivity * spread
        out_ref[c] = result
        turned = result.T
        span_of = out_ref.shape[1]
        cols_ref[0, :, c * span_of : (c + 1) * span_of] = turned[0:1, :]
        cols_ref[1, :, c * span_of : (c + 1) * span_of] = turned[width - 1 : width, :]
    for c in range(3):
        rows_ref[0, c] = out_ref[c, pl.ds(0, rows_ref.shape[2], stride=planes), :]
        rows_ref[1, c] = out_ref[c, pl.ds(planes - 1, rows_ref.shape[2], stride=planes), :]


def derivative_tables(radial_nodes, na_dev, nb_dev):
    _, _, matrix_list = gll_tables(P_SIZE)
    dmat = np.asarray(matrix_list, np.float32)
    radial = np.kron(dmat, np.eye(na_dev, dtype=np.float32))
    first = np.kron(np.eye(radial_nodes * na_dev // P_SIZE, dtype=np.float32), dmat)
    second = np.kron(np.eye(nb_dev // P_SIZE, dtype=np.float32), dmat)
    return jnp.asarray(np.stack([radial, first, second.T, radial.T, first.T, second]))


def legendre_value(point, degree):
    previous = 1.0
    current = point
    for order in range(1, degree):
        following = ((2 * order + 1) * point * current - order * previous) / (order + 1)
        previous = current
        current = following
    return current


def gll_tables(count):
    degree = count - 1
    points = [-1.0] + [-value for value in reversed(gll_interior)] + list(gll_interior) + [1.0]
    values = [legendre_value(point, degree) for point in points]
    weights = [2.0 / (degree * (degree + 1) * value * value) for value in values]
    matrix = [
        [
            values[row] / (values[col] * (points[row] - points[col])) if row != col else 0.0
            for col in range(count)
        ]
        for row in range(count)
    ]
    matrix[0][0] = -degree * (degree + 1) / 4.0
    matrix[count - 1][count - 1] = degree * (degree + 1) / 4.0
    return (points, weights, matrix)


def apply_along(values, axis_pos, matrix):
    shape = values.shape
    blocks = values.reshape(
        shape[:axis_pos] + (shape[axis_pos] // P_SIZE, P_SIZE) + shape[axis_pos + 1 :]
    )
    letters = list("abcdefg"[: blocks.ndim])
    source = list(letters)
    source[axis_pos + 1] = "p"
    target = list(letters)
    target[axis_pos + 1] = "q"
    formula = "".join(source) + ",qp->" + "".join(target)
    return jnp.einsum(formula, blocks, matrix, precision=highest).reshape(shape)


def assemble_dim(values, axis_pos, left, right):
    shape = values.shape
    count = shape[axis_pos] // P_SIZE
    blocks = values.reshape(shape[:axis_pos] + (count, P_SIZE) + shape[axis_pos + 1 :])
    edge_shape = shape[:axis_pos] + (1, 1) + shape[axis_pos + 1 :]
    first = lax.slice_in_dim(blocks, 0, 1, axis=axis_pos + 1)
    last = lax.slice_in_dim(blocks, P_SIZE - 1, P_SIZE, axis=axis_pos + 1)
    before = jnp.concatenate(
        [left.reshape(edge_shape), lax.slice_in_dim(last, 0, count - 1, axis=axis_pos)],
        axis=axis_pos,
    )
    after = jnp.concatenate(
        [lax.slice_in_dim(first, 1, count, axis=axis_pos), right.reshape(edge_shape)], axis=axis_pos
    )
    middle = lax.slice_in_dim(blocks, 1, P_SIZE - 1, axis=axis_pos + 1)
    joined = jnp.concatenate([first + before, middle, last + after], axis=axis_pos + 1)
    return joined.reshape(shape)


def assembled_weights(weights, count, lead, trail):
    position = jnp.arange(count * P_SIZE, dtype=jnp.int32)
    local_point = position % P_SIZE
    element = position // P_SIZE
    base = jnp.tile(weights, count)
    starts = (
        jnp.where(local_point == 0, jnp.where(element > 0, 1.0, lead), 0.0) * weights[P_SIZE - 1]
    )
    ends = (
        jnp.where(local_point == P_SIZE - 1, jnp.where(element < count - 1, 1.0, trail), 0.0)
        * weights[0]
    )
    return base + starts + ends


def static_assembled(weights, count, lead, trail):
    position = np.arange(count * P_SIZE)
    local_point = position % P_SIZE
    element = position // P_SIZE
    starts = np.where(local_point == 0, np.where(element > 0, 1.0, lead), 0.0) * weights[P_SIZE - 1]
    ends = np.where(local_point == P_SIZE - 1, np.where(element < count - 1, 1.0, trail), 0.0)
    return (np.tile(weights, count) + starts + ends * weights[0]).astype(np.float32)


def table_at(values, index):
    point = index % P_SIZE
    total = jnp.zeros(index.shape, jnp.float32)
    for p in range(P_SIZE):
        total = total + jnp.where(point == p, float(values[p]), 0.0)
    return total


def phases(waves, elem_start, elem_count, span, points):
    position = elem_start * P_SIZE + jnp.arange(elem_count * P_SIZE, dtype=jnp.int32)
    element = position // P_SIZE
    whole = waves[:, None] * (2 * element + 1)[None, :] % span
    fraction = waves.astype(jnp.float32)[:, None] * table_at(points, position)[None, :]
    return 2.0 * math.pi / span * (whole.astype(jnp.float32) + fraction)


def phases_at(waves, element, point_values, span):
    whole = waves[:, None] * (2 * element + 1)[None, :] % span
    fraction = waves.astype(jnp.float32)[:, None] * point_values[None, :]
    return 2.0 * math.pi / span * (whole.astype(jnp.float32) + fraction)


def shift_pairs(sizes, steps):
    count = sizes[0] * sizes[1]
    pairs = []
    for source in range(count):
        t, g = divmod(source, sizes[1])
        target = ((t + steps[0]) % sizes[0]) * sizes[1] + (g + steps[1]) % sizes[1]
        pairs.append((source, target))
    return pairs


def local(field, flow, match_ops, wave_of_slot):
    tiles = lax.axis_size("tile")
    groups = lax.axis_size("deg")
    both = ("tile", "deg")
    tile_index = lax.axis_index("tile")
    group_index = lax.axis_index("deg")
    radial_nodes = field.shape[1]
    na_dev = field.shape[2]
    nb_dev = field.shape[3]
    elems_a = na_dev // P_SIZE
    elems_b = nb_dev // P_SIZE
    nb = nb_dev * groups
    span = 2 * elems_a * tiles
    scale = P_SIZE / (na_dev * tiles)
    points_list, weights_list, _ = gll_tables(P_SIZE)
    points = np.asarray(points_list, np.float32)
    weights = np.asarray(weights_list, np.float32)
    lead = (group_index > 0).astype(jnp.float32)
    trail = (group_index < groups - 1).astype(jnp.float32)
    w_r = np.tile(weights, radial_nodes // P_SIZE)
    w_a = np.tile(weights, elems_a)
    w_b = np.tile(weights, elems_b)
    mass3 = w_r[:, None, None] * w_a[None, :, None] * w_b[None, None, :]
    origin = jnp.minimum(tile_index, 0)

    def assembled_at(length, lead_value, trail_value):
        position = origin + jnp.arange(length, dtype=jnp.int32)
        local_point = position % P_SIZE
        element = position // P_SIZE
        count = length // P_SIZE
        starts = jnp.where(
            local_point == 0, jnp.where(element > 0, 1.0, lead_value), 0.0
        ) * float(weights[P_SIZE - 1])
        ends = jnp.where(
            local_point == P_SIZE - 1, jnp.where(element < count - 1, 1.0, trail_value), 0.0
        ) * float(weights[0])
        return table_at(weights, position) + starts + ends

    assembled = (
        (
            assembled_at(radial_nodes, 0.0, 0.0)[:, None]
            * assembled_at(na_dev, 1.0, 1.0)[None, :]
        )[:, :, None]
        * assembled_at(nb_dev, lead, trail)[None, None, :]
    )
    rows_ext = (tile_index * na_dev - 1 + jnp.arange(na_dev + 2, dtype=jnp.int32)) % (na_dev * tiles)
    row_points = (np.arange(na_dev + 2) - 1) % P_SIZE
    col_points = (np.arange(nb_dev + 2) - 1) % P_SIZE
    cols_ext = group_index * nb_dev - 1 + jnp.arange(nb_dev + 2, dtype=jnp.int32)

    def weight_at(index):
        return table_at(weights, index)

    surface_ext = diffusivity * weight_at(rows_ext)[:, None] * weight_at(cols_ext)[None, :]

    rows = radial_nodes * na_dev
    mats = derivative_tables(radial_nodes, na_dev, nb_dev)
    flat_mass = mass3.reshape(rows, nb_dev)
    flat_flow = flow.reshape(3, rows, nb_dev)

    angle = phases(wave_of_slot, tile_index * elems_a, elems_a, span, points)
    analysis = (
        jnp.stack([jnp.cos(angle), jnp.sin(angle)], axis=1)
        * (scale * weight_at(tile_index * na_dev + jnp.arange(na_dev, dtype=jnp.int32)))[
            None, None, :
        ]
    ).reshape(-1, na_dev)

    def owner_map(partial):
        partial = partial.reshape(-1, 2, nb_dev)
        gathered = lax.all_to_all(partial, both, 0, 0, tiled=True)
        coeff = gathered.reshape(tiles, groups, 2, nb_dev).sum(axis=0)
        coeff = coeff.transpose(1, 0, 2).reshape(2, nb)
        owned = coeff.astype(jnp.bfloat16)
        mapped = jnp.einsum(
            "pq,cq->cp", match_ops[0], owned, preferred_element_type=jnp.float32
        )
        edged = jnp.concatenate([mapped[:, :1], mapped, mapped[:, -1:]], axis=1)
        pieces = jnp.stack(
            [edged[:, g * nb_dev : g * nb_dev + nb_dev + 2] for g in range(groups)], axis=0
        )
        return jnp.broadcast_to(pieces[None], (tiles,) + pieces.shape).reshape(
            tiles, groups, 2 * (nb_dev + 2)
        )

    def flux_of(returned):
        angle = phases_at(wave_of_slot, rows_ext // P_SIZE, table_at(points, rows_ext), span)
        synth = jnp.stack([jnp.cos(angle).T, jnp.sin(angle).T], axis=2).reshape(na_dev + 2, -1)
        flux = -jnp.dot(synth, returned.reshape(-1, nb_dev + 2), precision=highest)
        return surface_ext * flux

    mapped_len = 2 * (nb_dev + 2)
    slot_len = 3 * radial_nodes * na_dev
    carried_halo = tiles >= 3 and groups >= 3 and tiles * groups <= 64

    def joint_exchange(sent, stacked, edge_rows, edge_cols):
        a_lo = edge_rows[0].reshape(3, radial_nodes, 1, nb_dev)
        a_hi = edge_rows[1].reshape(3, radial_nodes, 1, nb_dev)
        up = [(i, (i + 1) % tiles) for i in range(tiles)]
        down = [(j, i) for i, j in up]
        from_up = lax.ppermute(a_hi, "tile", up)
        from_down = lax.ppermute(a_lo, "tile", down)
        b_lo = edge_cols[0:1]
        b_hi = edge_cols[1:2]
        out_pieces = [
            ((0, 1), b_hi),
            ((0, -1), b_lo),
            ((1, 1), b_hi),
            ((1, -1), b_lo),
            ((-1, 1), b_hi),
            ((-1, -1), b_lo),
        ]
        slots = jnp.zeros((tiles * groups, 1, slot_len), jnp.float32)
        for (dt, dg), flat in out_pieces:
            target = ((tile_index + dt) % tiles) * groups + (group_index + dg) % groups
            slots = lax.dynamic_update_slice(slots, flat, (target, 0, 0))
        message = jnp.concatenate([sent.reshape(tiles * groups, 1, -1), slots], axis=2)
        received = lax.all_to_all(message, both, 0, 0, tiled=True)
        returned = received[:, 0, :mapped_len].reshape(tiles * groups, 2, nb_dev + 2)

        def take(dt, dg):
            source = ((tile_index - dt) % tiles) * groups + (group_index - dg) % groups
            row = lax.dynamic_slice(received, (source, 0, mapped_len), (1, 1, slot_len))
            return row.reshape(3, radial_nodes, na_dev, 1)

        from_left = take(0, 1)
        from_right = take(0, -1)
        corner_ul = take(1, 1)[:, :, na_dev - 1 :, :]
        corner_ur = take(1, -1)[:, :, na_dev - 1 :, :]
        corner_dl = take(-1, 1)[:, :, :1, :]
        corner_dr = take(-1, -1)[:, :, :1, :]
        top = jnp.concatenate([corner_ul, from_up, corner_ur], axis=3)
        middle = jnp.concatenate([from_left, stacked, from_right], axis=3)
        bottom = jnp.concatenate([corner_dl, from_down, corner_dr], axis=3)
        return returned, jnp.concatenate([top, middle, bottom], axis=2)

    def halo(stacked):
        a_lo = lax.slice_in_dim(stacked, 0, 1, axis=2)
        a_hi = lax.slice_in_dim(stacked, na_dev - 1, na_dev, axis=2)
        b_lo = lax.slice_in_dim(stacked, 0, 1, axis=3)
        b_hi = lax.slice_in_dim(stacked, nb_dev - 1, nb_dev, axis=3)
        sizes = (tiles, groups)
        from_up = lax.ppermute(a_hi, both, shift_pairs(sizes, (1, 0)))
        from_down = lax.ppermute(a_lo, both, shift_pairs(sizes, (-1, 0)))
        from_left = lax.ppermute(b_hi, both, shift_pairs(sizes, (0, 1)))
        from_right = lax.ppermute(b_lo, both, shift_pairs(sizes, (0, -1)))
        corner_ul = lax.ppermute(a_hi[:, :, :, -1:], both, shift_pairs(sizes, (1, 1)))
        corner_ur = lax.ppermute(a_hi[:, :, :, :1], both, shift_pairs(sizes, (1, -1)))
        corner_dl = lax.ppermute(a_lo[:, :, :, -1:], both, shift_pairs(sizes, (-1, 1)))
        corner_dr = lax.ppermute(a_lo[:, :, :, :1], both, shift_pairs(sizes, (-1, -1)))
        top = jnp.concatenate([corner_ul, from_up, corner_ur], axis=3)
        middle = jnp.concatenate([from_left, stacked, from_right], axis=3)
        bottom = jnp.concatenate([corner_dl, from_down, corner_dr], axis=3)
        return jnp.concatenate([top, middle, bottom], axis=2)

    join_b = np.zeros((nb_dev + 2, nb_dev), np.float32)
    join_b[np.arange(nb_dev) + 1, np.arange(nb_dev)] = 1.0
    inner_first = np.arange(P_SIZE, nb_dev, P_SIZE)
    join_b[inner_first, inner_first] = 1.0
    inner_last = np.arange(P_SIZE - 1, nb_dev - 1, P_SIZE)
    join_b[inner_last + 2, inner_last] = 1.0
    edge_lead = np.zeros((nb_dev + 2, nb_dev), np.float32)
    edge_lead[0, 0] = 1.0
    edge_trail = np.zeros((nb_dev + 2, nb_dev), np.float32)
    edge_trail[nb_dev + 1, nb_dev - 1] = 1.0
    join_b = join_b + lead * edge_lead + trail * edge_trail

    mask_shape = (3, radial_nodes, 1, 1)
    outer_index = radial_nodes - 1 + jnp.minimum(tile_index, 0)
    plane_mask = jnp.where(
        (lax.broadcasted_iota(jnp.int32, mask_shape, 0) == 0)
        & (lax.broadcasted_iota(jnp.int32, mask_shape, 1) == outer_index),
        1.0,
        0.0,
    )

    def assemble_ext(padded):
        last = padded.ndim - 1
        along_a = assemble_dim(
            padded[..., 1:-1, :], last - 1, padded[..., 0:1, :], padded[..., -1:, :]
        )
        return jnp.dot(along_a, join_b, precision=highest)

    shapes = (
        jax.ShapeDtypeStruct((3, rows, nb_dev), jnp.float32),
        jax.ShapeDtypeStruct((2, 3, radial_nodes, nb_dev), jnp.float32),
        jax.ShapeDtypeStruct((2, 1, 3 * rows), jnp.float32),
    )
    first_outs = pl.pallas_call(
        first_volume_kernel,
        out_shape=shapes
        + (
            jax.ShapeDtypeStruct(analysis.shape[:1] + (nb_dev,), jnp.float32),
            jax.ShapeDtypeStruct((9, rows, nb_dev), jnp.float32),
        ),
    )(field.reshape(3, rows, nb_dev), flat_flow, mats, flat_mass, analysis)
    grads = first_outs[4]

    def tendency(parts, surface):
        if surface is None:
            stacked, edge_rows, edge_cols, partial = first_outs[:4]
        else:
            stacked, edge_rows, edge_cols = pl.pallas_call(volume_kernel, out_shape=shapes)(
                parts.reshape(3, rows, nb_dev), flat_flow, grads, mats, flat_mass
            )
            partial = jnp.dot(analysis, surface, precision=highest)
        stacked = stacked.reshape(parts.shape)
        sent = owner_map(partial)
        if carried_halo:
            returned, padded = joint_exchange(sent, stacked, edge_rows, edge_cols)
        else:
            returned = lax.all_to_all(
                sent.reshape(tiles * groups, -1), both, 0, 0, tiled=True
            ).reshape(tiles * groups, 2, nb_dev + 2)
            padded = halo(stacked)
        flux_term = flux_of(returned)
        outer = padded[0, radial_nodes - 1] + flux_term
        outer_rate = assemble_ext(outer) / assembled[radial_nodes - 1]
        padded = padded + plane_mask * flux_term
        plane_r = jnp.zeros_like(lax.slice_in_dim(padded, 0, 1, axis=1))
        padded = assemble_dim(padded, 1, plane_r, plane_r)
        return assemble_ext(padded) / assembled[None], outer_rate

    first_rate, first_outer = tendency(field, None)
    section = field + time_step * first_rate
    section_outer = field[0, radial_nodes - 1] + time_step * first_outer
    second_rate, _ = tendency(section, section_outer)
    return 0.5 * (field + section + time_step * second_rate)


def solution(mesh):
    placed = (
        P(None, None, "tile", "deg"),
        P(None, None, "tile", "deg"),
        P(("tile", "deg"), None, None),
        P(),
    )
    return jax.shard_map(
        local, mesh=mesh, in_specs=placed, out_specs=P(None, None, "tile", "deg"), check_vma=False
    )
```

```python
import math

import numpy as np
import jax
import jax.numpy as jnp
from jax import lax
from jax.sharding import PartitionSpec as P
from jax.experimental import pallas as pl

P_SIZE = 8


diffusivity = 0.05
time_step = 0.01
highest = lax.Precision.HIGHEST
gll_interior = [0.2092992179024789, 0.5917001814331423, 0.8717401485096066]


def padded_2(value, sides, width):
    for axis, dim in sides:
        size, length = (lax.axis_size(axis), value.shape[dim])
        up = [(i, (i + 1) % size) for i in range(size)]
        down = [(j, i) for i, j in up]
        last = lax.slice_in_dim(value, length - width, length, axis=dim)
        first = lax.slice_in_dim(value, 0, width, axis=dim)
        before = lax.ppermute(last, axis, up)
        after = lax.ppermute(first, axis, down)
        value = jnp.concatenate([before, value, after], axis=dim)
    return value


def product(a, b):
    return jnp.dot(a, b, precision=lax.Precision.HIGH, preferred_element_type=jnp.float32)


def gradient_kernel(flow_ref, mats_ref, out_ref):
    for component in range(3):
        x = flow_ref[component]
        out_ref[3 * component] = product(mats_ref[0], x)
        out_ref[3 * component + 1] = product(mats_ref[1], x)
        out_ref[3 * component + 2] = product(x, mats_ref[2])


def volume_kernel(parts_ref, flow_ref, grad_ref, mats_ref, mass_ref, *outs):
    volume_body(parts_ref, flow_ref, grad_ref, mats_ref, mass_ref, *outs)


def first_volume_kernel(parts_ref, flow_ref, mats_ref, mass_ref, table_ref, *outs):
    grad_ref = outs[4]
    gradient_kernel(flow_ref, mats_ref, grad_ref)
    volume_body(parts_ref, flow_ref, grad_ref, mats_ref, mass_ref, *outs[:3])
    depth = outs[0].shape[1] // outs[1].shape[2]
    surface = parts_ref[0, pl.ds(outs[0].shape[1] - depth, depth), :]
    outs[3][...] = product(table_ref[...], surface)


def volume_body(parts_ref, flow_ref, grad_ref, mats_ref, mass_ref, out_ref, rows_ref, cols_ref):
    mass = mass_ref[...]
    p = [parts_ref[i] for i in range(3)]
    f = [flow_ref[i] for i in range(3)]
    planes = out_ref.shape[1] // rows_ref.shape[2]
    width = out_ref.shape[2]
    for c in range(3):
        x = p[c]
        s0 = product(mats_ref[0], x)
        s1 = product(mats_ref[1], x)
        s2 = product(x, mats_ref[2])
        stretch = p[0] * grad_ref[3 * c] + p[1] * grad_ref[3 * c + 1] + p[2] * grad_ref[3 * c + 2]
        carried = f[0] * s0 + f[1] * s1 + f[2] * s2
        spread = (
            product(mats_ref[3], mass * s0)
            + product(mats_ref[4], mass * s1)
            + product(mass * s2, mats_ref[5])
        )
        result = mass * (stretch - carried) - diffusivity * spread
        out_ref[c] = result
        turned = result.T
        span_of = out_ref.shape[1]
        cols_ref[0, :, c * span_of : (c + 1) * span_of] = turned[0:1, :]
        cols_ref[1, :, c * span_of : (c + 1) * span_of] = turned[width - 1 : width, :]
    for c in range(3):
        rows_ref[0, c] = out_ref[c, pl.ds(0, rows_ref.shape[2], stride=planes), :]
        rows_ref[1, c] = out_ref[c, pl.ds(planes - 1, rows_ref.shape[2], stride=planes), :]


def derivative_tables(radial_nodes, na_dev, nb_dev):
    _, _, matrix_list = gll_tables(P_SIZE)
    dmat = np.asarray(matrix_list, np.float32)
    radial = np.kron(dmat, np.eye(na_dev, dtype=np.float32))
    first = np.kron(np.eye(radial_nodes * na_dev // P_SIZE, dtype=np.float32), dmat)
    second = np.kron(np.eye(nb_dev // P_SIZE, dtype=np.float32), dmat)
    return jnp.asarray(np.stack([radial, first, second.T, radial.T, first.T, second]))


def legendre_value(point, degree):
    previous = 1.0
    current = point
    for order in range(1, degree):
        following = ((2 * order + 1) * point * current - order * previous) / (order + 1)
        previous = current
        current = following
    return current


def gll_tables(count):
    degree = count - 1
    points = [-1.0] + [-value for value in reversed(gll_interior)] + list(gll_interior) + [1.0]
    values = [legendre_value(point, degree) for point in points]
    weights = [2.0 / (degree * (degree + 1) * value * value) for value in values]
    matrix = [
        [
            values[row] / (values[col] * (points[row] - points[col])) if row != col else 0.0
            for col in range(count)
        ]
        for row in range(count)
    ]
    matrix[0][0] = -degree * (degree + 1) / 4.0
    matrix[count - 1][count - 1] = degree * (degree + 1) / 4.0
    return (points, weights, matrix)


def apply_along(values, axis_pos, matrix):
    shape = values.shape
    blocks = values.reshape(
        shape[:axis_pos] + (shape[axis_pos] // P_SIZE, P_SIZE) + shape[axis_pos + 1 :]
    )
    letters = list("abcdefg"[: blocks.ndim])
    source = list(letters)
    source[axis_pos + 1] = "p"
    target = list(letters)
    target[axis_pos + 1] = "q"
    formula = "".join(source) + ",qp->" + "".join(target)
    return jnp.einsum(formula, blocks, matrix, precision=highest).reshape(shape)


def assemble_dim(values, axis_pos, left, right):
    shape = values.shape
    count = shape[axis_pos] // P_SIZE
    blocks = values.reshape(shape[:axis_pos] + (count, P_SIZE) + shape[axis_pos + 1 :])
    edge_shape = shape[:axis_pos] + (1, 1) + shape[axis_pos + 1 :]
    first = lax.slice_in_dim(blocks, 0, 1, axis=axis_pos + 1)
    last = lax.slice_in_dim(blocks, P_SIZE - 1, P_SIZE, axis=axis_pos + 1)
    before = jnp.concatenate(
        [left.reshape(edge_shape), lax.slice_in_dim(last, 0, count - 1, axis=axis_pos)],
        axis=axis_pos,
    )
    after = jnp.concatenate(
        [lax.slice_in_dim(first, 1, count, axis=axis_pos), right.reshape(edge_shape)], axis=axis_pos
    )
    middle = lax.slice_in_dim(blocks, 1, P_SIZE - 1, axis=axis_pos + 1)
    joined = jnp.concatenate([first + before, middle, last + after], axis=axis_pos + 1)
    return joined.reshape(shape)


def assembled_weights(weights, count, lead, trail):
    position = jnp.arange(count * P_SIZE, dtype=jnp.int32)
    local_point = position % P_SIZE
    element = position // P_SIZE
    base = jnp.tile(weights, count)
    starts = (
        jnp.where(local_point == 0, jnp.where(element > 0, 1.0, lead), 0.0) * weights[P_SIZE - 1]
    )
    ends = (
        jnp.where(local_point == P_SIZE - 1, jnp.where(element < count - 1, 1.0, trail), 0.0)
        * weights[0]
    )
    return base + starts + ends


def static_assembled(weights, count, lead, trail):
    position = np.arange(count * P_SIZE)
    local_point = position % P_SIZE
    element = position // P_SIZE
    starts = np.where(local_point == 0, np.where(element > 0, 1.0, lead), 0.0) * weights[P_SIZE - 1]
    ends = np.where(local_point == P_SIZE - 1, np.where(element < count - 1, 1.0, trail), 0.0)
    return (np.tile(weights, count) + starts + ends * weights[0]).astype(np.float32)


def table_at(values, index):
    point = index % P_SIZE
    total = jnp.zeros(index.shape, jnp.float32)
    for p in range(P_SIZE):
        total = total + jnp.where(point == p, float(values[p]), 0.0)
    return total


def phases(waves, elem_start, elem_count, span, points):
    position = elem_start * P_SIZE + jnp.arange(elem_count * P_SIZE, dtype=jnp.int32)
    element = position // P_SIZE
    whole = waves[:, None] * (2 * element + 1)[None, :] % span
    fraction = waves.astype(jnp.float32)[:, None] * table_at(points, position)[None, :]
    return 2.0 * math.pi / span * (whole.astype(jnp.float32) + fraction)


def phases_at(waves, element, point_values, span):
    whole = waves[:, None] * (2 * element + 1)[None, :] % span
    fraction = waves.astype(jnp.float32)[:, None] * point_values[None, :]
    return 2.0 * math.pi / span * (whole.astype(jnp.float32) + fraction)


def shift_pairs(sizes, steps):
    count = sizes[0] * sizes[1]
    pairs = []
    for source in range(count):
        t, g = divmod(source, sizes[1])
        target = ((t + steps[0]) % sizes[0]) * sizes[1] + (g + steps[1]) % sizes[1]
        pairs.append((source, target))
    return pairs


def local(field, flow, match_ops, wave_of_slot):
    tiles = lax.axis_size("tile")
    groups = lax.axis_size("deg")
    both = ("tile", "deg")
    tile_index = lax.axis_index("tile")
    group_index = lax.axis_index("deg")
    radial_nodes = field.shape[1]
    na_dev = field.shape[2]
    nb_dev = field.shape[3]
    elems_a = na_dev // P_SIZE
    elems_b = nb_dev // P_SIZE
    nb = nb_dev * groups
    span = 2 * elems_a * tiles
    scale = P_SIZE / (na_dev * tiles)
    points_list, weights_list, _ = gll_tables(P_SIZE)
    points = np.asarray(points_list, np.float32)
    weights = np.asarray(weights_list, np.float32)
    lead = (group_index > 0).astype(jnp.float32)
    trail = (group_index < groups - 1).astype(jnp.float32)
    w_r = np.tile(weights, radial_nodes // P_SIZE)
    w_a = np.tile(weights, elems_a)
    w_b = np.tile(weights, elems_b)
    mass3 = w_r[:, None, None] * w_a[None, :, None] * w_b[None, None, :]
    origin = jnp.minimum(tile_index, 0)

    def assembled_at(length, lead_value, trail_value):
        position = origin + jnp.arange(length, dtype=jnp.int32)
        local_point = position % P_SIZE
        element = position // P_SIZE
        count = length // P_SIZE
        starts = jnp.where(
            local_point == 0, jnp.where(element > 0, 1.0, lead_value), 0.0
        ) * float(weights[P_SIZE - 1])
        ends = jnp.where(
            local_point == P_SIZE - 1, jnp.where(element < count - 1, 1.0, trail_value), 0.0
        ) * float(weights[0])
        return table_at(weights, position) + starts + ends

    assembled = (
        (
            assembled_at(radial_nodes, 0.0, 0.0)[:, None]
            * assembled_at(na_dev, 1.0, 1.0)[None, :]
        )[:, :, None]
        * assembled_at(nb_dev, lead, trail)[None, None, :]
    )
    rows_ext = (tile_index * na_dev - 1 + jnp.arange(na_dev + 2, dtype=jnp.int32)) % (na_dev * tiles)
    row_points = (np.arange(na_dev + 2) - 1) % P_SIZE
    col_points = (np.arange(nb_dev + 2) - 1) % P_SIZE
    cols_ext = group_index * nb_dev - 1 + jnp.arange(nb_dev + 2, dtype=jnp.int32)

    def weight_at(index):
        return table_at(weights, index)

    surface_ext = diffusivity * weight_at(rows_ext)[:, None] * weight_at(cols_ext)[None, :]

    rows = radial_nodes * na_dev
    mats = derivative_tables(radial_nodes, na_dev, nb_dev)
    flat_mass = mass3.reshape(rows, nb_dev)
    flat_flow = flow.reshape(3, rows, nb_dev)

    angle = phases(wave_of_slot, tile_index * elems_a, elems_a, span, points)
    analysis = (
        jnp.stack([jnp.cos(angle), jnp.sin(angle)], axis=1)
        * (scale * weight_at(tile_index * na_dev + jnp.arange(na_dev, dtype=jnp.int32)))[
            None, None, :
        ]
    ).reshape(-1, na_dev)

    def owner_map(partial):
        partial = partial.reshape(-1, 2, nb_dev)
        gathered = lax.all_to_all(partial, both, 0, 0, tiled=True)
        coeff = gathered.reshape(tiles, groups, 2, nb_dev).sum(axis=0)
        coeff = coeff.transpose(1, 0, 2).reshape(2, nb)
        owned = coeff.astype(jnp.bfloat16)
        mapped = jnp.einsum(
            "pq,cq->cp", match_ops[0], owned, preferred_element_type=jnp.float32
        )
        edged = jnp.concatenate([mapped[:, :1], mapped, mapped[:, -1:]], axis=1)
        pieces = jnp.stack(
            [edged[:, g * nb_dev : g * nb_dev + nb_dev + 2] for g in range(groups)], axis=0
        )
        return jnp.broadcast_to(pieces[None], (tiles,) + pieces.shape).reshape(
            tiles, groups, 2 * (nb_dev + 2)
        )

    def flux_of(returned):
        angle = phases_at(wave_of_slot, rows_ext // P_SIZE, table_at(points, rows_ext), span)
        synth = jnp.stack([jnp.cos(angle).T, jnp.sin(angle).T], axis=2).reshape(na_dev + 2, -1)
        flux = -jnp.dot(synth, returned.reshape(-1, nb_dev + 2), precision=lax.Precision.HIGH)
        return surface_ext * flux

    mapped_len = 2 * (nb_dev + 2)
    slot_len = 3 * radial_nodes * na_dev
    carried_halo = tiles >= 3 and groups >= 3 and tiles * groups <= 64

    def joint_exchange(sent, stacked, edge_rows, edge_cols):
        a_lo = edge_rows[0].reshape(3, radial_nodes, 1, nb_dev)
        a_hi = edge_rows[1].reshape(3, radial_nodes, 1, nb_dev)
        up = [(i, (i + 1) % tiles) for i in range(tiles)]
        down = [(j, i) for i, j in up]
        from_up = lax.ppermute(a_hi, "tile", up)
        from_down = lax.ppermute(a_lo, "tile", down)
        b_lo = edge_cols[0:1]
        b_hi = edge_cols[1:2]
        out_pieces = [
            ((0, 1), b_hi),
            ((0, -1), b_lo),
            ((1, 1), b_hi),
            ((1, -1), b_lo),
            ((-1, 1), b_hi),
            ((-1, -1), b_lo),
        ]
        slots = jnp.zeros((tiles * groups, 1, slot_len), jnp.float32)
        for (dt, dg), flat in out_pieces:
            target = ((tile_index + dt) % tiles) * groups + (group_index + dg) % groups
            slots = lax.dynamic_update_slice(slots, flat, (target, 0, 0))
        message = jnp.concatenate([sent.reshape(tiles * groups, 1, -1), slots], axis=2)
        received = lax.all_to_all(message, both, 0, 0, tiled=True)
        returned = received[:, 0, :mapped_len].reshape(tiles * groups, 2, nb_dev + 2)

        def take(dt, dg):
            source = ((tile_index - dt) % tiles) * groups + (group_index - dg) % groups
            row = lax.dynamic_slice(received, (source, 0, mapped_len), (1, 1, slot_len))
            return row.reshape(3, radial_nodes, na_dev, 1)

        from_left = take(0, 1)
        from_right = take(0, -1)
        corner_ul = take(1, 1)[:, :, na_dev - 1 :, :]
        corner_ur = take(1, -1)[:, :, na_dev - 1 :, :]
        corner_dl = take(-1, 1)[:, :, :1, :]
        corner_dr = take(-1, -1)[:, :, :1, :]
        top = jnp.concatenate([corner_ul, from_up, corner_ur], axis=3)
        middle = jnp.concatenate([from_left, stacked, from_right], axis=3)
        bottom = jnp.concatenate([corner_dl, from_down, corner_dr], axis=3)
        return returned, jnp.concatenate([top, middle, bottom], axis=2)

    def halo(stacked):
        a_lo = lax.slice_in_dim(stacked, 0, 1, axis=2)
        a_hi = lax.slice_in_dim(stacked, na_dev - 1, na_dev, axis=2)
        b_lo = lax.slice_in_dim(stacked, 0, 1, axis=3)
        b_hi = lax.slice_in_dim(stacked, nb_dev - 1, nb_dev, axis=3)
        sizes = (tiles, groups)
        from_up = lax.ppermute(a_hi, both, shift_pairs(sizes, (1, 0)))
        from_down = lax.ppermute(a_lo, both, shift_pairs(sizes, (-1, 0)))
        from_left = lax.ppermute(b_hi, both, shift_pairs(sizes, (0, 1)))
        from_right = lax.ppermute(b_lo, both, shift_pairs(sizes, (0, -1)))
        corner_ul = lax.ppermute(a_hi[:, :, :, -1:], both, shift_pairs(sizes, (1, 1)))
        corner_ur = lax.ppermute(a_hi[:, :, :, :1], both, shift_pairs(sizes, (1, -1)))
        corner_dl = lax.ppermute(a_lo[:, :, :, -1:], both, shift_pairs(sizes, (-1, 1)))
        corner_dr = lax.ppermute(a_lo[:, :, :, :1], both, shift_pairs(sizes, (-1, -1)))
        top = jnp.concatenate([corner_ul, from_up, corner_ur], axis=3)
        middle = jnp.concatenate([from_left, stacked, from_right], axis=3)
        bottom = jnp.concatenate([corner_dl, from_down, corner_dr], axis=3)
        return jnp.concatenate([top, middle, bottom], axis=2)

    join_b = np.zeros((nb_dev + 2, nb_dev), np.float32)
    join_b[np.arange(nb_dev) + 1, np.arange(nb_dev)] = 1.0
    inner_first = np.arange(P_SIZE, nb_dev, P_SIZE)
    join_b[inner_first, inner_first] = 1.0
    inner_last = np.arange(P_SIZE - 1, nb_dev - 1, P_SIZE)
    join_b[inner_last + 2, inner_last] = 1.0
    edge_lead = np.zeros((nb_dev + 2, nb_dev), np.float32)
    edge_lead[0, 0] = 1.0
    edge_trail = np.zeros((nb_dev + 2, nb_dev), np.float32)
    edge_trail[nb_dev + 1, nb_dev - 1] = 1.0
    join_b = join_b + lead * edge_lead + trail * edge_trail

    mask_shape = (3, radial_nodes, 1, 1)
    outer_index = radial_nodes - 1 + jnp.minimum(tile_index, 0)
    plane_mask = jnp.where(
        (lax.broadcasted_iota(jnp.int32, mask_shape, 0) == 0)
        & (lax.broadcasted_iota(jnp.int32, mask_shape, 1) == outer_index),
        1.0,
        0.0,
    )

    def assemble_ext(padded):
        last = padded.ndim - 1
        along_a = assemble_dim(
            padded[..., 1:-1, :], last - 1, padded[..., 0:1, :], padded[..., -1:, :]
        )
        return jnp.dot(along_a, join_b, precision=lax.Precision.HIGH)

    shapes = (
        jax.ShapeDtypeStruct((3, rows, nb_dev), jnp.float32),
        jax.ShapeDtypeStruct((2, 3, radial_nodes, nb_dev), jnp.float32),
        jax.ShapeDtypeStruct((2, 1, 3 * rows), jnp.float32),
    )
    first_outs = pl.pallas_call(
        first_volume_kernel,
        out_shape=shapes
        + (
            jax.ShapeDtypeStruct(analysis.shape[:1] + (nb_dev,), jnp.float32),
            jax.ShapeDtypeStruct((9, rows, nb_dev), jnp.float32),
        ),
    )(field.reshape(3, rows, nb_dev), flat_flow, mats, flat_mass, analysis)
    grads = first_outs[4]

    def tendency(parts, surface):
        if surface is None:
            stacked, edge_rows, edge_cols, partial = first_outs[:4]
        else:
            stacked, edge_rows, edge_cols = pl.pallas_call(volume_kernel, out_shape=shapes)(
                parts.reshape(3, rows, nb_dev), flat_flow, grads, mats, flat_mass
            )
            partial = jnp.dot(analysis, surface, precision=lax.Precision.HIGH)
        stacked = stacked.reshape(parts.shape)
        sent = owner_map(partial)
        if carried_halo:
            returned, padded = joint_exchange(sent, stacked, edge_rows, edge_cols)
        else:
            returned = lax.all_to_all(
                sent.reshape(tiles * groups, -1), both, 0, 0, tiled=True
            ).reshape(tiles * groups, 2, nb_dev + 2)
            padded = halo(stacked)
        flux_term = flux_of(returned)
        outer = padded[0, radial_nodes - 1] + flux_term
        outer_rate = assemble_ext(outer) / assembled[radial_nodes - 1]
        padded = padded + plane_mask * flux_term
        plane_r = jnp.zeros_like(lax.slice_in_dim(padded, 0, 1, axis=1))
        padded = assemble_dim(padded, 1, plane_r, plane_r)
        return assemble_ext(padded) / assembled[None], outer_rate

    first_rate, first_outer = tendency(field, None)
    section = field + time_step * first_rate
    section_outer = field[0, radial_nodes - 1] + time_step * first_outer
    second_rate, _ = tendency(section, section_outer)
    return 0.5 * (field + section + time_step * second_rate)


def solution(mesh):
    placed = (
        P(None, None, "tile", "deg"),
        P(None, None, "tile", "deg"),
        P(("tile", "deg"), None, None),
        P(),
    )
    return jax.shard_map(
        local, mesh=mesh, in_specs=placed, out_specs=P(None, None, "tile", "deg"), check_vma=False
    )
```

```python
import math

import numpy as np
import jax
import jax.numpy as jnp
from jax import lax
from jax.sharding import PartitionSpec as P
from jax.experimental import pallas as pl

P_SIZE = 8


diffusivity = 0.05
time_step = 0.01
highest = lax.Precision.HIGHEST
gll_interior = [0.2092992179024789, 0.5917001814331423, 0.8717401485096066]


def padded_2(value, sides, width):
    for axis, dim in sides:
        size, length = (lax.axis_size(axis), value.shape[dim])
        up = [(i, (i + 1) % size) for i in range(size)]
        down = [(j, i) for i, j in up]
        last = lax.slice_in_dim(value, length - width, length, axis=dim)
        first = lax.slice_in_dim(value, 0, width, axis=dim)
        before = lax.ppermute(last, axis, up)
        after = lax.ppermute(first, axis, down)
        value = jnp.concatenate([before, value, after], axis=dim)
    return value


def product(a, b):
    return jnp.dot(a, b, precision=lax.Precision.HIGH, preferred_element_type=jnp.float32)


def gradient_kernel(flow_ref, mats_ref, out_ref):
    for component in range(3):
        x = flow_ref[component]
        out_ref[3 * component] = product(mats_ref[0], x)
        out_ref[3 * component + 1] = product(mats_ref[1], x)
        out_ref[3 * component + 2] = product(x, mats_ref[2])


def volume_kernel(parts_ref, flow_ref, grad_ref, mats_ref, mass_ref, *outs):
    volume_body(parts_ref, flow_ref, grad_ref, mats_ref, mass_ref, *outs)


def first_volume_kernel(parts_ref, flow_ref, mats_ref, mass_ref, table_ref, *outs):
    grad_ref = outs[4]
    gradient_kernel(flow_ref, mats_ref, grad_ref)
    volume_body(parts_ref, flow_ref, grad_ref, mats_ref, mass_ref, *outs[:3])
    depth = outs[0].shape[1] // outs[1].shape[2]
    surface = parts_ref[0, pl.ds(outs[0].shape[1] - depth, depth), :]
    outs[3][...] = product(table_ref[...], surface)


def partial_kernel(table_ref, surface_ref, out_ref):
    out_ref[...] = product(table_ref[...], surface_ref[...])


def volume_body(parts_ref, flow_ref, grad_ref, mats_ref, mass_ref, out_ref, rows_ref, cols_ref):
    mass = mass_ref[...]
    p = [parts_ref[i] for i in range(3)]
    f = [flow_ref[i] for i in range(3)]
    planes = out_ref.shape[1] // rows_ref.shape[2]
    width = out_ref.shape[2]
    for c in range(3):
        x = p[c]
        s0 = product(mats_ref[0], x)
        s1 = product(mats_ref[1], x)
        s2 = product(x, mats_ref[2])
        stretch = p[0] * grad_ref[3 * c] + p[1] * grad_ref[3 * c + 1] + p[2] * grad_ref[3 * c + 2]
        carried = f[0] * s0 + f[1] * s1 + f[2] * s2
        spread = (
            product(mats_ref[3], mass * s0)
            + product(mats_ref[4], mass * s1)
            + product(mass * s2, mats_ref[5])
        )
        result = mass * (stretch - carried) - diffusivity * spread
        out_ref[c] = result
        turned = result.T
        span_of = out_ref.shape[1]
        cols_ref[0, :, c * span_of : (c + 1) * span_of] = turned[0:1, :]
        cols_ref[1, :, c * span_of : (c + 1) * span_of] = turned[width - 1 : width, :]
    for c in range(3):
        rows_ref[0, c] = out_ref[c, pl.ds(0, rows_ref.shape[2], stride=planes), :]
        rows_ref[1, c] = out_ref[c, pl.ds(planes - 1, rows_ref.shape[2], stride=planes), :]


def derivative_tables(radial_nodes, na_dev, nb_dev):
    _, _, matrix_list = gll_tables(P_SIZE)
    dmat = np.asarray(matrix_list, np.float32)
    radial = np.kron(dmat, np.eye(na_dev, dtype=np.float32))
    first = np.kron(np.eye(radial_nodes * na_dev // P_SIZE, dtype=np.float32), dmat)
    second = np.kron(np.eye(nb_dev // P_SIZE, dtype=np.float32), dmat)
    return jnp.asarray(np.stack([radial, first, second.T, radial.T, first.T, second]))


def legendre_value(point, degree):
    previous = 1.0
    current = point
    for order in range(1, degree):
        following = ((2 * order + 1) * point * current - order * previous) / (order + 1)
        previous = current
        current = following
    return current


def gll_tables(count):
    degree = count - 1
    points = [-1.0] + [-value for value in reversed(gll_interior)] + list(gll_interior) + [1.0]
    values = [legendre_value(point, degree) for point in points]
    weights = [2.0 / (degree * (degree + 1) * value * value) for value in values]
    matrix = [
        [
            values[row] / (values[col] * (points[row] - points[col])) if row != col else 0.0
            for col in range(count)
        ]
        for row in range(count)
    ]
    matrix[0][0] = -degree * (degree + 1) / 4.0
    matrix[count - 1][count - 1] = degree * (degree + 1) / 4.0
    return (points, weights, matrix)


def apply_along(values, axis_pos, matrix):
    shape = values.shape
    blocks = values.reshape(
        shape[:axis_pos] + (shape[axis_pos] // P_SIZE, P_SIZE) + shape[axis_pos + 1 :]
    )
    letters = list("abcdefg"[: blocks.ndim])
    source = list(letters)
    source[axis_pos + 1] = "p"
    target = list(letters)
    target[axis_pos + 1] = "q"
    formula = "".join(source) + ",qp->" + "".join(target)
    return jnp.einsum(formula, blocks, matrix, precision=highest).reshape(shape)


def assemble_dim(values, axis_pos, left, right):
    shape = values.shape
    count = shape[axis_pos] // P_SIZE
    blocks = values.reshape(shape[:axis_pos] + (count, P_SIZE) + shape[axis_pos + 1 :])
    edge_shape = shape[:axis_pos] + (1, 1) + shape[axis_pos + 1 :]
    first = lax.slice_in_dim(blocks, 0, 1, axis=axis_pos + 1)
    last = lax.slice_in_dim(blocks, P_SIZE - 1, P_SIZE, axis=axis_pos + 1)
    before = jnp.concatenate(
        [left.reshape(edge_shape), lax.slice_in_dim(last, 0, count - 1, axis=axis_pos)],
        axis=axis_pos,
    )
    after = jnp.concatenate(
        [lax.slice_in_dim(first, 1, count, axis=axis_pos), right.reshape(edge_shape)], axis=axis_pos
    )
    middle = lax.slice_in_dim(blocks, 1, P_SIZE - 1, axis=axis_pos + 1)
    joined = jnp.concatenate([first + before, middle, last + after], axis=axis_pos + 1)
    return joined.reshape(shape)


def assembled_weights(weights, count, lead, trail):
    position = jnp.arange(count * P_SIZE, dtype=jnp.int32)
    local_point = position % P_SIZE
    element = position // P_SIZE
    base = jnp.tile(weights, count)
    starts = (
        jnp.where(local_point == 0, jnp.where(element > 0, 1.0, lead), 0.0) * weights[P_SIZE - 1]
    )
    ends = (
        jnp.where(local_point == P_SIZE - 1, jnp.where(element < count - 1, 1.0, trail), 0.0)
        * weights[0]
    )
    return base + starts + ends


def static_assembled(weights, count, lead, trail):
    position = np.arange(count * P_SIZE)
    local_point = position % P_SIZE
    element = position // P_SIZE
    starts = np.where(local_point == 0, np.where(element > 0, 1.0, lead), 0.0) * weights[P_SIZE - 1]
    ends = np.where(local_point == P_SIZE - 1, np.where(element < count - 1, 1.0, trail), 0.0)
    return (np.tile(weights, count) + starts + ends * weights[0]).astype(np.float32)


def table_at(values, index):
    point = index % P_SIZE
    total = jnp.zeros(index.shape, jnp.float32)
    for p in range(P_SIZE):
        total = total + jnp.where(point == p, float(values[p]), 0.0)
    return total


def phases(waves, elem_start, elem_count, span, points):
    position = elem_start * P_SIZE + jnp.arange(elem_count * P_SIZE, dtype=jnp.int32)
    element = position // P_SIZE
    whole = waves[:, None] * (2 * element + 1)[None, :] % span
    fraction = waves.astype(jnp.float32)[:, None] * table_at(points, position)[None, :]
    return 2.0 * math.pi / span * (whole.astype(jnp.float32) + fraction)


def phases_at(waves, element, point_values, span):
    whole = waves[:, None] * (2 * element + 1)[None, :] % span
    fraction = waves.astype(jnp.float32)[:, None] * point_values[None, :]
    return 2.0 * math.pi / span * (whole.astype(jnp.float32) + fraction)


def shift_pairs(sizes, steps):
    count = sizes[0] * sizes[1]
    pairs = []
    for source in range(count):
        t, g = divmod(source, sizes[1])
        target = ((t + steps[0]) % sizes[0]) * sizes[1] + (g + steps[1]) % sizes[1]
        pairs.append((source, target))
    return pairs


def local(field, flow, match_ops, wave_of_slot):
    tiles = lax.axis_size("tile")
    groups = lax.axis_size("deg")
    both = ("tile", "deg")
    tile_index = lax.axis_index("tile")
    group_index = lax.axis_index("deg")
    radial_nodes = field.shape[1]
    na_dev = field.shape[2]
    nb_dev = field.shape[3]
    elems_a = na_dev // P_SIZE
    elems_b = nb_dev // P_SIZE
    nb = nb_dev * groups
    span = 2 * elems_a * tiles
    scale = P_SIZE / (na_dev * tiles)
    points_list, weights_list, _ = gll_tables(P_SIZE)
    points = np.asarray(points_list, np.float32)
    weights = np.asarray(weights_list, np.float32)
    lead = (group_index > 0).astype(jnp.float32)
    trail = (group_index < groups - 1).astype(jnp.float32)
    w_r = np.tile(weights, radial_nodes // P_SIZE)
    w_a = np.tile(weights, elems_a)
    w_b = np.tile(weights, elems_b)
    mass3 = w_r[:, None, None] * w_a[None, :, None] * w_b[None, None, :]
    origin = jnp.minimum(tile_index, 0)

    def assembled_at(length, lead_value, trail_value):
        position = origin + jnp.arange(length, dtype=jnp.int32)
        local_point = position % P_SIZE
        element = position // P_SIZE
        count = length // P_SIZE
        starts = jnp.where(
            local_point == 0, jnp.where(element > 0, 1.0, lead_value), 0.0
        ) * float(weights[P_SIZE - 1])
        ends = jnp.where(
            local_point == P_SIZE - 1, jnp.where(element < count - 1, 1.0, trail_value), 0.0
        ) * float(weights[0])
        return table_at(weights, position) + starts + ends

    assembled = (
        (
            assembled_at(radial_nodes, 0.0, 0.0)[:, None]
            * assembled_at(na_dev, 1.0, 1.0)[None, :]
        )[:, :, None]
        * assembled_at(nb_dev, lead, trail)[None, None, :]
    )
    rows_ext = (tile_index * na_dev - 1 + jnp.arange(na_dev + 2, dtype=jnp.int32)) % (na_dev * tiles)
    row_points = (np.arange(na_dev + 2) - 1) % P_SIZE
    col_points = (np.arange(nb_dev + 2) - 1) % P_SIZE
    cols_ext = group_index * nb_dev - 1 + jnp.arange(nb_dev + 2, dtype=jnp.int32)

    def weight_at(index):
        return table_at(weights, index)

    surface_ext = diffusivity * weight_at(rows_ext)[:, None] * weight_at(cols_ext)[None, :]

    rows = radial_nodes * na_dev
    mats = derivative_tables(radial_nodes, na_dev, nb_dev)
    flat_mass = mass3.reshape(rows, nb_dev)
    flat_flow = flow.reshape(3, rows, nb_dev)

    angle = phases(wave_of_slot, tile_index * elems_a, elems_a, span, points)
    analysis = (
        jnp.stack([jnp.cos(angle), jnp.sin(angle)], axis=1)
        * (scale * weight_at(tile_index * na_dev + jnp.arange(na_dev, dtype=jnp.int32)))[
            None, None, :
        ]
    ).reshape(-1, na_dev)

    def owner_map(partial):
        partial = partial.reshape(-1, 2, nb_dev)
        gathered = lax.all_to_all(partial, both, 0, 0, tiled=True)
        coeff = gathered.reshape(tiles, groups, 2, nb_dev).sum(axis=0)
        coeff = coeff.transpose(1, 0, 2).reshape(2, nb)
        owned = coeff.astype(jnp.bfloat16)
        mapped = jnp.einsum(
            "pq,cq->cp", match_ops[0], owned, preferred_element_type=jnp.float32
        )
        edged = jnp.concatenate([mapped[:, :1], mapped, mapped[:, -1:]], axis=1)
        pieces = jnp.stack(
            [edged[:, g * nb_dev : g * nb_dev + nb_dev + 2] for g in range(groups)], axis=0
        )
        return jnp.broadcast_to(pieces[None], (tiles,) + pieces.shape).reshape(
            tiles, groups, 2 * (nb_dev + 2)
        )

    def flux_of(returned):
        angle = phases_at(wave_of_slot, rows_ext // P_SIZE, table_at(points, rows_ext), span)
        synth = jnp.stack([jnp.cos(angle).T, jnp.sin(angle).T], axis=2).reshape(na_dev + 2, -1)
        flux = -jnp.dot(synth, returned.reshape(-1, nb_dev + 2), precision=lax.Precision.HIGH)
        return surface_ext * flux

    mapped_len = 2 * (nb_dev + 2)
    slot_len = 3 * radial_nodes * na_dev
    carried_halo = tiles >= 3 and groups >= 3 and tiles * groups <= 64

    def joint_exchange(sent, stacked, edge_rows, edge_cols):
        a_lo = edge_rows[0].reshape(3, radial_nodes, 1, nb_dev)
        a_hi = edge_rows[1].reshape(3, radial_nodes, 1, nb_dev)
        up = [(i, (i + 1) % tiles) for i in range(tiles)]
        down = [(j, i) for i, j in up]
        from_up = lax.ppermute(a_hi, "tile", up)
        from_down = lax.ppermute(a_lo, "tile", down)
        b_lo = edge_cols[0:1]
        b_hi = edge_cols[1:2]
        out_pieces = [
            ((0, 1), b_hi),
            ((0, -1), b_lo),
            ((1, 1), b_hi),
            ((1, -1), b_lo),
            ((-1, 1), b_hi),
            ((-1, -1), b_lo),
        ]
        slots = jnp.zeros((tiles * groups, 1, slot_len), jnp.float32)
        for (dt, dg), flat in out_pieces:
            target = ((tile_index + dt) % tiles) * groups + (group_index + dg) % groups
            slots = lax.dynamic_update_slice(slots, flat, (target, 0, 0))
        message = jnp.concatenate([sent.reshape(tiles * groups, 1, -1), slots], axis=2)
        received = lax.all_to_all(message, both, 0, 0, tiled=True)
        returned = received[:, 0, :mapped_len].reshape(tiles * groups, 2, nb_dev + 2)

        def take(dt, dg):
            source = ((tile_index - dt) % tiles) * groups + (group_index - dg) % groups
            row = lax.dynamic_slice(received, (source, 0, mapped_len), (1, 1, slot_len))
            return row.reshape(3, radial_nodes, na_dev, 1)

        from_left = take(0, 1)
        from_right = take(0, -1)
        corner_ul = take(1, 1)[:, :, na_dev - 1 :, :]
        corner_ur = take(1, -1)[:, :, na_dev - 1 :, :]
        corner_dl = take(-1, 1)[:, :, :1, :]
        corner_dr = take(-1, -1)[:, :, :1, :]
        top = jnp.concatenate([corner_ul, from_up, corner_ur], axis=3)
        middle = jnp.concatenate([from_left, stacked, from_right], axis=3)
        bottom = jnp.concatenate([corner_dl, from_down, corner_dr], axis=3)
        return returned, jnp.concatenate([top, middle, bottom], axis=2)

    def halo(stacked):
        a_lo = lax.slice_in_dim(stacked, 0, 1, axis=2)
        a_hi = lax.slice_in_dim(stacked, na_dev - 1, na_dev, axis=2)
        b_lo = lax.slice_in_dim(stacked, 0, 1, axis=3)
        b_hi = lax.slice_in_dim(stacked, nb_dev - 1, nb_dev, axis=3)
        sizes = (tiles, groups)
        from_up = lax.ppermute(a_hi, both, shift_pairs(sizes, (1, 0)))
        from_down = lax.ppermute(a_lo, both, shift_pairs(sizes, (-1, 0)))
        from_left = lax.ppermute(b_hi, both, shift_pairs(sizes, (0, 1)))
        from_right = lax.ppermute(b_lo, both, shift_pairs(sizes, (0, -1)))
        corner_ul = lax.ppermute(a_hi[:, :, :, -1:], both, shift_pairs(sizes, (1, 1)))
        corner_ur = lax.ppermute(a_hi[:, :, :, :1], both, shift_pairs(sizes, (1, -1)))
        corner_dl = lax.ppermute(a_lo[:, :, :, -1:], both, shift_pairs(sizes, (-1, 1)))
        corner_dr = lax.ppermute(a_lo[:, :, :, :1], both, shift_pairs(sizes, (-1, -1)))
        top = jnp.concatenate([corner_ul, from_up, corner_ur], axis=3)
        middle = jnp.concatenate([from_left, stacked, from_right], axis=3)
        bottom = jnp.concatenate([corner_dl, from_down, corner_dr], axis=3)
        return jnp.concatenate([top, middle, bottom], axis=2)

    join_b = np.zeros((nb_dev + 2, nb_dev), np.float32)
    join_b[np.arange(nb_dev) + 1, np.arange(nb_dev)] = 1.0
    inner_first = np.arange(P_SIZE, nb_dev, P_SIZE)
    join_b[inner_first, inner_first] = 1.0
    inner_last = np.arange(P_SIZE - 1, nb_dev - 1, P_SIZE)
    join_b[inner_last + 2, inner_last] = 1.0
    edge_lead = np.zeros((nb_dev + 2, nb_dev), np.float32)
    edge_lead[0, 0] = 1.0
    edge_trail = np.zeros((nb_dev + 2, nb_dev), np.float32)
    edge_trail[nb_dev + 1, nb_dev - 1] = 1.0
    join_b = join_b + lead * edge_lead + trail * edge_trail

    mask_shape = (3, radial_nodes, 1, 1)
    outer_index = radial_nodes - 1 + jnp.minimum(tile_index, 0)
    plane_mask = jnp.where(
        (lax.broadcasted_iota(jnp.int32, mask_shape, 0) == 0)
        & (lax.broadcasted_iota(jnp.int32, mask_shape, 1) == outer_index),
        1.0,
        0.0,
    )

    def assemble_ext(padded):
        last = padded.ndim - 1
        along_a = assemble_dim(
            padded[..., 1:-1, :], last - 1, padded[..., 0:1, :], padded[..., -1:, :]
        )
        return jnp.dot(along_a, join_b, precision=lax.Precision.HIGH)

    shapes = (
        jax.ShapeDtypeStruct((3, rows, nb_dev), jnp.float32),
        jax.ShapeDtypeStruct((2, 3, radial_nodes, nb_dev), jnp.float32),
        jax.ShapeDtypeStruct((2, 1, 3 * rows), jnp.float32),
    )
    first_outs = pl.pallas_call(
        first_volume_kernel,
        out_shape=shapes
        + (
            jax.ShapeDtypeStruct(analysis.shape[:1] + (nb_dev,), jnp.float32),
            jax.ShapeDtypeStruct((9, rows, nb_dev), jnp.float32),
        ),
    )(field.reshape(3, rows, nb_dev), flat_flow, mats, flat_mass, analysis)
    grads = first_outs[4]

    def tendency(parts, surface):
        if surface is None:
            stacked, edge_rows, edge_cols, partial = first_outs[:4]
        else:
            stacked, edge_rows, edge_cols = pl.pallas_call(volume_kernel, out_shape=shapes)(
                parts.reshape(3, rows, nb_dev), flat_flow, grads, mats, flat_mass
            )
            partial = pl.pallas_call(
                partial_kernel,
                out_shape=jax.ShapeDtypeStruct(analysis.shape[:1] + (nb_dev,), jnp.float32),
            )(analysis, surface)
        stacked = stacked.reshape(parts.shape)
        sent = owner_map(partial)
        if carried_halo:
            returned, padded = joint_exchange(sent, stacked, edge_rows, edge_cols)
        else:
            returned = lax.all_to_all(
                sent.reshape(tiles * groups, -1), both, 0, 0, tiled=True
            ).reshape(tiles * groups, 2, nb_dev + 2)
            padded = halo(stacked)
        flux_term = flux_of(returned)
        outer = padded[0, radial_nodes - 1] + flux_term
        outer_rate = assemble_ext(outer) / assembled[radial_nodes - 1]
        padded = padded + plane_mask * flux_term
        plane_r = jnp.zeros_like(lax.slice_in_dim(padded, 0, 1, axis=1))
        padded = assemble_dim(padded, 1, plane_r, plane_r)
        return assemble_ext(padded) / assembled[None], outer_rate

    first_rate, first_outer = tendency(field, None)
    section = field + time_step * first_rate
    section_outer = field[0, radial_nodes - 1] + time_step * first_outer
    second_rate, _ = tendency(section, section_outer)
    return 0.5 * (field + section + time_step * second_rate)


def solution(mesh):
    placed = (
        P(None, None, "tile", "deg"),
        P(None, None, "tile", "deg"),
        P(("tile", "deg"), None, None),
        P(),
    )
    return jax.shard_map(
        local, mesh=mesh, in_specs=placed, out_specs=P(None, None, "tile", "deg"), check_vma=False
    )
```

```python
import math

import numpy as np
import jax
import jax.numpy as jnp
from jax import lax
from jax.sharding import PartitionSpec as P
from jax.experimental import pallas as pl

P_SIZE = 8


diffusivity = 0.05
time_step = 0.01
highest = lax.Precision.HIGHEST
gll_interior = [0.2092992179024789, 0.5917001814331423, 0.8717401485096066]


def padded_2(value, sides, width):
    for axis, dim in sides:
        size, length = (lax.axis_size(axis), value.shape[dim])
        up = [(i, (i + 1) % size) for i in range(size)]
        down = [(j, i) for i, j in up]
        last = lax.slice_in_dim(value, length - width, length, axis=dim)
        first = lax.slice_in_dim(value, 0, width, axis=dim)
        before = lax.ppermute(last, axis, up)
        after = lax.ppermute(first, axis, down)
        value = jnp.concatenate([before, value, after], axis=dim)
    return value


def product(a, b):
    return jnp.dot(a, b, precision=lax.Precision.HIGH, preferred_element_type=jnp.float32)


def gradient_kernel(flow_ref, mats_ref, out_ref):
    for component in range(3):
        x = flow_ref[component]
        out_ref[3 * component] = product(mats_ref[0], x)
        out_ref[3 * component + 1] = product(mats_ref[1], x)
        out_ref[3 * component + 2] = product(x, mats_ref[2])


def volume_kernel(parts_ref, flow_ref, grad_ref, mats_ref, mass_ref, *outs):
    volume_body(parts_ref, flow_ref, grad_ref, mats_ref, mass_ref, *outs)


def first_volume_kernel(parts_ref, flow_ref, mats_ref, mass_ref, table_ref, *outs):
    grad_ref = outs[4]
    gradient_kernel(flow_ref, mats_ref, grad_ref)
    volume_body(parts_ref, flow_ref, grad_ref, mats_ref, mass_ref, *outs[:3])
    depth = outs[0].shape[1] // outs[1].shape[2]
    surface = parts_ref[0, pl.ds(outs[0].shape[1] - depth, depth), :]
    outs[3][...] = product(table_ref[...], surface)


def volume_body(parts_ref, flow_ref, grad_ref, mats_ref, mass_ref, out_ref, rows_ref, cols_ref):
    mass = mass_ref[...]
    p = [parts_ref[i] for i in range(3)]
    f = [flow_ref[i] for i in range(3)]
    planes = out_ref.shape[1] // rows_ref.shape[2]
    width = out_ref.shape[2]
    for c in range(3):
        x = p[c]
        s0 = product(mats_ref[0], x)
        s1 = product(mats_ref[1], x)
        s2 = product(x, mats_ref[2])
        stretch = p[0] * grad_ref[3 * c] + p[1] * grad_ref[3 * c + 1] + p[2] * grad_ref[3 * c + 2]
        carried = f[0] * s0 + f[1] * s1 + f[2] * s2
        spread = (
            product(mats_ref[3], mass * s0)
            + product(mats_ref[4], mass * s1)
            + product(mass * s2, mats_ref[5])
        )
        result = mass * (stretch - carried) - diffusivity * spread
        out_ref[c] = result
        turned = result.T
        span_of = out_ref.shape[1]
        cols_ref[0, :, c * span_of : (c + 1) * span_of] = turned[0:1, :]
        cols_ref[1, :, c * span_of : (c + 1) * span_of] = turned[width - 1 : width, :]
    for c in range(3):
        rows_ref[0, c] = out_ref[c, pl.ds(0, rows_ref.shape[2], stride=planes), :]
        rows_ref[1, c] = out_ref[c, pl.ds(planes - 1, rows_ref.shape[2], stride=planes), :]


def derivative_tables(radial_nodes, na_dev, nb_dev):
    _, _, matrix_list = gll_tables(P_SIZE)
    dmat = np.asarray(matrix_list, np.float32)
    radial = np.kron(dmat, np.eye(na_dev, dtype=np.float32))
    first = np.kron(np.eye(radial_nodes * na_dev // P_SIZE, dtype=np.float32), dmat)
    second = np.kron(np.eye(nb_dev // P_SIZE, dtype=np.float32), dmat)
    return jnp.asarray(np.stack([radial, first, second.T, radial.T, first.T, second]))


def legendre_value(point, degree):
    previous = 1.0
    current = point
    for order in range(1, degree):
        following = ((2 * order + 1) * point * current - order * previous) / (order + 1)
        previous = current
        current = following
    return current


def gll_tables(count):
    degree = count - 1
    points = [-1.0] + [-value for value in reversed(gll_interior)] + list(gll_interior) + [1.0]
    values = [legendre_value(point, degree) for point in points]
    weights = [2.0 / (degree * (degree + 1) * value * value) for value in values]
    matrix = [
        [
            values[row] / (values[col] * (points[row] - points[col])) if row != col else 0.0
            for col in range(count)
        ]
        for row in range(count)
    ]
    matrix[0][0] = -degree * (degree + 1) / 4.0
    matrix[count - 1][count - 1] = degree * (degree + 1) / 4.0
    return (points, weights, matrix)


def apply_along(values, axis_pos, matrix):
    shape = values.shape
    blocks = values.reshape(
        shape[:axis_pos] + (shape[axis_pos] // P_SIZE, P_SIZE) + shape[axis_pos + 1 :]
    )
    letters = list("abcdefg"[: blocks.ndim])
    source = list(letters)
    source[axis_pos + 1] = "p"
    target = list(letters)
    target[axis_pos + 1] = "q"
    formula = "".join(source) + ",qp->" + "".join(target)
    return jnp.einsum(formula, blocks, matrix, precision=highest).reshape(shape)


def assemble_dim(values, axis_pos, left, right):
    shape = values.shape
    count = shape[axis_pos] // P_SIZE
    blocks = values.reshape(shape[:axis_pos] + (count, P_SIZE) + shape[axis_pos + 1 :])
    edge_shape = shape[:axis_pos] + (1, 1) + shape[axis_pos + 1 :]
    first = lax.slice_in_dim(blocks, 0, 1, axis=axis_pos + 1)
    last = lax.slice_in_dim(blocks, P_SIZE - 1, P_SIZE, axis=axis_pos + 1)
    before = jnp.concatenate(
        [left.reshape(edge_shape), lax.slice_in_dim(last, 0, count - 1, axis=axis_pos)],
        axis=axis_pos,
    )
    after = jnp.concatenate(
        [lax.slice_in_dim(first, 1, count, axis=axis_pos), right.reshape(edge_shape)], axis=axis_pos
    )
    middle = lax.slice_in_dim(blocks, 1, P_SIZE - 1, axis=axis_pos + 1)
    joined = jnp.concatenate([first + before, middle, last + after], axis=axis_pos + 1)
    return joined.reshape(shape)


def assembled_weights(weights, count, lead, trail):
    position = jnp.arange(count * P_SIZE, dtype=jnp.int32)
    local_point = position % P_SIZE
    element = position // P_SIZE
    base = jnp.tile(weights, count)
    starts = (
        jnp.where(local_point == 0, jnp.where(element > 0, 1.0, lead), 0.0) * weights[P_SIZE - 1]
    )
    ends = (
        jnp.where(local_point == P_SIZE - 1, jnp.where(element < count - 1, 1.0, trail), 0.0)
        * weights[0]
    )
    return base + starts + ends


def static_assembled(weights, count, lead, trail):
    position = np.arange(count * P_SIZE)
    local_point = position % P_SIZE
    element = position // P_SIZE
    starts = np.where(local_point == 0, np.where(element > 0, 1.0, lead), 0.0) * weights[P_SIZE - 1]
    ends = np.where(local_point == P_SIZE - 1, np.where(element < count - 1, 1.0, trail), 0.0)
    return (np.tile(weights, count) + starts + ends * weights[0]).astype(np.float32)


def table_at(values, index):
    point = index % P_SIZE
    total = jnp.zeros(index.shape, jnp.float32)
    for p in range(P_SIZE):
        total = total + jnp.where(point == p, float(values[p]), 0.0)
    return total


def phases(waves, elem_start, elem_count, span, points):
    position = elem_start * P_SIZE + jnp.arange(elem_count * P_SIZE, dtype=jnp.int32)
    element = position // P_SIZE
    whole = waves[:, None] * (2 * element + 1)[None, :] % span
    fraction = waves.astype(jnp.float32)[:, None] * table_at(points, position)[None, :]
    return 2.0 * math.pi / span * (whole.astype(jnp.float32) + fraction)


def phases_at(waves, element, point_values, span):
    whole = waves[:, None] * (2 * element + 1)[None, :] % span
    fraction = waves.astype(jnp.float32)[:, None] * point_values[None, :]
    return 2.0 * math.pi / span * (whole.astype(jnp.float32) + fraction)


def shift_pairs(sizes, steps):
    count = sizes[0] * sizes[1]
    pairs = []
    for source in range(count):
        t, g = divmod(source, sizes[1])
        target = ((t + steps[0]) % sizes[0]) * sizes[1] + (g + steps[1]) % sizes[1]
        pairs.append((source, target))
    return pairs


def local(field, flow, match_ops, wave_of_slot):
    tiles = lax.axis_size("tile")
    groups = lax.axis_size("deg")
    both = ("tile", "deg")
    tile_index = lax.axis_index("tile")
    group_index = lax.axis_index("deg")
    radial_nodes = field.shape[1]
    na_dev = field.shape[2]
    nb_dev = field.shape[3]
    elems_a = na_dev // P_SIZE
    elems_b = nb_dev // P_SIZE
    nb = nb_dev * groups
    span = 2 * elems_a * tiles
    scale = P_SIZE / (na_dev * tiles)
    points_list, weights_list, _ = gll_tables(P_SIZE)
    points = np.asarray(points_list, np.float32)
    weights = np.asarray(weights_list, np.float32)
    lead = (group_index > 0).astype(jnp.float32)
    trail = (group_index < groups - 1).astype(jnp.float32)
    w_r = np.tile(weights, radial_nodes // P_SIZE)
    w_a = np.tile(weights, elems_a)
    w_b = np.tile(weights, elems_b)
    mass3 = w_r[:, None, None] * w_a[None, :, None] * w_b[None, None, :]
    origin = jnp.minimum(tile_index, 0)

    def assembled_at(length, lead_value, trail_value):
        position = origin + jnp.arange(length, dtype=jnp.int32)
        local_point = position % P_SIZE
        element = position // P_SIZE
        count = length // P_SIZE
        starts = jnp.where(
            local_point == 0, jnp.where(element > 0, 1.0, lead_value), 0.0
        ) * float(weights[P_SIZE - 1])
        ends = jnp.where(
            local_point == P_SIZE - 1, jnp.where(element < count - 1, 1.0, trail_value), 0.0
        ) * float(weights[0])
        return table_at(weights, position) + starts + ends

    assembled = (
        (
            assembled_at(radial_nodes, 0.0, 0.0)[:, None]
            * assembled_at(na_dev, 1.0, 1.0)[None, :]
        )[:, :, None]
        * assembled_at(nb_dev, lead, trail)[None, None, :]
    )
    rows_ext = (tile_index * na_dev - 1 + jnp.arange(na_dev + 2, dtype=jnp.int32)) % (na_dev * tiles)
    row_points = (np.arange(na_dev + 2) - 1) % P_SIZE
    col_points = (np.arange(nb_dev + 2) - 1) % P_SIZE
    cols_ext = group_index * nb_dev - 1 + jnp.arange(nb_dev + 2, dtype=jnp.int32)

    def weight_at(index):
        return table_at(weights, index)

    surface_ext = diffusivity * weight_at(rows_ext)[:, None] * weight_at(cols_ext)[None, :]

    rows = radial_nodes * na_dev
    mats = derivative_tables(radial_nodes, na_dev, nb_dev)
    flat_mass = mass3.reshape(rows, nb_dev)
    flat_flow = flow.reshape(3, rows, nb_dev)

    angle = phases(wave_of_slot, tile_index * elems_a, elems_a, span, points)
    analysis = (
        jnp.stack([jnp.cos(angle), jnp.sin(angle)], axis=1)
        * (scale * weight_at(tile_index * na_dev + jnp.arange(na_dev, dtype=jnp.int32)))[
            None, None, :
        ]
    ).reshape(-1, na_dev)

    def owner_map(partial):
        partial = partial.reshape(-1, 2, nb_dev)
        gathered = lax.all_to_all(partial, both, 0, 0, tiled=True)
        coeff = gathered.reshape(tiles, groups, 2, nb_dev).sum(axis=0)
        coeff = coeff.transpose(1, 0, 2).reshape(2, nb)
        owned = coeff.astype(jnp.bfloat16)
        mapped = jnp.einsum(
            "pq,cq->cp", match_ops[0], owned, preferred_element_type=jnp.float32
        )
        edged = jnp.concatenate([mapped[:, :1], mapped, mapped[:, -1:]], axis=1)
        pieces = jnp.stack(
            [edged[:, g * nb_dev : g * nb_dev + nb_dev + 2] for g in range(groups)], axis=0
        )
        return jnp.broadcast_to(pieces[None], (tiles,) + pieces.shape).reshape(
            tiles, groups, 2 * (nb_dev + 2)
        )

    def flux_of(returned):
        angle = phases_at(wave_of_slot, rows_ext // P_SIZE, table_at(points, rows_ext), span)
        synth = jnp.stack([jnp.cos(angle).T, jnp.sin(angle).T], axis=2).reshape(na_dev + 2, -1)
        flux = -jnp.dot(synth, returned.reshape(-1, nb_dev + 2), precision=lax.Precision.HIGH)
        return surface_ext * flux

    mapped_len = 2 * (nb_dev + 2)
    slot_len = 3 * radial_nodes * na_dev
    carried_halo = tiles >= 3 and groups >= 3 and tiles * groups <= 64

    def joint_exchange(sent, stacked, edge_rows, edge_cols):
        a_lo = edge_rows[0].reshape(3, radial_nodes, 1, nb_dev)
        a_hi = edge_rows[1].reshape(3, radial_nodes, 1, nb_dev)
        up = [(i, (i + 1) % tiles) for i in range(tiles)]
        down = [(j, i) for i, j in up]
        from_up = lax.ppermute(a_hi, "tile", up)
        from_down = lax.ppermute(a_lo, "tile", down)
        b_lo = edge_cols[0:1]
        b_hi = edge_cols[1:2]
        out_pieces = [
            ((0, 1), b_hi),
            ((0, -1), b_lo),
            ((1, 1), b_hi),
            ((1, -1), b_lo),
            ((-1, 1), b_hi),
            ((-1, -1), b_lo),
        ]
        slots = jnp.zeros((tiles * groups, 1, slot_len), jnp.float32)
        for (dt, dg), flat in out_pieces:
            target = ((tile_index + dt) % tiles) * groups + (group_index + dg) % groups
            slots = lax.dynamic_update_slice(slots, flat, (target, 0, 0))
        message = jnp.concatenate([sent.reshape(tiles * groups, 1, -1), slots], axis=2)
        received = lax.all_to_all(message, both, 0, 0, tiled=True)
        returned = received[:, 0, :mapped_len].reshape(tiles * groups, 2, nb_dev + 2)

        def take(dt, dg):
            source = ((tile_index - dt) % tiles) * groups + (group_index - dg) % groups
            row = lax.dynamic_slice(received, (source, 0, mapped_len), (1, 1, slot_len))
            return row.reshape(3, radial_nodes, na_dev, 1)

        from_left = take(0, 1)
        from_right = take(0, -1)
        corner_ul = take(1, 1)[:, :, na_dev - 1 :, :]
        corner_ur = take(1, -1)[:, :, na_dev - 1 :, :]
        corner_dl = take(-1, 1)[:, :, :1, :]
        corner_dr = take(-1, -1)[:, :, :1, :]
        top = jnp.concatenate([corner_ul, from_up, corner_ur], axis=3)
        middle = jnp.concatenate([from_left, stacked, from_right], axis=3)
        bottom = jnp.concatenate([corner_dl, from_down, corner_dr], axis=3)
        return returned, jnp.concatenate([top, middle, bottom], axis=2)

    def halo(stacked):
        a_lo = lax.slice_in_dim(stacked, 0, 1, axis=2)
        a_hi = lax.slice_in_dim(stacked, na_dev - 1, na_dev, axis=2)
        b_lo = lax.slice_in_dim(stacked, 0, 1, axis=3)
        b_hi = lax.slice_in_dim(stacked, nb_dev - 1, nb_dev, axis=3)
        sizes = (tiles, groups)
        from_up = lax.ppermute(a_hi, both, shift_pairs(sizes, (1, 0)))
        from_down = lax.ppermute(a_lo, both, shift_pairs(sizes, (-1, 0)))
        from_left = lax.ppermute(b_hi, both, shift_pairs(sizes, (0, 1)))
        from_right = lax.ppermute(b_lo, both, shift_pairs(sizes, (0, -1)))
        corner_ul = lax.ppermute(a_hi[:, :, :, -1:], both, shift_pairs(sizes, (1, 1)))
        corner_ur = lax.ppermute(a_hi[:, :, :, :1], both, shift_pairs(sizes, (1, -1)))
        corner_dl = lax.ppermute(a_lo[:, :, :, -1:], both, shift_pairs(sizes, (-1, 1)))
        corner_dr = lax.ppermute(a_lo[:, :, :, :1], both, shift_pairs(sizes, (-1, -1)))
        top = jnp.concatenate([corner_ul, from_up, corner_ur], axis=3)
        middle = jnp.concatenate([from_left, stacked, from_right], axis=3)
        bottom = jnp.concatenate([corner_dl, from_down, corner_dr], axis=3)
        return jnp.concatenate([top, middle, bottom], axis=2)

    join_b = np.zeros((nb_dev + 2, nb_dev), np.float32)
    join_b[np.arange(nb_dev) + 1, np.arange(nb_dev)] = 1.0
    inner_first = np.arange(P_SIZE, nb_dev, P_SIZE)
    join_b[inner_first, inner_first] = 1.0
    inner_last = np.arange(P_SIZE - 1, nb_dev - 1, P_SIZE)
    join_b[inner_last + 2, inner_last] = 1.0
    edge_lead = np.zeros((nb_dev + 2, nb_dev), np.float32)
    edge_lead[0, 0] = 1.0
    edge_trail = np.zeros((nb_dev + 2, nb_dev), np.float32)
    edge_trail[nb_dev + 1, nb_dev - 1] = 1.0
    join_b = join_b + lead * edge_lead + trail * edge_trail

    mask_shape = (3, radial_nodes, 1, 1)
    outer_index = radial_nodes - 1 + jnp.minimum(tile_index, 0)
    plane_mask = jnp.where(
        (lax.broadcasted_iota(jnp.int32, mask_shape, 0) == 0)
        & (lax.broadcasted_iota(jnp.int32, mask_shape, 1) == outer_index),
        1.0,
        0.0,
    )

    def assemble_ext(padded):
        last = padded.ndim - 1
        along_a = assemble_dim(
            padded[..., 1:-1, :], last - 1, padded[..., 0:1, :], padded[..., -1:, :]
        )
        return jnp.dot(along_a, join_b, precision=lax.Precision.HIGH)

    shapes = (
        jax.ShapeDtypeStruct((3, rows, nb_dev), jnp.float32),
        jax.ShapeDtypeStruct((2, 3, radial_nodes, nb_dev), jnp.float32),
        jax.ShapeDtypeStruct((2, 1, 3 * rows), jnp.float32),
    )
    first_outs = pl.pallas_call(
        first_volume_kernel,
        out_shape=shapes
        + (
            jax.ShapeDtypeStruct(analysis.shape[:1] + (nb_dev,), jnp.float32),
            jax.ShapeDtypeStruct((9, rows, nb_dev), jnp.float32),
        ),
    )(field.reshape(3, rows, nb_dev), flat_flow, mats, flat_mass, analysis)
    grads = first_outs[4]

    def tendency(parts, surface):
        if surface is None:
            stacked, edge_rows, edge_cols, partial = first_outs[:4]
        else:
            stacked, edge_rows, edge_cols = pl.pallas_call(volume_kernel, out_shape=shapes)(
                parts.reshape(3, rows, nb_dev), flat_flow, grads, mats, flat_mass
            )
            partial = jnp.dot(analysis, surface, precision=lax.Precision.HIGH)
        stacked = stacked.reshape(parts.shape)
        sent = owner_map(partial)
        if carried_halo:
            returned, padded = joint_exchange(sent, stacked, edge_rows, edge_cols)
        else:
            returned = lax.all_to_all(
                sent.reshape(tiles * groups, -1), both, 0, 0, tiled=True
            ).reshape(tiles * groups, 2, nb_dev + 2)
            padded = halo(stacked)
        flux_term = flux_of(returned)
        outer = padded[0, radial_nodes - 1] + flux_term
        outer_rate = assemble_ext(outer) / assembled[radial_nodes - 1]
        padded = padded + plane_mask * flux_term
        plane_r = jnp.zeros_like(lax.slice_in_dim(padded, 0, 1, axis=1))
        padded = assemble_dim(padded, 1, plane_r, plane_r)
        return assemble_ext(padded) / assembled[None], outer_rate

    first_rate, first_outer = tendency(field, None)
    section = field + time_step * first_rate
    section_outer = field[0, radial_nodes - 1] + time_step * first_outer
    second_rate, _ = tendency(section, section_outer)
    settled = lax.optimization_barrier(0.5 * (field + section))
    return settled + (0.5 * time_step) * second_rate


def solution(mesh):
    placed = (
        P(None, None, "tile", "deg"),
        P(None, None, "tile", "deg"),
        P(("tile", "deg"), None, None),
        P(),
    )
    return jax.shard_map(
        local, mesh=mesh, in_specs=placed, out_specs=P(None, None, "tile", "deg"), check_vma=False
    )
```

```python
import math

import numpy as np
import jax
import jax.numpy as jnp
from jax import lax
from jax.sharding import PartitionSpec as P
from jax.experimental import pallas as pl

P_SIZE = 8


diffusivity = 0.05
time_step = 0.01
highest = lax.Precision.HIGHEST
gll_interior = [0.2092992179024789, 0.5917001814331423, 0.8717401485096066]


def padded_2(value, sides, width):
    for axis, dim in sides:
        size, length = (lax.axis_size(axis), value.shape[dim])
        up = [(i, (i + 1) % size) for i in range(size)]
        down = [(j, i) for i, j in up]
        last = lax.slice_in_dim(value, length - width, length, axis=dim)
        first = lax.slice_in_dim(value, 0, width, axis=dim)
        before = lax.ppermute(last, axis, up)
        after = lax.ppermute(first, axis, down)
        value = jnp.concatenate([before, value, after], axis=dim)
    return value


def product(a, b):
    return jnp.dot(a, b, precision=lax.Precision.HIGH, preferred_element_type=jnp.float32)


def gradient_kernel(flow_ref, mats_ref, out_ref):
    for component in range(3):
        x = flow_ref[component]
        out_ref[3 * component] = product(mats_ref[0], x)
        out_ref[3 * component + 1] = product(mats_ref[1], x)
        out_ref[3 * component + 2] = product(x, mats_ref[2])


def volume_kernel(parts_ref, flow_ref, grad_ref, mats_ref, mass_ref, *outs):
    volume_body(parts_ref, flow_ref, grad_ref, mats_ref, mass_ref, *outs)


def first_volume_kernel(parts_ref, flow_ref, mats_ref, mass_ref, table_ref, *outs):
    grad_ref = outs[4]
    gradient_kernel(flow_ref, mats_ref, grad_ref)
    volume_body(parts_ref, flow_ref, grad_ref, mats_ref, mass_ref, *outs[:3])
    depth = outs[0].shape[1] // outs[1].shape[2]
    surface = parts_ref[0, pl.ds(outs[0].shape[1] - depth, depth), :]
    outs[3][...] = product(table_ref[...], surface)


def volume_body(parts_ref, flow_ref, grad_ref, mats_ref, mass_ref, out_ref, rows_ref, cols_ref):
    mass = mass_ref[...]
    p = [parts_ref[i] for i in range(3)]
    f = [flow_ref[i] for i in range(3)]
    planes = out_ref.shape[1] // rows_ref.shape[2]
    width = out_ref.shape[2]
    for c in range(3):
        x = p[c]
        s0 = product(mats_ref[0], x)
        s1 = product(mats_ref[1], x)
        s2 = product(x, mats_ref[2])
        stretch = p[0] * grad_ref[3 * c] + p[1] * grad_ref[3 * c + 1] + p[2] * grad_ref[3 * c + 2]
        carried = f[0] * s0 + f[1] * s1 + f[2] * s2
        spread = (
            product(mats_ref[3], mass * s0)
            + product(mats_ref[4], mass * s1)
            + product(mass * s2, mats_ref[5])
        )
        result = mass * (stretch - carried) - diffusivity * spread
        out_ref[c] = result
        turned = result.T
        span_of = out_ref.shape[1]
        cols_ref[0, :, c * span_of : (c + 1) * span_of] = turned[0:1, :]
        cols_ref[1, :, c * span_of : (c + 1) * span_of] = turned[width - 1 : width, :]
    for c in range(3):
        rows_ref[0, c] = out_ref[c, pl.ds(0, rows_ref.shape[2], stride=planes), :]
        rows_ref[1, c] = out_ref[c, pl.ds(planes - 1, rows_ref.shape[2], stride=planes), :]


def derivative_tables(radial_nodes, na_dev, nb_dev):
    _, _, matrix_list = gll_tables(P_SIZE)
    dmat = np.asarray(matrix_list, np.float32)
    radial = np.kron(dmat, np.eye(na_dev, dtype=np.float32))
    first = np.kron(np.eye(radial_nodes * na_dev // P_SIZE, dtype=np.float32), dmat)
    second = np.kron(np.eye(nb_dev // P_SIZE, dtype=np.float32), dmat)
    return jnp.asarray(np.stack([radial, first, second.T, radial.T, first.T, second]))


def legendre_value(point, degree):
    previous = 1.0
    current = point
    for order in range(1, degree):
        following = ((2 * order + 1) * point * current - order * previous) / (order + 1)
        previous = current
        current = following
    return current


def gll_tables(count):
    degree = count - 1
    points = [-1.0] + [-value for value in reversed(gll_interior)] + list(gll_interior) + [1.0]
    values = [legendre_value(point, degree) for point in points]
    weights = [2.0 / (degree * (degree + 1) * value * value) for value in values]
    matrix = [
        [
            values[row] / (values[col] * (points[row] - points[col])) if row != col else 0.0
            for col in range(count)
        ]
        for row in range(count)
    ]
    matrix[0][0] = -degree * (degree + 1) / 4.0
    matrix[count - 1][count - 1] = degree * (degree + 1) / 4.0
    return (points, weights, matrix)


def apply_along(values, axis_pos, matrix):
    shape = values.shape
    blocks = values.reshape(
        shape[:axis_pos] + (shape[axis_pos] // P_SIZE, P_SIZE) + shape[axis_pos + 1 :]
    )
    letters = list("abcdefg"[: blocks.ndim])
    source = list(letters)
    source[axis_pos + 1] = "p"
    target = list(letters)
    target[axis_pos + 1] = "q"
    formula = "".join(source) + ",qp->" + "".join(target)
    return jnp.einsum(formula, blocks, matrix, precision=highest).reshape(shape)


def assemble_dim(values, axis_pos, left, right):
    shape = values.shape
    count = shape[axis_pos] // P_SIZE
    blocks = values.reshape(shape[:axis_pos] + (count, P_SIZE) + shape[axis_pos + 1 :])
    edge_shape = shape[:axis_pos] + (1, 1) + shape[axis_pos + 1 :]
    first = lax.slice_in_dim(blocks, 0, 1, axis=axis_pos + 1)
    last = lax.slice_in_dim(blocks, P_SIZE - 1, P_SIZE, axis=axis_pos + 1)
    before = jnp.concatenate(
        [left.reshape(edge_shape), lax.slice_in_dim(last, 0, count - 1, axis=axis_pos)],
        axis=axis_pos,
    )
    after = jnp.concatenate(
        [lax.slice_in_dim(first, 1, count, axis=axis_pos), right.reshape(edge_shape)], axis=axis_pos
    )
    middle = lax.slice_in_dim(blocks, 1, P_SIZE - 1, axis=axis_pos + 1)
    joined = jnp.concatenate([first + before, middle, last + after], axis=axis_pos + 1)
    return joined.reshape(shape)


def assembled_weights(weights, count, lead, trail):
    position = jnp.arange(count * P_SIZE, dtype=jnp.int32)
    local_point = position % P_SIZE
    element = position // P_SIZE
    base = jnp.tile(weights, count)
    starts = (
        jnp.where(local_point == 0, jnp.where(element > 0, 1.0, lead), 0.0) * weights[P_SIZE - 1]
    )
    ends = (
        jnp.where(local_point == P_SIZE - 1, jnp.where(element < count - 1, 1.0, trail), 0.0)
        * weights[0]
    )
    return base + starts + ends


def static_assembled(weights, count, lead, trail):
    position = np.arange(count * P_SIZE)
    local_point = position % P_SIZE
    element = position // P_SIZE
    starts = np.where(local_point == 0, np.where(element > 0, 1.0, lead), 0.0) * weights[P_SIZE - 1]
    ends = np.where(local_point == P_SIZE - 1, np.where(element < count - 1, 1.0, trail), 0.0)
    return (np.tile(weights, count) + starts + ends * weights[0]).astype(np.float32)


def table_at(values, index):
    point = index % P_SIZE
    total = jnp.zeros(index.shape, jnp.float32)
    for p in range(P_SIZE):
        total = total + jnp.where(point == p, float(values[p]), 0.0)
    return total


def phases(waves, elem_start, elem_count, span, points):
    position = elem_start * P_SIZE + jnp.arange(elem_count * P_SIZE, dtype=jnp.int32)
    element = position // P_SIZE
    whole = waves[:, None] * (2 * element + 1)[None, :] % span
    fraction = waves.astype(jnp.float32)[:, None] * table_at(points, position)[None, :]
    return 2.0 * math.pi / span * (whole.astype(jnp.float32) + fraction)


def phases_at(waves, element, point_values, span):
    whole = waves[:, None] * (2 * element + 1)[None, :] % span
    fraction = waves.astype(jnp.float32)[:, None] * point_values[None, :]
    return 2.0 * math.pi / span * (whole.astype(jnp.float32) + fraction)


def shift_pairs(sizes, steps):
    count = sizes[0] * sizes[1]
    pairs = []
    for source in range(count):
        t, g = divmod(source, sizes[1])
        target = ((t + steps[0]) % sizes[0]) * sizes[1] + (g + steps[1]) % sizes[1]
        pairs.append((source, target))
    return pairs


def local(field, flow, match_ops, wave_of_slot):
    tiles = lax.axis_size("tile")
    groups = lax.axis_size("deg")
    both = ("tile", "deg")
    tile_index = lax.axis_index("tile")
    group_index = lax.axis_index("deg")
    radial_nodes = field.shape[1]
    na_dev = field.shape[2]
    nb_dev = field.shape[3]
    elems_a = na_dev // P_SIZE
    elems_b = nb_dev // P_SIZE
    nb = nb_dev * groups
    span = 2 * elems_a * tiles
    scale = P_SIZE / (na_dev * tiles)
    points_list, weights_list, _ = gll_tables(P_SIZE)
    points = np.asarray(points_list, np.float32)
    weights = np.asarray(weights_list, np.float32)
    lead = (group_index > 0).astype(jnp.float32)
    trail = (group_index < groups - 1).astype(jnp.float32)
    w_r = np.tile(weights, radial_nodes // P_SIZE)
    w_a = np.tile(weights, elems_a)
    w_b = np.tile(weights, elems_b)
    mass3 = w_r[:, None, None] * w_a[None, :, None] * w_b[None, None, :]
    origin = jnp.minimum(tile_index, 0)

    def assembled_at(length, lead_value, trail_value):
        position = origin + jnp.arange(length, dtype=jnp.int32)
        local_point = position % P_SIZE
        element = position // P_SIZE
        count = length // P_SIZE
        starts = jnp.where(
            local_point == 0, jnp.where(element > 0, 1.0, lead_value), 0.0
        ) * float(weights[P_SIZE - 1])
        ends = jnp.where(
            local_point == P_SIZE - 1, jnp.where(element < count - 1, 1.0, trail_value), 0.0
        ) * float(weights[0])
        return table_at(weights, position) + starts + ends

    assembled = (
        (
            assembled_at(radial_nodes, 0.0, 0.0)[:, None]
            * assembled_at(na_dev, 1.0, 1.0)[None, :]
        )[:, :, None]
        * assembled_at(nb_dev, lead, trail)[None, None, :]
    )
    rows_ext = (tile_index * na_dev - 1 + jnp.arange(na_dev + 2, dtype=jnp.int32)) % (na_dev * tiles)
    row_points = (np.arange(na_dev + 2) - 1) % P_SIZE
    col_points = (np.arange(nb_dev + 2) - 1) % P_SIZE
    cols_ext = group_index * nb_dev - 1 + jnp.arange(nb_dev + 2, dtype=jnp.int32)

    def weight_at(index):
        return table_at(weights, index)

    surface_ext = diffusivity * weight_at(rows_ext)[:, None] * weight_at(cols_ext)[None, :]

    rows = radial_nodes * na_dev
    mats = derivative_tables(radial_nodes, na_dev, nb_dev)
    flat_mass = mass3.reshape(rows, nb_dev)
    flat_flow = flow.reshape(3, rows, nb_dev)

    angle = phases(wave_of_slot, tile_index * elems_a, elems_a, span, points)
    analysis = (
        jnp.stack([jnp.cos(angle), jnp.sin(angle)], axis=1)
        * (scale * weight_at(tile_index * na_dev + jnp.arange(na_dev, dtype=jnp.int32)))[
            None, None, :
        ]
    ).reshape(-1, na_dev)

    def owner_map(partial):
        partial = partial.reshape(-1, 2, nb_dev)
        gathered = lax.all_to_all(partial, both, 0, 0, tiled=True)
        coeff = gathered.reshape(tiles, groups, 2, nb_dev).sum(axis=0)
        coeff = coeff.transpose(1, 0, 2).reshape(2, nb)
        owned = coeff.astype(jnp.bfloat16)
        mapped = jnp.einsum(
            "pq,cq->cp", match_ops[0], owned, preferred_element_type=jnp.float32
        )
        edged = jnp.concatenate([mapped[:, :1], mapped, mapped[:, -1:]], axis=1)
        pieces = jnp.stack(
            [edged[:, g * nb_dev : g * nb_dev + nb_dev + 2] for g in range(groups)], axis=0
        )
        return jnp.broadcast_to(pieces[None], (tiles,) + pieces.shape).reshape(
            tiles, groups, 2 * (nb_dev + 2)
        )

    def flux_of(returned):
        angle = phases_at(wave_of_slot, rows_ext // P_SIZE, table_at(points, rows_ext), span)
        synth = jnp.stack([jnp.cos(angle).T, jnp.sin(angle).T], axis=2).reshape(na_dev + 2, -1)
        flux = -jnp.dot(synth, returned.reshape(-1, nb_dev + 2), precision=lax.Precision.HIGH)
        return surface_ext * flux

    mapped_len = 2 * (nb_dev + 2)
    slot_len = 3 * radial_nodes * na_dev
    carried_halo = tiles >= 3 and groups >= 3 and tiles * groups <= 64

    def joint_exchange(sent, stacked, edge_rows, edge_cols):
        a_lo = edge_rows[0].reshape(3, radial_nodes, 1, nb_dev)
        a_hi = edge_rows[1].reshape(3, radial_nodes, 1, nb_dev)
        up = [(i, (i + 1) % tiles) for i in range(tiles)]
        down = [(j, i) for i, j in up]
        from_up = lax.ppermute(a_hi, "tile", up)
        from_down = lax.ppermute(a_lo, "tile", down)
        b_lo = edge_cols[0:1]
        b_hi = edge_cols[1:2]
        out_pieces = [
            ((0, 1), b_hi),
            ((0, -1), b_lo),
            ((1, 1), b_hi),
            ((1, -1), b_lo),
            ((-1, 1), b_hi),
            ((-1, -1), b_lo),
        ]
        slots = jnp.zeros((tiles * groups, 1, slot_len), jnp.float32)
        for (dt, dg), flat in out_pieces:
            target = ((tile_index + dt) % tiles) * groups + (group_index + dg) % groups
            slots = lax.dynamic_update_slice(slots, flat, (target, 0, 0))
        message = jnp.concatenate([sent.reshape(tiles * groups, 1, -1), slots], axis=2)
        received = lax.all_to_all(message, both, 0, 0, tiled=True)
        returned = received[:, 0, :mapped_len].reshape(tiles * groups, 2, nb_dev + 2)

        def take(dt, dg):
            source = ((tile_index - dt) % tiles) * groups + (group_index - dg) % groups
            row = lax.dynamic_slice(received, (source, 0, mapped_len), (1, 1, slot_len))
            return row.reshape(3, radial_nodes, na_dev, 1)

        from_left = take(0, 1)
        from_right = take(0, -1)
        corner_ul = take(1, 1)[:, :, na_dev - 1 :, :]
        corner_ur = take(1, -1)[:, :, na_dev - 1 :, :]
        corner_dl = take(-1, 1)[:, :, :1, :]
        corner_dr = take(-1, -1)[:, :, :1, :]
        top = jnp.concatenate([corner_ul, from_up, corner_ur], axis=3)
        middle = jnp.concatenate([from_left, stacked, from_right], axis=3)
        bottom = jnp.concatenate([corner_dl, from_down, corner_dr], axis=3)
        return returned, jnp.concatenate([top, middle, bottom], axis=2)

    def halo(stacked):
        a_lo = lax.slice_in_dim(stacked, 0, 1, axis=2)
        a_hi = lax.slice_in_dim(stacked, na_dev - 1, na_dev, axis=2)
        b_lo = lax.slice_in_dim(stacked, 0, 1, axis=3)
        b_hi = lax.slice_in_dim(stacked, nb_dev - 1, nb_dev, axis=3)
        sizes = (tiles, groups)
        from_up = lax.ppermute(a_hi, both, shift_pairs(sizes, (1, 0)))
        from_down = lax.ppermute(a_lo, both, shift_pairs(sizes, (-1, 0)))
        from_left = lax.ppermute(b_hi, both, shift_pairs(sizes, (0, 1)))
        from_right = lax.ppermute(b_lo, both, shift_pairs(sizes, (0, -1)))
        corner_ul = lax.ppermute(a_hi[:, :, :, -1:], both, shift_pairs(sizes, (1, 1)))
        corner_ur = lax.ppermute(a_hi[:, :, :, :1], both, shift_pairs(sizes, (1, -1)))
        corner_dl = lax.ppermute(a_lo[:, :, :, -1:], both, shift_pairs(sizes, (-1, 1)))
        corner_dr = lax.ppermute(a_lo[:, :, :, :1], both, shift_pairs(sizes, (-1, -1)))
        top = jnp.concatenate([corner_ul, from_up, corner_ur], axis=3)
        middle = jnp.concatenate([from_left, stacked, from_right], axis=3)
        bottom = jnp.concatenate([corner_dl, from_down, corner_dr], axis=3)
        return jnp.concatenate([top, middle, bottom], axis=2)

    join_b = np.zeros((nb_dev + 2, nb_dev), np.float32)
    join_b[np.arange(nb_dev) + 1, np.arange(nb_dev)] = 1.0
    inner_first = np.arange(P_SIZE, nb_dev, P_SIZE)
    join_b[inner_first, inner_first] = 1.0
    inner_last = np.arange(P_SIZE - 1, nb_dev - 1, P_SIZE)
    join_b[inner_last + 2, inner_last] = 1.0
    edge_lead = np.zeros((nb_dev + 2, nb_dev), np.float32)
    edge_lead[0, 0] = 1.0
    edge_trail = np.zeros((nb_dev + 2, nb_dev), np.float32)
    edge_trail[nb_dev + 1, nb_dev - 1] = 1.0
    join_b = join_b + lead * edge_lead + trail * edge_trail

    mask_shape = (3, radial_nodes, 1, 1)
    outer_index = radial_nodes - 1 + jnp.minimum(tile_index, 0)
    plane_mask = jnp.where(
        (lax.broadcasted_iota(jnp.int32, mask_shape, 0) == 0)
        & (lax.broadcasted_iota(jnp.int32, mask_shape, 1) == outer_index),
        1.0,
        0.0,
    )

    def assemble_ext(padded):
        last = padded.ndim - 1
        along_a = assemble_dim(
            padded[..., 1:-1, :], last - 1, padded[..., 0:1, :], padded[..., -1:, :]
        )
        return jnp.dot(along_a, join_b, precision=lax.Precision.HIGH)

    shapes = (
        jax.ShapeDtypeStruct((3, rows, nb_dev), jnp.float32),
        jax.ShapeDtypeStruct((2, 3, radial_nodes, nb_dev), jnp.float32),
        jax.ShapeDtypeStruct((2, 1, 3 * rows), jnp.float32),
    )
    first_outs = pl.pallas_call(
        first_volume_kernel,
        out_shape=shapes
        + (
            jax.ShapeDtypeStruct(analysis.shape[:1] + (nb_dev,), jnp.float32),
            jax.ShapeDtypeStruct((9, rows, nb_dev), jnp.float32),
        ),
    )(field.reshape(3, rows, nb_dev), flat_flow, mats, flat_mass, analysis)
    grads = first_outs[4]

    def tendency(parts, surface):
        if surface is None:
            stacked, edge_rows, edge_cols, partial = first_outs[:4]
        else:
            stacked, edge_rows, edge_cols = pl.pallas_call(volume_kernel, out_shape=shapes)(
                parts.reshape(3, rows, nb_dev), flat_flow, grads, mats, flat_mass
            )
            partial = jnp.dot(analysis, surface, precision=lax.Precision.HIGH)
        stacked = stacked.reshape(parts.shape)
        sent = owner_map(partial)
        if carried_halo:
            returned, padded = joint_exchange(sent, stacked, edge_rows, edge_cols)
        else:
            returned = lax.all_to_all(
                sent.reshape(tiles * groups, -1), both, 0, 0, tiled=True
            ).reshape(tiles * groups, 2, nb_dev + 2)
            padded = halo(stacked)
        flux_term = flux_of(returned)
        outer = padded[0, radial_nodes - 1] + flux_term
        outer_rate = assemble_ext(outer) / assembled[radial_nodes - 1]
        padded = padded + plane_mask * flux_term
        plane_r = jnp.zeros_like(lax.slice_in_dim(padded, 0, 1, axis=1))
        padded = assemble_dim(padded, 1, plane_r, plane_r)
        return assemble_ext(padded) / assembled[None], outer_rate

    first_rate, first_outer = tendency(field, None)
    section = field + time_step * first_rate
    field_outer = lax.optimization_barrier(field[0, radial_nodes - 1])
    section_outer = field_outer + time_step * first_outer
    second_rate, _ = tendency(section, section_outer)
    settled = lax.optimization_barrier(0.5 * (field + section))
    return settled + (0.5 * time_step) * second_rate


def solution(mesh):
    placed = (
        P(None, None, "tile", "deg"),
        P(None, None, "tile", "deg"),
        P(("tile", "deg"), None, None),
        P(),
    )
    return jax.shard_map(
        local, mesh=mesh, in_specs=placed, out_specs=P(None, None, "tile", "deg"), check_vma=False
    )
```
